32 devices in a mesh: gx: 4 (over x, core), gy: 8 (over z, y).
Axes of the slice: x: 2, y: 2, z: 4, core: 2. Of those that a mesh axis runs over, the one named last changes fastest.
Arguments:
- fine_wave: float32 [9, 12, 24, 3072], P(None, None, 'gx', 'gy'), may hold values from -6 to 6
- fine_memory: float32 [6, 12, 24, 3072], P(None, None, 'gx', 'gy'), may hold values from -6 to 6
- fine_material: int32 [12, 24, 3072], P(None, 'gx', 'gy'), may hold values from 0 to 7
- fine_mechanism: int32 [12, 24, 3072], P(None, 'gx', 'gy'), may hold values from 0 to 3
- fine_metric: float32 [12, 24, 3072], P(None, 'gx', 'gy'), may hold values from 0.7 to 1.4
- coarse_wave: float32 [9, 8, 8, 1024], P(None, None, 'gx', 'gy'), may hold values from -6 to 6
- coarse_memory: float32 [6, 8, 8, 1024], P(None, None, 'gx', 'gy'), may hold values from -6 to 6
- coarse_material: int32 [8, 8, 1024], P(None, 'gx', 'gy'), may hold values from 0 to 7
- coarse_mechanism: int32 [8, 8, 1024], P(None, 'gx', 'gy'), may hold values from 0 to 3
- material_table: float32 [3, 8], replicated, may hold values from 0.4 to 1.5
- attenuation_table: float32 [2, 4], replicated, may hold values from 0.2 to 0.9
Outputs:
- fine_wavefield_output: float32 [9, 12, 24, 3072], P(None, None, 'gx', 'gy')
- fine_memory_out: float32 [6, 12, 24, 3072], P(None, None, 'gx', 'gy')
- coarse_wave_out: float32 [9, 8, 8, 1024], P(None, None, 'gx', 'gy')
- coarse_memory_out: float32 [6, 8, 8, 1024], P(None, None, 'gx', 'gy')
The draws below stay inside these ranges and needn't reach their ends.
All inputs are finite; a program needn't handle non-finite values.
Results may differ from the reference program's by a relative error of at most 0.000062.
Values sent between devices are 32-bit elements; how exact they have to be, the bound alone decides.
No kernel may reach another device: no remote copies, remote signals or barrier semaphores. Data moves between devices by JAX's collectives and lax.ppermute only.
A program may use at most 64 MiB of HBM per device.

```python
import math
import jax
import jax.numpy as jnp
import numpy as np
from jax import lax

FZ = 12
CZ = 8
NMAT = 8
NMECH = 4
NXF = 24
NYF = 3072
NXC = 8
NYC = 1024


def touch_ends(values, key, smallest, high):
    dims = values.shape
    index_at = [jax.random.randint(jax.random.fold_in(key, axis), (), 0, dims[axis]) for axis in range(len(dims))]
    values = values.at[tuple(index_at)].set(smallest)
    longest = dims.index(max(dims))
    index_at[longest] = (index_at[longest] + 1) % dims[longest]
    return values.at[tuple(index_at)].set(high)


def level_of(stream_key, dims, shards, low, top_value):
    gain, own = 1.0, jax.random.fold_in(stream_key, 6)
    for dim, shards_of in shards:
        steps = jnp.exp(jax.random.uniform(jax.random.fold_in(own, dim), (shards_of,), jnp.float32, low / len(shards), top_value / len(shards)))
        gain = gain * jnp.repeat(steps, dims[dim] // shards_of).reshape([-1 if axis == dim else 1 for axis in range(len(dims))])
    return gain


def gaussian(stream_key, shape, spread, limit, split=(), kind=jnp.bfloat16):
    values = jax.random.normal(stream_key, shape, jnp.float32) * spread
    if len(split) > 0:
        values = level_of(stream_key, shape, split, -0.22, 0.18) * values
    return jnp.clip(values, min=-limit, max=limit).astype(kind)


def setup_inputs(seed: int = 0) -> dict:
    streams_of = jax.random.split(jax.random.key(seed), 12)
    return {
        "fine_wave": gaussian(streams_of[0], (9, FZ, NXF, NYF), 1.0, 6.0, ((2, 4), (3, 8)), jnp.float32),
        "fine_memory": gaussian(streams_of[1], (6, FZ, NXF, NYF), 1.0, 6.0, ((2, 4), (3, 8)), jnp.float32),
        "fine_material": touch_ends(jax.random.randint(streams_of[2], (FZ, NXF, NYF), 0, NMAT), jax.random.fold_in(streams_of[2], 1), 0, NMAT - 1).astype(jnp.int32),
        "fine_mechanism": touch_ends(jax.random.randint(streams_of[3], (FZ, NXF, NYF), 0, NMECH), jax.random.fold_in(streams_of[3], 1), 0, NMECH - 1).astype(jnp.int32),
        "fine_metric": jnp.clip(jnp.exp(math.log(1.4) - 0.6931472 * jax.random.uniform(streams_of[4], (FZ, NXF, NYF), jnp.float32) ** level_of(streams_of[4], (FZ, NXF, NYF), ((1, 4), (2, 8)), -0.2, 0.2)), 0.7, 1.4),
        "coarse_wave": gaussian(streams_of[5], (9, CZ, NXC, NYC), 1.0, 6.0, ((2, 4), (3, 8)), jnp.float32),
        "coarse_memory": gaussian(streams_of[6], (6, CZ, NXC, NYC), 1.0, 6.0, ((2, 4), (3, 8)), jnp.float32),
        "coarse_material": touch_ends(jax.random.randint(streams_of[7], (CZ, NXC, NYC), 0, NMAT), jax.random.fold_in(streams_of[7], 1), 0, NMAT - 1).astype(jnp.int32),
        "coarse_mechanism": touch_ends(jax.random.randint(streams_of[8], (CZ, NXC, NYC), 0, NMECH), jax.random.fold_in(streams_of[8], 1), 0, NMECH - 1).astype(jnp.int32),
        "material_table": jnp.clip(jax.random.uniform(streams_of[9], (3, NMAT), jnp.float32, 0.4, 1.5), 0.4, 1.5),
        "attenuation_table": jnp.clip(jax.random.uniform(streams_of[10], (2, NMECH), jnp.float32, 0.2, 0.9), 0.2, 0.9),
    }


step_size = 0.1
penalty = 0.1 * 48.0 / 17.0
closure = [[-24.0 / 17.0, 59.0 / 34.0, -4.0 / 17.0, -3.0 / 34.0, 0.0, 0.0],
           [-0.5, 0.0, 0.5, 0.0, 0.0, 0.0],
           [4.0 / 43.0, -59.0 / 86.0, 0.0, 59.0 / 86.0, -4.0 / 43.0, 0.0],
           [3.0 / 98.0, 0.0, -59.0 / 98.0, 0.0, 32.0 / 49.0, -4.0 / 49.0]]
face_rows = np.array([0, 1, 2, 7, 8, 5])


def sbp_table(layers, spacing):
    table = np.zeros((layers, layers))
    for line_at in range(4):
        for column in range(6):
            table[line_at, column] = closure[line_at][column]
            table[layers - 1 - line_at, layers - 1 - column] = -closure[line_at][column]
    for line_at in range(4, layers - 4):
        table[line_at, line_at - 2:line_at + 3] = [1.0 / 12.0, -2.0 / 3.0, 0.0, 2.0 / 3.0, -1.0 / 12.0]
    return jnp.asarray(table / spacing, dtype=jnp.float32)


def shifted(padded, offset, length, along):
    return lax.slice_in_dim(padded, offset, offset + length, axis=along)


def central_diff(padded, along, spacing):
    length = padded.shape[along] - 4
    return (shifted(padded, 0, length, along) - 8.0 * shifted(padded, 1, length, along)
            + 8.0 * shifted(padded, 3, length, along) - shifted(padded, 4, length, along)) / (12.0 * spacing)


def vertical_diff(fields, matrix):
    return jnp.einsum("kz,czxy->ckxy", matrix, fields, precision=lax.Precision.HIGHEST)


def lookup_table(grid_cell_index, values):
    result = jnp.zeros(grid_cell_index.shape, jnp.float32)
    for kind_at in range(values.shape[0]):
        result = result + jnp.where(grid_cell_index == kind_at, values[kind_at], jnp.float32(0.0))
    return result


def velocity_rate(stress_pad, buoyancy, metric, matrix, spacing):
    slope_x = central_diff(stress_pad[:, :, :, 2:-2], 2, spacing)
    slope_y = central_diff(stress_pad[:, :, 2:-2, :], 3, spacing)
    slope_z = metric * vertical_diff(stress_pad[:, :, 2:-2, 2:-2], matrix)
    rate_x = slope_x[0] + slope_y[3] + slope_z[4]
    rate_y = slope_x[3] + slope_y[1] + slope_z[5]
    rate_z = slope_x[4] + slope_y[5] + slope_z[2]
    return buoyancy * jnp.stack([rate_x, rate_y, rate_z])


def stress_rate(velocity_pad, lame, shear, metric, matrix, spacing):
    slope_x = central_diff(velocity_pad[:, :, :, 2:-2], 2, spacing)
    slope_y = central_diff(velocity_pad[:, :, 2:-2, :], 3, spacing)
    slope_z = metric * vertical_diff(velocity_pad[:, :, 2:-2, 2:-2], matrix)
    cell_volume = lame * (slope_x[0] + slope_y[1] + slope_z[2])
    return jnp.stack([cell_volume + 2.0 * shear * slope_x[0], cell_volume + 2.0 * shear * slope_y[1],
                      cell_volume + 2.0 * shear * slope_z[2], shear * (slope_y[0] + slope_x[1]),
                      shear * (slope_z[0] + slope_x[2]), shear * (slope_z[1] + slope_y[2])])


def finish_stress(wave, memory, velocity_pad, lame, shear, decay, strength, metric, matrix, spacing):
    rate = stress_rate(velocity_pad, lame, shear, metric, matrix, spacing)
    memory_new = decay * memory + (1.0 - decay) * strength * rate
    stress = wave[3:] + step_size * (rate - memory_new)
    return stress, memory_new


def pad_sides(fields, width):
    return jnp.pad(fields, ((0, 0), (0, 0), (width, width), (width, width)))


def face_of(velocity, stress, depth):
    return jnp.stack([velocity[0, depth], velocity[1, depth], velocity[2, depth],
                      stress[4, depth], stress[5, depth], stress[2, depth]])


def prolong_axis(padded, along):
    length = padded.shape[along] - 2
    left = shifted(padded, 0, length, along)
    middle = shifted(padded, 1, length, along)
    right = shifted(padded, 2, length, along)
    parts = jnp.stack([(left + 2.0 * middle) / 3.0, middle, (2.0 * middle + right) / 3.0], axis=along + 1)
    shape = list(middle.shape)
    shape[along] = shape[along] * 3
    return parts.reshape(tuple(shape))


def split_three(padded, offset, length, along):
    part = shifted(padded, offset, 3 * length, along)
    return part.reshape(part.shape[:along] + (length, 3) + part.shape[along + 1:])


def pick_part(parts, number, along):
    return lax.index_in_dim(parts, number, along + 1, keepdims=False)


def restrict_axis(padded, along):
    length = (padded.shape[along] - 2) // 3
    first = split_three(padded, 0, length, along)
    middle = split_three(padded, 1, length, along)
    last = split_three(padded, 2, length, along)
    return (pick_part(first, 0, along) + 2.0 * pick_part(middle, 0, along) + 3.0 * pick_part(middle, 1, along)
            + 2.0 * pick_part(middle, 2, along) + pick_part(last, 2, along)) / 9.0


def reference(fine_wave, fine_memory, fine_material, fine_mechanism, fine_metric, coarse_wave, coarse_memory,
              coarse_material, coarse_mechanism, material_table, attenuation_table):
    fine_matrix = sbp_table(fine_wave.shape[1], 1.0)
    coarse_matrix = sbp_table(coarse_wave.shape[1], 3.0)
    fine_buoy = lookup_table(fine_material, material_table[0])
    fine_lame_moduli = lookup_table(fine_material, material_table[1])
    fine_shear = lookup_table(fine_material, material_table[2])
    fine_decay = lookup_table(fine_mechanism, attenuation_table[0])
    fine_strength = lookup_table(fine_mechanism, attenuation_table[1])
    coarse_buoy = lookup_table(coarse_material, material_table[0])
    coarse_lame = lookup_table(coarse_material, material_table[1])
    coarse_shear = lookup_table(coarse_material, material_table[2])
    coarse_decay = lookup_table(coarse_mechanism, attenuation_table[0])
    coarse_strength = lookup_table(coarse_mechanism, attenuation_table[1])

    fine_velocity = fine_wave[:3] + step_size * velocity_rate(pad_sides(fine_wave[3:], 2), fine_buoy, fine_metric, fine_matrix, 1.0)
    fine_grid_stress, fine_mem = finish_stress(fine_wave, fine_memory, pad_sides(fine_velocity, 2), fine_lame_moduli, fine_shear,
                                          fine_decay, fine_strength, fine_metric, fine_matrix, 1.0)
    coarse_grid_velocity = coarse_wave[:3] + step_size * velocity_rate(pad_sides(coarse_wave[3:], 2), coarse_buoy, 1.0, coarse_matrix, 3.0)
    coarse_stress, coarse_mem = finish_stress(coarse_wave, coarse_memory, pad_sides(coarse_grid_velocity, 2), coarse_lame,
                                              coarse_shear, coarse_decay, coarse_strength, 1.0, coarse_matrix, 3.0)

    depth = fine_wave.shape[1] - 1
    fine_face = face_of(fine_velocity, fine_grid_stress, depth)
    coarse_face = face_of(coarse_grid_velocity, coarse_stress, 0)
    coarse_padded = jnp.pad(coarse_face, ((0, 0), (1, 1), (1, 1)))
    fine_padded = jnp.pad(fine_face, ((0, 0), (1, 1), (1, 1)))
    fine_new = fine_face - penalty * (fine_face - prolong_axis(prolong_axis(coarse_padded, 1), 2))
    coarse_updated_fields = coarse_face - penalty * (coarse_face - restrict_axis(restrict_axis(fine_padded, 1), 2))
    fine_out = jnp.concatenate([fine_velocity, fine_grid_stress]).at[face_rows, depth].set(fine_new)
    coarse_out = jnp.concatenate([coarse_grid_velocity, coarse_stress]).at[face_rows, 0].set(coarse_updated_fields)
    return (fine_out, fine_mem, coarse_out, coarse_mem)
```

```python
import math

import jax
import jax.numpy as jnp
import numpy as np
from jax import lax
from jax.sharding import PartitionSpec as P

step_size = 0.1
penalty = 0.1 * 48.0 / 17.0
closure = [
    [-24.0 / 17.0, 59.0 / 34.0, -4.0 / 17.0, -3.0 / 34.0, 0.0, 0.0],
    [-0.5, 0.0, 0.5, 0.0, 0.0, 0.0],
    [4.0 / 43.0, -59.0 / 86.0, 0.0, 59.0 / 86.0, -4.0 / 43.0, 0.0],
    [3.0 / 98.0, 0.0, -59.0 / 98.0, 0.0, 32.0 / 49.0, -4.0 / 49.0],
]


def sbp_table(layers, spacing):
    table = np.zeros((layers, layers))
    for line_at in range(4):
        for column in range(6):
            table[line_at, column] = closure[line_at][column]
            table[layers - 1 - line_at, layers - 1 - column] = -closure[line_at][column]
    for line_at in range(4, layers - 4):
        table[line_at, line_at - 2 : line_at + 3] = [
            1.0 / 12.0,
            -2.0 / 3.0,
            0.0,
            2.0 / 3.0,
            -1.0 / 12.0,
        ]
    return jnp.asarray(table / spacing, dtype=jnp.float32)


def shift_from(block, axis, offset):
    count = lax.axis_size(axis)
    pairs = [(i, i + offset) for i in range(count) if 0 <= i + offset < count]
    return lax.ppermute(block, axis, pairs)


def packed_shift(blocks, axis, offset):
    sizes = [math.prod(b.shape) for b in blocks]
    joined = jnp.concatenate([b.reshape(-1) for b in blocks])
    moved = shift_from(joined, axis, offset)
    out, start = [], 0
    for b, size in zip(blocks, sizes):
        out.append(moved[start : start + size].reshape(b.shape))
        start += size
    return out


def exchange(blocks, width):
    x_lo = packed_shift([b[..., -width:, :] for b in blocks], "gx", 1)
    x_hi = packed_shift([b[..., :width, :] for b in blocks], "gx", -1)
    y_lo = packed_shift([b[..., -width:] for b in blocks], "gy", 1)
    y_hi = packed_shift([b[..., :width] for b in blocks], "gy", -1)
    return [(x_lo[i], x_hi[i], y_lo[i], y_hi[i]) for i in range(len(blocks))]


def central_diff(padded, along, spacing):
    length = padded.shape[along] - 4
    s = lambda o: lax.slice_in_dim(padded, o, o + length, axis=along)
    return (s(0) - 8.0 * s(1) + 8.0 * s(3) - s(4)) / (12.0 * spacing)


def diff_x(block, halo, spacing):
    x_lo, x_hi, _, _ = halo
    return central_diff(jnp.concatenate([x_lo, block, x_hi], axis=-2), block.ndim - 2, spacing)


def diff_y(block, halo, spacing):
    _, _, y_lo, y_hi = halo
    return central_diff(jnp.concatenate([y_lo, block, y_hi], axis=-1), block.ndim - 1, spacing)


def vertical_diff(fields, matrix):
    return jnp.einsum("kz,czxy->ckxy", matrix, fields, precision=lax.Precision.HIGHEST)


def lookup_table(grid_cell_index, values):
    result = jnp.zeros(grid_cell_index.shape, jnp.float32)
    for kind_at in range(values.shape[0]):
        result = jnp.where(grid_cell_index == kind_at, values[kind_at], result)
    return result


def velocity_step(wave, halo_x3, halo_y3, buoyancy, metric, matrix, spacing):
    sx = jnp.stack([wave[3], wave[6], wave[7]])
    sy = jnp.stack([wave[6], wave[4], wave[8]])
    slope_x = diff_x(sx, halo_x3, spacing)
    slope_y = diff_y(sy, halo_y3, spacing)
    slope_z = metric * vertical_diff(jnp.stack([wave[7], wave[8], wave[5]]), matrix)
    rate_x = slope_x[0] + slope_y[0] + slope_z[0]
    rate_y = slope_x[1] + slope_y[1] + slope_z[1]
    rate_z = slope_x[2] + slope_y[2] + slope_z[2]
    return wave[:3] + step_size * (buoyancy * jnp.stack([rate_x, rate_y, rate_z]))


def stress_step(wave, memory, velocity, halo, lame, shear, decay, strength, metric, matrix, spacing):
    slope_x = diff_x(velocity, halo, spacing)
    slope_y = diff_y(velocity, halo, spacing)
    slope_z = metric * vertical_diff(velocity, matrix)
    cell_volume = lame * (slope_x[0] + slope_y[1] + slope_z[2])
    rate = jnp.stack(
        [
            cell_volume + 2.0 * shear * slope_x[0],
            cell_volume + 2.0 * shear * slope_y[1],
            cell_volume + 2.0 * shear * slope_z[2],
            shear * (slope_y[0] + slope_x[1]),
            shear * (slope_z[0] + slope_x[2]),
            shear * (slope_z[1] + slope_y[2]),
        ]
    )
    memory_new = decay * memory + (1.0 - decay) * strength * rate
    stress = wave[3:] + step_size * (rate - memory_new)
    return stress, memory_new


def face_of(velocity, stress, depth):
    return jnp.stack(
        [
            velocity[0, depth],
            velocity[1, depth],
            velocity[2, depth],
            stress[4, depth],
            stress[5, depth],
            stress[2, depth],
        ]
    )


def pad_faces(faces):
    x_lo = packed_shift([f[:, -1:, :] for f in faces], "gx", 1)
    x_hi = packed_shift([f[:, :1, :] for f in faces], "gx", -1)
    faces = [jnp.concatenate([lo, f, hi], axis=1) for lo, f, hi in zip(x_lo, faces, x_hi)]
    y_lo = packed_shift([f[:, :, -1:] for f in faces], "gy", 1)
    y_hi = packed_shift([f[:, :, :1] for f in faces], "gy", -1)
    return [jnp.concatenate([lo, f, hi], axis=2) for lo, f, hi in zip(y_lo, faces, y_hi)]


def shifted(padded, offset, length, along):
    return lax.slice_in_dim(padded, offset, offset + length, axis=along)


def prolong_axis(padded, along):
    length = padded.shape[along] - 2
    left = shifted(padded, 0, length, along)
    middle = shifted(padded, 1, length, along)
    right = shifted(padded, 2, length, along)
    parts = jnp.stack(
        [(left + 2.0 * middle) / 3.0, middle, (2.0 * middle + right) / 3.0], axis=along + 1
    )
    shape = list(middle.shape)
    shape[along] = shape[along] * 3
    return parts.reshape(tuple(shape))


def split_three(padded, offset, length, along):
    part = shifted(padded, offset, 3 * length, along)
    return part.reshape(part.shape[:along] + (length, 3) + part.shape[along + 1 :])


def pick_part(parts, number, along):
    return lax.index_in_dim(parts, number, along + 1, keepdims=False)


def restrict_axis(padded, along):
    length = (padded.shape[along] - 2) // 3
    first = split_three(padded, 0, length, along)
    middle = split_three(padded, 1, length, along)
    last = split_three(padded, 2, length, along)
    return (
        pick_part(first, 0, along)
        + 2.0 * pick_part(middle, 0, along)
        + 3.0 * pick_part(middle, 1, along)
        + 2.0 * pick_part(middle, 2, along)
        + pick_part(last, 2, along)
    ) / 9.0


def assemble(velocity, stress, face, depth):
    replace = {0: face[0], 1: face[1], 2: face[2], 7: face[3], 8: face[4], 5: face[5]}
    fields = [velocity[0], velocity[1], velocity[2]] + [stress[k] for k in range(6)]
    rows = []
    for k, field in enumerate(fields):
        if k in replace:
            field = lax.dynamic_update_slice_in_dim(field, replace[k][None], depth, axis=0)
        rows.append(field)
    return jnp.stack(rows)


def local(
    fine_wave,
    fine_memory,
    fine_material,
    fine_mechanism,
    fine_metric,
    coarse_wave,
    coarse_memory,
    coarse_material,
    coarse_mechanism,
    material_table,
    attenuation_table,
):
    fine_matrix = sbp_table(fine_wave.shape[1], 1.0)
    coarse_matrix = sbp_table(coarse_wave.shape[1], 3.0)
    fine_buoy = lookup_table(fine_material, material_table[0])
    fine_lame = lookup_table(fine_material, material_table[1])
    fine_shear = lookup_table(fine_material, material_table[2])
    fine_decay = lookup_table(fine_mechanism, attenuation_table[0])
    fine_strength = lookup_table(fine_mechanism, attenuation_table[1])
    coarse_buoy = lookup_table(coarse_material, material_table[0])
    coarse_lame = lookup_table(coarse_material, material_table[1])
    coarse_shear = lookup_table(coarse_material, material_table[2])
    coarse_decay = lookup_table(coarse_mechanism, attenuation_table[0])
    coarse_strength = lookup_table(coarse_mechanism, attenuation_table[1])

    def x_parts(w):
        return jnp.stack([w[3], w[6], w[7]])

    def y_parts(w):
        return jnp.stack([w[6], w[4], w[8]])

    fx, fy, cx, cy = x_parts(fine_wave), y_parts(fine_wave), x_parts(coarse_wave), y_parts(coarse_wave)
    x_lo = packed_shift([fx[..., -2:, :], cx[..., -2:, :]], "gx", 1)
    x_hi = packed_shift([fx[..., :2, :], cx[..., :2, :]], "gx", -1)
    y_lo = packed_shift([fy[..., -2:], cy[..., -2:]], "gy", 1)
    y_hi = packed_shift([fy[..., :2], cy[..., :2]], "gy", -1)
    fine_hx = (x_lo[0], x_hi[0], None, None)
    fine_hy = (None, None, y_lo[0], y_hi[0])
    coarse_hx = (x_lo[1], x_hi[1], None, None)
    coarse_hy = (None, None, y_lo[1], y_hi[1])

    fine_velocity = velocity_step(fine_wave, fine_hx, fine_hy, fine_buoy, fine_metric, fine_matrix, 1.0)
    coarse_velocity = velocity_step(coarse_wave, coarse_hx, coarse_hy, coarse_buoy, 1.0, coarse_matrix, 3.0)

    fine_vh, coarse_vh = exchange([fine_velocity, coarse_velocity], 2)
    fine_stress, fine_mem = stress_step(
        fine_wave, fine_memory, fine_velocity, fine_vh, fine_lame, fine_shear, fine_decay, fine_strength,
        fine_metric, fine_matrix, 1.0,
    )
    coarse_stress, coarse_mem = stress_step(
        coarse_wave, coarse_memory, coarse_velocity, coarse_vh, coarse_lame, coarse_shear, coarse_decay,
        coarse_strength, 1.0, coarse_matrix, 3.0,
    )

    depth = fine_wave.shape[1] - 1
    fine_face = face_of(fine_velocity, fine_stress, depth)
    coarse_face = face_of(coarse_velocity, coarse_stress, 0)
    fine_padded, coarse_padded = pad_faces([fine_face, coarse_face])
    fine_new = fine_face - penalty * (fine_face - prolong_axis(prolong_axis(coarse_padded, 1), 2))
    coarse_new = coarse_face - penalty * (coarse_face - restrict_axis(restrict_axis(fine_padded, 1), 2))
    fine_out = assemble(fine_velocity, fine_stress, fine_new, depth)
    coarse_out = assemble(coarse_velocity, coarse_stress, coarse_new, 0)
    return (fine_out, fine_mem, coarse_out, coarse_mem)


def solution(mesh):
    in_specs = (
        P(None, None, "gx", "gy"),
        P(None, None, "gx", "gy"),
        P(None, "gx", "gy"),
        P(None, "gx", "gy"),
        P(None, "gx", "gy"),
        P(None, None, "gx", "gy"),
        P(None, None, "gx", "gy"),
        P(None, "gx", "gy"),
        P(None, "gx", "gy"),
        P(),
        P(),
    )
    out_specs = (
        P(None, None, "gx", "gy"),
        P(None, None, "gx", "gy"),
        P(None, None, "gx", "gy"),
        P(None, None, "gx", "gy"),
    )
    return jax.shard_map(local, mesh=mesh, in_specs=in_specs, out_specs=out_specs, check_vma=False)
```

```python
import functools
import math

import jax
import jax.numpy as jnp
import numpy as np
from jax import lax
from jax.sharding import PartitionSpec as P

step_size = 0.1
penalty = 0.1 * 48.0 / 17.0
closure = [
    [-24.0 / 17.0, 59.0 / 34.0, -4.0 / 17.0, -3.0 / 34.0, 0.0, 0.0],
    [-0.5, 0.0, 0.5, 0.0, 0.0, 0.0],
    [4.0 / 43.0, -59.0 / 86.0, 0.0, 59.0 / 86.0, -4.0 / 43.0, 0.0],
    [3.0 / 98.0, 0.0, -59.0 / 98.0, 0.0, 32.0 / 49.0, -4.0 / 49.0],
]


def sbp_table(layers, spacing):
    return jnp.asarray(sbp_numpy(layers, spacing))


def sbp_numpy(layers, spacing):
    table = np.zeros((layers, layers))
    for line_at in range(4):
        for column in range(6):
            table[line_at, column] = closure[line_at][column]
            table[layers - 1 - line_at, layers - 1 - column] = -closure[line_at][column]
    for line_at in range(4, layers - 4):
        table[line_at, line_at - 2 : line_at + 3] = [
            1.0 / 12.0,
            -2.0 / 3.0,
            0.0,
            2.0 / 3.0,
            -1.0 / 12.0,
        ]
    return (table / spacing).astype(np.float32)


def shift_from(block, axis, offset):
    count = lax.axis_size(axis)
    pairs = [(i, i + offset) for i in range(count) if 0 <= i + offset < count]
    return lax.ppermute(block, axis, pairs)


def packed_shift(blocks, axis, offset):
    sizes = [math.prod(b.shape) for b in blocks]
    joined = jnp.concatenate([b.reshape(-1) for b in blocks])
    moved = shift_from(joined, axis, offset)
    out, start = [], 0
    for b, size in zip(blocks, sizes):
        out.append(moved[start : start + size].reshape(b.shape))
        start += size
    return out


def exchange(blocks, width):
    x_lo = packed_shift([b[..., -width:, :] for b in blocks], "gx", 1)
    x_hi = packed_shift([b[..., :width, :] for b in blocks], "gx", -1)
    y_lo = packed_shift([b[..., -width:] for b in blocks], "gy", 1)
    y_hi = packed_shift([b[..., :width] for b in blocks], "gy", -1)
    return [(x_lo[i], x_hi[i], y_lo[i], y_hi[i]) for i in range(len(blocks))]


def central_diff(padded, along, spacing):
    length = padded.shape[along] - 4
    s = lambda o: lax.slice_in_dim(padded, o, o + length, axis=along)
    return (s(0) - 8.0 * s(1) + 8.0 * s(3) - s(4)) / (12.0 * spacing)


def diff_x(block, halo, spacing):
    x_lo, x_hi, _, _ = halo
    return central_diff(jnp.concatenate([x_lo, block, x_hi], axis=-2), block.ndim - 2, spacing)


def diff_y(block, halo, spacing):
    _, _, y_lo, y_hi = halo
    return central_diff(jnp.concatenate([y_lo, block, y_hi], axis=-1), block.ndim - 1, spacing)


def vertical_diff(fields, matrix):
    return jnp.einsum("kz,czxy->ckxy", matrix, fields, precision=lax.Precision.HIGHEST)


def lookup_table(grid_cell_index, values):
    result = jnp.zeros(grid_cell_index.shape, jnp.float32)
    for kind_at in range(values.shape[0]):
        result = jnp.where(grid_cell_index == kind_at, values[kind_at], result)
    return result


def velocity_step(wave, halo_x3, halo_y3, buoyancy, metric, matrix, spacing):
    sx = jnp.stack([wave[3], wave[6], wave[7]])
    sy = jnp.stack([wave[6], wave[4], wave[8]])
    slope_x = diff_x(sx, halo_x3, spacing)
    slope_y = diff_y(sy, halo_y3, spacing)
    slope_z = metric * vertical_diff(jnp.stack([wave[7], wave[8], wave[5]]), matrix)
    rate_x = slope_x[0] + slope_y[0] + slope_z[0]
    rate_y = slope_x[1] + slope_y[1] + slope_z[1]
    rate_z = slope_x[2] + slope_y[2] + slope_z[2]
    return wave[:3] + step_size * (buoyancy * jnp.stack([rate_x, rate_y, rate_z]))


def stress_step(wave, memory, velocity, halo, lame, shear, decay, strength, metric, matrix, spacing):
    slope_x = diff_x(velocity, halo, spacing)
    slope_y = diff_y(velocity, halo, spacing)
    slope_z = metric * vertical_diff(velocity, matrix)
    cell_volume = lame * (slope_x[0] + slope_y[1] + slope_z[2])
    rate = jnp.stack(
        [
            cell_volume + 2.0 * shear * slope_x[0],
            cell_volume + 2.0 * shear * slope_y[1],
            cell_volume + 2.0 * shear * slope_z[2],
            shear * (slope_y[0] + slope_x[1]),
            shear * (slope_z[0] + slope_x[2]),
            shear * (slope_z[1] + slope_y[2]),
        ]
    )
    memory_new = decay * memory + (1.0 - decay) * strength * rate
    stress = wave[3:] + step_size * (rate - memory_new)
    return stress, memory_new


def face_of(velocity, stress, depth):
    return jnp.stack(
        [
            velocity[0, depth],
            velocity[1, depth],
            velocity[2, depth],
            stress[4, depth],
            stress[5, depth],
            stress[2, depth],
        ]
    )


def pad_faces(faces):
    x_lo = packed_shift([f[:, -1:, :] for f in faces], "gx", 1)
    x_hi = packed_shift([f[:, :1, :] for f in faces], "gx", -1)
    faces = [jnp.concatenate([lo, f, hi], axis=1) for lo, f, hi in zip(x_lo, faces, x_hi)]
    y_lo = packed_shift([f[:, :, -1:] for f in faces], "gy", 1)
    y_hi = packed_shift([f[:, :, :1] for f in faces], "gy", -1)
    return [jnp.concatenate([lo, f, hi], axis=2) for lo, f, hi in zip(y_lo, faces, y_hi)]


def shifted(padded, offset, length, along):
    return lax.slice_in_dim(padded, offset, offset + length, axis=along)


def prolong_axis(padded, along):
    length = padded.shape[along] - 2
    left = shifted(padded, 0, length, along)
    middle = shifted(padded, 1, length, along)
    right = shifted(padded, 2, length, along)
    parts = jnp.stack(
        [(left + 2.0 * middle) / 3.0, middle, (2.0 * middle + right) / 3.0], axis=along + 1
    )
    shape = list(middle.shape)
    shape[along] = shape[along] * 3
    return parts.reshape(tuple(shape))


def split_three(padded, offset, length, along):
    part = shifted(padded, offset, 3 * length, along)
    return part.reshape(part.shape[:along] + (length, 3) + part.shape[along + 1 :])


def pick_part(parts, number, along):
    return lax.index_in_dim(parts, number, along + 1, keepdims=False)


def restrict_axis(padded, along):
    length = (padded.shape[along] - 2) // 3
    first = split_three(padded, 0, length, along)
    middle = split_three(padded, 1, length, along)
    last = split_three(padded, 2, length, along)
    return (
        pick_part(first, 0, along)
        + 2.0 * pick_part(middle, 0, along)
        + 3.0 * pick_part(middle, 1, along)
        + 2.0 * pick_part(middle, 2, along)
        + pick_part(last, 2, along)
    ) / 9.0


def assemble(velocity, stress, face, depth):
    replace = {0: face[0], 1: face[1], 2: face[2], 7: face[3], 8: face[4], 5: face[5]}
    fields = [velocity[0], velocity[1], velocity[2]] + [stress[k] for k in range(6)]
    rows = []
    for k, field in enumerate(fields):
        if k in replace:
            field = lax.dynamic_update_slice_in_dim(field, replace[k][None], depth, axis=0)
        rows.append(field)
    return jnp.stack(rows)


from jax.experimental import pallas as pl
from jax.experimental.pallas import tpu as pltpu


def sbp_rows(layers, spacing):
    table = sbp_numpy(layers, spacing)
    return [[(j, float(table[k, j])) for j in range(layers) if table[k, j] != 0.0] for k in range(layers)]


def pick(values_ref, row, index):
    result = jnp.zeros(index.shape, jnp.float32)
    for kind_at in range(values_ref.shape[1]):
        result = jnp.where(index == kind_at, values_ref[row, kind_at], result)
    return result


def fill_x(scratch, slot, lo, block, hi):
    width = lo.shape[-2]
    size = block.shape[-2]
    scratch[slot, :, 0:width, :] = lo
    scratch[slot, :, width : width + size, :] = block
    scratch[slot, :, width + size :, :] = hi


def slope_x(scratch, slot, z, size, spacing):
    s = lambda o: scratch[slot, z, o : o + size, :]
    return (s(0) - 8.0 * s(1) + 8.0 * s(3) - s(4)) / (12.0 * spacing)


def slope_y(f, lo, hi, spacing):
    n = f.shape[-1]
    lane = lax.broadcasted_iota(jnp.int32, f.shape, f.ndim - 1)
    m1 = jnp.where(lane == 0, lo[:, 1:2], pltpu.roll(f, 1, f.ndim - 1))
    m2 = jnp.where(lane == 0, lo[:, 0:1], jnp.where(lane == 1, lo[:, 1:2], pltpu.roll(f, 2, f.ndim - 1)))
    p1 = jnp.where(lane == n - 1, hi[:, 0:1], pltpu.roll(f, n - 1, f.ndim - 1))
    p2 = jnp.where(lane == n - 2, hi[:, 0:1], jnp.where(lane == n - 1, hi[:, 1:2], pltpu.roll(f, n - 2, f.ndim - 1)))
    return (m2 - 8.0 * m1 + 8.0 * p1 - p2) / (12.0 * spacing)


def slope_z(field_ref, index, row):
    total = None
    for j, weight in row:
        term = jnp.float32(weight) * field_ref[index, j]
        total = term if total is None else total + term
    return total


def velocity_kernel(rows, spacing, has_metric, *refs):
    if has_metric:
        w, xlo, xhi, ylo, yhi, mat, metric, table, out, sx = refs
    else:
        w, xlo, xhi, ylo, yhi, mat, table, out, sx = refs
        metric = None
    layers, size = w.shape[1], w.shape[2]
    for slot, field in enumerate((3, 6, 7)):
        fill_x(sx, slot, xlo[slot], w[field], xhi[slot])
    for z in range(layers):
        dx = [slope_x(sx, slot, z, size, spacing) for slot in range(3)]
        dy = [slope_y(w[field, z], ylo[slot, z], yhi[slot, z], spacing) for slot, field in enumerate((6, 4, 8))]
        dz = [slope_z(w, field, rows[z]) for field in (7, 8, 5)]
        if metric is not None:
            m = metric[z]
            dz = [m * d for d in dz]
        buoy = pick(table, 0, mat[z])
        for k in range(3):
            out[k, z] = w[k, z] + step_size * (buoy * (dx[k] + dy[k] + dz[k]))


def stress_kernel(rows, spacing, has_metric, depth, *refs):
    if has_metric:
        w, mem, vel, xlo, xhi, ylo, yhi, mat, mech, metric, mtab, atab, out, mem_out, face, sx = refs
    else:
        w, mem, vel, xlo, xhi, ylo, yhi, mat, mech, mtab, atab, out, mem_out, face, sx = refs
        metric = None
    layers, size = w.shape[1], w.shape[2]
    for slot in range(3):
        fill_x(sx, slot, xlo[slot], vel[slot], xhi[slot])
    for z in range(layers):
        dx = [slope_x(sx, slot, z, size, spacing) for slot in range(3)]
        dy = [slope_y(vel[slot, z], ylo[slot, z], yhi[slot, z], spacing) for slot in range(3)]
        dz = [slope_z(vel, slot, rows[z]) for slot in range(3)]
        if metric is not None:
            m = metric[z]
            dz = [m * d for d in dz]
        kind, mechanism = mat[z], mech[z]
        lame, shear = pick(mtab, 1, kind), pick(mtab, 2, kind)
        decay, strength = pick(atab, 0, mechanism), pick(atab, 1, mechanism)
        cell_volume = lame * (dx[0] + dy[1] + dz[2])
        rate = [
            cell_volume + 2.0 * shear * dx[0],
            cell_volume + 2.0 * shear * dy[1],
            cell_volume + 2.0 * shear * dz[2],
            shear * (dy[0] + dx[1]),
            shear * (dz[0] + dx[2]),
            shear * (dz[1] + dy[2]),
        ]
        values = []
        for k in range(3):
            v = vel[k, z]
            out[k, z] = v
            values.append(v)
        for k in range(6):
            memory_new = decay * mem[k, z] + (1.0 - decay) * strength * rate[k]
            mem_out[k, z] = memory_new
            stress = w[3 + k, z] + step_size * (rate[k] - memory_new)
            out[3 + k, z] = stress
            values.append(stress)
        if z == depth:
            for i, k in enumerate((0, 1, 2, 7, 8, 5)):
                face[i] = values[k]


def vmem_specs(count):
    return [pl.BlockSpec(memory_space=pltpu.VMEM)] * count


def velocity_call(wave, halo_x, halo_y, material, metric, table, spacing):
    layers, size, lanes = wave.shape[1:]
    rows = sbp_rows(layers, spacing)
    args = [wave, halo_x[0], halo_x[1], halo_y[0], halo_y[1], material]
    if metric is not None:
        args.append(metric)
    kernel = functools.partial(velocity_kernel, rows, spacing, metric is not None)
    return pl.pallas_call(
        kernel,
        out_shape=jax.ShapeDtypeStruct((3, layers, size, lanes), jnp.float32),
        in_specs=vmem_specs(len(args)) + [pl.BlockSpec(memory_space=pltpu.SMEM)],
        out_specs=pl.BlockSpec(memory_space=pltpu.VMEM),
        scratch_shapes=[pltpu.VMEM((3, layers, size + 4, lanes), jnp.float32)],
    )(*args, table)


def stress_call(wave, memory, velocity, halo, material, mechanism, metric, mtab, atab, spacing, depth):
    layers, size, lanes = wave.shape[1:]
    rows = sbp_rows(layers, spacing)
    args = [wave, memory, velocity, halo[0], halo[1], halo[2], halo[3], material, mechanism]
    if metric is not None:
        args.append(metric)
    kernel = functools.partial(stress_kernel, rows, spacing, metric is not None, depth)
    return pl.pallas_call(
        kernel,
        out_shape=(
            jax.ShapeDtypeStruct(wave.shape, jnp.float32),
            jax.ShapeDtypeStruct(memory.shape, jnp.float32),
            jax.ShapeDtypeStruct((6, size, lanes), jnp.float32),
        ),
        in_specs=vmem_specs(len(args)) + [pl.BlockSpec(memory_space=pltpu.SMEM)] * 2,
        out_specs=tuple(vmem_specs(3)),
        scratch_shapes=[pltpu.VMEM((3, layers, size + 4, lanes), jnp.float32)],
    )(*args, mtab, atab)


def put_face(out, face, depth):
    out = lax.dynamic_update_slice(out, face[0:3][:, None], (0, depth, 0, 0))
    out = lax.dynamic_update_slice(out, face[5:6][:, None], (5, depth, 0, 0))
    out = lax.dynamic_update_slice(out, face[3:5][:, None], (7, depth, 0, 0))
    return out


def local(
    fine_wave,
    fine_memory,
    fine_material,
    fine_mechanism,
    fine_metric,
    coarse_wave,
    coarse_memory,
    coarse_material,
    coarse_mechanism,
    material_table,
    attenuation_table,
):
    def x_parts(w):
        return jnp.stack([w[3], w[6], w[7]])

    def y_parts(w):
        return jnp.stack([w[6], w[4], w[8]])

    fx, fy, cx, cy = x_parts(fine_wave), y_parts(fine_wave), x_parts(coarse_wave), y_parts(coarse_wave)
    x_lo = packed_shift([fx[..., -2:, :], cx[..., -2:, :]], "gx", 1)
    x_hi = packed_shift([fx[..., :2, :], cx[..., :2, :]], "gx", -1)
    y_lo = packed_shift([fy[..., -2:], cy[..., -2:]], "gy", 1)
    y_hi = packed_shift([fy[..., :2], cy[..., :2]], "gy", -1)

    fine_velocity = velocity_call(
        fine_wave, (x_lo[0], x_hi[0]), (y_lo[0], y_hi[0]), fine_material, fine_metric, material_table, 1.0
    )
    coarse_velocity = velocity_call(
        coarse_wave, (x_lo[1], x_hi[1]), (y_lo[1], y_hi[1]), coarse_material, None, material_table, 3.0
    )

    fine_vh, coarse_vh = exchange([fine_velocity, coarse_velocity], 2)
    depth = fine_wave.shape[1] - 1
    fine_out, fine_mem, fine_face = stress_call(
        fine_wave, fine_memory, fine_velocity, fine_vh, fine_material, fine_mechanism, fine_metric,
        material_table, attenuation_table, 1.0, depth,
    )
    coarse_out, coarse_mem, coarse_face = stress_call(
        coarse_wave, coarse_memory, coarse_velocity, coarse_vh, coarse_material, coarse_mechanism, None,
        material_table, attenuation_table, 3.0, 0,
    )

    fine_padded, coarse_padded = pad_faces([fine_face, coarse_face])
    fine_new = fine_face - penalty * (fine_face - prolong_axis(prolong_axis(coarse_padded, 1), 2))
    coarse_new = coarse_face - penalty * (coarse_face - restrict_axis(restrict_axis(fine_padded, 1), 2))
    return (put_face(fine_out, fine_new, depth), fine_mem, put_face(coarse_out, coarse_new, 0), coarse_mem)


def solution(mesh):
    in_specs = (
        P(None, None, "gx", "gy"),
        P(None, None, "gx", "gy"),
        P(None, "gx", "gy"),
        P(None, "gx", "gy"),
        P(None, "gx", "gy"),
        P(None, None, "gx", "gy"),
        P(None, None, "gx", "gy"),
        P(None, "gx", "gy"),
        P(None, "gx", "gy"),
        P(),
        P(),
    )
    out_specs = (
        P(None, None, "gx", "gy"),
        P(None, None, "gx", "gy"),
        P(None, None, "gx", "gy"),
        P(None, None, "gx", "gy"),
    )
    return jax.shard_map(local, mesh=mesh, in_specs=in_specs, out_specs=out_specs, check_vma=False)
```

```python
import functools
import math

import jax
import jax.numpy as jnp
import numpy as np
from jax import lax
from jax.sharding import PartitionSpec as P

step_size = 0.1
penalty = 0.1 * 48.0 / 17.0
closure = [
    [-24.0 / 17.0, 59.0 / 34.0, -4.0 / 17.0, -3.0 / 34.0, 0.0, 0.0],
    [-0.5, 0.0, 0.5, 0.0, 0.0, 0.0],
    [4.0 / 43.0, -59.0 / 86.0, 0.0, 59.0 / 86.0, -4.0 / 43.0, 0.0],
    [3.0 / 98.0, 0.0, -59.0 / 98.0, 0.0, 32.0 / 49.0, -4.0 / 49.0],
]


def sbp_table(layers, spacing):
    return jnp.asarray(sbp_numpy(layers, spacing))


def sbp_numpy(layers, spacing):
    table = np.zeros((layers, layers))
    for line_at in range(4):
        for column in range(6):
            table[line_at, column] = closure[line_at][column]
            table[layers - 1 - line_at, layers - 1 - column] = -closure[line_at][column]
    for line_at in range(4, layers - 4):
        table[line_at, line_at - 2 : line_at + 3] = [
            1.0 / 12.0,
            -2.0 / 3.0,
            0.0,
            2.0 / 3.0,
            -1.0 / 12.0,
        ]
    return (table / spacing).astype(np.float32)


def shift_from(block, axis, offset):
    count = lax.axis_size(axis)
    pairs = [(i, i + offset) for i in range(count) if 0 <= i + offset < count]
    return lax.ppermute(block, axis, pairs)


def packed_shift(blocks, axis, offset):
    sizes = [math.prod(b.shape) for b in blocks]
    joined = jnp.concatenate([b.reshape(-1) for b in blocks])
    moved = shift_from(joined, axis, offset)
    out, start = [], 0
    for b, size in zip(blocks, sizes):
        out.append(moved[start : start + size].reshape(b.shape))
        start += size
    return out


def exchange(blocks, width):
    x_lo = packed_shift([b[..., -width:, :] for b in blocks], "gx", 1)
    x_hi = packed_shift([b[..., :width, :] for b in blocks], "gx", -1)
    y_lo = packed_shift([b[..., -width:] for b in blocks], "gy", 1)
    y_hi = packed_shift([b[..., :width] for b in blocks], "gy", -1)
    return [(x_lo[i], x_hi[i], y_lo[i], y_hi[i]) for i in range(len(blocks))]


def central_diff(padded, along, spacing):
    length = padded.shape[along] - 4
    s = lambda o: lax.slice_in_dim(padded, o, o + length, axis=along)
    return (s(0) - 8.0 * s(1) + 8.0 * s(3) - s(4)) / (12.0 * spacing)


def diff_x(block, halo, spacing):
    x_lo, x_hi, _, _ = halo
    return central_diff(jnp.concatenate([x_lo, block, x_hi], axis=-2), block.ndim - 2, spacing)


def diff_y(block, halo, spacing):
    _, _, y_lo, y_hi = halo
    return central_diff(jnp.concatenate([y_lo, block, y_hi], axis=-1), block.ndim - 1, spacing)


def vertical_diff(fields, matrix):
    return jnp.einsum("kz,czxy->ckxy", matrix, fields, precision=lax.Precision.HIGHEST)


def lookup_table(grid_cell_index, values):
    result = jnp.zeros(grid_cell_index.shape, jnp.float32)
    for kind_at in range(values.shape[0]):
        result = jnp.where(grid_cell_index == kind_at, values[kind_at], result)
    return result


def velocity_step(wave, halo_x3, halo_y3, buoyancy, metric, matrix, spacing):
    sx = jnp.stack([wave[3], wave[6], wave[7]])
    sy = jnp.stack([wave[6], wave[4], wave[8]])
    slope_x = diff_x(sx, halo_x3, spacing)
    slope_y = diff_y(sy, halo_y3, spacing)
    slope_z = metric * vertical_diff(jnp.stack([wave[7], wave[8], wave[5]]), matrix)
    rate_x = slope_x[0] + slope_y[0] + slope_z[0]
    rate_y = slope_x[1] + slope_y[1] + slope_z[1]
    rate_z = slope_x[2] + slope_y[2] + slope_z[2]
    return wave[:3] + step_size * (buoyancy * jnp.stack([rate_x, rate_y, rate_z]))


def stress_step(wave, memory, velocity, halo, lame, shear, decay, strength, metric, matrix, spacing):
    slope_x = diff_x(velocity, halo, spacing)
    slope_y = diff_y(velocity, halo, spacing)
    slope_z = metric * vertical_diff(velocity, matrix)
    cell_volume = lame * (slope_x[0] + slope_y[1] + slope_z[2])
    rate = jnp.stack(
        [
            cell_volume + 2.0 * shear * slope_x[0],
            cell_volume + 2.0 * shear * slope_y[1],
            cell_volume + 2.0 * shear * slope_z[2],
            shear * (slope_y[0] + slope_x[1]),
            shear * (slope_z[0] + slope_x[2]),
            shear * (slope_z[1] + slope_y[2]),
        ]
    )
    memory_new = decay * memory + (1.0 - decay) * strength * rate
    stress = wave[3:] + step_size * (rate - memory_new)
    return stress, memory_new


def face_of(velocity, stress, depth):
    return jnp.stack(
        [
            velocity[0, depth],
            velocity[1, depth],
            velocity[2, depth],
            stress[4, depth],
            stress[5, depth],
            stress[2, depth],
        ]
    )


def pad_faces(faces):
    x_lo = packed_shift([f[:, -1:, :] for f in faces], "gx", 1)
    x_hi = packed_shift([f[:, :1, :] for f in faces], "gx", -1)
    faces = [jnp.concatenate([lo, f, hi], axis=1) for lo, f, hi in zip(x_lo, faces, x_hi)]
    y_lo = packed_shift([f[:, :, -1:] for f in faces], "gy", 1)
    y_hi = packed_shift([f[:, :, :1] for f in faces], "gy", -1)
    return [jnp.concatenate([lo, f, hi], axis=2) for lo, f, hi in zip(y_lo, faces, y_hi)]


def shifted(padded, offset, length, along):
    return lax.slice_in_dim(padded, offset, offset + length, axis=along)


def prolong_axis(padded, along):
    length = padded.shape[along] - 2
    left = shifted(padded, 0, length, along)
    middle = shifted(padded, 1, length, along)
    right = shifted(padded, 2, length, along)
    parts = jnp.stack(
        [(left + 2.0 * middle) / 3.0, middle, (2.0 * middle + right) / 3.0], axis=along + 1
    )
    shape = list(middle.shape)
    shape[along] = shape[along] * 3
    return parts.reshape(tuple(shape))


def split_three(padded, offset, length, along):
    part = shifted(padded, offset, 3 * length, along)
    return part.reshape(part.shape[:along] + (length, 3) + part.shape[along + 1 :])


def pick_part(parts, number, along):
    return lax.index_in_dim(parts, number, along + 1, keepdims=False)


def restrict_axis(padded, along):
    length = (padded.shape[along] - 2) // 3
    first = split_three(padded, 0, length, along)
    middle = split_three(padded, 1, length, along)
    last = split_three(padded, 2, length, along)
    return (
        pick_part(first, 0, along)
        + 2.0 * pick_part(middle, 0, along)
        + 3.0 * pick_part(middle, 1, along)
        + 2.0 * pick_part(middle, 2, along)
        + pick_part(last, 2, along)
    ) / 9.0


def assemble(velocity, stress, face, depth):
    replace = {0: face[0], 1: face[1], 2: face[2], 7: face[3], 8: face[4], 5: face[5]}
    fields = [velocity[0], velocity[1], velocity[2]] + [stress[k] for k in range(6)]
    rows = []
    for k, field in enumerate(fields):
        if k in replace:
            field = lax.dynamic_update_slice_in_dim(field, replace[k][None], depth, axis=0)
        rows.append(field)
    return jnp.stack(rows)


from jax.experimental import pallas as pl
from jax.experimental.pallas import tpu as pltpu


def sbp_rows(layers, spacing):
    table = sbp_numpy(layers, spacing)
    return [[(j, float(table[k, j])) for j in range(layers) if table[k, j] != 0.0] for k in range(layers)]


def pick(values_ref, row, index):
    result = jnp.zeros(index.shape, jnp.float32)
    for kind_at in range(values_ref.shape[1]):
        result = jnp.where(index == kind_at, values_ref[row, kind_at], result)
    return result


def fill_x(scratch, slot, lo, block, hi):
    width = lo.shape[-2]
    size = block.shape[-2]
    scratch[slot, :, 0:width, :] = lo
    scratch[slot, :, width : width + size, :] = block
    scratch[slot, :, width + size :, :] = hi


def slope_x(scratch, slot, z, size, spacing):
    s = lambda o: scratch[slot, z, o : o + size, :]
    return (s(0) - 8.0 * s(1) + 8.0 * s(3) - s(4)) / (12.0 * spacing)


def slope_y(f, lo, hi, spacing):
    n = f.shape[-1]
    lane = lax.broadcasted_iota(jnp.int32, f.shape, f.ndim - 1)
    m1 = jnp.where(lane == 0, lo[:, 1:2], pltpu.roll(f, 1, f.ndim - 1))
    m2 = jnp.where(lane == 0, lo[:, 0:1], jnp.where(lane == 1, lo[:, 1:2], pltpu.roll(f, 2, f.ndim - 1)))
    p1 = jnp.where(lane == n - 1, hi[:, 0:1], pltpu.roll(f, n - 1, f.ndim - 1))
    p2 = jnp.where(lane == n - 2, hi[:, 0:1], jnp.where(lane == n - 1, hi[:, 1:2], pltpu.roll(f, n - 2, f.ndim - 1)))
    return (m2 - 8.0 * m1 + 8.0 * p1 - p2) / (12.0 * spacing)


def slope_z(field_ref, index, row):
    total = None
    for j, weight in row:
        term = jnp.float32(weight) * field_ref[index, j]
        total = term if total is None else total + term
    return total


class Block:
    def __init__(self, shape, spacing, has_metric, x_base, y_base):
        self.layers, self.size, self.lanes = shape
        self.chunks = self.lanes // 128
        self.spacing = spacing
        self.has_metric = has_metric
        self.rows = sbp_rows(self.layers, spacing)
        self.x_base, self.y_base = x_base, y_base

    @property
    def x_rows(self):
        return 3 * self.layers * self.chunks * 2

    @property
    def y_rows(self):
        return self.layers * self.size


def plan_blocks(fine_shape, coarse_shape):
    fine = Block(fine_shape, 1.0, True, 0, 0)
    coarse = Block(coarse_shape, 3.0, False, fine.x_rows, fine.y_rows)
    return fine, coarse, fine.x_rows + coarse.x_rows, fine.y_rows + coarse.y_rows


def write_rims(b, src, fields, x_prev, x_next, y_prev, y_next):
    size, lanes = b.size, b.lanes
    for c, field in enumerate(fields):
        for z in range(b.layers):
            lo = src[field, z, 0:2, :]
            hi = src[field, z, size - 2 : size, :]
            for j in range(b.chunks):
                row = b.x_base + ((c * b.layers + z) * b.chunks + j) * 2
                x_prev[row : row + 2, :] = lo[:, j * 128 : (j + 1) * 128]
                x_next[row : row + 2, :] = hi[:, j * 128 : (j + 1) * 128]
    lane = lax.broadcasted_iota(jnp.int32, (size, 128), 1)
    for z in range(b.layers):
        acc_lo = jnp.zeros((size, 128), jnp.float32)
        acc_hi = jnp.zeros((size, 128), jnp.float32)
        for c, field in enumerate(fields):
            v = src[field, z]
            rl = v if c == 0 else pltpu.roll(v, 2 * c, 1)
            rh = pltpu.roll(v, (2 * c + 2) % lanes, 1)
            keep = (lane >= 2 * c) & (lane < 2 * c + 2)
            acc_lo = jnp.where(keep, rl[:, 0:128], acc_lo)
            acc_hi = jnp.where(keep, rh[:, 0:128], acc_hi)
        row = b.y_base + z * size
        y_prev[row : row + size, :] = acc_lo
        y_next[row : row + size, :] = acc_hi


def read_x_halo(b, buf, c, z):
    parts = [buf[pl.ds(b.x_base + ((c * b.layers + z) * b.chunks + j) * 2, 2), :] for j in range(b.chunks)]
    return parts[0] if len(parts) == 1 else jnp.concatenate(parts, axis=1)


def read_y_halo(b, buf, c, z):
    row = b.y_base + z * b.size
    return buf[pl.ds(row, b.size), pl.ds(2 * c, 1)], buf[pl.ds(row, b.size), pl.ds(2 * c + 1, 1)]


def fill_x2(b, scratch, slot, src, field, lo_buf, hi_buf):
    size = b.size
    scratch[slot, :, 2 : 2 + size, :] = src[field]
    for z in range(b.layers):
        scratch[slot, z, 0:2, :] = read_x_halo(b, lo_buf, slot, z)
        scratch[slot, z, 2 + size :, :] = read_x_halo(b, hi_buf, slot, z)


def slope_y2(f, lo, hi, spacing):
    n = f.shape[-1]
    lane = lax.broadcasted_iota(jnp.int32, f.shape, 1)
    m1 = jnp.where(lane == 0, lo[1], pltpu.roll(f, 1, 1))
    m2 = jnp.where(lane == 0, lo[0], jnp.where(lane == 1, lo[1], pltpu.roll(f, 2, 1)))
    p1 = jnp.where(lane == n - 1, hi[0], pltpu.roll(f, n - 1, 1))
    p2 = jnp.where(lane == n - 2, hi[0], jnp.where(lane == n - 1, hi[1], pltpu.roll(f, n - 2, 1)))
    return (m2 - 8.0 * m1 + 8.0 * p1 - p2) / (12.0 * spacing)


STRESS_X = (3, 6, 7)
STRESS_Y = (6, 4, 8)
VELOCITY = (0, 1, 2)


def pack_kernel(blocks, fw, cw, x_prev, x_next, y_prev, y_next):
    for b, w in zip(blocks, (fw, cw)):
        write_rims_split(b, w, x_prev, x_next, y_prev, y_next)


def write_rims_split(b, w, x_prev, x_next, y_prev, y_next):
    size, lanes = b.size, b.lanes
    for c, field in enumerate(STRESS_X):
        for z in range(b.layers):
            lo = w[field, z, 0:2, :]
            hi = w[field, z, size - 2 : size, :]
            for j in range(b.chunks):
                row = b.x_base + ((c * b.layers + z) * b.chunks + j) * 2
                x_prev[row : row + 2, :] = lo[:, j * 128 : (j + 1) * 128]
                x_next[row : row + 2, :] = hi[:, j * 128 : (j + 1) * 128]
    lane = lax.broadcasted_iota(jnp.int32, (size, 128), 1)
    for z in range(b.layers):
        acc_lo = jnp.zeros((size, 128), jnp.float32)
        acc_hi = jnp.zeros((size, 128), jnp.float32)
        for c, field in enumerate(STRESS_Y):
            v = w[field, z]
            rl = v if c == 0 else pltpu.roll(v, 2 * c, 1)
            rh = pltpu.roll(v, (2 * c + 2) % lanes, 1)
            keep = (lane >= 2 * c) & (lane < 2 * c + 2)
            acc_lo = jnp.where(keep, rl[:, 0:128], acc_lo)
            acc_hi = jnp.where(keep, rh[:, 0:128], acc_hi)
        row = b.y_base + z * size
        y_prev[row : row + size, :] = acc_lo
        y_next[row : row + size, :] = acc_hi


def velocity_block(b, w, mat, metric, table, out, sx, hx_lo, hx_hi, hy_lo, hy_hi):
    for slot, field in enumerate(STRESS_X):
        fill_x2(b, sx, slot, w, field, hx_lo, hx_hi)
    for z in range(b.layers):
        dx = [slope_x(sx, slot, z, b.size, b.spacing) for slot in range(3)]
        dy = [
            slope_y2(w[field, z], read_y_halo(b, hy_lo, slot, z), read_y_halo(b, hy_hi, slot, z), b.spacing)
            for slot, field in enumerate(STRESS_Y)
        ]
        dz = [slope_z(w, field, b.rows[z]) for field in (7, 8, 5)]
        if metric is not None:
            m = metric[z]
            dz = [m * d for d in dz]
        buoy = pick(table, 0, mat[z])
        for k in range(3):
            out[k, z] = w[k, z] + step_size * (buoy * (dx[k] + dy[k] + dz[k]))


def velocity_kernel(blocks, fw, cw, hx_lo, hx_hi, hy_lo, hy_hi, fmat, fmetric, cmat, table,
                    fvel, cvel, vx_prev, vx_next, vy_prev, vy_next, sx_f, sx_c):
    fine, coarse = blocks
    velocity_block(fine, fw, fmat, fmetric, table, fvel, sx_f, hx_lo, hx_hi, hy_lo, hy_hi)
    velocity_block(coarse, cw, cmat, None, table, cvel, sx_c, hx_lo, hx_hi, hy_lo, hy_hi)
    write_rims(fine, fvel, VELOCITY, vx_prev, vx_next, vy_prev, vy_next)
    write_rims(coarse, cvel, VELOCITY, vx_prev, vx_next, vy_prev, vy_next)


def stress_block(b, depth, w, mem, vel, mat, mech, metric, mtab, atab, out, mem_out, face, sx,
                 hx_lo, hx_hi, hy_lo, hy_hi):
    for slot in range(3):
        fill_x2(b, sx, slot, vel, slot, hx_lo, hx_hi)
    for z in range(b.layers):
        dx = [slope_x(sx, slot, z, b.size, b.spacing) for slot in range(3)]
        dy = [
            slope_y2(vel[slot, z], read_y_halo(b, hy_lo, slot, z), read_y_halo(b, hy_hi, slot, z), b.spacing)
            for slot in range(3)
        ]
        dz = [slope_z(vel, slot, b.rows[z]) for slot in range(3)]
        if metric is not None:
            m = metric[z]
            dz = [m * d for d in dz]
        kind, mechanism = mat[z], mech[z]
        lame, shear = pick(mtab, 1, kind), pick(mtab, 2, kind)
        decay, strength = pick(atab, 0, mechanism), pick(atab, 1, mechanism)
        cell_volume = lame * (dx[0] + dy[1] + dz[2])
        rate = [
            cell_volume + 2.0 * shear * dx[0],
            cell_volume + 2.0 * shear * dy[1],
            cell_volume + 2.0 * shear * dz[2],
            shear * (dy[0] + dx[1]),
            shear * (dz[0] + dx[2]),
            shear * (dz[1] + dy[2]),
        ]
        values = []
        for k in range(3):
            v = vel[k, z]
            out[k, z] = v
            values.append(v)
        for k in range(6):
            memory_new = decay * mem[k, z] + (1.0 - decay) * strength * rate[k]
            mem_out[k, z] = memory_new
            stress = w[3 + k, z] + step_size * (rate[k] - memory_new)
            out[3 + k, z] = stress
            values.append(stress)
        if z == depth:
            for i, k in enumerate((0, 1, 2, 7, 8, 5)):
                face[i] = values[k]


def stress_kernel(blocks, fw, fmem, fvel, cw, cmem, cvel, hx_lo, hx_hi, hy_lo, hy_hi,
                  fmat, fmech, fmetric, cmat, cmech, mtab, atab,
                  fout, fmem_out, fface, cout, cmem_out, cface, sx_f, sx_c):
    fine, coarse = blocks
    stress_block(fine, fine.layers - 1, fw, fmem, fvel, fmat, fmech, fmetric, mtab, atab, fout, fmem_out,
                 fface, sx_f, hx_lo, hx_hi, hy_lo, hy_hi)
    stress_block(coarse, 0, cw, cmem, cvel, cmat, cmech, None, mtab, atab, cout, cmem_out,
                 cface, sx_c, hx_lo, hx_hi, hy_lo, hy_hi)


def vmem_specs(count):
    return [pl.BlockSpec(memory_space=pltpu.VMEM)] * count


def f32(shape):
    return jax.ShapeDtypeStruct(shape, jnp.float32)


def halo_shapes(x_rows, y_rows):
    return (f32((x_rows, 128)), f32((x_rows, 128)), f32((y_rows, 128)), f32((y_rows, 128)))


def scratch_for(b):
    return pltpu.VMEM((3, b.layers, b.size + 4, b.lanes), jnp.float32)


def receive(buffers):
    x_prev, x_next, y_prev, y_next = buffers
    return (
        shift_from(x_next, "gx", 1),
        shift_from(x_prev, "gx", -1),
        shift_from(y_next, "gy", 1),
        shift_from(y_prev, "gy", -1),
    )


def put_face(out, face, depth):
    out = lax.dynamic_update_slice(out, face[0:3][:, None], (0, depth, 0, 0))
    out = lax.dynamic_update_slice(out, face[5:6][:, None], (5, depth, 0, 0))
    out = lax.dynamic_update_slice(out, face[3:5][:, None], (7, depth, 0, 0))
    return out


def local(
    fine_wave,
    fine_memory,
    fine_material,
    fine_mechanism,
    fine_metric,
    coarse_wave,
    coarse_memory,
    coarse_material,
    coarse_mechanism,
    material_table,
    attenuation_table,
):
    fine, coarse, x_rows, y_rows = plan_blocks(fine_wave.shape[1:], coarse_wave.shape[1:])
    blocks = (fine, coarse)
    smem = pl.BlockSpec(memory_space=pltpu.SMEM)

    rims = pl.pallas_call(
        functools.partial(pack_kernel, blocks),
        out_shape=halo_shapes(x_rows, y_rows),
        in_specs=vmem_specs(2),
        out_specs=tuple(vmem_specs(4)),
    )(fine_wave, coarse_wave)
    halos = receive(rims)

    fine_velocity, coarse_velocity, *vrims = pl.pallas_call(
        functools.partial(velocity_kernel, blocks),
        out_shape=(f32((3,) + fine_wave.shape[1:]), f32((3,) + coarse_wave.shape[1:])) + halo_shapes(x_rows, y_rows),
        in_specs=vmem_specs(9) + [smem],
        out_specs=tuple(vmem_specs(6)),
        scratch_shapes=[scratch_for(fine), scratch_for(coarse)],
    )(fine_wave, coarse_wave, *halos, fine_material, fine_metric, coarse_material, material_table)

    vhalos = receive(vrims)
    fine_out, fine_mem, fine_face, coarse_out, coarse_mem, coarse_face = pl.pallas_call(
        functools.partial(stress_kernel, blocks),
        out_shape=(
            f32(fine_wave.shape), f32(fine_memory.shape), f32((6,) + fine_wave.shape[2:]),
            f32(coarse_wave.shape), f32(coarse_memory.shape), f32((6,) + coarse_wave.shape[2:]),
        ),
        in_specs=vmem_specs(15) + [smem, smem],
        out_specs=tuple(vmem_specs(6)),
        scratch_shapes=[scratch_for(fine), scratch_for(coarse)],
    )(fine_wave, fine_memory, fine_velocity, coarse_wave, coarse_memory, coarse_velocity, *vhalos,
      fine_material, fine_mechanism, fine_metric, coarse_material, coarse_mechanism, material_table,
      attenuation_table)

    depth = fine_wave.shape[1] - 1
    fine_padded, coarse_padded = pad_faces([fine_face, coarse_face])
    fine_new = fine_face - penalty * (fine_face - prolong_axis(prolong_axis(coarse_padded, 1), 2))
    coarse_new = coarse_face - penalty * (coarse_face - restrict_axis(restrict_axis(fine_padded, 1), 2))
    return (put_face(fine_out, fine_new, depth), fine_mem, put_face(coarse_out, coarse_new, 0), coarse_mem)


def solution(mesh):
    in_specs = (
        P(None, None, "gx", "gy"),
        P(None, None, "gx", "gy"),
        P(None, "gx", "gy"),
        P(None, "gx", "gy"),
        P(None, "gx", "gy"),
        P(None, None, "gx", "gy"),
        P(None, None, "gx", "gy"),
        P(None, "gx", "gy"),
        P(None, "gx", "gy"),
        P(),
        P(),
    )
    out_specs = (
        P(None, None, "gx", "gy"),
        P(None, None, "gx", "gy"),
        P(None, None, "gx", "gy"),
        P(None, None, "gx", "gy"),
    )
    return jax.shard_map(local, mesh=mesh, in_specs=in_specs, out_specs=out_specs, check_vma=False)
```

```python
import functools
import math

import jax
import jax.numpy as jnp
import numpy as np
from jax import lax
from jax.sharding import PartitionSpec as P

step_size = 0.1
penalty = 0.1 * 48.0 / 17.0
closure = [
    [-24.0 / 17.0, 59.0 / 34.0, -4.0 / 17.0, -3.0 / 34.0, 0.0, 0.0],
    [-0.5, 0.0, 0.5, 0.0, 0.0, 0.0],
    [4.0 / 43.0, -59.0 / 86.0, 0.0, 59.0 / 86.0, -4.0 / 43.0, 0.0],
    [3.0 / 98.0, 0.0, -59.0 / 98.0, 0.0, 32.0 / 49.0, -4.0 / 49.0],
]


def sbp_table(layers, spacing):
    return jnp.asarray(sbp_numpy(layers, spacing))


def sbp_numpy(layers, spacing):
    table = np.zeros((layers, layers))
    for line_at in range(4):
        for column in range(6):
            table[line_at, column] = closure[line_at][column]
            table[layers - 1 - line_at, layers - 1 - column] = -closure[line_at][column]
    for line_at in range(4, layers - 4):
        table[line_at, line_at - 2 : line_at + 3] = [
            1.0 / 12.0,
            -2.0 / 3.0,
            0.0,
            2.0 / 3.0,
            -1.0 / 12.0,
        ]
    return (table / spacing).astype(np.float32)


def shift_from(block, axis, offset):
    count = lax.axis_size(axis)
    pairs = [(i, i + offset) for i in range(count) if 0 <= i + offset < count]
    return lax.ppermute(block, axis, pairs)


def packed_shift(blocks, axis, offset):
    sizes = [math.prod(b.shape) for b in blocks]
    joined = jnp.concatenate([b.reshape(-1) for b in blocks])
    moved = shift_from(joined, axis, offset)
    out, start = [], 0
    for b, size in zip(blocks, sizes):
        out.append(moved[start : start + size].reshape(b.shape))
        start += size
    return out


def exchange(blocks, width):
    x_lo = packed_shift([b[..., -width:, :] for b in blocks], "gx", 1)
    x_hi = packed_shift([b[..., :width, :] for b in blocks], "gx", -1)
    y_lo = packed_shift([b[..., -width:] for b in blocks], "gy", 1)
    y_hi = packed_shift([b[..., :width] for b in blocks], "gy", -1)
    return [(x_lo[i], x_hi[i], y_lo[i], y_hi[i]) for i in range(len(blocks))]


def central_diff(padded, along, spacing):
    length = padded.shape[along] - 4
    s = lambda o: lax.slice_in_dim(padded, o, o + length, axis=along)
    return (s(0) - 8.0 * s(1) + 8.0 * s(3) - s(4)) / (12.0 * spacing)


def diff_x(block, halo, spacing):
    x_lo, x_hi, _, _ = halo
    return central_diff(jnp.concatenate([x_lo, block, x_hi], axis=-2), block.ndim - 2, spacing)


def diff_y(block, halo, spacing):
    _, _, y_lo, y_hi = halo
    return central_diff(jnp.concatenate([y_lo, block, y_hi], axis=-1), block.ndim - 1, spacing)


def vertical_diff(fields, matrix):
    return jnp.einsum("kz,czxy->ckxy", matrix, fields, precision=lax.Precision.HIGHEST)


def lookup_table(grid_cell_index, values):
    result = jnp.zeros(grid_cell_index.shape, jnp.float32)
    for kind_at in range(values.shape[0]):
        result = jnp.where(grid_cell_index == kind_at, values[kind_at], result)
    return result


def velocity_step(wave, halo_x3, halo_y3, buoyancy, metric, matrix, spacing):
    sx = jnp.stack([wave[3], wave[6], wave[7]])
    sy = jnp.stack([wave[6], wave[4], wave[8]])
    slope_x = diff_x(sx, halo_x3, spacing)
    slope_y = diff_y(sy, halo_y3, spacing)
    slope_z = metric * vertical_diff(jnp.stack([wave[7], wave[8], wave[5]]), matrix)
    rate_x = slope_x[0] + slope_y[0] + slope_z[0]
    rate_y = slope_x[1] + slope_y[1] + slope_z[1]
    rate_z = slope_x[2] + slope_y[2] + slope_z[2]
    return wave[:3] + step_size * (buoyancy * jnp.stack([rate_x, rate_y, rate_z]))


def stress_step(wave, memory, velocity, halo, lame, shear, decay, strength, metric, matrix, spacing):
    slope_x = diff_x(velocity, halo, spacing)
    slope_y = diff_y(velocity, halo, spacing)
    slope_z = metric * vertical_diff(velocity, matrix)
    cell_volume = lame * (slope_x[0] + slope_y[1] + slope_z[2])
    rate = jnp.stack(
        [
            cell_volume + 2.0 * shear * slope_x[0],
            cell_volume + 2.0 * shear * slope_y[1],
            cell_volume + 2.0 * shear * slope_z[2],
            shear * (slope_y[0] + slope_x[1]),
            shear * (slope_z[0] + slope_x[2]),
            shear * (slope_z[1] + slope_y[2]),
        ]
    )
    memory_new = decay * memory + (1.0 - decay) * strength * rate
    stress = wave[3:] + step_size * (rate - memory_new)
    return stress, memory_new


def face_of(velocity, stress, depth):
    return jnp.stack(
        [
            velocity[0, depth],
            velocity[1, depth],
            velocity[2, depth],
            stress[4, depth],
            stress[5, depth],
            stress[2, depth],
        ]
    )


def pad_faces(faces):
    x_lo = packed_shift([f[:, -1:, :] for f in faces], "gx", 1)
    x_hi = packed_shift([f[:, :1, :] for f in faces], "gx", -1)
    faces = [jnp.concatenate([lo, f, hi], axis=1) for lo, f, hi in zip(x_lo, faces, x_hi)]
    y_lo = packed_shift([f[:, :, -1:] for f in faces], "gy", 1)
    y_hi = packed_shift([f[:, :, :1] for f in faces], "gy", -1)
    return [jnp.concatenate([lo, f, hi], axis=2) for lo, f, hi in zip(y_lo, faces, y_hi)]


def shifted(padded, offset, length, along):
    return lax.slice_in_dim(padded, offset, offset + length, axis=along)


def prolong_axis(padded, along):
    length = padded.shape[along] - 2
    left = shifted(padded, 0, length, along)
    middle = shifted(padded, 1, length, along)
    right = shifted(padded, 2, length, along)
    parts = jnp.stack(
        [(left + 2.0 * middle) / 3.0, middle, (2.0 * middle + right) / 3.0], axis=along + 1
    )
    shape = list(middle.shape)
    shape[along] = shape[along] * 3
    return parts.reshape(tuple(shape))


def split_three(padded, offset, length, along):
    part = shifted(padded, offset, 3 * length, along)
    return part.reshape(part.shape[:along] + (length, 3) + part.shape[along + 1 :])


def pick_part(parts, number, along):
    return lax.index_in_dim(parts, number, along + 1, keepdims=False)


def restrict_axis(padded, along):
    length = (padded.shape[along] - 2) // 3
    first = split_three(padded, 0, length, along)
    middle = split_three(padded, 1, length, along)
    last = split_three(padded, 2, length, along)
    return (
        pick_part(first, 0, along)
        + 2.0 * pick_part(middle, 0, along)
        + 3.0 * pick_part(middle, 1, along)
        + 2.0 * pick_part(middle, 2, along)
        + pick_part(last, 2, along)
    ) / 9.0


def assemble(velocity, stress, face, depth):
    replace = {0: face[0], 1: face[1], 2: face[2], 7: face[3], 8: face[4], 5: face[5]}
    fields = [velocity[0], velocity[1], velocity[2]] + [stress[k] for k in range(6)]
    rows = []
    for k, field in enumerate(fields):
        if k in replace:
            field = lax.dynamic_update_slice_in_dim(field, replace[k][None], depth, axis=0)
        rows.append(field)
    return jnp.stack(rows)


from jax.experimental import pallas as pl
from jax.experimental.pallas import tpu as pltpu


def sbp_rows(layers, spacing):
    table = sbp_numpy(layers, spacing)
    return [[(j, float(table[k, j])) for j in range(layers) if table[k, j] != 0.0] for k in range(layers)]


def pick(values_ref, row, index):
    result = jnp.zeros(index.shape, jnp.float32)
    for kind_at in range(values_ref.shape[1]):
        result = jnp.where(index == kind_at, values_ref[row, kind_at], result)
    return result


def fill_x(scratch, slot, lo, block, hi):
    width = lo.shape[-2]
    size = block.shape[-2]
    scratch[slot, :, 0:width, :] = lo
    scratch[slot, :, width : width + size, :] = block
    scratch[slot, :, width + size :, :] = hi


def slope_x(scratch, slot, z, size, spacing):
    s = lambda o: scratch[slot, z, o : o + size, :]
    return (s(0) - 8.0 * s(1) + 8.0 * s(3) - s(4)) / (12.0 * spacing)


def slope_y(f, lo, hi, spacing):
    n = f.shape[-1]
    lane = lax.broadcasted_iota(jnp.int32, f.shape, f.ndim - 1)
    m1 = jnp.where(lane == 0, lo[:, 1:2], pltpu.roll(f, 1, f.ndim - 1))
    m2 = jnp.where(lane == 0, lo[:, 0:1], jnp.where(lane == 1, lo[:, 1:2], pltpu.roll(f, 2, f.ndim - 1)))
    p1 = jnp.where(lane == n - 1, hi[:, 0:1], pltpu.roll(f, n - 1, f.ndim - 1))
    p2 = jnp.where(lane == n - 2, hi[:, 0:1], jnp.where(lane == n - 1, hi[:, 1:2], pltpu.roll(f, n - 2, f.ndim - 1)))
    return (m2 - 8.0 * m1 + 8.0 * p1 - p2) / (12.0 * spacing)


def slope_z(field_ref, index, row):
    total = None
    for j, weight in row:
        term = jnp.float32(weight) * field_ref[index, j]
        total = term if total is None else total + term
    return total


class Block:
    def __init__(self, shape, spacing, has_metric, x_base, y_base):
        self.layers, self.size, self.lanes = shape
        self.chunks = self.lanes // 128
        self.spacing = spacing
        self.has_metric = has_metric
        self.rows = sbp_rows(self.layers, spacing)
        self.x_base, self.y_base = x_base, y_base

    @property
    def x_rows(self):
        return 3 * self.layers * self.chunks * 2

    @property
    def y_rows(self):
        return self.layers * self.size


def plan_blocks(fine_shape, coarse_shape):
    fine = Block(fine_shape, 1.0, True, 0, 0)
    coarse = Block(coarse_shape, 3.0, False, fine.x_rows, fine.y_rows)
    fine.fx_base, fine.fy_base = 0, 0
    coarse.fx_base, coarse.fy_base = 6 * fine.chunks, fine.size
    return fine, coarse, fine.x_rows + coarse.x_rows, fine.y_rows + coarse.y_rows


def round8(n):
    return -(-n // 8) * 8


def write_rims(b, src, fields, x_prev, x_next, y_prev, y_next):
    size, lanes = b.size, b.lanes
    for c, field in enumerate(fields):
        for z in range(b.layers):
            lo = src[field, z, 0:2, :]
            hi = src[field, z, size - 2 : size, :]
            for j in range(b.chunks):
                row = b.x_base + ((c * b.layers + z) * b.chunks + j) * 2
                x_prev[row : row + 2, :] = lo[:, j * 128 : (j + 1) * 128]
                x_next[row : row + 2, :] = hi[:, j * 128 : (j + 1) * 128]
    lane = lax.broadcasted_iota(jnp.int32, (size, 128), 1)
    for z in range(b.layers):
        acc_lo = jnp.zeros((size, 128), jnp.float32)
        acc_hi = jnp.zeros((size, 128), jnp.float32)
        for c, field in enumerate(fields):
            v = src[field, z]
            rl = v if c == 0 else pltpu.roll(v, 2 * c, 1)
            rh = pltpu.roll(v, (2 * c + 2) % lanes, 1)
            keep = (lane >= 2 * c) & (lane < 2 * c + 2)
            acc_lo = jnp.where(keep, rl[:, 0:128], acc_lo)
            acc_hi = jnp.where(keep, rh[:, 0:128], acc_hi)
        row = b.y_base + z * size
        y_prev[row : row + size, :] = acc_lo
        y_next[row : row + size, :] = acc_hi


def read_x_halo(b, buf, c, z):
    parts = [buf[pl.ds(b.x_base + ((c * b.layers + z) * b.chunks + j) * 2, 2), :] for j in range(b.chunks)]
    return parts[0] if len(parts) == 1 else jnp.concatenate(parts, axis=1)


def read_y_halo(b, buf, c, z):
    row = b.y_base + z * b.size
    return buf[pl.ds(row, b.size), pl.ds(2 * c, 1)], buf[pl.ds(row, b.size), pl.ds(2 * c + 1, 1)]


def fill_x2(b, scratch, slot, src, field, lo_buf, hi_buf):
    size = b.size
    scratch[slot, :, 2 : 2 + size, :] = src[field]
    for z in range(b.layers):
        scratch[slot, z, 0:2, :] = read_x_halo(b, lo_buf, slot, z)
        scratch[slot, z, 2 + size :, :] = read_x_halo(b, hi_buf, slot, z)


def slope_y2(f, lo, hi, spacing):
    n = f.shape[-1]
    lane = lax.broadcasted_iota(jnp.int32, f.shape, 1)
    m1 = jnp.where(lane == 0, lo[1], pltpu.roll(f, 1, 1))
    m2 = jnp.where(lane == 0, lo[0], jnp.where(lane == 1, lo[1], pltpu.roll(f, 2, 1)))
    p1 = jnp.where(lane == n - 1, hi[0], pltpu.roll(f, n - 1, 1))
    p2 = jnp.where(lane == n - 2, hi[0], jnp.where(lane == n - 1, hi[1], pltpu.roll(f, n - 2, 1)))
    return (m2 - 8.0 * m1 + 8.0 * p1 - p2) / (12.0 * spacing)


STRESS_X = (3, 6, 7)
STRESS_Y = (6, 4, 8)
VELOCITY = (0, 1, 2)


def pack_kernel(blocks, fw, cw, x_prev, x_next, y_prev, y_next):
    for b, w in zip(blocks, (fw, cw)):
        write_rims_split(b, w, x_prev, x_next, y_prev, y_next)


def write_rims_split(b, w, x_prev, x_next, y_prev, y_next):
    size, lanes = b.size, b.lanes
    for c, field in enumerate(STRESS_X):
        for z in range(b.layers):
            lo = w[field, z, 0:2, :]
            hi = w[field, z, size - 2 : size, :]
            for j in range(b.chunks):
                row = b.x_base + ((c * b.layers + z) * b.chunks + j) * 2
                x_prev[row : row + 2, :] = lo[:, j * 128 : (j + 1) * 128]
                x_next[row : row + 2, :] = hi[:, j * 128 : (j + 1) * 128]
    lane = lax.broadcasted_iota(jnp.int32, (size, 128), 1)
    for z in range(b.layers):
        acc_lo = jnp.zeros((size, 128), jnp.float32)
        acc_hi = jnp.zeros((size, 128), jnp.float32)
        for c, field in enumerate(STRESS_Y):
            v = w[field, z]
            rl = v if c == 0 else pltpu.roll(v, 2 * c, 1)
            rh = pltpu.roll(v, (2 * c + 2) % lanes, 1)
            keep = (lane >= 2 * c) & (lane < 2 * c + 2)
            acc_lo = jnp.where(keep, rl[:, 0:128], acc_lo)
            acc_hi = jnp.where(keep, rh[:, 0:128], acc_hi)
        row = b.y_base + z * size
        y_prev[row : row + size, :] = acc_lo
        y_next[row : row + size, :] = acc_hi


def velocity_block(b, w, mat, metric, table, out, sx, hx_lo, hx_hi, hy_lo, hy_hi):
    for slot, field in enumerate(STRESS_X):
        fill_x2(b, sx, slot, w, field, hx_lo, hx_hi)
    for z in range(b.layers):
        dx = [slope_x(sx, slot, z, b.size, b.spacing) for slot in range(3)]
        dy = [
            slope_y2(w[field, z], read_y_halo(b, hy_lo, slot, z), read_y_halo(b, hy_hi, slot, z), b.spacing)
            for slot, field in enumerate(STRESS_Y)
        ]
        dz = [slope_z(w, field, b.rows[z]) for field in (7, 8, 5)]
        if metric is not None:
            m = metric[z]
            dz = [m * d for d in dz]
        buoy = pick(table, 0, mat[z])
        for k in range(3):
            out[k, z] = w[k, z] + step_size * (buoy * (dx[k] + dy[k] + dz[k]))


def velocity_kernel(blocks, fw, cw, hx_lo, hx_hi, hy_lo, hy_hi, fmat, fmetric, cmat, table,
                    fvel, cvel, vx_prev, vx_next, vy_prev, vy_next, sx_f, sx_c):
    fine, coarse = blocks
    velocity_block(fine, fw, fmat, fmetric, table, fvel, sx_f, hx_lo, hx_hi, hy_lo, hy_hi)
    velocity_block(coarse, cw, cmat, None, table, cvel, sx_c, hx_lo, hx_hi, hy_lo, hy_hi)
    write_rims(fine, fvel, VELOCITY, vx_prev, vx_next, vy_prev, vy_next)
    write_rims(coarse, cvel, VELOCITY, vx_prev, vx_next, vy_prev, vy_next)


def stress_block(b, depth, w, mem, vel, mat, mech, metric, mtab, atab, out, mem_out, face, sx,
                 hx_lo, hx_hi, hy_lo, hy_hi, face_rims):
    for slot in range(3):
        fill_x2(b, sx, slot, vel, slot, hx_lo, hx_hi)
    for z in range(b.layers):
        dx = [slope_x(sx, slot, z, b.size, b.spacing) for slot in range(3)]
        dy = [
            slope_y2(vel[slot, z], read_y_halo(b, hy_lo, slot, z), read_y_halo(b, hy_hi, slot, z), b.spacing)
            for slot in range(3)
        ]
        dz = [slope_z(vel, slot, b.rows[z]) for slot in range(3)]
        if metric is not None:
            m = metric[z]
            dz = [m * d for d in dz]
        kind, mechanism = mat[z], mech[z]
        lame, shear = pick(mtab, 1, kind), pick(mtab, 2, kind)
        decay, strength = pick(atab, 0, mechanism), pick(atab, 1, mechanism)
        cell_volume = lame * (dx[0] + dy[1] + dz[2])
        rate = [
            cell_volume + 2.0 * shear * dx[0],
            cell_volume + 2.0 * shear * dy[1],
            cell_volume + 2.0 * shear * dz[2],
            shear * (dy[0] + dx[1]),
            shear * (dz[0] + dx[2]),
            shear * (dz[1] + dy[2]),
        ]
        values = []
        for k in range(3):
            v = vel[k, z]
            out[k, z] = v
            values.append(v)
        for k in range(6):
            memory_new = decay * mem[k, z] + (1.0 - decay) * strength * rate[k]
            mem_out[k, z] = memory_new
            stress = w[3 + k, z] + step_size * (rate[k] - memory_new)
            out[3 + k, z] = stress
            values.append(stress)
        if z == depth:
            for i, k in enumerate((0, 1, 2, 7, 8, 5)):
                face[i] = values[k]
            write_face_rims(b, [values[k] for k in (0, 1, 2, 7, 8, 5)], *face_rims)


def write_face_rims(b, planes, x_prev, x_next, y_prev, y_next):
    size, lanes = b.size, b.lanes
    for i, v in enumerate(planes):
        for j in range(b.chunks):
            row = b.fx_base + i * b.chunks + j
            x_prev[row : row + 1, :] = v[0:1, j * 128 : (j + 1) * 128]
            x_next[row : row + 1, :] = v[size - 1 : size, j * 128 : (j + 1) * 128]
    lane = lax.broadcasted_iota(jnp.int32, (size, 128), 1)
    acc_lo = jnp.zeros((size, 128), jnp.float32)
    acc_hi = jnp.zeros((size, 128), jnp.float32)
    for i, v in enumerate(planes):
        rl = v if i == 0 else pltpu.roll(v, i, 1)
        rh = pltpu.roll(v, (i + 1) % lanes, 1)
        acc_lo = jnp.where(lane == i, rl[:, 0:128], acc_lo)
        acc_hi = jnp.where(lane == i, rh[:, 0:128], acc_hi)
    y_prev[b.fy_base : b.fy_base + size, :] = acc_lo
    y_next[b.fy_base : b.fy_base + size, :] = acc_hi


def stress_kernel(blocks, fw, fmem, fvel, cw, cmem, cvel, hx_lo, hx_hi, hy_lo, hy_hi,
                  fmat, fmech, fmetric, cmat, cmech, mtab, atab,
                  fout, fmem_out, fface, cout, cmem_out, cface, rx_prev, rx_next, ry_prev, ry_next, sx_f, sx_c):
    fine, coarse = blocks
    rims = (rx_prev, rx_next, ry_prev, ry_next)
    stress_block(fine, fine.layers - 1, fw, fmem, fvel, fmat, fmech, fmetric, mtab, atab, fout, fmem_out,
                 fface, sx_f, hx_lo, hx_hi, hy_lo, hy_hi, rims)
    stress_block(coarse, 0, cw, cmem, cvel, cmat, cmech, None, mtab, atab, cout, cmem_out,
                 cface, sx_c, hx_lo, hx_hi, hy_lo, hy_hi, rims)


def vmem_specs(count):
    return [pl.BlockSpec(memory_space=pltpu.VMEM)] * count


def f32(shape):
    return jax.ShapeDtypeStruct(shape, jnp.float32)


def halo_shapes(x_rows, y_rows):
    return (f32((x_rows, 128)), f32((x_rows, 128)), f32((y_rows, 128)), f32((y_rows, 128)))


def scratch_for(b):
    return pltpu.VMEM((3, b.layers, b.size + 4, b.lanes), jnp.float32)


def receive(buffers):
    x_prev, x_next, y_prev, y_next = buffers
    return (
        shift_from(x_next, "gx", 1),
        shift_from(x_prev, "gx", -1),
        shift_from(y_next, "gy", 1),
        shift_from(y_prev, "gy", -1),
    )


def put_face(out, face, depth):
    out = lax.dynamic_update_slice(out, face[0:3][:, None], (0, depth, 0, 0))
    out = lax.dynamic_update_slice(out, face[5:6][:, None], (5, depth, 0, 0))
    out = lax.dynamic_update_slice(out, face[3:5][:, None], (7, depth, 0, 0))
    return out


def prolong_y_matrix(coarse_lanes):
    m = np.zeros((coarse_lanes, 3 * coarse_lanes), np.float32)
    for d in range(coarse_lanes):
        m[d, 3 * d] = 2.0 / 3.0
        m[d, 3 * d + 1] = 1.0
        m[d, 3 * d + 2] = 2.0 / 3.0
        if d >= 1:
            m[d - 1, 3 * d] = 1.0 / 3.0
        if d + 1 < coarse_lanes:
            m[d + 1, 3 * d + 2] = 1.0 / 3.0
    return m


def restrict_y_matrix(coarse_lanes):
    m = np.zeros((3 * coarse_lanes, coarse_lanes), np.float32)
    for c in range(coarse_lanes):
        for offset, weight in ((-1, 1.0), (0, 2.0), (1, 3.0), (2, 2.0), (3, 1.0)):
            f = 3 * c + offset
            if 0 <= f < 3 * coarse_lanes:
                m[f, c] = weight / 9.0
    return m


def padded_rows(b, face, hx_lo, hx_hi, hy_lo, hy_hi, c_mm, c_pm, c_mp, c_pp, i):
    size = b.size

    def x_row(buf):
        parts = [buf[pl.ds(b.fx_base + i * b.chunks + j, 1), :] for j in range(b.chunks)]
        return parts[0] if len(parts) == 1 else jnp.concatenate(parts, axis=1)

    def lane_of(buf, row):
        return buf[pl.ds(b.fy_base + row, 1), pl.ds(i, 1)]

    rows = [(x_row(hx_lo), lane_of(c_mm, size - 1), lane_of(c_mp, size - 1))]
    for x in range(size):
        rows.append((face[i, pl.ds(x, 1), :], lane_of(hy_lo, x), lane_of(hy_hi, x)))
    rows.append((x_row(hx_hi), lane_of(c_pm, 0), lane_of(c_pp, 0)))
    return rows


def combine(terms):
    out = []
    for part in range(3):
        total = None
        for weight, row in terms:
            v = row[part] if weight == 1.0 else weight * row[part]
            total = v if total is None else total + v
        out.append(total)
    return out


def face_kernel(blocks, fine_depth, fout_in, cout_in, fface, cface, hx_lo, hx_hi, hy_lo, hy_hi,
                c_mm, c_pm, c_mp, c_pp, py, ry, fout, cout, fnew, cnew, stage_p, stage_r, sems):
    fine, coarse = blocks
    halos = (hx_lo, hx_hi, hy_lo, hy_hi, c_mm, c_pm, c_mp, c_pp)
    lane_f = lax.broadcasted_iota(jnp.int32, (1, fine.lanes), 1)
    p_lo, p_hi = [], []
    for i in range(6):
        rows = padded_rows(coarse, cface, *halos, i)
        for c in range(coarse.size):
            left, middle, right = rows[c], rows[c + 1], rows[c + 2]
            parts = [
                [(1.0, left), (2.0, middle)],
                [(1.0, middle)],
                [(2.0, middle), (1.0, right)],
            ]
            for a, terms in enumerate(parts):
                interior, lo, hi = combine(terms)
                if a != 1:
                    interior, lo, hi = interior / 3.0, lo / 3.0, hi / 3.0
                r = i * fine.size + 3 * c + a
                stage_p[pl.ds(r, 1), :] = interior
                p_lo.append(lo)
                p_hi.append(hi)
    prolonged = jnp.dot(stage_p[...], py[...], precision=lax.Precision.HIGHEST, preferred_element_type=jnp.float32)
    for i in range(6):
        for x in range(fine.size):
            r = i * fine.size + x
            value = prolonged[r : r + 1, :]
            value = value + jnp.where(lane_f == 0, p_lo[r] / 3.0, 0.0) + jnp.where(lane_f == fine.lanes - 1, p_hi[r] / 3.0, 0.0)
            own = fface[i, pl.ds(x, 1), :]
            fnew[i, 0, pl.ds(x, 1), :] = own - penalty * (own - value)
    lane_c = lax.broadcasted_iota(jnp.int32, (1, coarse.lanes), 1)
    r_lo, r_hi = [], []
    for i in range(6):
        rows = padded_rows(fine, fface, *halos, i)
        for c in range(coarse.size):
            terms = [(1.0, rows[3 * c]), (2.0, rows[3 * c + 1]), (3.0, rows[3 * c + 2]), (2.0, rows[3 * c + 3]),
                     (1.0, rows[3 * c + 4])]
            interior, lo, hi = combine(terms)
            r = i * coarse.size + c
            stage_r[pl.ds(r, 1), :] = interior / 9.0
            r_lo.append(lo / 9.0)
            r_hi.append(hi / 9.0)
    restricted = jnp.dot(stage_r[...], ry[...], precision=lax.Precision.HIGHEST, preferred_element_type=jnp.float32)
    for i in range(6):
        for c in range(coarse.size):
            r = i * coarse.size + c
            value = restricted[r : r + 1, :]
            value = value + jnp.where(lane_c == 0, r_lo[r] / 9.0, 0.0) + jnp.where(lane_c == coarse.lanes - 1, r_hi[r] / 9.0, 0.0)
            own = cface[i, pl.ds(c, 1), :]
            cnew[i, 0, pl.ds(c, 1), :] = own - penalty * (own - value)
    copies = []
    for n, (src, dst, depth) in enumerate(((fnew, fout, fine_depth), (cnew, cout, 0))):
        for k, (first, count, field) in enumerate(((0, 3, 0), (5, 1, 5), (3, 2, 7))):
            copy = pltpu.make_async_copy(
                src.at[pl.ds(first, count)], dst.at[pl.ds(field, count), pl.ds(depth, 1)], sems.at[3 * n + k]
            )
            copy.start()
            copies.append(copy)
    for copy in copies:
        copy.wait()


def diag_from(block, dx, dy):
    nx, ny = lax.axis_size("gx"), lax.axis_size("gy")
    pairs = []
    for i in range(nx):
        for j in range(ny):
            if 0 <= i + dx < nx and 0 <= j + dy < ny:
                pairs.append((i * ny + j, (i + dx) * ny + (j + dy)))
    return lax.ppermute(block, ("gx", "gy"), pairs)


def face_call(blocks, fine_out, coarse_out, fine_face, coarse_face, rims):
    fine, coarse = blocks
    x_prev, x_next, y_prev, y_next = rims
    received = (
        shift_from(x_next, "gx", 1),
        shift_from(x_prev, "gx", -1),
        shift_from(y_next, "gy", 1),
        shift_from(y_prev, "gy", -1),
        diag_from(y_next, 1, 1),
        diag_from(y_next, -1, 1),
        diag_from(y_prev, 1, -1),
        diag_from(y_prev, -1, -1),
    )
    py = jnp.asarray(prolong_y_matrix(coarse.lanes))
    ry = jnp.asarray(restrict_y_matrix(coarse.lanes))
    anyspace = pl.BlockSpec(memory_space=pl.ANY)
    return pl.pallas_call(
        functools.partial(face_kernel, blocks, fine.layers - 1),
        out_shape=(f32(fine_out.shape), f32(coarse_out.shape)),
        in_specs=[anyspace, anyspace] + vmem_specs(12),
        out_specs=(anyspace, anyspace),
        input_output_aliases={0: 0, 1: 1},
        scratch_shapes=[
            pltpu.VMEM((6, 1, fine.size, fine.lanes), jnp.float32),
            pltpu.VMEM((6, 1, coarse.size, coarse.lanes), jnp.float32),
            pltpu.VMEM((round8(6 * fine.size), coarse.lanes), jnp.float32),
            pltpu.VMEM((round8(6 * coarse.size), fine.lanes), jnp.float32),
            pltpu.SemaphoreType.DMA((6,)),
        ],
    )(fine_out, coarse_out, fine_face, coarse_face, *received, py, ry)


def local(
    fine_wave,
    fine_memory,
    fine_material,
    fine_mechanism,
    fine_metric,
    coarse_wave,
    coarse_memory,
    coarse_material,
    coarse_mechanism,
    material_table,
    attenuation_table,
):
    fine, coarse, x_rows, y_rows = plan_blocks(fine_wave.shape[1:], coarse_wave.shape[1:])
    blocks = (fine, coarse)
    smem = pl.BlockSpec(memory_space=pltpu.SMEM)

    rims = pl.pallas_call(
        functools.partial(pack_kernel, blocks),
        out_shape=halo_shapes(x_rows, y_rows),
        in_specs=vmem_specs(2),
        out_specs=tuple(vmem_specs(4)),
    )(fine_wave, coarse_wave)
    halos = receive(rims)

    fine_velocity, coarse_velocity, *vrims = pl.pallas_call(
        functools.partial(velocity_kernel, blocks),
        out_shape=(f32((3,) + fine_wave.shape[1:]), f32((3,) + coarse_wave.shape[1:])) + halo_shapes(x_rows, y_rows),
        in_specs=vmem_specs(9) + [smem],
        out_specs=tuple(vmem_specs(6)),
        scratch_shapes=[scratch_for(fine), scratch_for(coarse)],
    )(fine_wave, coarse_wave, *halos, fine_material, fine_metric, coarse_material, material_table)

    vhalos = receive(vrims)
    fx_rows = 6 * (fine.chunks + coarse.chunks)
    fy_rows = round8(fine.size + coarse.size)
    fine_out, fine_mem, fine_face, coarse_out, coarse_mem, coarse_face, *face_rims = pl.pallas_call(
        functools.partial(stress_kernel, blocks),
        out_shape=(
            f32(fine_wave.shape), f32(fine_memory.shape), f32((6,) + fine_wave.shape[2:]),
            f32(coarse_wave.shape), f32(coarse_memory.shape), f32((6,) + coarse_wave.shape[2:]),
            f32((fx_rows, 128)), f32((fx_rows, 128)), f32((fy_rows, 128)), f32((fy_rows, 128)),
        ),
        in_specs=vmem_specs(15) + [smem, smem],
        out_specs=tuple(vmem_specs(10)),
        scratch_shapes=[scratch_for(fine), scratch_for(coarse)],
    )(fine_wave, fine_memory, fine_velocity, coarse_wave, coarse_memory, coarse_velocity, *vhalos,
      fine_material, fine_mechanism, fine_metric, coarse_material, coarse_mechanism, material_table,
      attenuation_table)

    fine_out, coarse_out = face_call(blocks, fine_out, coarse_out, fine_face, coarse_face, face_rims)
    return (fine_out, fine_mem, coarse_out, coarse_mem)


def solution(mesh):
    in_specs = (
        P(None, None, "gx", "gy"),
        P(None, None, "gx", "gy"),
        P(None, "gx", "gy"),
        P(None, "gx", "gy"),
        P(None, "gx", "gy"),
        P(None, None, "gx", "gy"),
        P(None, None, "gx", "gy"),
        P(None, "gx", "gy"),
        P(None, "gx", "gy"),
        P(),
        P(),
    )
    out_specs = (
        P(None, None, "gx", "gy"),
        P(None, None, "gx", "gy"),
        P(None, None, "gx", "gy"),
        P(None, None, "gx", "gy"),
    )
    return jax.shard_map(local, mesh=mesh, in_specs=in_specs, out_specs=out_specs, check_vma=False)
```

```python
import functools
import math

import jax
import jax.numpy as jnp
import numpy as np
from jax import lax
from jax.sharding import PartitionSpec as P

step_size = 0.1
penalty = 0.1 * 48.0 / 17.0
closure = [
    [-24.0 / 17.0, 59.0 / 34.0, -4.0 / 17.0, -3.0 / 34.0, 0.0, 0.0],
    [-0.5, 0.0, 0.5, 0.0, 0.0, 0.0],
    [4.0 / 43.0, -59.0 / 86.0, 0.0, 59.0 / 86.0, -4.0 / 43.0, 0.0],
    [3.0 / 98.0, 0.0, -59.0 / 98.0, 0.0, 32.0 / 49.0, -4.0 / 49.0],
]


def sbp_table(layers, spacing):
    return jnp.asarray(sbp_numpy(layers, spacing))


def sbp_numpy(layers, spacing):
    table = np.zeros((layers, layers))
    for line_at in range(4):
        for column in range(6):
            table[line_at, column] = closure[line_at][column]
            table[layers - 1 - line_at, layers - 1 - column] = -closure[line_at][column]
    for line_at in range(4, layers - 4):
        table[line_at, line_at - 2 : line_at + 3] = [
            1.0 / 12.0,
            -2.0 / 3.0,
            0.0,
            2.0 / 3.0,
            -1.0 / 12.0,
        ]
    return (table / spacing).astype(np.float32)


def shift_from(block, axis, offset):
    count = lax.axis_size(axis)
    pairs = [(i, i + offset) for i in range(count) if 0 <= i + offset < count]
    return lax.ppermute(block, axis, pairs)


def packed_shift(blocks, axis, offset):
    sizes = [math.prod(b.shape) for b in blocks]
    joined = jnp.concatenate([b.reshape(-1) for b in blocks])
    moved = shift_from(joined, axis, offset)
    out, start = [], 0
    for b, size in zip(blocks, sizes):
        out.append(moved[start : start + size].reshape(b.shape))
        start += size
    return out


def exchange(blocks, width):
    x_lo = packed_shift([b[..., -width:, :] for b in blocks], "gx", 1)
    x_hi = packed_shift([b[..., :width, :] for b in blocks], "gx", -1)
    y_lo = packed_shift([b[..., -width:] for b in blocks], "gy", 1)
    y_hi = packed_shift([b[..., :width] for b in blocks], "gy", -1)
    return [(x_lo[i], x_hi[i], y_lo[i], y_hi[i]) for i in range(len(blocks))]


def central_diff(padded, along, spacing):
    length = padded.shape[along] - 4
    s = lambda o: lax.slice_in_dim(padded, o, o + length, axis=along)
    return (s(0) - 8.0 * s(1) + 8.0 * s(3) - s(4)) / (12.0 * spacing)


def diff_x(block, halo, spacing):
    x_lo, x_hi, _, _ = halo
    return central_diff(jnp.concatenate([x_lo, block, x_hi], axis=-2), block.ndim - 2, spacing)


def diff_y(block, halo, spacing):
    _, _, y_lo, y_hi = halo
    return central_diff(jnp.concatenate([y_lo, block, y_hi], axis=-1), block.ndim - 1, spacing)


def vertical_diff(fields, matrix):
    return jnp.einsum("kz,czxy->ckxy", matrix, fields, precision=lax.Precision.HIGHEST)


def lookup_table(grid_cell_index, values):
    result = jnp.zeros(grid_cell_index.shape, jnp.float32)
    for kind_at in range(values.shape[0]):
        result = jnp.where(grid_cell_index == kind_at, values[kind_at], result)
    return result


def velocity_step(wave, halo_x3, halo_y3, buoyancy, metric, matrix, spacing):
    sx = jnp.stack([wave[3], wave[6], wave[7]])
    sy = jnp.stack([wave[6], wave[4], wave[8]])
    slope_x = diff_x(sx, halo_x3, spacing)
    slope_y = diff_y(sy, halo_y3, spacing)
    slope_z = metric * vertical_diff(jnp.stack([wave[7], wave[8], wave[5]]), matrix)
    rate_x = slope_x[0] + slope_y[0] + slope_z[0]
    rate_y = slope_x[1] + slope_y[1] + slope_z[1]
    rate_z = slope_x[2] + slope_y[2] + slope_z[2]
    return wave[:3] + step_size * (buoyancy * jnp.stack([rate_x, rate_y, rate_z]))


def stress_step(wave, memory, velocity, halo, lame, shear, decay, strength, metric, matrix, spacing):
    slope_x = diff_x(velocity, halo, spacing)
    slope_y = diff_y(velocity, halo, spacing)
    slope_z = metric * vertical_diff(velocity, matrix)
    cell_volume = lame * (slope_x[0] + slope_y[1] + slope_z[2])
    rate = jnp.stack(
        [
            cell_volume + 2.0 * shear * slope_x[0],
            cell_volume + 2.0 * shear * slope_y[1],
            cell_volume + 2.0 * shear * slope_z[2],
            shear * (slope_y[0] + slope_x[1]),
            shear * (slope_z[0] + slope_x[2]),
            shear * (slope_z[1] + slope_y[2]),
        ]
    )
    memory_new = decay * memory + (1.0 - decay) * strength * rate
    stress = wave[3:] + step_size * (rate - memory_new)
    return stress, memory_new


def face_of(velocity, stress, depth):
    return jnp.stack(
        [
            velocity[0, depth],
            velocity[1, depth],
            velocity[2, depth],
            stress[4, depth],
            stress[5, depth],
            stress[2, depth],
        ]
    )


def pad_faces(faces):
    x_lo = packed_shift([f[:, -1:, :] for f in faces], "gx", 1)
    x_hi = packed_shift([f[:, :1, :] for f in faces], "gx", -1)
    faces = [jnp.concatenate([lo, f, hi], axis=1) for lo, f, hi in zip(x_lo, faces, x_hi)]
    y_lo = packed_shift([f[:, :, -1:] for f in faces], "gy", 1)
    y_hi = packed_shift([f[:, :, :1] for f in faces], "gy", -1)
    return [jnp.concatenate([lo, f, hi], axis=2) for lo, f, hi in zip(y_lo, faces, y_hi)]


def shifted(padded, offset, length, along):
    return lax.slice_in_dim(padded, offset, offset + length, axis=along)


def prolong_axis(padded, along):
    length = padded.shape[along] - 2
    left = shifted(padded, 0, length, along)
    middle = shifted(padded, 1, length, along)
    right = shifted(padded, 2, length, along)
    parts = jnp.stack(
        [(left + 2.0 * middle) / 3.0, middle, (2.0 * middle + right) / 3.0], axis=along + 1
    )
    shape = list(middle.shape)
    shape[along] = shape[along] * 3
    return parts.reshape(tuple(shape))


def split_three(padded, offset, length, along):
    part = shifted(padded, offset, 3 * length, along)
    return part.reshape(part.shape[:along] + (length, 3) + part.shape[along + 1 :])


def pick_part(parts, number, along):
    return lax.index_in_dim(parts, number, along + 1, keepdims=False)


def restrict_axis(padded, along):
    length = (padded.shape[along] - 2) // 3
    first = split_three(padded, 0, length, along)
    middle = split_three(padded, 1, length, along)
    last = split_three(padded, 2, length, along)
    return (
        pick_part(first, 0, along)
        + 2.0 * pick_part(middle, 0, along)
        + 3.0 * pick_part(middle, 1, along)
        + 2.0 * pick_part(middle, 2, along)
        + pick_part(last, 2, along)
    ) / 9.0


def assemble(velocity, stress, face, depth):
    replace = {0: face[0], 1: face[1], 2: face[2], 7: face[3], 8: face[4], 5: face[5]}
    fields = [velocity[0], velocity[1], velocity[2]] + [stress[k] for k in range(6)]
    rows = []
    for k, field in enumerate(fields):
        if k in replace:
            field = lax.dynamic_update_slice_in_dim(field, replace[k][None], depth, axis=0)
        rows.append(field)
    return jnp.stack(rows)


from jax.experimental import pallas as pl
from jax.experimental.pallas import tpu as pltpu


def sbp_rows(layers, spacing):
    table = sbp_numpy(layers, spacing)
    return [[(j, float(table[k, j])) for j in range(layers) if table[k, j] != 0.0] for k in range(layers)]


def pick(values_ref, row, index):
    result = jnp.zeros(index.shape, jnp.float32)
    for kind_at in range(values_ref.shape[1]):
        result = jnp.where(index == kind_at, values_ref[row, kind_at], result)
    return result


def fill_x(scratch, slot, lo, block, hi):
    width = lo.shape[-2]
    size = block.shape[-2]
    scratch[slot, :, 0:width, :] = lo
    scratch[slot, :, width : width + size, :] = block
    scratch[slot, :, width + size :, :] = hi


def slope_x(scratch, slot, z, size, spacing):
    s = lambda o: scratch[slot, z, o : o + size, :]
    return (s(0) - 8.0 * s(1) + 8.0 * s(3) - s(4)) / (12.0 * spacing)


def slope_y(f, lo, hi, spacing):
    n = f.shape[-1]
    lane = lax.broadcasted_iota(jnp.int32, f.shape, f.ndim - 1)
    m1 = jnp.where(lane == 0, lo[:, 1:2], pltpu.roll(f, 1, f.ndim - 1))
    m2 = jnp.where(lane == 0, lo[:, 0:1], jnp.where(lane == 1, lo[:, 1:2], pltpu.roll(f, 2, f.ndim - 1)))
    p1 = jnp.where(lane == n - 1, hi[:, 0:1], pltpu.roll(f, n - 1, f.ndim - 1))
    p2 = jnp.where(lane == n - 2, hi[:, 0:1], jnp.where(lane == n - 1, hi[:, 1:2], pltpu.roll(f, n - 2, f.ndim - 1)))
    return (m2 - 8.0 * m1 + 8.0 * p1 - p2) / (12.0 * spacing)


def slope_z(field_ref, index, row):
    total = None
    for j, weight in row:
        term = jnp.float32(weight) * field_ref[index, j]
        total = term if total is None else total + term
    return total


class Block:
    def __init__(self, shape, spacing, has_metric, x_base, y_base):
        self.layers, self.size, self.lanes = shape
        self.chunks = self.lanes // 128
        self.spacing = spacing
        self.has_metric = has_metric
        self.rows = sbp_rows(self.layers, spacing)
        self.x_base, self.y_base = x_base, y_base

    @property
    def x_rows(self):
        return 3 * self.layers * self.chunks * 2

    @property
    def y_rows(self):
        return self.layers * self.size


def plan_blocks(fine_shape, coarse_shape):
    fine = Block(fine_shape, 1.0, True, 0, 0)
    coarse = Block(coarse_shape, 3.0, False, fine.x_rows, fine.y_rows)
    fine.fx_base, fine.fy_base = 0, 0
    coarse.fx_base, coarse.fy_base = 6 * fine.chunks, fine.size
    corner_base = fine.size + coarse.size
    fine.corner_rows = (corner_base, corner_base + 1)
    coarse.corner_rows = (corner_base + 2, corner_base + 3)
    return fine, coarse, fine.x_rows + coarse.x_rows, fine.y_rows + coarse.y_rows


def round8(n):
    return -(-n // 8) * 8


def write_rims(b, src, fields, x_prev, x_next, y_prev, y_next):
    size, lanes = b.size, b.lanes
    for c, field in enumerate(fields):
        for z in range(b.layers):
            lo = src[field, z, 0:2, :]
            hi = src[field, z, size - 2 : size, :]
            for j in range(b.chunks):
                row = b.x_base + ((c * b.layers + z) * b.chunks + j) * 2
                x_prev[row : row + 2, :] = lo[:, j * 128 : (j + 1) * 128]
                x_next[row : row + 2, :] = hi[:, j * 128 : (j + 1) * 128]
    lane = lax.broadcasted_iota(jnp.int32, (size, 128), 1)
    for z in range(b.layers):
        acc_lo = jnp.zeros((size, 128), jnp.float32)
        acc_hi = jnp.zeros((size, 128), jnp.float32)
        for c, field in enumerate(fields):
            v = src[field, z]
            rl = v if c == 0 else pltpu.roll(v, 2 * c, 1)
            rh = pltpu.roll(v, (2 * c + 2) % lanes, 1)
            keep = (lane >= 2 * c) & (lane < 2 * c + 2)
            acc_lo = jnp.where(keep, rl[:, 0:128], acc_lo)
            acc_hi = jnp.where(keep, rh[:, 0:128], acc_hi)
        row = b.y_base + z * size
        y_prev[row : row + size, :] = acc_lo
        y_next[row : row + size, :] = acc_hi


def read_x_halo(b, buf, c, z):
    parts = [buf[pl.ds(b.x_base + ((c * b.layers + z) * b.chunks + j) * 2, 2), :] for j in range(b.chunks)]
    return parts[0] if len(parts) == 1 else jnp.concatenate(parts, axis=1)


def read_y_halo(b, buf, c, z):
    row = b.y_base + z * b.size
    return buf[pl.ds(row, b.size), pl.ds(2 * c, 1)], buf[pl.ds(row, b.size), pl.ds(2 * c + 1, 1)]


def fill_x2(b, scratch, slot, src, field, lo_buf, hi_buf):
    size = b.size
    scratch[slot, :, 2 : 2 + size, :] = src[field]
    for z in range(b.layers):
        scratch[slot, z, 0:2, :] = read_x_halo(b, lo_buf, slot, z)
        scratch[slot, z, 2 + size :, :] = read_x_halo(b, hi_buf, slot, z)


def slope_y2(f, lo, hi, spacing):
    n = f.shape[-1]
    lane = lax.broadcasted_iota(jnp.int32, f.shape, 1)
    m1 = jnp.where(lane == 0, lo[1], pltpu.roll(f, 1, 1))
    m2 = jnp.where(lane == 0, lo[0], jnp.where(lane == 1, lo[1], pltpu.roll(f, 2, 1)))
    p1 = jnp.where(lane == n - 1, hi[0], pltpu.roll(f, n - 1, 1))
    p2 = jnp.where(lane == n - 2, hi[0], jnp.where(lane == n - 1, hi[1], pltpu.roll(f, n - 2, 1)))
    return (m2 - 8.0 * m1 + 8.0 * p1 - p2) / (12.0 * spacing)


STRESS_X = (3, 6, 7)
STRESS_Y = (6, 4, 8)
VELOCITY = (0, 1, 2)


def pack_kernel(blocks, fw, cw, x_prev, x_next, y_prev, y_next):
    for b, w in zip(blocks, (fw, cw)):
        write_rims_split(b, w, x_prev, x_next, y_prev, y_next)


def write_rims_split(b, w, x_prev, x_next, y_prev, y_next):
    size, lanes = b.size, b.lanes
    for c, field in enumerate(STRESS_X):
        for z in range(b.layers):
            lo = w[field, z, 0:2, :]
            hi = w[field, z, size - 2 : size, :]
            for j in range(b.chunks):
                row = b.x_base + ((c * b.layers + z) * b.chunks + j) * 2
                x_prev[row : row + 2, :] = lo[:, j * 128 : (j + 1) * 128]
                x_next[row : row + 2, :] = hi[:, j * 128 : (j + 1) * 128]
    lane = lax.broadcasted_iota(jnp.int32, (size, 128), 1)
    for z in range(b.layers):
        acc_lo = jnp.zeros((size, 128), jnp.float32)
        acc_hi = jnp.zeros((size, 128), jnp.float32)
        for c, field in enumerate(STRESS_Y):
            v = w[field, z]
            rl = v if c == 0 else pltpu.roll(v, 2 * c, 1)
            rh = pltpu.roll(v, (2 * c + 2) % lanes, 1)
            keep = (lane >= 2 * c) & (lane < 2 * c + 2)
            acc_lo = jnp.where(keep, rl[:, 0:128], acc_lo)
            acc_hi = jnp.where(keep, rh[:, 0:128], acc_hi)
        row = b.y_base + z * size
        y_prev[row : row + size, :] = acc_lo
        y_next[row : row + size, :] = acc_hi


def velocity_block(b, w, mat, metric, table, out, sx, hx_lo, hx_hi, hy_lo, hy_hi):
    for slot, field in enumerate(STRESS_X):
        fill_x2(b, sx, slot, w, field, hx_lo, hx_hi)
    for z in range(b.layers):
        dx = [slope_x(sx, slot, z, b.size, b.spacing) for slot in range(3)]
        dy = [
            slope_y2(w[field, z], read_y_halo(b, hy_lo, slot, z), read_y_halo(b, hy_hi, slot, z), b.spacing)
            for slot, field in enumerate(STRESS_Y)
        ]
        dz = [slope_z(w, field, b.rows[z]) for field in (7, 8, 5)]
        if metric is not None:
            m = metric[z]
            dz = [m * d for d in dz]
        buoy = pick(table, 0, mat[z])
        for k in range(3):
            out[k, z] = w[k, z] + step_size * (buoy * (dx[k] + dy[k] + dz[k]))


def velocity_kernel(blocks, fw, cw, hx_lo, hx_hi, hy_lo, hy_hi, fmat, fmetric, cmat, table,
                    fvel, cvel, vx_prev, vx_next, vy_prev, vy_next, sx_f, sx_c):
    fine, coarse = blocks
    velocity_block(fine, fw, fmat, fmetric, table, fvel, sx_f, hx_lo, hx_hi, hy_lo, hy_hi)
    velocity_block(coarse, cw, cmat, None, table, cvel, sx_c, hx_lo, hx_hi, hy_lo, hy_hi)
    write_rims(fine, fvel, VELOCITY, vx_prev, vx_next, vy_prev, vy_next)
    write_rims(coarse, cvel, VELOCITY, vx_prev, vx_next, vy_prev, vy_next)


def stress_block(b, depth, w, mem, vel, mat, mech, metric, mtab, atab, out, mem_out, face, sx,
                 hx_lo, hx_hi, hy_lo, hy_hi, face_rims):
    for slot in range(3):
        fill_x2(b, sx, slot, vel, slot, hx_lo, hx_hi)
    for z in range(b.layers):
        dx = [slope_x(sx, slot, z, b.size, b.spacing) for slot in range(3)]
        dy = [
            slope_y2(vel[slot, z], read_y_halo(b, hy_lo, slot, z), read_y_halo(b, hy_hi, slot, z), b.spacing)
            for slot in range(3)
        ]
        dz = [slope_z(vel, slot, b.rows[z]) for slot in range(3)]
        if metric is not None:
            m = metric[z]
            dz = [m * d for d in dz]
        kind, mechanism = mat[z], mech[z]
        lame, shear = pick(mtab, 1, kind), pick(mtab, 2, kind)
        decay, strength = pick(atab, 0, mechanism), pick(atab, 1, mechanism)
        cell_volume = lame * (dx[0] + dy[1] + dz[2])
        rate = [
            cell_volume + 2.0 * shear * dx[0],
            cell_volume + 2.0 * shear * dy[1],
            cell_volume + 2.0 * shear * dz[2],
            shear * (dy[0] + dx[1]),
            shear * (dz[0] + dx[2]),
            shear * (dz[1] + dy[2]),
        ]
        values = []
        for k in range(3):
            v = vel[k, z]
            out[k, z] = v
            values.append(v)
        for k in range(6):
            memory_new = decay * mem[k, z] + (1.0 - decay) * strength * rate[k]
            mem_out[k, z] = memory_new
            stress = w[3 + k, z] + step_size * (rate[k] - memory_new)
            out[3 + k, z] = stress
            values.append(stress)
        if z == depth:
            for i, k in enumerate((0, 1, 2, 7, 8, 5)):
                face[i] = values[k]
            write_face_rims(b, [values[k] for k in (0, 1, 2, 7, 8, 5)], *face_rims)


def write_face_rims(b, planes, x_prev, x_next, y_prev, y_next):
    size, lanes = b.size, b.lanes
    for i, v in enumerate(planes):
        for j in range(b.chunks):
            row = b.fx_base + i * b.chunks + j
            x_prev[row : row + 1, :] = v[0:1, j * 128 : (j + 1) * 128]
            x_next[row : row + 1, :] = v[size - 1 : size, j * 128 : (j + 1) * 128]
    lane = lax.broadcasted_iota(jnp.int32, (size, 128), 1)
    acc_lo = jnp.zeros((size, 128), jnp.float32)
    acc_hi = jnp.zeros((size, 128), jnp.float32)
    for i, v in enumerate(planes):
        rl = v if i == 0 else pltpu.roll(v, i, 1)
        rh = pltpu.roll(v, (i + 1) % lanes, 1)
        acc_lo = jnp.where(lane == i, rl[:, 0:128], acc_lo)
        acc_hi = jnp.where(lane == i, rh[:, 0:128], acc_hi)
    y_prev[b.fy_base : b.fy_base + size, :] = acc_lo
    y_next[b.fy_base : b.fy_base + size, :] = acc_hi


def stress_kernel(blocks, fw, fmem, fvel, cw, cmem, cvel, hx_lo, hx_hi, hy_lo, hy_hi,
                  fmat, fmech, fmetric, cmat, cmech, mtab, atab,
                  fout, fmem_out, fface, cout, cmem_out, cface, rx_prev, rx_next, ry_prev, ry_next, sx_f, sx_c):
    fine, coarse = blocks
    rims = (rx_prev, rx_next, ry_prev, ry_next)
    stress_block(fine, fine.layers - 1, fw, fmem, fvel, fmat, fmech, fmetric, mtab, atab, fout, fmem_out,
                 fface, sx_f, hx_lo, hx_hi, hy_lo, hy_hi, rims)
    stress_block(coarse, 0, cw, cmem, cvel, cmat, cmech, None, mtab, atab, cout, cmem_out,
                 cface, sx_c, hx_lo, hx_hi, hy_lo, hy_hi, rims)


def vmem_specs(count):
    return [pl.BlockSpec(memory_space=pltpu.VMEM)] * count


def f32(shape):
    return jax.ShapeDtypeStruct(shape, jnp.float32)


def halo_shapes(x_rows, y_rows):
    return (f32((x_rows, 128)), f32((x_rows, 128)), f32((y_rows, 128)), f32((y_rows, 128)))


def scratch_for(b):
    return pltpu.VMEM((3, b.layers, b.size + 4, b.lanes), jnp.float32)


def receive(buffers):
    x_prev, x_next, y_prev, y_next = buffers
    return (
        shift_from(x_next, "gx", 1),
        shift_from(x_prev, "gx", -1),
        shift_from(y_next, "gy", 1),
        shift_from(y_prev, "gy", -1),
    )


def put_face(out, face, depth):
    out = lax.dynamic_update_slice(out, face[0:3][:, None], (0, depth, 0, 0))
    out = lax.dynamic_update_slice(out, face[5:6][:, None], (5, depth, 0, 0))
    out = lax.dynamic_update_slice(out, face[3:5][:, None], (7, depth, 0, 0))
    return out


def prolong_y_matrix(coarse_lanes):
    m = np.zeros((coarse_lanes, 3 * coarse_lanes), np.float32)
    for d in range(coarse_lanes):
        m[d, 3 * d] = 2.0 / 3.0
        m[d, 3 * d + 1] = 1.0
        m[d, 3 * d + 2] = 2.0 / 3.0
        if d >= 1:
            m[d - 1, 3 * d] = 1.0 / 3.0
        if d + 1 < coarse_lanes:
            m[d + 1, 3 * d + 2] = 1.0 / 3.0
    return m


def restrict_y_matrix(coarse_lanes):
    m = np.zeros((3 * coarse_lanes, coarse_lanes), np.float32)
    for c in range(coarse_lanes):
        for offset, weight in ((-1, 1.0), (0, 2.0), (1, 3.0), (2, 2.0), (3, 1.0)):
            f = 3 * c + offset
            if 0 <= f < 3 * coarse_lanes:
                m[f, c] = weight / 9.0
    return m


def padded_rows(b, face, hx_lo, hx_hi, hy_lo, hy_hi, i):
    size = b.size

    def x_row(buf):
        parts = [buf[pl.ds(b.fx_base + i * b.chunks + j, 1), :] for j in range(b.chunks)]
        return parts[0] if len(parts) == 1 else jnp.concatenate(parts, axis=1)

    def lane_of(buf, row):
        return buf[pl.ds(row, 1), pl.ds(i, 1)]

    lo_row, hi_row = b.corner_rows
    rows = [(x_row(hx_lo), lane_of(hy_lo, lo_row), lane_of(hy_hi, lo_row))]
    for x in range(size):
        rows.append((face[i, pl.ds(x, 1), :], lane_of(hy_lo, b.fy_base + x), lane_of(hy_hi, b.fy_base + x)))
    rows.append((x_row(hx_hi), lane_of(hy_lo, hi_row), lane_of(hy_hi, hi_row)))
    return rows


def combine(terms):
    out = []
    for part in range(3):
        total = None
        for weight, row in terms:
            v = row[part] if weight == 1.0 else weight * row[part]
            total = v if total is None else total + v
        out.append(total)
    return out


def face_kernel(blocks, fine_depth, fout_in, cout_in, fface, cface, hx_lo, hx_hi, hy_lo, hy_hi,
                py, ry, fout, cout, fnew, cnew, stage_p, stage_r, sems):
    fine, coarse = blocks
    halos = (hx_lo, hx_hi, hy_lo, hy_hi)
    lane_f = lax.broadcasted_iota(jnp.int32, (1, fine.lanes), 1)
    p_lo, p_hi = [], []
    for i in range(6):
        rows = padded_rows(coarse, cface, *halos, i)
        for c in range(coarse.size):
            left, middle, right = rows[c], rows[c + 1], rows[c + 2]
            parts = [
                [(1.0, left), (2.0, middle)],
                [(1.0, middle)],
                [(2.0, middle), (1.0, right)],
            ]
            for a, terms in enumerate(parts):
                interior, lo, hi = combine(terms)
                if a != 1:
                    interior, lo, hi = interior / 3.0, lo / 3.0, hi / 3.0
                r = i * fine.size + 3 * c + a
                stage_p[pl.ds(r, 1), :] = interior
                p_lo.append(lo)
                p_hi.append(hi)
    prolonged = jnp.dot(stage_p[...], py[...], precision=lax.Precision.HIGHEST, preferred_element_type=jnp.float32)
    for i in range(6):
        for x in range(fine.size):
            r = i * fine.size + x
            value = prolonged[r : r + 1, :]
            value = value + jnp.where(lane_f == 0, p_lo[r] / 3.0, 0.0) + jnp.where(lane_f == fine.lanes - 1, p_hi[r] / 3.0, 0.0)
            own = fface[i, pl.ds(x, 1), :]
            fnew[i, 0, pl.ds(x, 1), :] = own - penalty * (own - value)
    lane_c = lax.broadcasted_iota(jnp.int32, (1, coarse.lanes), 1)
    r_lo, r_hi = [], []
    for i in range(6):
        rows = padded_rows(fine, fface, *halos, i)
        for c in range(coarse.size):
            terms = [(1.0, rows[3 * c]), (2.0, rows[3 * c + 1]), (3.0, rows[3 * c + 2]), (2.0, rows[3 * c + 3]),
                     (1.0, rows[3 * c + 4])]
            interior, lo, hi = combine(terms)
            r = i * coarse.size + c
            stage_r[pl.ds(r, 1), :] = interior / 9.0
            r_lo.append(lo / 9.0)
            r_hi.append(hi / 9.0)
    restricted = jnp.dot(stage_r[...], ry[...], precision=lax.Precision.HIGHEST, preferred_element_type=jnp.float32)
    for i in range(6):
        for c in range(coarse.size):
            r = i * coarse.size + c
            value = restricted[r : r + 1, :]
            value = value + jnp.where(lane_c == 0, r_lo[r] / 9.0, 0.0) + jnp.where(lane_c == coarse.lanes - 1, r_hi[r] / 9.0, 0.0)
            own = cface[i, pl.ds(c, 1), :]
            cnew[i, 0, pl.ds(c, 1), :] = own - penalty * (own - value)
    copies = []
    for n, (src, dst, depth) in enumerate(((fnew, fout, fine_depth), (cnew, cout, 0))):
        for k, (first, count, field) in enumerate(((0, 3, 0), (5, 1, 5), (3, 2, 7))):
            copy = pltpu.make_async_copy(
                src.at[pl.ds(first, count)], dst.at[pl.ds(field, count), pl.ds(depth, 1)], sems.at[3 * n + k]
            )
            copy.start()
            copies.append(copy)
    for copy in copies:
        copy.wait()


def diag_from(block, dx, dy):
    nx, ny = lax.axis_size("gx"), lax.axis_size("gy")
    pairs = []
    for i in range(nx):
        for j in range(ny):
            if 0 <= i + dx < nx and 0 <= j + dy < ny:
                pairs.append((i * ny + j, (i + dx) * ny + (j + dy)))
    return lax.ppermute(block, ("gx", "gy"), pairs)


def row_ends(buf, blocks, at_end):
    out = []
    for b in blocks:
        chunk = b.chunks - 1 if at_end else 0
        rows = [b.fx_base + i * b.chunks + chunk for i in range(6)]
        out.append(buf[jnp.asarray(rows), 127 if at_end else 0])
    return jnp.stack(out)


def with_corners(y_rim, x_lo, x_hi, blocks, at_end):
    lo, hi = row_ends(x_lo, blocks, at_end), row_ends(x_hi, blocks, at_end)
    extra = jnp.stack([lo, hi], axis=1).reshape(2 * len(blocks), 6)
    extra = jnp.pad(extra, ((0, 0), (0, 128 - 6)))
    joined = jnp.concatenate([y_rim, extra])
    return jnp.pad(joined, ((0, round8(joined.shape[0]) - joined.shape[0]), (0, 0)))


def face_call(blocks, fine_out, coarse_out, fine_face, coarse_face, rims):
    fine, coarse = blocks
    x_prev, x_next, y_prev, y_next = rims
    x_lo = shift_from(x_next, "gx", 1)
    x_hi = shift_from(x_prev, "gx", -1)
    y_lo = shift_from(with_corners(y_next, x_lo, x_hi, blocks, True), "gy", 1)
    y_hi = shift_from(with_corners(y_prev, x_lo, x_hi, blocks, False), "gy", -1)
    received = (x_lo, x_hi, y_lo, y_hi)
    py = jnp.asarray(prolong_y_matrix(coarse.lanes))
    ry = jnp.asarray(restrict_y_matrix(coarse.lanes))
    anyspace = pl.BlockSpec(memory_space=pl.ANY)
    return pl.pallas_call(
        functools.partial(face_kernel, blocks, fine.layers - 1),
        out_shape=(f32(fine_out.shape), f32(coarse_out.shape)),
        in_specs=[anyspace, anyspace] + vmem_specs(8),
        out_specs=(anyspace, anyspace),
        input_output_aliases={0: 0, 1: 1},
        scratch_shapes=[
            pltpu.VMEM((6, 1, fine.size, fine.lanes), jnp.float32),
            pltpu.VMEM((6, 1, coarse.size, coarse.lanes), jnp.float32),
            pltpu.VMEM((round8(6 * fine.size), coarse.lanes), jnp.float32),
            pltpu.VMEM((round8(6 * coarse.size), fine.lanes), jnp.float32),
            pltpu.SemaphoreType.DMA((6,)),
        ],
    )(fine_out, coarse_out, fine_face, coarse_face, *received, py, ry)


def local(
    fine_wave,
    fine_memory,
    fine_material,
    fine_mechanism,
    fine_metric,
    coarse_wave,
    coarse_memory,
    coarse_material,
    coarse_mechanism,
    material_table,
    attenuation_table,
):
    fine, coarse, x_rows, y_rows = plan_blocks(fine_wave.shape[1:], coarse_wave.shape[1:])
    blocks = (fine, coarse)
    smem = pl.BlockSpec(memory_space=pltpu.SMEM)

    rims = pl.pallas_call(
        functools.partial(pack_kernel, blocks),
        out_shape=halo_shapes(x_rows, y_rows),
        in_specs=vmem_specs(2),
        out_specs=tuple(vmem_specs(4)),
    )(fine_wave, coarse_wave)
    halos = receive(rims)

    fine_velocity, coarse_velocity, *vrims = pl.pallas_call(
        functools.partial(velocity_kernel, blocks),
        out_shape=(f32((3,) + fine_wave.shape[1:]), f32((3,) + coarse_wave.shape[1:])) + halo_shapes(x_rows, y_rows),
        in_specs=vmem_specs(9) + [smem],
        out_specs=tuple(vmem_specs(6)),
        scratch_shapes=[scratch_for(fine), scratch_for(coarse)],
    )(fine_wave, coarse_wave, *halos, fine_material, fine_metric, coarse_material, material_table)

    vhalos = receive(vrims)
    fx_rows = 6 * (fine.chunks + coarse.chunks)
    fy_rows = round8(fine.size + coarse.size)
    fine_out, fine_mem, fine_face, coarse_out, coarse_mem, coarse_face, *face_rims = pl.pallas_call(
        functools.partial(stress_kernel, blocks),
        out_shape=(
            f32(fine_wave.shape), f32(fine_memory.shape), f32((6,) + fine_wave.shape[2:]),
            f32(coarse_wave.shape), f32(coarse_memory.shape), f32((6,) + coarse_wave.shape[2:]),
            f32((fx_rows, 128)), f32((fx_rows, 128)), f32((fy_rows, 128)), f32((fy_rows, 128)),
        ),
        in_specs=vmem_specs(15) + [smem, smem],
        out_specs=tuple(vmem_specs(10)),
        scratch_shapes=[scratch_for(fine), scratch_for(coarse)],
    )(fine_wave, fine_memory, fine_velocity, coarse_wave, coarse_memory, coarse_velocity, *vhalos,
      fine_material, fine_mechanism, fine_metric, coarse_material, coarse_mechanism, material_table,
      attenuation_table)

    fine_out, coarse_out = face_call(blocks, fine_out, coarse_out, fine_face, coarse_face, face_rims)
    return (fine_out, fine_mem, coarse_out, coarse_mem)


def solution(mesh):
    in_specs = (
        P(None, None, "gx", "gy"),
        P(None, None, "gx", "gy"),
        P(None, "gx", "gy"),
        P(None, "gx", "gy"),
        P(None, "gx", "gy"),
        P(None, None, "gx", "gy"),
        P(None, None, "gx", "gy"),
        P(None, "gx", "gy"),
        P(None, "gx", "gy"),
        P(),
        P(),
    )
    out_specs = (
        P(None, None, "gx", "gy"),
        P(None, None, "gx", "gy"),
        P(None, None, "gx", "gy"),
        P(None, None, "gx", "gy"),
    )
    return jax.shard_map(local, mesh=mesh, in_specs=in_specs, out_specs=out_specs, check_vma=False)
```

```python
import functools
import math

import jax
import jax.numpy as jnp
import numpy as np
from jax import lax
from jax.sharding import PartitionSpec as P

step_size = 0.1
penalty = 0.1 * 48.0 / 17.0
closure = [
    [-24.0 / 17.0, 59.0 / 34.0, -4.0 / 17.0, -3.0 / 34.0, 0.0, 0.0],
    [-0.5, 0.0, 0.5, 0.0, 0.0, 0.0],
    [4.0 / 43.0, -59.0 / 86.0, 0.0, 59.0 / 86.0, -4.0 / 43.0, 0.0],
    [3.0 / 98.0, 0.0, -59.0 / 98.0, 0.0, 32.0 / 49.0, -4.0 / 49.0],
]


def sbp_table(layers, spacing):
    return jnp.asarray(sbp_numpy(layers, spacing))


def sbp_numpy(layers, spacing):
    table = np.zeros((layers, layers))
    for line_at in range(4):
        for column in range(6):
            table[line_at, column] = closure[line_at][column]
            table[layers - 1 - line_at, layers - 1 - column] = -closure[line_at][column]
    for line_at in range(4, layers - 4):
        table[line_at, line_at - 2 : line_at + 3] = [
            1.0 / 12.0,
            -2.0 / 3.0,
            0.0,
            2.0 / 3.0,
            -1.0 / 12.0,
        ]
    return (table / spacing).astype(np.float32)


def shift_from(block, axis, offset):
    count = lax.axis_size(axis)
    pairs = [(i, i + offset) for i in range(count) if 0 <= i + offset < count]
    return lax.ppermute(block, axis, pairs)


def packed_shift(blocks, axis, offset):
    sizes = [math.prod(b.shape) for b in blocks]
    joined = jnp.concatenate([b.reshape(-1) for b in blocks])
    moved = shift_from(joined, axis, offset)
    out, start = [], 0
    for b, size in zip(blocks, sizes):
        out.append(moved[start : start + size].reshape(b.shape))
        start += size
    return out


def exchange(blocks, width):
    x_lo = packed_shift([b[..., -width:, :] for b in blocks], "gx", 1)
    x_hi = packed_shift([b[..., :width, :] for b in blocks], "gx", -1)
    y_lo = packed_shift([b[..., -width:] for b in blocks], "gy", 1)
    y_hi = packed_shift([b[..., :width] for b in blocks], "gy", -1)
    return [(x_lo[i], x_hi[i], y_lo[i], y_hi[i]) for i in range(len(blocks))]


def central_diff(padded, along, spacing):
    length = padded.shape[along] - 4
    s = lambda o: lax.slice_in_dim(padded, o, o + length, axis=along)
    return (s(0) - 8.0 * s(1) + 8.0 * s(3) - s(4)) / (12.0 * spacing)


def diff_x(block, halo, spacing):
    x_lo, x_hi, _, _ = halo
    return central_diff(jnp.concatenate([x_lo, block, x_hi], axis=-2), block.ndim - 2, spacing)


def diff_y(block, halo, spacing):
    _, _, y_lo, y_hi = halo
    return central_diff(jnp.concatenate([y_lo, block, y_hi], axis=-1), block.ndim - 1, spacing)


def vertical_diff(fields, matrix):
    return jnp.einsum("kz,czxy->ckxy", matrix, fields, precision=lax.Precision.HIGHEST)


def lookup_table(grid_cell_index, values):
    result = jnp.zeros(grid_cell_index.shape, jnp.float32)
    for kind_at in range(values.shape[0]):
        result = jnp.where(grid_cell_index == kind_at, values[kind_at], result)
    return result


def velocity_step(wave, halo_x3, halo_y3, buoyancy, metric, matrix, spacing):
    sx = jnp.stack([wave[3], wave[6], wave[7]])
    sy = jnp.stack([wave[6], wave[4], wave[8]])
    slope_x = diff_x(sx, halo_x3, spacing)
    slope_y = diff_y(sy, halo_y3, spacing)
    slope_z = metric * vertical_diff(jnp.stack([wave[7], wave[8], wave[5]]), matrix)
    rate_x = slope_x[0] + slope_y[0] + slope_z[0]
    rate_y = slope_x[1] + slope_y[1] + slope_z[1]
    rate_z = slope_x[2] + slope_y[2] + slope_z[2]
    return wave[:3] + step_size * (buoyancy * jnp.stack([rate_x, rate_y, rate_z]))


def stress_step(wave, memory, velocity, halo, lame, shear, decay, strength, metric, matrix, spacing):
    slope_x = diff_x(velocity, halo, spacing)
    slope_y = diff_y(velocity, halo, spacing)
    slope_z = metric * vertical_diff(velocity, matrix)
    cell_volume = lame * (slope_x[0] + slope_y[1] + slope_z[2])
    rate = jnp.stack(
        [
            cell_volume + 2.0 * shear * slope_x[0],
            cell_volume + 2.0 * shear * slope_y[1],
            cell_volume + 2.0 * shear * slope_z[2],
            shear * (slope_y[0] + slope_x[1]),
            shear * (slope_z[0] + slope_x[2]),
            shear * (slope_z[1] + slope_y[2]),
        ]
    )
    memory_new = decay * memory + (1.0 - decay) * strength * rate
    stress = wave[3:] + step_size * (rate - memory_new)
    return stress, memory_new


def face_of(velocity, stress, depth):
    return jnp.stack(
        [
            velocity[0, depth],
            velocity[1, depth],
            velocity[2, depth],
            stress[4, depth],
            stress[5, depth],
            stress[2, depth],
        ]
    )


def pad_faces(faces):
    x_lo = packed_shift([f[:, -1:, :] for f in faces], "gx", 1)
    x_hi = packed_shift([f[:, :1, :] for f in faces], "gx", -1)
    faces = [jnp.concatenate([lo, f, hi], axis=1) for lo, f, hi in zip(x_lo, faces, x_hi)]
    y_lo = packed_shift([f[:, :, -1:] for f in faces], "gy", 1)
    y_hi = packed_shift([f[:, :, :1] for f in faces], "gy", -1)
    return [jnp.concatenate([lo, f, hi], axis=2) for lo, f, hi in zip(y_lo, faces, y_hi)]


def shifted(padded, offset, length, along):
    return lax.slice_in_dim(padded, offset, offset + length, axis=along)


def prolong_axis(padded, along):
    length = padded.shape[along] - 2
    left = shifted(padded, 0, length, along)
    middle = shifted(padded, 1, length, along)
    right = shifted(padded, 2, length, along)
    parts = jnp.stack(
        [(left + 2.0 * middle) / 3.0, middle, (2.0 * middle + right) / 3.0], axis=along + 1
    )
    shape = list(middle.shape)
    shape[along] = shape[along] * 3
    return parts.reshape(tuple(shape))


def split_three(padded, offset, length, along):
    part = shifted(padded, offset, 3 * length, along)
    return part.reshape(part.shape[:along] + (length, 3) + part.shape[along + 1 :])


def pick_part(parts, number, along):
    return lax.index_in_dim(parts, number, along + 1, keepdims=False)


def restrict_axis(padded, along):
    length = (padded.shape[along] - 2) // 3
    first = split_three(padded, 0, length, along)
    middle = split_three(padded, 1, length, along)
    last = split_three(padded, 2, length, along)
    return (
        pick_part(first, 0, along)
        + 2.0 * pick_part(middle, 0, along)
        + 3.0 * pick_part(middle, 1, along)
        + 2.0 * pick_part(middle, 2, along)
        + pick_part(last, 2, along)
    ) / 9.0


def assemble(velocity, stress, face, depth):
    replace = {0: face[0], 1: face[1], 2: face[2], 7: face[3], 8: face[4], 5: face[5]}
    fields = [velocity[0], velocity[1], velocity[2]] + [stress[k] for k in range(6)]
    rows = []
    for k, field in enumerate(fields):
        if k in replace:
            field = lax.dynamic_update_slice_in_dim(field, replace[k][None], depth, axis=0)
        rows.append(field)
    return jnp.stack(rows)


from jax.experimental import pallas as pl
from jax.experimental.pallas import tpu as pltpu


def sbp_rows(layers, spacing):
    table = sbp_numpy(layers, spacing)
    return [[(j, float(table[k, j])) for j in range(layers) if table[k, j] != 0.0] for k in range(layers)]


def pick(values_ref, row, index):
    result = jnp.zeros(index.shape, jnp.float32)
    for kind_at in range(values_ref.shape[1]):
        result = jnp.where(index == kind_at, values_ref[row, kind_at], result)
    return result


def fill_x(scratch, slot, lo, block, hi):
    width = lo.shape[-2]
    size = block.shape[-2]
    scratch[slot, :, 0:width, :] = lo
    scratch[slot, :, width : width + size, :] = block
    scratch[slot, :, width + size :, :] = hi


def slope_x(scratch, slot, z, size, spacing):
    s = lambda o: scratch[slot, z, o : o + size, :]
    return (s(0) - 8.0 * s(1) + 8.0 * s(3) - s(4)) / (12.0 * spacing)


def slope_y(f, lo, hi, spacing):
    n = f.shape[-1]
    lane = lax.broadcasted_iota(jnp.int32, f.shape, f.ndim - 1)
    m1 = jnp.where(lane == 0, lo[:, 1:2], pltpu.roll(f, 1, f.ndim - 1))
    m2 = jnp.where(lane == 0, lo[:, 0:1], jnp.where(lane == 1, lo[:, 1:2], pltpu.roll(f, 2, f.ndim - 1)))
    p1 = jnp.where(lane == n - 1, hi[:, 0:1], pltpu.roll(f, n - 1, f.ndim - 1))
    p2 = jnp.where(lane == n - 2, hi[:, 0:1], jnp.where(lane == n - 1, hi[:, 1:2], pltpu.roll(f, n - 2, f.ndim - 1)))
    return (m2 - 8.0 * m1 + 8.0 * p1 - p2) / (12.0 * spacing)


def slope_z(field_ref, index, row):
    total = None
    for j, weight in row:
        term = jnp.float32(weight) * field_ref[index, j]
        total = term if total is None else total + term
    return total


class Block:
    def __init__(self, shape, spacing, has_metric, x_base, y_base):
        self.layers, self.size, self.lanes = shape
        self.chunks = self.lanes // 128
        self.spacing = spacing
        self.has_metric = has_metric
        self.rows = sbp_rows(self.layers, spacing)
        self.x_base, self.y_base = x_base, y_base

    @property
    def x_rows(self):
        return 3 * self.layers * self.chunks * 2

    @property
    def y_rows(self):
        return self.layers * self.size


def plan_blocks(fine_shape, coarse_shape):
    fine = Block(fine_shape, 1.0, True, 0, 0)
    coarse = Block(coarse_shape, 3.0, False, fine.x_rows, fine.y_rows)
    fine.fx_base, fine.fy_base = 0, 0
    coarse.fx_base, coarse.fy_base = 6 * fine.chunks, fine.size
    corner_base = fine.size + coarse.size
    fine.corner_rows = (corner_base, corner_base + 1)
    coarse.corner_rows = (corner_base + 2, corner_base + 3)
    return fine, coarse, fine.x_rows + coarse.x_rows, fine.y_rows + coarse.y_rows


def round8(n):
    return -(-n // 8) * 8


def write_rims(b, src, fields, x_prev, x_next, y_prev, y_next):
    size, lanes = b.size, b.lanes
    for c, field in enumerate(fields):
        for z in range(b.layers):
            lo = src[field, z, 0:2, :]
            hi = src[field, z, size - 2 : size, :]
            for j in range(b.chunks):
                row = b.x_base + ((c * b.layers + z) * b.chunks + j) * 2
                x_prev[row : row + 2, :] = lo[:, j * 128 : (j + 1) * 128]
                x_next[row : row + 2, :] = hi[:, j * 128 : (j + 1) * 128]
    lane = lax.broadcasted_iota(jnp.int32, (size, 128), 1)
    for z in range(b.layers):
        acc_lo = jnp.zeros((size, 128), jnp.float32)
        acc_hi = jnp.zeros((size, 128), jnp.float32)
        for c, field in enumerate(fields):
            v = src[field, z]
            rl = v if c == 0 else pltpu.roll(v, 2 * c, 1)
            rh = pltpu.roll(v, (2 * c + 2) % lanes, 1)
            keep = (lane >= 2 * c) & (lane < 2 * c + 2)
            acc_lo = jnp.where(keep, rl[:, 0:128], acc_lo)
            acc_hi = jnp.where(keep, rh[:, 0:128], acc_hi)
        row = b.y_base + z * size
        y_prev[row : row + size, :] = acc_lo
        y_next[row : row + size, :] = acc_hi


def read_x_halo(b, buf, c, z):
    parts = [buf[pl.ds(b.x_base + ((c * b.layers + z) * b.chunks + j) * 2, 2), :] for j in range(b.chunks)]
    return parts[0] if len(parts) == 1 else jnp.concatenate(parts, axis=1)


def read_y_halo(b, buf, c, z):
    row = b.y_base + z * b.size
    return buf[pl.ds(row, b.size), pl.ds(2 * c, 1)], buf[pl.ds(row, b.size), pl.ds(2 * c + 1, 1)]


def fill_x2(b, scratch, slot, src, field, lo_buf, hi_buf):
    size = b.size
    scratch[slot, :, 2 : 2 + size, :] = src[field]
    for z in range(b.layers):
        scratch[slot, z, 0:2, :] = read_x_halo(b, lo_buf, slot, z)
        scratch[slot, z, 2 + size :, :] = read_x_halo(b, hi_buf, slot, z)


def slope_y2(f, lo, hi, spacing):
    n = f.shape[-1]
    lane = lax.broadcasted_iota(jnp.int32, f.shape, 1)
    m1 = jnp.where(lane == 0, lo[1], pltpu.roll(f, 1, 1))
    m2 = jnp.where(lane == 0, lo[0], jnp.where(lane == 1, lo[1], pltpu.roll(f, 2, 1)))
    p1 = jnp.where(lane == n - 1, hi[0], pltpu.roll(f, n - 1, 1))
    p2 = jnp.where(lane == n - 2, hi[0], jnp.where(lane == n - 1, hi[1], pltpu.roll(f, n - 2, 1)))
    return (m2 - 8.0 * m1 + 8.0 * p1 - p2) / (12.0 * spacing)


STRESS_X = (3, 6, 7)
STRESS_Y = (6, 4, 8)
VELOCITY = (0, 1, 2)


def pack_kernel(blocks, fw, cw, x_prev, x_next, y_prev, y_next):
    for b, w in zip(blocks, (fw, cw)):
        write_rims_split(b, w, x_prev, x_next, y_prev, y_next)


def write_rims_split(b, w, x_prev, x_next, y_prev, y_next):
    size, lanes = b.size, b.lanes
    for c, field in enumerate(STRESS_X):
        for z in range(b.layers):
            lo = w[field, z, 0:2, :]
            hi = w[field, z, size - 2 : size, :]
            for j in range(b.chunks):
                row = b.x_base + ((c * b.layers + z) * b.chunks + j) * 2
                x_prev[row : row + 2, :] = lo[:, j * 128 : (j + 1) * 128]
                x_next[row : row + 2, :] = hi[:, j * 128 : (j + 1) * 128]
    lane = lax.broadcasted_iota(jnp.int32, (size, 128), 1)
    for z in range(b.layers):
        acc_lo = jnp.zeros((size, 128), jnp.float32)
        acc_hi = jnp.zeros((size, 128), jnp.float32)
        for c, field in enumerate(STRESS_Y):
            v = w[field, z]
            rl = v if c == 0 else pltpu.roll(v, 2 * c, 1)
            rh = pltpu.roll(v, (2 * c + 2) % lanes, 1)
            keep = (lane >= 2 * c) & (lane < 2 * c + 2)
            acc_lo = jnp.where(keep, rl[:, 0:128], acc_lo)
            acc_hi = jnp.where(keep, rh[:, 0:128], acc_hi)
        row = b.y_base + z * size
        y_prev[row : row + size, :] = acc_lo
        y_next[row : row + size, :] = acc_hi


def velocity_block(b, w, mat, metric, table, out, sx, hx_lo, hx_hi, hy_lo, hy_hi):
    for slot, field in enumerate(STRESS_X):
        fill_x2(b, sx, slot, w, field, hx_lo, hx_hi)
    for z in range(b.layers):
        dx = [slope_x(sx, slot, z, b.size, b.spacing) for slot in range(3)]
        dy = [
            slope_y2(w[field, z], read_y_halo(b, hy_lo, slot, z), read_y_halo(b, hy_hi, slot, z), b.spacing)
            for slot, field in enumerate(STRESS_Y)
        ]
        dz = [slope_z(w, field, b.rows[z]) for field in (7, 8, 5)]
        if metric is not None:
            m = metric[z]
            dz = [m * d for d in dz]
        buoy = pick(table, 0, mat[z])
        for k in range(3):
            out[k, z] = w[k, z] + step_size * (buoy * (dx[k] + dy[k] + dz[k]))


def velocity_kernel(blocks, fw, cw, hx_lo, hx_hi, hy_lo, hy_hi, fmat, fmetric, cmat, table,
                    fvel, cvel, vx_prev, vx_next, vy_prev, vy_next, sx_f, sx_c):
    fine, coarse = blocks
    velocity_block(fine, fw, fmat, fmetric, table, fvel, sx_f, hx_lo, hx_hi, hy_lo, hy_hi)
    velocity_block(coarse, cw, cmat, None, table, cvel, sx_c, hx_lo, hx_hi, hy_lo, hy_hi)
    write_rims(fine, fvel, VELOCITY, vx_prev, vx_next, vy_prev, vy_next)
    write_rims(coarse, cvel, VELOCITY, vx_prev, vx_next, vy_prev, vy_next)


def stress_block(b, depth, w, mem, vel, mat, mech, metric, mtab, atab, out, mem_out, face, sx,
                 hx_lo, hx_hi, hy_lo, hy_hi, face_rims):
    for slot in range(3):
        fill_x2(b, sx, slot, vel, slot, hx_lo, hx_hi)
    for z in range(b.layers):
        dx = [slope_x(sx, slot, z, b.size, b.spacing) for slot in range(3)]
        dy = [
            slope_y2(vel[slot, z], read_y_halo(b, hy_lo, slot, z), read_y_halo(b, hy_hi, slot, z), b.spacing)
            for slot in range(3)
        ]
        dz = [slope_z(vel, slot, b.rows[z]) for slot in range(3)]
        if metric is not None:
            m = metric[z]
            dz = [m * d for d in dz]
        kind, mechanism = mat[z], mech[z]
        lame, shear = pick(mtab, 1, kind), pick(mtab, 2, kind)
        decay, strength = pick(atab, 0, mechanism), pick(atab, 1, mechanism)
        cell_volume = lame * (dx[0] + dy[1] + dz[2])
        rate = [
            cell_volume + 2.0 * shear * dx[0],
            cell_volume + 2.0 * shear * dy[1],
            cell_volume + 2.0 * shear * dz[2],
            shear * (dy[0] + dx[1]),
            shear * (dz[0] + dx[2]),
            shear * (dz[1] + dy[2]),
        ]
        values = []
        for k in range(3):
            v = vel[k, z]
            out[k, z] = v
            values.append(v)
        for k in range(6):
            memory_new = decay * mem[k, z] + (1.0 - decay) * strength * rate[k]
            mem_out[k, z] = memory_new
            stress = w[3 + k, z] + step_size * (rate[k] - memory_new)
            out[3 + k, z] = stress
            values.append(stress)
        if z == depth:
            for i, k in enumerate((0, 1, 2, 7, 8, 5)):
                face[i] = values[k]
            write_face_rims(b, [values[k] for k in (0, 1, 2, 7, 8, 5)], *face_rims)


def write_face_rims(b, planes, x_prev, x_next, y_prev, y_next):
    size, lanes = b.size, b.lanes
    for i, v in enumerate(planes):
        for j in range(b.chunks):
            row = b.fx_base + i * b.chunks + j
            x_prev[row : row + 1, :] = v[0:1, j * 128 : (j + 1) * 128]
            x_next[row : row + 1, :] = v[size - 1 : size, j * 128 : (j + 1) * 128]
    lane = lax.broadcasted_iota(jnp.int32, (size, 128), 1)
    acc_lo = jnp.zeros((size, 128), jnp.float32)
    acc_hi = jnp.zeros((size, 128), jnp.float32)
    for i, v in enumerate(planes):
        rl = v if i == 0 else pltpu.roll(v, i, 1)
        rh = pltpu.roll(v, (i + 1) % lanes, 1)
        acc_lo = jnp.where(lane == i, rl[:, 0:128], acc_lo)
        acc_hi = jnp.where(lane == i, rh[:, 0:128], acc_hi)
    y_prev[b.fy_base : b.fy_base + size, :] = acc_lo
    y_next[b.fy_base : b.fy_base + size, :] = acc_hi


def stress_kernel(blocks, fw, fmem, fvel, cw, cmem, cvel, hx_lo, hx_hi, hy_lo, hy_hi,
                  fmat, fmech, fmetric, cmat, cmech, mtab, atab,
                  fout, fmem_out, fface, cout, cmem_out, cface, rx_prev, rx_next, ry_prev, ry_next, sx_f, sx_c):
    fine, coarse = blocks
    rims = (rx_prev, rx_next, ry_prev, ry_next)
    stress_block(fine, fine.layers - 1, fw, fmem, fvel, fmat, fmech, fmetric, mtab, atab, fout, fmem_out,
                 fface, sx_f, hx_lo, hx_hi, hy_lo, hy_hi, rims)
    stress_block(coarse, 0, cw, cmem, cvel, cmat, cmech, None, mtab, atab, cout, cmem_out,
                 cface, sx_c, hx_lo, hx_hi, hy_lo, hy_hi, rims)


def vmem_specs(count):
    return [pl.BlockSpec(memory_space=pltpu.VMEM)] * count


def f32(shape):
    return jax.ShapeDtypeStruct(shape, jnp.float32)


def halo_shapes(x_rows, y_rows):
    return (f32((x_rows, 128)), f32((x_rows, 128)), f32((y_rows, 128)), f32((y_rows, 128)))


def scratch_for(b):
    return pltpu.VMEM((3, b.layers, b.size + 4, b.lanes), jnp.float32)


def receive(buffers):
    x_prev, x_next, y_prev, y_next = buffers
    y_lo = shift_from(y_next, "gy", 1)
    y_hi = shift_from(y_prev, "gy", -1)
    x_lo = shift_from(x_next, "gx", 1)
    x_hi = shift_from(x_prev, "gx", -1)
    return x_lo, x_hi, y_lo, y_hi


def put_face(out, face, depth):
    out = lax.dynamic_update_slice(out, face[0:3][:, None], (0, depth, 0, 0))
    out = lax.dynamic_update_slice(out, face[5:6][:, None], (5, depth, 0, 0))
    out = lax.dynamic_update_slice(out, face[3:5][:, None], (7, depth, 0, 0))
    return out


def prolong_y_matrix(coarse_lanes):
    m = np.zeros((coarse_lanes, 3 * coarse_lanes), np.float32)
    for d in range(coarse_lanes):
        m[d, 3 * d] = 2.0 / 3.0
        m[d, 3 * d + 1] = 1.0
        m[d, 3 * d + 2] = 2.0 / 3.0
        if d >= 1:
            m[d - 1, 3 * d] = 1.0 / 3.0
        if d + 1 < coarse_lanes:
            m[d + 1, 3 * d + 2] = 1.0 / 3.0
    return m


def restrict_y_matrix(coarse_lanes):
    m = np.zeros((3 * coarse_lanes, coarse_lanes), np.float32)
    for c in range(coarse_lanes):
        for offset, weight in ((-1, 1.0), (0, 2.0), (1, 3.0), (2, 2.0), (3, 1.0)):
            f = 3 * c + offset
            if 0 <= f < 3 * coarse_lanes:
                m[f, c] = weight / 9.0
    return m


def padded_rows(b, face, hx_lo, hx_hi, hy_lo, hy_hi, i):
    size = b.size

    def x_row(buf):
        parts = [buf[pl.ds(b.fx_base + i * b.chunks + j, 1), :] for j in range(b.chunks)]
        return parts[0] if len(parts) == 1 else jnp.concatenate(parts, axis=1)

    def lane_of(buf, row):
        return buf[pl.ds(row, 1), pl.ds(i, 1)]

    lo_row, hi_row = b.corner_rows
    rows = [(x_row(hx_lo), lane_of(hy_lo, lo_row), lane_of(hy_hi, lo_row))]
    for x in range(size):
        rows.append((face[i, pl.ds(x, 1), :], lane_of(hy_lo, b.fy_base + x), lane_of(hy_hi, b.fy_base + x)))
    rows.append((x_row(hx_hi), lane_of(hy_lo, hi_row), lane_of(hy_hi, hi_row)))
    return rows


def combine(terms):
    out = []
    for part in range(3):
        total = None
        for weight, row in terms:
            v = row[part] if weight == 1.0 else weight * row[part]
            total = v if total is None else total + v
        out.append(total)
    return out


def face_kernel(blocks, fine_depth, fout_in, cout_in, fface, cface, hx_lo, hx_hi, hy_lo, hy_hi,
                py, ry, fout, cout, fnew, cnew, stage_p, stage_r, sems):
    fine, coarse = blocks
    halos = (hx_lo, hx_hi, hy_lo, hy_hi)
    lane_f = lax.broadcasted_iota(jnp.int32, (1, fine.lanes), 1)
    p_lo, p_hi = [], []
    for i in range(6):
        rows = padded_rows(coarse, cface, *halos, i)
        for c in range(coarse.size):
            left, middle, right = rows[c], rows[c + 1], rows[c + 2]
            parts = [
                [(1.0, left), (2.0, middle)],
                [(1.0, middle)],
                [(2.0, middle), (1.0, right)],
            ]
            for a, terms in enumerate(parts):
                interior, lo, hi = combine(terms)
                if a != 1:
                    interior, lo, hi = interior / 3.0, lo / 3.0, hi / 3.0
                r = i * fine.size + 3 * c + a
                stage_p[pl.ds(r, 1), :] = interior
                p_lo.append(lo)
                p_hi.append(hi)
    prolonged = jnp.dot(stage_p[...], py[...], precision=lax.Precision.HIGHEST, preferred_element_type=jnp.float32)
    for i in range(6):
        for x in range(fine.size):
            r = i * fine.size + x
            value = prolonged[r : r + 1, :]
            value = value + jnp.where(lane_f == 0, p_lo[r] / 3.0, 0.0) + jnp.where(lane_f == fine.lanes - 1, p_hi[r] / 3.0, 0.0)
            own = fface[i, pl.ds(x, 1), :]
            fnew[i, 0, pl.ds(x, 1), :] = own - penalty * (own - value)
    lane_c = lax.broadcasted_iota(jnp.int32, (1, coarse.lanes), 1)
    r_lo, r_hi = [], []
    for i in range(6):
        rows = padded_rows(fine, fface, *halos, i)
        for c in range(coarse.size):
            terms = [(1.0, rows[3 * c]), (2.0, rows[3 * c + 1]), (3.0, rows[3 * c + 2]), (2.0, rows[3 * c + 3]),
                     (1.0, rows[3 * c + 4])]
            interior, lo, hi = combine(terms)
            r = i * coarse.size + c
            stage_r[pl.ds(r, 1), :] = interior / 9.0
            r_lo.append(lo / 9.0)
            r_hi.append(hi / 9.0)
    restricted = jnp.dot(stage_r[...], ry[...], precision=lax.Precision.HIGHEST, preferred_element_type=jnp.float32)
    for i in range(6):
        for c in range(coarse.size):
            r = i * coarse.size + c
            value = restricted[r : r + 1, :]
            value = value + jnp.where(lane_c == 0, r_lo[r] / 9.0, 0.0) + jnp.where(lane_c == coarse.lanes - 1, r_hi[r] / 9.0, 0.0)
            own = cface[i, pl.ds(c, 1), :]
            cnew[i, 0, pl.ds(c, 1), :] = own - penalty * (own - value)
    copies = []
    for n, (src, dst, depth) in enumerate(((fnew, fout, fine_depth), (cnew, cout, 0))):
        for k, (first, count, field) in enumerate(((0, 3, 0), (5, 1, 5), (3, 2, 7))):
            copy = pltpu.make_async_copy(
                src.at[pl.ds(first, count)], dst.at[pl.ds(field, count), pl.ds(depth, 1)], sems.at[3 * n + k]
            )
            copy.start()
            copies.append(copy)
    for copy in copies:
        copy.wait()


def diag_from(block, dx, dy):
    nx, ny = lax.axis_size("gx"), lax.axis_size("gy")
    pairs = []
    for i in range(nx):
        for j in range(ny):
            if 0 <= i + dx < nx and 0 <= j + dy < ny:
                pairs.append((i * ny + j, (i + dx) * ny + (j + dy)))
    return lax.ppermute(block, ("gx", "gy"), pairs)


def row_ends(buf, blocks, at_end):
    out = []
    for b in blocks:
        chunk = b.chunks - 1 if at_end else 0
        first = b.fx_base + chunk
        lane = 127 if at_end else 0
        out.append(lax.slice(buf, (first, lane), (first + 5 * b.chunks + 1, lane + 1), (b.chunks, 1))[:, 0])
    return jnp.stack(out)


def with_corners(y_rim, x_lo, x_hi, blocks, at_end):
    lo, hi = row_ends(x_lo, blocks, at_end), row_ends(x_hi, blocks, at_end)
    extra = jnp.stack([lo, hi], axis=1).reshape(2 * len(blocks), 6)
    extra = jnp.pad(extra, ((0, 0), (0, 128 - 6)))
    joined = jnp.concatenate([y_rim, extra])
    return jnp.pad(joined, ((0, round8(joined.shape[0]) - joined.shape[0]), (0, 0)))


def face_call(blocks, fine_out, coarse_out, fine_face, coarse_face, rims):
    fine, coarse = blocks
    x_prev, x_next, y_prev, y_next = rims
    x_lo = shift_from(x_next, "gx", 1)
    x_hi = shift_from(x_prev, "gx", -1)
    y_lo = shift_from(with_corners(y_next, x_lo, x_hi, blocks, True), "gy", 1)
    y_hi = shift_from(with_corners(y_prev, x_lo, x_hi, blocks, False), "gy", -1)
    received = (x_lo, x_hi, y_lo, y_hi)
    py = jnp.asarray(prolong_y_matrix(coarse.lanes))
    ry = jnp.asarray(restrict_y_matrix(coarse.lanes))
    anyspace = pl.BlockSpec(memory_space=pl.ANY)
    return pl.pallas_call(
        functools.partial(face_kernel, blocks, fine.layers - 1),
        out_shape=(f32(fine_out.shape), f32(coarse_out.shape)),
        in_specs=[anyspace, anyspace] + vmem_specs(8),
        out_specs=(anyspace, anyspace),
        input_output_aliases={0: 0, 1: 1},
        scratch_shapes=[
            pltpu.VMEM((6, 1, fine.size, fine.lanes), jnp.float32),
            pltpu.VMEM((6, 1, coarse.size, coarse.lanes), jnp.float32),
            pltpu.VMEM((round8(6 * fine.size), coarse.lanes), jnp.float32),
            pltpu.VMEM((round8(6 * coarse.size), fine.lanes), jnp.float32),
            pltpu.SemaphoreType.DMA((6,)),
        ],
    )(fine_out, coarse_out, fine_face, coarse_face, *received, py, ry)


def local(
    fine_wave,
    fine_memory,
    fine_material,
    fine_mechanism,
    fine_metric,
    coarse_wave,
    coarse_memory,
    coarse_material,
    coarse_mechanism,
    material_table,
    attenuation_table,
):
    fine, coarse, x_rows, y_rows = plan_blocks(fine_wave.shape[1:], coarse_wave.shape[1:])
    blocks = (fine, coarse)
    smem = pl.BlockSpec(memory_space=pltpu.SMEM)

    rims = pl.pallas_call(
        functools.partial(pack_kernel, blocks),
        out_shape=halo_shapes(x_rows, y_rows),
        in_specs=vmem_specs(2),
        out_specs=tuple(vmem_specs(4)),
    )(fine_wave, coarse_wave)
    halos = receive(rims)

    fine_velocity, coarse_velocity, *vrims = pl.pallas_call(
        functools.partial(velocity_kernel, blocks),
        out_shape=(f32((3,) + fine_wave.shape[1:]), f32((3,) + coarse_wave.shape[1:])) + halo_shapes(x_rows, y_rows),
        in_specs=vmem_specs(9) + [smem],
        out_specs=tuple(vmem_specs(6)),
        scratch_shapes=[scratch_for(fine), scratch_for(coarse)],
    )(fine_wave, coarse_wave, *halos, fine_material, fine_metric, coarse_material, material_table)

    vhalos = receive(vrims)
    fx_rows = 6 * (fine.chunks + coarse.chunks)
    fy_rows = round8(fine.size + coarse.size)
    fine_out, fine_mem, fine_face, coarse_out, coarse_mem, coarse_face, *face_rims = pl.pallas_call(
        functools.partial(stress_kernel, blocks),
        out_shape=(
            f32(fine_wave.shape), f32(fine_memory.shape), f32((6,) + fine_wave.shape[2:]),
            f32(coarse_wave.shape), f32(coarse_memory.shape), f32((6,) + coarse_wave.shape[2:]),
            f32((fx_rows, 128)), f32((fx_rows, 128)), f32((fy_rows, 128)), f32((fy_rows, 128)),
        ),
        in_specs=vmem_specs(15) + [smem, smem],
        out_specs=tuple(vmem_specs(10)),
        scratch_shapes=[scratch_for(fine), scratch_for(coarse)],
    )(fine_wave, fine_memory, fine_velocity, coarse_wave, coarse_memory, coarse_velocity, *vhalos,
      fine_material, fine_mechanism, fine_metric, coarse_material, coarse_mechanism, material_table,
      attenuation_table)

    fine_out, coarse_out = face_call(blocks, fine_out, coarse_out, fine_face, coarse_face, face_rims)
    return (fine_out, fine_mem, coarse_out, coarse_mem)


def solution(mesh):
    in_specs = (
        P(None, None, "gx", "gy"),
        P(None, None, "gx", "gy"),
        P(None, "gx", "gy"),
        P(None, "gx", "gy"),
        P(None, "gx", "gy"),
        P(None, None, "gx", "gy"),
        P(None, None, "gx", "gy"),
        P(None, "gx", "gy"),
        P(None, "gx", "gy"),
        P(),
        P(),
    )
    out_specs = (
        P(None, None, "gx", "gy"),
        P(None, None, "gx", "gy"),
        P(None, None, "gx", "gy"),
        P(None, None, "gx", "gy"),
    )
    return jax.shard_map(local, mesh=mesh, in_specs=in_specs, out_specs=out_specs, check_vma=False)
```

```python
import functools
import math

import jax
import jax.numpy as jnp
import numpy as np
from jax import lax
from jax.sharding import PartitionSpec as P

step_size = 0.1
penalty = 0.1 * 48.0 / 17.0
closure = [
    [-24.0 / 17.0, 59.0 / 34.0, -4.0 / 17.0, -3.0 / 34.0, 0.0, 0.0],
    [-0.5, 0.0, 0.5, 0.0, 0.0, 0.0],
    [4.0 / 43.0, -59.0 / 86.0, 0.0, 59.0 / 86.0, -4.0 / 43.0, 0.0],
    [3.0 / 98.0, 0.0, -59.0 / 98.0, 0.0, 32.0 / 49.0, -4.0 / 49.0],
]


def sbp_table(layers, spacing):
    return jnp.asarray(sbp_numpy(layers, spacing))


def sbp_numpy(layers, spacing):
    table = np.zeros((layers, layers))
    for line_at in range(4):
        for column in range(6):
            table[line_at, column] = closure[line_at][column]
            table[layers - 1 - line_at, layers - 1 - column] = -closure[line_at][column]
    for line_at in range(4, layers - 4):
        table[line_at, line_at - 2 : line_at + 3] = [
            1.0 / 12.0,
            -2.0 / 3.0,
            0.0,
            2.0 / 3.0,
            -1.0 / 12.0,
        ]
    return (table / spacing).astype(np.float32)


def shift_from(block, axis, offset):
    count = lax.axis_size(axis)
    pairs = [(i, (i + offset) % count) for i in range(count)]
    return lax.ppermute(block, axis, pairs)


def edge_flags():
    gx, gy = lax.axis_index("gx"), lax.axis_index("gy")
    nx, ny = lax.axis_size("gx"), lax.axis_size("gy")
    return jnp.stack([gx > 0, gx < nx - 1, gy > 0, gy < ny - 1]).astype(jnp.int32)


def valid_of(flags):
    return tuple(flags[k] != 0 for k in range(4))


def keep(ok, value):
    return jnp.where(ok, value, 0.0)


def packed_shift(blocks, axis, offset):
    sizes = [math.prod(b.shape) for b in blocks]
    joined = jnp.concatenate([b.reshape(-1) for b in blocks])
    moved = shift_from(joined, axis, offset)
    out, start = [], 0
    for b, size in zip(blocks, sizes):
        out.append(moved[start : start + size].reshape(b.shape))
        start += size
    return out


def exchange(blocks, width):
    x_lo = packed_shift([b[..., -width:, :] for b in blocks], "gx", 1)
    x_hi = packed_shift([b[..., :width, :] for b in blocks], "gx", -1)
    y_lo = packed_shift([b[..., -width:] for b in blocks], "gy", 1)
    y_hi = packed_shift([b[..., :width] for b in blocks], "gy", -1)
    return [(x_lo[i], x_hi[i], y_lo[i], y_hi[i]) for i in range(len(blocks))]


def central_diff(padded, along, spacing):
    length = padded.shape[along] - 4
    s = lambda o: lax.slice_in_dim(padded, o, o + length, axis=along)
    return (s(0) - 8.0 * s(1) + 8.0 * s(3) - s(4)) / (12.0 * spacing)


def diff_x(block, halo, spacing):
    x_lo, x_hi, _, _ = halo
    return central_diff(jnp.concatenate([x_lo, block, x_hi], axis=-2), block.ndim - 2, spacing)


def diff_y(block, halo, spacing):
    _, _, y_lo, y_hi = halo
    return central_diff(jnp.concatenate([y_lo, block, y_hi], axis=-1), block.ndim - 1, spacing)


def vertical_diff(fields, matrix):
    return jnp.einsum("kz,czxy->ckxy", matrix, fields, precision=lax.Precision.HIGHEST)


def lookup_table(grid_cell_index, values):
    result = jnp.zeros(grid_cell_index.shape, jnp.float32)
    for kind_at in range(values.shape[0]):
        result = jnp.where(grid_cell_index == kind_at, values[kind_at], result)
    return result


def velocity_step(wave, halo_x3, halo_y3, buoyancy, metric, matrix, spacing):
    sx = jnp.stack([wave[3], wave[6], wave[7]])
    sy = jnp.stack([wave[6], wave[4], wave[8]])
    slope_x = diff_x(sx, halo_x3, spacing)
    slope_y = diff_y(sy, halo_y3, spacing)
    slope_z = metric * vertical_diff(jnp.stack([wave[7], wave[8], wave[5]]), matrix)
    rate_x = slope_x[0] + slope_y[0] + slope_z[0]
    rate_y = slope_x[1] + slope_y[1] + slope_z[1]
    rate_z = slope_x[2] + slope_y[2] + slope_z[2]
    return wave[:3] + step_size * (buoyancy * jnp.stack([rate_x, rate_y, rate_z]))


def stress_step(wave, memory, velocity, halo, lame, shear, decay, strength, metric, matrix, spacing):
    slope_x = diff_x(velocity, halo, spacing)
    slope_y = diff_y(velocity, halo, spacing)
    slope_z = metric * vertical_diff(velocity, matrix)
    cell_volume = lame * (slope_x[0] + slope_y[1] + slope_z[2])
    rate = jnp.stack(
        [
            cell_volume + 2.0 * shear * slope_x[0],
            cell_volume + 2.0 * shear * slope_y[1],
            cell_volume + 2.0 * shear * slope_z[2],
            shear * (slope_y[0] + slope_x[1]),
            shear * (slope_z[0] + slope_x[2]),
            shear * (slope_z[1] + slope_y[2]),
        ]
    )
    memory_new = decay * memory + (1.0 - decay) * strength * rate
    stress = wave[3:] + step_size * (rate - memory_new)
    return stress, memory_new


def face_of(velocity, stress, depth):
    return jnp.stack(
        [
            velocity[0, depth],
            velocity[1, depth],
            velocity[2, depth],
            stress[4, depth],
            stress[5, depth],
            stress[2, depth],
        ]
    )


def pad_faces(faces):
    x_lo = packed_shift([f[:, -1:, :] for f in faces], "gx", 1)
    x_hi = packed_shift([f[:, :1, :] for f in faces], "gx", -1)
    faces = [jnp.concatenate([lo, f, hi], axis=1) for lo, f, hi in zip(x_lo, faces, x_hi)]
    y_lo = packed_shift([f[:, :, -1:] for f in faces], "gy", 1)
    y_hi = packed_shift([f[:, :, :1] for f in faces], "gy", -1)
    return [jnp.concatenate([lo, f, hi], axis=2) for lo, f, hi in zip(y_lo, faces, y_hi)]


def shifted(padded, offset, length, along):
    return lax.slice_in_dim(padded, offset, offset + length, axis=along)


def prolong_axis(padded, along):
    length = padded.shape[along] - 2
    left = shifted(padded, 0, length, along)
    middle = shifted(padded, 1, length, along)
    right = shifted(padded, 2, length, along)
    parts = jnp.stack(
        [(left + 2.0 * middle) / 3.0, middle, (2.0 * middle + right) / 3.0], axis=along + 1
    )
    shape = list(middle.shape)
    shape[along] = shape[along] * 3
    return parts.reshape(tuple(shape))


def split_three(padded, offset, length, along):
    part = shifted(padded, offset, 3 * length, along)
    return part.reshape(part.shape[:along] + (length, 3) + part.shape[along + 1 :])


def pick_part(parts, number, along):
    return lax.index_in_dim(parts, number, along + 1, keepdims=False)


def restrict_axis(padded, along):
    length = (padded.shape[along] - 2) // 3
    first = split_three(padded, 0, length, along)
    middle = split_three(padded, 1, length, along)
    last = split_three(padded, 2, length, along)
    return (
        pick_part(first, 0, along)
        + 2.0 * pick_part(middle, 0, along)
        + 3.0 * pick_part(middle, 1, along)
        + 2.0 * pick_part(middle, 2, along)
        + pick_part(last, 2, along)
    ) / 9.0


def assemble(velocity, stress, face, depth):
    replace = {0: face[0], 1: face[1], 2: face[2], 7: face[3], 8: face[4], 5: face[5]}
    fields = [velocity[0], velocity[1], velocity[2]] + [stress[k] for k in range(6)]
    rows = []
    for k, field in enumerate(fields):
        if k in replace:
            field = lax.dynamic_update_slice_in_dim(field, replace[k][None], depth, axis=0)
        rows.append(field)
    return jnp.stack(rows)


from jax.experimental import pallas as pl
from jax.experimental.pallas import tpu as pltpu


def sbp_rows(layers, spacing):
    table = sbp_numpy(layers, spacing)
    return [[(j, float(table[k, j])) for j in range(layers) if table[k, j] != 0.0] for k in range(layers)]


def pick(values_ref, row, index):
    result = jnp.zeros(index.shape, jnp.float32)
    for kind_at in range(values_ref.shape[1]):
        result = jnp.where(index == kind_at, values_ref[row, kind_at], result)
    return result


def fill_x(scratch, slot, lo, block, hi):
    width = lo.shape[-2]
    size = block.shape[-2]
    scratch[slot, :, 0:width, :] = lo
    scratch[slot, :, width : width + size, :] = block
    scratch[slot, :, width + size :, :] = hi


def slope_x(scratch, slot, z, size, spacing):
    s = lambda o: scratch[slot, z, o : o + size, :]
    return (s(0) - 8.0 * s(1) + 8.0 * s(3) - s(4)) / (12.0 * spacing)


def slope_y(f, lo, hi, spacing):
    n = f.shape[-1]
    lane = lax.broadcasted_iota(jnp.int32, f.shape, f.ndim - 1)
    m1 = jnp.where(lane == 0, lo[:, 1:2], pltpu.roll(f, 1, f.ndim - 1))
    m2 = jnp.where(lane == 0, lo[:, 0:1], jnp.where(lane == 1, lo[:, 1:2], pltpu.roll(f, 2, f.ndim - 1)))
    p1 = jnp.where(lane == n - 1, hi[:, 0:1], pltpu.roll(f, n - 1, f.ndim - 1))
    p2 = jnp.where(lane == n - 2, hi[:, 0:1], jnp.where(lane == n - 1, hi[:, 1:2], pltpu.roll(f, n - 2, f.ndim - 1)))
    return (m2 - 8.0 * m1 + 8.0 * p1 - p2) / (12.0 * spacing)


def slope_z(field_ref, index, row):
    total = None
    for j, weight in row:
        term = jnp.float32(weight) * field_ref[index, j]
        total = term if total is None else total + term
    return total


class Block:
    def __init__(self, shape, spacing, has_metric, x_base, y_base):
        self.layers, self.size, self.lanes = shape
        self.chunks = self.lanes // 128
        self.spacing = spacing
        self.has_metric = has_metric
        self.rows = sbp_rows(self.layers, spacing)
        self.x_base, self.y_base = x_base, y_base

    @property
    def x_rows(self):
        return 3 * self.layers * self.chunks * 2

    @property
    def y_rows(self):
        return self.layers * self.size


def plan_blocks(fine_shape, coarse_shape):
    fine = Block(fine_shape, 1.0, True, 0, 0)
    coarse = Block(coarse_shape, 3.0, False, fine.x_rows, fine.y_rows)
    fine.fx_base, fine.fy_base = 0, 0
    coarse.fx_base, coarse.fy_base = 6 * fine.chunks, fine.size
    corner_base = fine.size + coarse.size
    fine.corner_rows = (corner_base, corner_base + 1)
    coarse.corner_rows = (corner_base + 2, corner_base + 3)
    return fine, coarse, fine.x_rows + coarse.x_rows, fine.y_rows + coarse.y_rows


def round8(n):
    return -(-n // 8) * 8


def write_rims(b, src, fields, x_prev, x_next, y_prev, y_next):
    size, lanes = b.size, b.lanes
    for c, field in enumerate(fields):
        for z in range(b.layers):
            lo = src[field, z, 0:2, :]
            hi = src[field, z, size - 2 : size, :]
            for j in range(b.chunks):
                row = b.x_base + ((c * b.layers + z) * b.chunks + j) * 2
                x_prev[row : row + 2, :] = lo[:, j * 128 : (j + 1) * 128]
                x_next[row : row + 2, :] = hi[:, j * 128 : (j + 1) * 128]
    lane = lax.broadcasted_iota(jnp.int32, (size, 128), 1)
    for z in range(b.layers):
        acc_lo = jnp.zeros((size, 128), jnp.float32)
        acc_hi = jnp.zeros((size, 128), jnp.float32)
        for c, field in enumerate(fields):
            v = src[field, z]
            rl = v if c == 0 else pltpu.roll(v, 2 * c, 1)
            rh = pltpu.roll(v, (2 * c + 2) % lanes, 1)
            keep = (lane >= 2 * c) & (lane < 2 * c + 2)
            acc_lo = jnp.where(keep, rl[:, 0:128], acc_lo)
            acc_hi = jnp.where(keep, rh[:, 0:128], acc_hi)
        row = b.y_base + z * size
        y_prev[row : row + size, :] = acc_lo
        y_next[row : row + size, :] = acc_hi


def read_x_halo(b, buf, c, z):
    parts = [buf[pl.ds(b.x_base + ((c * b.layers + z) * b.chunks + j) * 2, 2), :] for j in range(b.chunks)]
    return parts[0] if len(parts) == 1 else jnp.concatenate(parts, axis=1)


def read_y_halo(b, buf, c, z, ok):
    row = b.y_base + z * b.size
    return keep(ok, buf[pl.ds(row, b.size), pl.ds(2 * c, 1)]), keep(ok, buf[pl.ds(row, b.size), pl.ds(2 * c + 1, 1)])


def fill_x2(b, scratch, slot, src, field, lo_buf, hi_buf, valid):
    size = b.size
    scratch[slot, :, 2 : 2 + size, :] = src[field]
    for z in range(b.layers):
        scratch[slot, z, 0:2, :] = keep(valid[0], read_x_halo(b, lo_buf, slot, z))
        scratch[slot, z, 2 + size :, :] = keep(valid[1], read_x_halo(b, hi_buf, slot, z))


def slope_y2(f, lo, hi, spacing):
    n = f.shape[-1]
    lane = lax.broadcasted_iota(jnp.int32, f.shape, 1)
    m1 = jnp.where(lane == 0, lo[1], pltpu.roll(f, 1, 1))
    m2 = jnp.where(lane == 0, lo[0], jnp.where(lane == 1, lo[1], pltpu.roll(f, 2, 1)))
    p1 = jnp.where(lane == n - 1, hi[0], pltpu.roll(f, n - 1, 1))
    p2 = jnp.where(lane == n - 2, hi[0], jnp.where(lane == n - 1, hi[1], pltpu.roll(f, n - 2, 1)))
    return (m2 - 8.0 * m1 + 8.0 * p1 - p2) / (12.0 * spacing)


STRESS_X = (3, 6, 7)
STRESS_Y = (6, 4, 8)
VELOCITY = (0, 1, 2)


def pack_kernel(blocks, fw, cw, x_prev, x_next, y_prev, y_next):
    for b, w in zip(blocks, (fw, cw)):
        write_rims_split(b, w, x_prev, x_next, y_prev, y_next)


def write_rims_split(b, w, x_prev, x_next, y_prev, y_next):
    size, lanes = b.size, b.lanes
    for c, field in enumerate(STRESS_X):
        for z in range(b.layers):
            lo = w[field, z, 0:2, :]
            hi = w[field, z, size - 2 : size, :]
            for j in range(b.chunks):
                row = b.x_base + ((c * b.layers + z) * b.chunks + j) * 2
                x_prev[row : row + 2, :] = lo[:, j * 128 : (j + 1) * 128]
                x_next[row : row + 2, :] = hi[:, j * 128 : (j + 1) * 128]
    lane = lax.broadcasted_iota(jnp.int32, (size, 128), 1)
    for z in range(b.layers):
        acc_lo = jnp.zeros((size, 128), jnp.float32)
        acc_hi = jnp.zeros((size, 128), jnp.float32)
        for c, field in enumerate(STRESS_Y):
            v = w[field, z]
            rl = v if c == 0 else pltpu.roll(v, 2 * c, 1)
            rh = pltpu.roll(v, (2 * c + 2) % lanes, 1)
            keep = (lane >= 2 * c) & (lane < 2 * c + 2)
            acc_lo = jnp.where(keep, rl[:, 0:128], acc_lo)
            acc_hi = jnp.where(keep, rh[:, 0:128], acc_hi)
        row = b.y_base + z * size
        y_prev[row : row + size, :] = acc_lo
        y_next[row : row + size, :] = acc_hi


def velocity_block(b, w, mat, metric, table, out, sx, hx_lo, hx_hi, hy_lo, hy_hi, valid):
    for slot, field in enumerate(STRESS_X):
        fill_x2(b, sx, slot, w, field, hx_lo, hx_hi, valid)
    for z in range(b.layers):
        dx = [slope_x(sx, slot, z, b.size, b.spacing) for slot in range(3)]
        dy = [
            slope_y2(w[field, z], read_y_halo(b, hy_lo, slot, z, valid[2]), read_y_halo(b, hy_hi, slot, z, valid[3]),
                     b.spacing)
            for slot, field in enumerate(STRESS_Y)
        ]
        dz = [slope_z(w, field, b.rows[z]) for field in (7, 8, 5)]
        if metric is not None:
            m = metric[z]
            dz = [m * d for d in dz]
        buoy = pick(table, 0, mat[z])
        for k in range(3):
            out[k, z] = w[k, z] + step_size * (buoy * (dx[k] + dy[k] + dz[k]))


def velocity_kernel(blocks, fw, cw, hx_lo, hx_hi, hy_lo, hy_hi, fmat, fmetric, cmat, table, flags,
                    fvel, cvel, vx_prev, vx_next, vy_prev, vy_next, sx_f, sx_c):
    fine, coarse = blocks
    valid = valid_of(flags)
    velocity_block(fine, fw, fmat, fmetric, table, fvel, sx_f, hx_lo, hx_hi, hy_lo, hy_hi, valid)
    velocity_block(coarse, cw, cmat, None, table, cvel, sx_c, hx_lo, hx_hi, hy_lo, hy_hi, valid)
    write_rims(fine, fvel, VELOCITY, vx_prev, vx_next, vy_prev, vy_next)
    write_rims(coarse, cvel, VELOCITY, vx_prev, vx_next, vy_prev, vy_next)


def stress_block(b, depth, w, mem, vel, mat, mech, metric, mtab, atab, out, mem_out, face, sx,
                 hx_lo, hx_hi, hy_lo, hy_hi, face_rims, valid):
    for slot in range(3):
        fill_x2(b, sx, slot, vel, slot, hx_lo, hx_hi, valid)
    for z in range(b.layers):
        dx = [slope_x(sx, slot, z, b.size, b.spacing) for slot in range(3)]
        dy = [
            slope_y2(vel[slot, z], read_y_halo(b, hy_lo, slot, z, valid[2]), read_y_halo(b, hy_hi, slot, z, valid[3]),
                     b.spacing)
            for slot in range(3)
        ]
        dz = [slope_z(vel, slot, b.rows[z]) for slot in range(3)]
        if metric is not None:
            m = metric[z]
            dz = [m * d for d in dz]
        kind, mechanism = mat[z], mech[z]
        lame, shear = pick(mtab, 1, kind), pick(mtab, 2, kind)
        decay, strength = pick(atab, 0, mechanism), pick(atab, 1, mechanism)
        cell_volume = lame * (dx[0] + dy[1] + dz[2])
        rate = [
            cell_volume + 2.0 * shear * dx[0],
            cell_volume + 2.0 * shear * dy[1],
            cell_volume + 2.0 * shear * dz[2],
            shear * (dy[0] + dx[1]),
            shear * (dz[0] + dx[2]),
            shear * (dz[1] + dy[2]),
        ]
        values = []
        for k in range(3):
            v = vel[k, z]
            out[k, z] = v
            values.append(v)
        for k in range(6):
            memory_new = decay * mem[k, z] + (1.0 - decay) * strength * rate[k]
            mem_out[k, z] = memory_new
            stress = w[3 + k, z] + step_size * (rate[k] - memory_new)
            out[3 + k, z] = stress
            values.append(stress)
        if z == depth:
            for i, k in enumerate((0, 1, 2, 7, 8, 5)):
                face[i] = values[k]
            write_face_rims(b, [values[k] for k in (0, 1, 2, 7, 8, 5)], *face_rims)


def write_face_rims(b, planes, x_prev, x_next, y_prev, y_next):
    size, lanes = b.size, b.lanes
    for i, v in enumerate(planes):
        for j in range(b.chunks):
            row = b.fx_base + i * b.chunks + j
            x_prev[row : row + 1, :] = v[0:1, j * 128 : (j + 1) * 128]
            x_next[row : row + 1, :] = v[size - 1 : size, j * 128 : (j + 1) * 128]
    lane = lax.broadcasted_iota(jnp.int32, (size, 128), 1)
    acc_lo = jnp.zeros((size, 128), jnp.float32)
    acc_hi = jnp.zeros((size, 128), jnp.float32)
    for i, v in enumerate(planes):
        rl = v if i == 0 else pltpu.roll(v, i, 1)
        rh = pltpu.roll(v, (i + 1) % lanes, 1)
        acc_lo = jnp.where(lane == i, rl[:, 0:128], acc_lo)
        acc_hi = jnp.where(lane == i, rh[:, 0:128], acc_hi)
    y_prev[b.fy_base : b.fy_base + size, :] = acc_lo
    y_next[b.fy_base : b.fy_base + size, :] = acc_hi


def stress_kernel(blocks, fw, fmem, fvel, cw, cmem, cvel, hx_lo, hx_hi, hy_lo, hy_hi,
                  fmat, fmech, fmetric, cmat, cmech, mtab, atab, flags,
                  fout, fmem_out, fface, cout, cmem_out, cface, rx_prev, rx_next, ry_prev, ry_next, sx_f, sx_c):
    fine, coarse = blocks
    valid = valid_of(flags)
    rims = (rx_prev, rx_next, ry_prev, ry_next)
    stress_block(fine, fine.layers - 1, fw, fmem, fvel, fmat, fmech, fmetric, mtab, atab, fout, fmem_out,
                 fface, sx_f, hx_lo, hx_hi, hy_lo, hy_hi, rims, valid)
    stress_block(coarse, 0, cw, cmem, cvel, cmat, cmech, None, mtab, atab, cout, cmem_out,
                 cface, sx_c, hx_lo, hx_hi, hy_lo, hy_hi, rims, valid)


def vmem_specs(count):
    return [pl.BlockSpec(memory_space=pltpu.VMEM)] * count


def f32(shape):
    return jax.ShapeDtypeStruct(shape, jnp.float32)


def halo_shapes(x_rows, y_rows):
    return (f32((x_rows, 128)), f32((x_rows, 128)), f32((y_rows, 128)), f32((y_rows, 128)))


def scratch_for(b):
    return pltpu.VMEM((3, b.layers, b.size + 4, b.lanes), jnp.float32)


def receive(buffers):
    x_prev, x_next, y_prev, y_next = buffers
    y_lo = shift_from(y_next, "gy", 1)
    y_hi = shift_from(y_prev, "gy", -1)
    x_lo = shift_from(x_next, "gx", 1)
    x_hi = shift_from(x_prev, "gx", -1)
    return x_lo, x_hi, y_lo, y_hi


def put_face(out, face, depth):
    out = lax.dynamic_update_slice(out, face[0:3][:, None], (0, depth, 0, 0))
    out = lax.dynamic_update_slice(out, face[5:6][:, None], (5, depth, 0, 0))
    out = lax.dynamic_update_slice(out, face[3:5][:, None], (7, depth, 0, 0))
    return out


def prolong_y_matrix(coarse_lanes):
    m = np.zeros((coarse_lanes, 3 * coarse_lanes), np.float32)
    for d in range(coarse_lanes):
        m[d, 3 * d] = 2.0 / 3.0
        m[d, 3 * d + 1] = 1.0
        m[d, 3 * d + 2] = 2.0 / 3.0
        if d >= 1:
            m[d - 1, 3 * d] = 1.0 / 3.0
        if d + 1 < coarse_lanes:
            m[d + 1, 3 * d + 2] = 1.0 / 3.0
    return m


def restrict_y_matrix(coarse_lanes):
    m = np.zeros((3 * coarse_lanes, coarse_lanes), np.float32)
    for c in range(coarse_lanes):
        for offset, weight in ((-1, 1.0), (0, 2.0), (1, 3.0), (2, 2.0), (3, 1.0)):
            f = 3 * c + offset
            if 0 <= f < 3 * coarse_lanes:
                m[f, c] = weight / 9.0
    return m


def padded_rows(b, face, hx_lo, hx_hi, hy_lo, hy_hi, valid, i):
    size = b.size

    def x_row(buf):
        parts = [buf[pl.ds(b.fx_base + i * b.chunks + j, 1), :] for j in range(b.chunks)]
        return parts[0] if len(parts) == 1 else jnp.concatenate(parts, axis=1)

    def lane_of(buf, row, ok):
        return keep(ok, buf[pl.ds(row, 1), pl.ds(i, 1)])

    x_lo_ok, x_hi_ok, y_lo_ok, y_hi_ok = valid
    lo_row, hi_row = b.corner_rows
    rows = [(keep(x_lo_ok, x_row(hx_lo)), lane_of(hy_lo, lo_row, x_lo_ok & y_lo_ok),
             lane_of(hy_hi, lo_row, x_lo_ok & y_hi_ok))]
    for x in range(size):
        rows.append((face[i, pl.ds(x, 1), :], lane_of(hy_lo, b.fy_base + x, y_lo_ok),
                     lane_of(hy_hi, b.fy_base + x, y_hi_ok)))
    rows.append((keep(x_hi_ok, x_row(hx_hi)), lane_of(hy_lo, hi_row, x_hi_ok & y_lo_ok),
                 lane_of(hy_hi, hi_row, x_hi_ok & y_hi_ok)))
    return rows


def combine(terms):
    out = []
    for part in range(3):
        total = None
        for weight, row in terms:
            v = row[part] if weight == 1.0 else weight * row[part]
            total = v if total is None else total + v
        out.append(total)
    return out


def face_kernel(blocks, fine_depth, fout_in, cout_in, fface, cface, hx_lo, hx_hi, hy_lo, hy_hi,
                py, ry, flags, fout, cout, fnew, cnew, stage_p, stage_r, sems):
    fine, coarse = blocks
    halos = (hx_lo, hx_hi, hy_lo, hy_hi, valid_of(flags))
    lane_f = lax.broadcasted_iota(jnp.int32, (1, fine.lanes), 1)
    p_lo, p_hi = [], []
    for i in range(6):
        rows = padded_rows(coarse, cface, *halos, i)
        for c in range(coarse.size):
            left, middle, right = rows[c], rows[c + 1], rows[c + 2]
            parts = [
                [(1.0, left), (2.0, middle)],
                [(1.0, middle)],
                [(2.0, middle), (1.0, right)],
            ]
            for a, terms in enumerate(parts):
                interior, lo, hi = combine(terms)
                if a != 1:
                    interior, lo, hi = interior / 3.0, lo / 3.0, hi / 3.0
                r = i * fine.size + 3 * c + a
                stage_p[pl.ds(r, 1), :] = interior
                p_lo.append(lo)
                p_hi.append(hi)
    prolonged = jnp.dot(stage_p[...], py[...], precision=lax.Precision.HIGHEST, preferred_element_type=jnp.float32)
    for i in range(6):
        for x in range(fine.size):
            r = i * fine.size + x
            value = prolonged[r : r + 1, :]
            value = value + jnp.where(lane_f == 0, p_lo[r] / 3.0, 0.0) + jnp.where(lane_f == fine.lanes - 1, p_hi[r] / 3.0, 0.0)
            own = fface[i, pl.ds(x, 1), :]
            fnew[i, 0, pl.ds(x, 1), :] = own - penalty * (own - value)
    lane_c = lax.broadcasted_iota(jnp.int32, (1, coarse.lanes), 1)
    r_lo, r_hi = [], []
    for i in range(6):
        rows = padded_rows(fine, fface, *halos, i)
        for c in range(coarse.size):
            terms = [(1.0, rows[3 * c]), (2.0, rows[3 * c + 1]), (3.0, rows[3 * c + 2]), (2.0, rows[3 * c + 3]),
                     (1.0, rows[3 * c + 4])]
            interior, lo, hi = combine(terms)
            r = i * coarse.size + c
            stage_r[pl.ds(r, 1), :] = interior / 9.0
            r_lo.append(lo / 9.0)
            r_hi.append(hi / 9.0)
    restricted = jnp.dot(stage_r[...], ry[...], precision=lax.Precision.HIGHEST, preferred_element_type=jnp.float32)
    for i in range(6):
        for c in range(coarse.size):
            r = i * coarse.size + c
            value = restricted[r : r + 1, :]
            value = value + jnp.where(lane_c == 0, r_lo[r] / 9.0, 0.0) + jnp.where(lane_c == coarse.lanes - 1, r_hi[r] / 9.0, 0.0)
            own = cface[i, pl.ds(c, 1), :]
            cnew[i, 0, pl.ds(c, 1), :] = own - penalty * (own - value)
    copies = []
    for n, (src, dst, depth) in enumerate(((fnew, fout, fine_depth), (cnew, cout, 0))):
        for k, (first, count, field) in enumerate(((0, 3, 0), (5, 1, 5), (3, 2, 7))):
            copy = pltpu.make_async_copy(
                src.at[pl.ds(first, count)], dst.at[pl.ds(field, count), pl.ds(depth, 1)], sems.at[3 * n + k]
            )
            copy.start()
            copies.append(copy)
    for copy in copies:
        copy.wait()


def diag_from(block, dx, dy):
    nx, ny = lax.axis_size("gx"), lax.axis_size("gy")
    pairs = []
    for i in range(nx):
        for j in range(ny):
            if 0 <= i + dx < nx and 0 <= j + dy < ny:
                pairs.append((i * ny + j, (i + dx) * ny + (j + dy)))
    return lax.ppermute(block, ("gx", "gy"), pairs)


def row_ends(buf, blocks, at_end):
    out = []
    for b in blocks:
        chunk = b.chunks - 1 if at_end else 0
        first = b.fx_base + chunk
        lane = 127 if at_end else 0
        out.append(lax.slice(buf, (first, lane), (first + 5 * b.chunks + 1, lane + 1), (b.chunks, 1))[:, 0])
    return jnp.stack(out)


def with_corners(y_rim, x_lo, x_hi, blocks, at_end):
    lo, hi = row_ends(x_lo, blocks, at_end), row_ends(x_hi, blocks, at_end)
    extra = jnp.stack([lo, hi], axis=1).reshape(2 * len(blocks), 6)
    extra = jnp.pad(extra, ((0, 0), (0, 128 - 6)))
    joined = jnp.concatenate([y_rim, extra])
    return jnp.pad(joined, ((0, round8(joined.shape[0]) - joined.shape[0]), (0, 0)))


def face_call(blocks, fine_out, coarse_out, fine_face, coarse_face, rims):
    fine, coarse = blocks
    x_prev, x_next, y_prev, y_next = rims
    x_lo = shift_from(x_next, "gx", 1)
    x_hi = shift_from(x_prev, "gx", -1)
    y_lo = shift_from(with_corners(y_next, x_lo, x_hi, blocks, True), "gy", 1)
    y_hi = shift_from(with_corners(y_prev, x_lo, x_hi, blocks, False), "gy", -1)
    received = (x_lo, x_hi, y_lo, y_hi)
    py = jnp.asarray(prolong_y_matrix(coarse.lanes))
    ry = jnp.asarray(restrict_y_matrix(coarse.lanes))
    anyspace = pl.BlockSpec(memory_space=pl.ANY)
    return pl.pallas_call(
        functools.partial(face_kernel, blocks, fine.layers - 1),
        out_shape=(f32(fine_out.shape), f32(coarse_out.shape)),
        in_specs=[anyspace, anyspace] + vmem_specs(8) + [pl.BlockSpec(memory_space=pltpu.SMEM)],
        out_specs=(anyspace, anyspace),
        input_output_aliases={0: 0, 1: 1},
        scratch_shapes=[
            pltpu.VMEM((6, 1, fine.size, fine.lanes), jnp.float32),
            pltpu.VMEM((6, 1, coarse.size, coarse.lanes), jnp.float32),
            pltpu.VMEM((round8(6 * fine.size), coarse.lanes), jnp.float32),
            pltpu.VMEM((round8(6 * coarse.size), fine.lanes), jnp.float32),
            pltpu.SemaphoreType.DMA((6,)),
        ],
    )(fine_out, coarse_out, fine_face, coarse_face, *received, py, ry, edge_flags())


def local(
    fine_wave,
    fine_memory,
    fine_material,
    fine_mechanism,
    fine_metric,
    coarse_wave,
    coarse_memory,
    coarse_material,
    coarse_mechanism,
    material_table,
    attenuation_table,
):
    fine, coarse, x_rows, y_rows = plan_blocks(fine_wave.shape[1:], coarse_wave.shape[1:])
    blocks = (fine, coarse)
    smem = pl.BlockSpec(memory_space=pltpu.SMEM)
    flags = edge_flags()

    rims = pl.pallas_call(
        functools.partial(pack_kernel, blocks),
        out_shape=halo_shapes(x_rows, y_rows),
        in_specs=vmem_specs(2),
        out_specs=tuple(vmem_specs(4)),
    )(fine_wave, coarse_wave)
    halos = receive(rims)

    fine_velocity, coarse_velocity, *vrims = pl.pallas_call(
        functools.partial(velocity_kernel, blocks),
        out_shape=(f32((3,) + fine_wave.shape[1:]), f32((3,) + coarse_wave.shape[1:])) + halo_shapes(x_rows, y_rows),
        in_specs=vmem_specs(9) + [smem, smem],
        out_specs=tuple(vmem_specs(6)),
        scratch_shapes=[scratch_for(fine), scratch_for(coarse)],
    )(fine_wave, coarse_wave, *halos, fine_material, fine_metric, coarse_material, material_table, flags)

    vhalos = receive(vrims)
    fx_rows = 6 * (fine.chunks + coarse.chunks)
    fy_rows = round8(fine.size + coarse.size)
    fine_out, fine_mem, fine_face, coarse_out, coarse_mem, coarse_face, *face_rims = pl.pallas_call(
        functools.partial(stress_kernel, blocks),
        out_shape=(
            f32(fine_wave.shape), f32(fine_memory.shape), f32((6,) + fine_wave.shape[2:]),
            f32(coarse_wave.shape), f32(coarse_memory.shape), f32((6,) + coarse_wave.shape[2:]),
            f32((fx_rows, 128)), f32((fx_rows, 128)), f32((fy_rows, 128)), f32((fy_rows, 128)),
        ),
        in_specs=vmem_specs(15) + [smem, smem, smem],
        out_specs=tuple(vmem_specs(10)),
        scratch_shapes=[scratch_for(fine), scratch_for(coarse)],
    )(fine_wave, fine_memory, fine_velocity, coarse_wave, coarse_memory, coarse_velocity, *vhalos,
      fine_material, fine_mechanism, fine_metric, coarse_material, coarse_mechanism, material_table,
      attenuation_table, flags)

    fine_out, coarse_out = face_call(blocks, fine_out, coarse_out, fine_face, coarse_face, face_rims)
    return (fine_out, fine_mem, coarse_out, coarse_mem)


def solution(mesh):
    in_specs = (
        P(None, None, "gx", "gy"),
        P(None, None, "gx", "gy"),
        P(None, "gx", "gy"),
        P(None, "gx", "gy"),
        P(None, "gx", "gy"),
        P(None, None, "gx", "gy"),
        P(None, None, "gx", "gy"),
        P(None, "gx", "gy"),
        P(None, "gx", "gy"),
        P(),
        P(),
    )
    out_specs = (
        P(None, None, "gx", "gy"),
        P(None, None, "gx", "gy"),
        P(None, None, "gx", "gy"),
        P(None, None, "gx", "gy"),
    )
    return jax.shard_map(local, mesh=mesh, in_specs=in_specs, out_specs=out_specs, check_vma=False)
```

```python
import functools
import math

import jax
import jax.numpy as jnp
import numpy as np
from jax import lax
from jax.sharding import PartitionSpec as P

step_size = 0.1
penalty = 0.1 * 48.0 / 17.0
closure = [
    [-24.0 / 17.0, 59.0 / 34.0, -4.0 / 17.0, -3.0 / 34.0, 0.0, 0.0],
    [-0.5, 0.0, 0.5, 0.0, 0.0, 0.0],
    [4.0 / 43.0, -59.0 / 86.0, 0.0, 59.0 / 86.0, -4.0 / 43.0, 0.0],
    [3.0 / 98.0, 0.0, -59.0 / 98.0, 0.0, 32.0 / 49.0, -4.0 / 49.0],
]


def sbp_table(layers, spacing):
    return jnp.asarray(sbp_numpy(layers, spacing))


def sbp_numpy(layers, spacing):
    table = np.zeros((layers, layers))
    for line_at in range(4):
        for column in range(6):
            table[line_at, column] = closure[line_at][column]
            table[layers - 1 - line_at, layers - 1 - column] = -closure[line_at][column]
    for line_at in range(4, layers - 4):
        table[line_at, line_at - 2 : line_at + 3] = [
            1.0 / 12.0,
            -2.0 / 3.0,
            0.0,
            2.0 / 3.0,
            -1.0 / 12.0,
        ]
    return (table / spacing).astype(np.float32)


def shift_from(block, axis, offset):
    count = lax.axis_size(axis)
    pairs = [(i, (i + offset) % count) for i in range(count)]
    return lax.ppermute(block, axis, pairs)


def edge_flags():
    gx, gy = lax.axis_index("gx"), lax.axis_index("gy")
    nx, ny = lax.axis_size("gx"), lax.axis_size("gy")
    return jnp.stack([gx > 0, gx < nx - 1, gy > 0, gy < ny - 1]).astype(jnp.int32)


def valid_of(flags):
    return tuple(flags[k] != 0 for k in range(4))


def keep(ok, value):
    return jnp.where(ok, value, 0.0)


def packed_shift(blocks, axis, offset):
    sizes = [math.prod(b.shape) for b in blocks]
    joined = jnp.concatenate([b.reshape(-1) for b in blocks])
    moved = shift_from(joined, axis, offset)
    out, start = [], 0
    for b, size in zip(blocks, sizes):
        out.append(moved[start : start + size].reshape(b.shape))
        start += size
    return out


def exchange(blocks, width):
    x_lo = packed_shift([b[..., -width:, :] for b in blocks], "gx", 1)
    x_hi = packed_shift([b[..., :width, :] for b in blocks], "gx", -1)
    y_lo = packed_shift([b[..., -width:] for b in blocks], "gy", 1)
    y_hi = packed_shift([b[..., :width] for b in blocks], "gy", -1)
    return [(x_lo[i], x_hi[i], y_lo[i], y_hi[i]) for i in range(len(blocks))]


def central_diff(padded, along, spacing):
    length = padded.shape[along] - 4
    s = lambda o: lax.slice_in_dim(padded, o, o + length, axis=along)
    return (s(0) - 8.0 * s(1) + 8.0 * s(3) - s(4)) / (12.0 * spacing)


def diff_x(block, halo, spacing):
    x_lo, x_hi, _, _ = halo
    return central_diff(jnp.concatenate([x_lo, block, x_hi], axis=-2), block.ndim - 2, spacing)


def diff_y(block, halo, spacing):
    _, _, y_lo, y_hi = halo
    return central_diff(jnp.concatenate([y_lo, block, y_hi], axis=-1), block.ndim - 1, spacing)


def vertical_diff(fields, matrix):
    return jnp.einsum("kz,czxy->ckxy", matrix, fields, precision=lax.Precision.HIGHEST)


def lookup_table(grid_cell_index, values):
    result = jnp.zeros(grid_cell_index.shape, jnp.float32)
    for kind_at in range(values.shape[0]):
        result = jnp.where(grid_cell_index == kind_at, values[kind_at], result)
    return result


def velocity_step(wave, halo_x3, halo_y3, buoyancy, metric, matrix, spacing):
    sx = jnp.stack([wave[3], wave[6], wave[7]])
    sy = jnp.stack([wave[6], wave[4], wave[8]])
    slope_x = diff_x(sx, halo_x3, spacing)
    slope_y = diff_y(sy, halo_y3, spacing)
    slope_z = metric * vertical_diff(jnp.stack([wave[7], wave[8], wave[5]]), matrix)
    rate_x = slope_x[0] + slope_y[0] + slope_z[0]
    rate_y = slope_x[1] + slope_y[1] + slope_z[1]
    rate_z = slope_x[2] + slope_y[2] + slope_z[2]
    return wave[:3] + step_size * (buoyancy * jnp.stack([rate_x, rate_y, rate_z]))


def stress_step(wave, memory, velocity, halo, lame, shear, decay, strength, metric, matrix, spacing):
    slope_x = diff_x(velocity, halo, spacing)
    slope_y = diff_y(velocity, halo, spacing)
    slope_z = metric * vertical_diff(velocity, matrix)
    cell_volume = lame * (slope_x[0] + slope_y[1] + slope_z[2])
    rate = jnp.stack(
        [
            cell_volume + 2.0 * shear * slope_x[0],
            cell_volume + 2.0 * shear * slope_y[1],
            cell_volume + 2.0 * shear * slope_z[2],
            shear * (slope_y[0] + slope_x[1]),
            shear * (slope_z[0] + slope_x[2]),
            shear * (slope_z[1] + slope_y[2]),
        ]
    )
    memory_new = decay * memory + (1.0 - decay) * strength * rate
    stress = wave[3:] + step_size * (rate - memory_new)
    return stress, memory_new


def face_of(velocity, stress, depth):
    return jnp.stack(
        [
            velocity[0, depth],
            velocity[1, depth],
            velocity[2, depth],
            stress[4, depth],
            stress[5, depth],
            stress[2, depth],
        ]
    )


def pad_faces(faces):
    x_lo = packed_shift([f[:, -1:, :] for f in faces], "gx", 1)
    x_hi = packed_shift([f[:, :1, :] for f in faces], "gx", -1)
    faces = [jnp.concatenate([lo, f, hi], axis=1) for lo, f, hi in zip(x_lo, faces, x_hi)]
    y_lo = packed_shift([f[:, :, -1:] for f in faces], "gy", 1)
    y_hi = packed_shift([f[:, :, :1] for f in faces], "gy", -1)
    return [jnp.concatenate([lo, f, hi], axis=2) for lo, f, hi in zip(y_lo, faces, y_hi)]


def shifted(padded, offset, length, along):
    return lax.slice_in_dim(padded, offset, offset + length, axis=along)


def prolong_axis(padded, along):
    length = padded.shape[along] - 2
    left = shifted(padded, 0, length, along)
    middle = shifted(padded, 1, length, along)
    right = shifted(padded, 2, length, along)
    parts = jnp.stack(
        [(left + 2.0 * middle) / 3.0, middle, (2.0 * middle + right) / 3.0], axis=along + 1
    )
    shape = list(middle.shape)
    shape[along] = shape[along] * 3
    return parts.reshape(tuple(shape))


def split_three(padded, offset, length, along):
    part = shifted(padded, offset, 3 * length, along)
    return part.reshape(part.shape[:along] + (length, 3) + part.shape[along + 1 :])


def pick_part(parts, number, along):
    return lax.index_in_dim(parts, number, along + 1, keepdims=False)


def restrict_axis(padded, along):
    length = (padded.shape[along] - 2) // 3
    first = split_three(padded, 0, length, along)
    middle = split_three(padded, 1, length, along)
    last = split_three(padded, 2, length, along)
    return (
        pick_part(first, 0, along)
        + 2.0 * pick_part(middle, 0, along)
        + 3.0 * pick_part(middle, 1, along)
        + 2.0 * pick_part(middle, 2, along)
        + pick_part(last, 2, along)
    ) / 9.0


def assemble(velocity, stress, face, depth):
    replace = {0: face[0], 1: face[1], 2: face[2], 7: face[3], 8: face[4], 5: face[5]}
    fields = [velocity[0], velocity[1], velocity[2]] + [stress[k] for k in range(6)]
    rows = []
    for k, field in enumerate(fields):
        if k in replace:
            field = lax.dynamic_update_slice_in_dim(field, replace[k][None], depth, axis=0)
        rows.append(field)
    return jnp.stack(rows)


from jax.experimental import pallas as pl
from jax.experimental.pallas import tpu as pltpu


def sbp_rows(layers, spacing):
    table = sbp_numpy(layers, spacing)
    return [[(j, float(table[k, j])) for j in range(layers) if table[k, j] != 0.0] for k in range(layers)]


def pick(values_ref, row, index):
    result = jnp.zeros(index.shape, jnp.float32)
    for kind_at in range(values_ref.shape[1]):
        result = jnp.where(index == kind_at, values_ref[row, kind_at], result)
    return result


def fill_x(scratch, slot, lo, block, hi):
    width = lo.shape[-2]
    size = block.shape[-2]
    scratch[slot, :, 0:width, :] = lo
    scratch[slot, :, width : width + size, :] = block
    scratch[slot, :, width + size :, :] = hi


def slope_x(scratch, slot, z, size, spacing):
    s = lambda o: scratch[slot, z, o : o + size, :]
    return (s(0) - 8.0 * s(1) + 8.0 * s(3) - s(4)) / (12.0 * spacing)


def slope_y(f, lo, hi, spacing):
    n = f.shape[-1]
    lane = lax.broadcasted_iota(jnp.int32, f.shape, f.ndim - 1)
    m1 = jnp.where(lane == 0, lo[:, 1:2], pltpu.roll(f, 1, f.ndim - 1))
    m2 = jnp.where(lane == 0, lo[:, 0:1], jnp.where(lane == 1, lo[:, 1:2], pltpu.roll(f, 2, f.ndim - 1)))
    p1 = jnp.where(lane == n - 1, hi[:, 0:1], pltpu.roll(f, n - 1, f.ndim - 1))
    p2 = jnp.where(lane == n - 2, hi[:, 0:1], jnp.where(lane == n - 1, hi[:, 1:2], pltpu.roll(f, n - 2, f.ndim - 1)))
    return (m2 - 8.0 * m1 + 8.0 * p1 - p2) / (12.0 * spacing)


def slope_z(field_ref, index, row):
    total = None
    for j, weight in row:
        term = jnp.float32(weight) * field_ref[index, j]
        total = term if total is None else total + term
    return total


class Block:
    def __init__(self, shape, spacing, has_metric, x_base, y_base):
        self.layers, self.size, self.lanes = shape
        self.chunks = self.lanes // 128
        self.spacing = spacing
        self.has_metric = has_metric
        self.rows = sbp_rows(self.layers, spacing)
        self.x_base, self.y_base = x_base, y_base

    @property
    def x_rows(self):
        return 3 * self.layers * self.chunks * 2

    @property
    def y_rows(self):
        return self.layers * self.size


def plan_blocks(fine_shape, coarse_shape):
    fine = Block(fine_shape, 1.0, True, 0, 0)
    coarse = Block(coarse_shape, 3.0, False, fine.x_rows, fine.y_rows)
    fine.fx_base, fine.fy_base = 0, 0
    coarse.fx_base, coarse.fy_base = 6 * fine.chunks, fine.size
    corner_base = fine.size + coarse.size
    fine.corner_rows = (corner_base, corner_base + 1)
    coarse.corner_rows = (corner_base + 2, corner_base + 3)
    return fine, coarse, fine.x_rows + coarse.x_rows, fine.y_rows + coarse.y_rows


def round8(n):
    return -(-n // 8) * 8


def write_rims(b, src, fields, x_prev, x_next, y_prev, y_next):
    size, lanes = b.size, b.lanes
    for c, field in enumerate(fields):
        for z in range(b.layers):
            lo = src[field, z, 0:2, :]
            hi = src[field, z, size - 2 : size, :]
            for j in range(b.chunks):
                row = b.x_base + ((c * b.layers + z) * b.chunks + j) * 2
                x_prev[row : row + 2, :] = lo[:, j * 128 : (j + 1) * 128]
                x_next[row : row + 2, :] = hi[:, j * 128 : (j + 1) * 128]
    lane = lax.broadcasted_iota(jnp.int32, (size, 128), 1)
    for z in range(b.layers):
        acc_lo = jnp.zeros((size, 128), jnp.float32)
        acc_hi = jnp.zeros((size, 128), jnp.float32)
        for c, field in enumerate(fields):
            v = src[field, z]
            rl = v if c == 0 else pltpu.roll(v, 2 * c, 1)
            rh = pltpu.roll(v, (2 * c + 2) % lanes, 1)
            keep = (lane >= 2 * c) & (lane < 2 * c + 2)
            acc_lo = jnp.where(keep, rl[:, 0:128], acc_lo)
            acc_hi = jnp.where(keep, rh[:, 0:128], acc_hi)
        row = b.y_base + z * size
        y_prev[row : row + size, :] = acc_lo
        y_next[row : row + size, :] = acc_hi


def read_x_halo(b, buf, c, z):
    parts = [buf[pl.ds(b.x_base + ((c * b.layers + z) * b.chunks + j) * 2, 2), :] for j in range(b.chunks)]
    return parts[0] if len(parts) == 1 else jnp.concatenate(parts, axis=1)


def read_y_halo(b, buf, c, z, ok):
    row = b.y_base + z * b.size
    return keep(ok, buf[pl.ds(row, b.size), pl.ds(2 * c, 1)]), keep(ok, buf[pl.ds(row, b.size), pl.ds(2 * c + 1, 1)])


def fill_x2(b, scratch, slot, src, field, lo_buf, hi_buf, valid):
    size = b.size
    scratch[slot, :, 2 : 2 + size, :] = src[field]
    for z in range(b.layers):
        scratch[slot, z, 0:2, :] = keep(valid[0], read_x_halo(b, lo_buf, slot, z))
        scratch[slot, z, 2 + size :, :] = keep(valid[1], read_x_halo(b, hi_buf, slot, z))


def slope_y2(f, lo, hi, spacing):
    n = f.shape[-1]
    lane = lax.broadcasted_iota(jnp.int32, f.shape, 1)
    m1 = jnp.where(lane == 0, lo[1], pltpu.roll(f, 1, 1))
    m2 = jnp.where(lane == 0, lo[0], jnp.where(lane == 1, lo[1], pltpu.roll(f, 2, 1)))
    p1 = jnp.where(lane == n - 1, hi[0], pltpu.roll(f, n - 1, 1))
    p2 = jnp.where(lane == n - 2, hi[0], jnp.where(lane == n - 1, hi[1], pltpu.roll(f, n - 2, 1)))
    return (m2 - 8.0 * m1 + 8.0 * p1 - p2) / (12.0 * spacing)


STRESS_X = (3, 6, 7)
STRESS_Y = (6, 4, 8)
VELOCITY = (0, 1, 2)


def pack_kernel(blocks, fw, cw, x_prev, x_next, y_prev, y_next):
    for b, w in zip(blocks, (fw, cw)):
        write_rims_split(b, w, x_prev, x_next, y_prev, y_next)


def write_rims_split(b, w, x_prev, x_next, y_prev, y_next):
    size, lanes = b.size, b.lanes
    for c, field in enumerate(STRESS_X):
        for z in range(b.layers):
            lo = w[field, z, 0:2, :]
            hi = w[field, z, size - 2 : size, :]
            for j in range(b.chunks):
                row = b.x_base + ((c * b.layers + z) * b.chunks + j) * 2
                x_prev[row : row + 2, :] = lo[:, j * 128 : (j + 1) * 128]
                x_next[row : row + 2, :] = hi[:, j * 128 : (j + 1) * 128]
    lane = lax.broadcasted_iota(jnp.int32, (size, 128), 1)
    for z in range(b.layers):
        acc_lo = jnp.zeros((size, 128), jnp.float32)
        acc_hi = jnp.zeros((size, 128), jnp.float32)
        for c, field in enumerate(STRESS_Y):
            v = w[field, z]
            rl = v if c == 0 else pltpu.roll(v, 2 * c, 1)
            rh = pltpu.roll(v, (2 * c + 2) % lanes, 1)
            keep = (lane >= 2 * c) & (lane < 2 * c + 2)
            acc_lo = jnp.where(keep, rl[:, 0:128], acc_lo)
            acc_hi = jnp.where(keep, rh[:, 0:128], acc_hi)
        row = b.y_base + z * size
        y_prev[row : row + size, :] = acc_lo
        y_next[row : row + size, :] = acc_hi


def velocity_block(b, w, mat, metric, table, out, sx, hx_lo, hx_hi, hy_lo, hy_hi, valid):
    for slot, field in enumerate(STRESS_X):
        fill_x2(b, sx, slot, w, field, hx_lo, hx_hi, valid)
    for z in range(b.layers):
        dx = [slope_x(sx, slot, z, b.size, b.spacing) for slot in range(3)]
        dy = [
            slope_y2(w[field, z], read_y_halo(b, hy_lo, slot, z, valid[2]), read_y_halo(b, hy_hi, slot, z, valid[3]),
                     b.spacing)
            for slot, field in enumerate(STRESS_Y)
        ]
        dz = [slope_z(w, field, b.rows[z]) for field in (7, 8, 5)]
        if metric is not None:
            m = metric[z]
            dz = [m * d for d in dz]
        buoy = pick(table, 0, mat[z])
        for k in range(3):
            out[k, z] = w[k, z] + step_size * (buoy * (dx[k] + dy[k] + dz[k]))


def velocity_kernel(blocks, fw, cw, hx_lo, hx_hi, hy_lo, hy_hi, fmat, fmetric, cmat, table, flags,
                    fvel, cvel, vx_prev, vx_next, vy_prev, vy_next, sx_f, sx_c):
    fine, coarse = blocks
    valid = valid_of(flags)
    velocity_block(fine, fw, fmat, fmetric, table, fvel, sx_f, hx_lo, hx_hi, hy_lo, hy_hi, valid)
    velocity_block(coarse, cw, cmat, None, table, cvel, sx_c, hx_lo, hx_hi, hy_lo, hy_hi, valid)
    write_rims(fine, fvel, VELOCITY, vx_prev, vx_next, vy_prev, vy_next)
    write_rims(coarse, cvel, VELOCITY, vx_prev, vx_next, vy_prev, vy_next)


def stress_block(b, depth, face_only, w, mem, vel, mat, mech, metric, mtab, atab, outputs, sx,
                 hx_lo, hx_hi, hy_lo, hy_hi, valid):
    for slot in range(3):
        fill_x2(b, sx, slot, vel, slot, hx_lo, hx_hi, valid)
    for z in ([depth] if face_only else range(b.layers)):
        dx = [slope_x(sx, slot, z, b.size, b.spacing) for slot in range(3)]
        dy = [
            slope_y2(vel[slot, z], read_y_halo(b, hy_lo, slot, z, valid[2]), read_y_halo(b, hy_hi, slot, z, valid[3]),
                     b.spacing)
            for slot in range(3)
        ]
        dz = [slope_z(vel, slot, b.rows[z]) for slot in range(3)]
        if metric is not None:
            m = metric[z]
            dz = [m * d for d in dz]
        kind, mechanism = mat[z], mech[z]
        lame, shear = pick(mtab, 1, kind), pick(mtab, 2, kind)
        decay, strength = pick(atab, 0, mechanism), pick(atab, 1, mechanism)
        cell_volume = lame * (dx[0] + dy[1] + dz[2])
        rate = [
            cell_volume + 2.0 * shear * dx[0],
            cell_volume + 2.0 * shear * dy[1],
            cell_volume + 2.0 * shear * dz[2],
            shear * (dy[0] + dx[1]),
            shear * (dz[0] + dx[2]),
            shear * (dz[1] + dy[2]),
        ]
        values = [vel[k, z] for k in range(3)]
        for k in range(6):
            memory_new = decay * mem[k, z] + (1.0 - decay) * strength * rate[k]
            stress = w[3 + k, z] + step_size * (rate[k] - memory_new)
            values.append(stress)
            if not face_only:
                outputs[1][k, z] = memory_new
        if face_only:
            planes = [values[k] for k in (0, 1, 2, 7, 8, 5)]
            for i, v in enumerate(planes):
                outputs[0][i] = v
            write_face_rims(b, planes, *outputs[1])
        else:
            for k in range(9):
                outputs[0][k, z] = values[k]


def write_face_rims(b, planes, x_prev, x_next, y_prev, y_next):
    size, lanes = b.size, b.lanes
    for i, v in enumerate(planes):
        for j in range(b.chunks):
            row = b.fx_base + i * b.chunks + j
            x_prev[row : row + 1, :] = v[0:1, j * 128 : (j + 1) * 128]
            x_next[row : row + 1, :] = v[size - 1 : size, j * 128 : (j + 1) * 128]
    lane = lax.broadcasted_iota(jnp.int32, (size, 128), 1)
    acc_lo = jnp.zeros((size, 128), jnp.float32)
    acc_hi = jnp.zeros((size, 128), jnp.float32)
    for i, v in enumerate(planes):
        rl = v if i == 0 else pltpu.roll(v, i, 1)
        rh = pltpu.roll(v, (i + 1) % lanes, 1)
        acc_lo = jnp.where(lane == i, rl[:, 0:128], acc_lo)
        acc_hi = jnp.where(lane == i, rh[:, 0:128], acc_hi)
    y_prev[b.fy_base : b.fy_base + size, :] = acc_lo
    y_next[b.fy_base : b.fy_base + size, :] = acc_hi


def stress_kernel(blocks, face_only, fw, fmem, fvel, cw, cmem, cvel, hx_lo, hx_hi, hy_lo, hy_hi,
                  fmat, fmech, fmetric, cmat, cmech, mtab, atab, flags, *outs):
    fine, coarse = blocks
    valid = valid_of(flags)
    if face_only:
        fface, cface, rx_prev, rx_next, ry_prev, ry_next, sx_f, sx_c = outs
        rims = (rx_prev, rx_next, ry_prev, ry_next)
        fine_outputs, coarse_outputs = (fface, rims), (cface, rims)
    else:
        fout, fmem_out, cout, cmem_out, sx_f, sx_c = outs
        fine_outputs, coarse_outputs = (fout, fmem_out), (cout, cmem_out)
    stress_block(fine, fine.layers - 1, face_only, fw, fmem, fvel, fmat, fmech, fmetric, mtab, atab, fine_outputs,
                 sx_f, hx_lo, hx_hi, hy_lo, hy_hi, valid)
    stress_block(coarse, 0, face_only, cw, cmem, cvel, cmat, cmech, None, mtab, atab, coarse_outputs,
                 sx_c, hx_lo, hx_hi, hy_lo, hy_hi, valid)


def vmem_specs(count):
    return [pl.BlockSpec(memory_space=pltpu.VMEM)] * count


def f32(shape):
    return jax.ShapeDtypeStruct(shape, jnp.float32)


def halo_shapes(x_rows, y_rows):
    return (f32((x_rows, 128)), f32((x_rows, 128)), f32((y_rows, 128)), f32((y_rows, 128)))


def scratch_for(b):
    return pltpu.VMEM((3, b.layers, b.size + 4, b.lanes), jnp.float32)


def receive(buffers):
    x_prev, x_next, y_prev, y_next = buffers
    y_lo = shift_from(y_next, "gy", 1)
    y_hi = shift_from(y_prev, "gy", -1)
    x_lo = shift_from(x_next, "gx", 1)
    x_hi = shift_from(x_prev, "gx", -1)
    return x_lo, x_hi, y_lo, y_hi


def put_face(out, face, depth):
    out = lax.dynamic_update_slice(out, face[0:3][:, None], (0, depth, 0, 0))
    out = lax.dynamic_update_slice(out, face[5:6][:, None], (5, depth, 0, 0))
    out = lax.dynamic_update_slice(out, face[3:5][:, None], (7, depth, 0, 0))
    return out


def prolong_y_matrix(coarse_lanes):
    m = np.zeros((coarse_lanes, 3 * coarse_lanes), np.float32)
    for d in range(coarse_lanes):
        m[d, 3 * d] = 2.0 / 3.0
        m[d, 3 * d + 1] = 1.0
        m[d, 3 * d + 2] = 2.0 / 3.0
        if d >= 1:
            m[d - 1, 3 * d] = 1.0 / 3.0
        if d + 1 < coarse_lanes:
            m[d + 1, 3 * d + 2] = 1.0 / 3.0
    return m


def restrict_y_matrix(coarse_lanes):
    m = np.zeros((3 * coarse_lanes, coarse_lanes), np.float32)
    for c in range(coarse_lanes):
        for offset, weight in ((-1, 1.0), (0, 2.0), (1, 3.0), (2, 2.0), (3, 1.0)):
            f = 3 * c + offset
            if 0 <= f < 3 * coarse_lanes:
                m[f, c] = weight / 9.0
    return m


def padded_rows(b, face, hx_lo, hx_hi, hy_lo, hy_hi, valid, i):
    size = b.size

    def x_row(buf):
        parts = [buf[pl.ds(b.fx_base + i * b.chunks + j, 1), :] for j in range(b.chunks)]
        return parts[0] if len(parts) == 1 else jnp.concatenate(parts, axis=1)

    def lane_of(buf, row, ok):
        return keep(ok, buf[pl.ds(row, 1), pl.ds(i, 1)])

    x_lo_ok, x_hi_ok, y_lo_ok, y_hi_ok = valid
    lo_row, hi_row = b.corner_rows
    rows = [(keep(x_lo_ok, x_row(hx_lo)), lane_of(hy_lo, lo_row, x_lo_ok & y_lo_ok),
             lane_of(hy_hi, lo_row, x_lo_ok & y_hi_ok))]
    for x in range(size):
        rows.append((face[i, pl.ds(x, 1), :], lane_of(hy_lo, b.fy_base + x, y_lo_ok),
                     lane_of(hy_hi, b.fy_base + x, y_hi_ok)))
    rows.append((keep(x_hi_ok, x_row(hx_hi)), lane_of(hy_lo, hi_row, x_hi_ok & y_lo_ok),
                 lane_of(hy_hi, hi_row, x_hi_ok & y_hi_ok)))
    return rows


def combine(terms):
    out = []
    for part in range(3):
        total = None
        for weight, row in terms:
            v = row[part] if weight == 1.0 else weight * row[part]
            total = v if total is None else total + v
        out.append(total)
    return out


def face_kernel(blocks, fine_depth, fout_in, cout_in, fface, cface, hx_lo, hx_hi, hy_lo, hy_hi,
                py, ry, flags, fout, cout, fnew, cnew, stage_p, stage_r, sems):
    fine, coarse = blocks
    halos = (hx_lo, hx_hi, hy_lo, hy_hi, valid_of(flags))
    lane_f = lax.broadcasted_iota(jnp.int32, (1, fine.lanes), 1)
    p_lo, p_hi = [], []
    for i in range(6):
        rows = padded_rows(coarse, cface, *halos, i)
        for c in range(coarse.size):
            left, middle, right = rows[c], rows[c + 1], rows[c + 2]
            parts = [
                [(1.0, left), (2.0, middle)],
                [(1.0, middle)],
                [(2.0, middle), (1.0, right)],
            ]
            for a, terms in enumerate(parts):
                interior, lo, hi = combine(terms)
                if a != 1:
                    interior, lo, hi = interior / 3.0, lo / 3.0, hi / 3.0
                r = i * fine.size + 3 * c + a
                stage_p[pl.ds(r, 1), :] = interior
                p_lo.append(lo)
                p_hi.append(hi)
    prolonged = jnp.dot(stage_p[...], py[...], precision=lax.Precision.HIGHEST, preferred_element_type=jnp.float32)
    for i in range(6):
        for x in range(fine.size):
            r = i * fine.size + x
            value = prolonged[r : r + 1, :]
            value = value + jnp.where(lane_f == 0, p_lo[r] / 3.0, 0.0) + jnp.where(lane_f == fine.lanes - 1, p_hi[r] / 3.0, 0.0)
            own = fface[i, pl.ds(x, 1), :]
            fnew[i, 0, pl.ds(x, 1), :] = own - penalty * (own - value)
    lane_c = lax.broadcasted_iota(jnp.int32, (1, coarse.lanes), 1)
    r_lo, r_hi = [], []
    for i in range(6):
        rows = padded_rows(fine, fface, *halos, i)
        for c in range(coarse.size):
            terms = [(1.0, rows[3 * c]), (2.0, rows[3 * c + 1]), (3.0, rows[3 * c + 2]), (2.0, rows[3 * c + 3]),
                     (1.0, rows[3 * c + 4])]
            interior, lo, hi = combine(terms)
            r = i * coarse.size + c
            stage_r[pl.ds(r, 1), :] = interior / 9.0
            r_lo.append(lo / 9.0)
            r_hi.append(hi / 9.0)
    restricted = jnp.dot(stage_r[...], ry[...], precision=lax.Precision.HIGHEST, preferred_element_type=jnp.float32)
    for i in range(6):
        for c in range(coarse.size):
            r = i * coarse.size + c
            value = restricted[r : r + 1, :]
            value = value + jnp.where(lane_c == 0, r_lo[r] / 9.0, 0.0) + jnp.where(lane_c == coarse.lanes - 1, r_hi[r] / 9.0, 0.0)
            own = cface[i, pl.ds(c, 1), :]
            cnew[i, 0, pl.ds(c, 1), :] = own - penalty * (own - value)
    copies = []
    for n, (src, dst, depth) in enumerate(((fnew, fout, fine_depth), (cnew, cout, 0))):
        for k, (first, count, field) in enumerate(((0, 3, 0), (5, 1, 5), (3, 2, 7))):
            copy = pltpu.make_async_copy(
                src.at[pl.ds(first, count)], dst.at[pl.ds(field, count), pl.ds(depth, 1)], sems.at[3 * n + k]
            )
            copy.start()
            copies.append(copy)
    for copy in copies:
        copy.wait()


def diag_from(block, dx, dy):
    nx, ny = lax.axis_size("gx"), lax.axis_size("gy")
    pairs = []
    for i in range(nx):
        for j in range(ny):
            if 0 <= i + dx < nx and 0 <= j + dy < ny:
                pairs.append((i * ny + j, (i + dx) * ny + (j + dy)))
    return lax.ppermute(block, ("gx", "gy"), pairs)


def row_ends(buf, blocks, at_end):
    out = []
    for b in blocks:
        chunk = b.chunks - 1 if at_end else 0
        first = b.fx_base + chunk
        lane = 127 if at_end else 0
        out.append(lax.slice(buf, (first, lane), (first + 5 * b.chunks + 1, lane + 1), (b.chunks, 1))[:, 0])
    return jnp.stack(out)


def with_corners(y_rim, x_lo, x_hi, blocks, at_end):
    lo, hi = row_ends(x_lo, blocks, at_end), row_ends(x_hi, blocks, at_end)
    extra = jnp.stack([lo, hi], axis=1).reshape(2 * len(blocks), 6)
    extra = jnp.pad(extra, ((0, 0), (0, 128 - 6)))
    joined = jnp.concatenate([y_rim, extra])
    return jnp.pad(joined, ((0, round8(joined.shape[0]) - joined.shape[0]), (0, 0)))


def face_call(blocks, fine_out, coarse_out, fine_face, coarse_face, rims):
    fine, coarse = blocks
    x_prev, x_next, y_prev, y_next = rims
    x_lo = shift_from(x_next, "gx", 1)
    x_hi = shift_from(x_prev, "gx", -1)
    y_lo = shift_from(with_corners(y_next, x_lo, x_hi, blocks, True), "gy", 1)
    y_hi = shift_from(with_corners(y_prev, x_lo, x_hi, blocks, False), "gy", -1)
    received = (x_lo, x_hi, y_lo, y_hi)
    py = jnp.asarray(prolong_y_matrix(coarse.lanes))
    ry = jnp.asarray(restrict_y_matrix(coarse.lanes))
    anyspace = pl.BlockSpec(memory_space=pl.ANY)
    return pl.pallas_call(
        functools.partial(face_kernel, blocks, fine.layers - 1),
        out_shape=(f32(fine_out.shape), f32(coarse_out.shape)),
        in_specs=[anyspace, anyspace] + vmem_specs(8) + [pl.BlockSpec(memory_space=pltpu.SMEM)],
        out_specs=(anyspace, anyspace),
        input_output_aliases={0: 0, 1: 1},
        scratch_shapes=[
            pltpu.VMEM((6, 1, fine.size, fine.lanes), jnp.float32),
            pltpu.VMEM((6, 1, coarse.size, coarse.lanes), jnp.float32),
            pltpu.VMEM((round8(6 * fine.size), coarse.lanes), jnp.float32),
            pltpu.VMEM((round8(6 * coarse.size), fine.lanes), jnp.float32),
            pltpu.SemaphoreType.DMA((6,)),
        ],
    )(fine_out, coarse_out, fine_face, coarse_face, *received, py, ry, edge_flags())


def local(
    fine_wave,
    fine_memory,
    fine_material,
    fine_mechanism,
    fine_metric,
    coarse_wave,
    coarse_memory,
    coarse_material,
    coarse_mechanism,
    material_table,
    attenuation_table,
):
    fine, coarse, x_rows, y_rows = plan_blocks(fine_wave.shape[1:], coarse_wave.shape[1:])
    blocks = (fine, coarse)
    smem = pl.BlockSpec(memory_space=pltpu.SMEM)
    flags = edge_flags()

    rims = pl.pallas_call(
        functools.partial(pack_kernel, blocks),
        out_shape=halo_shapes(x_rows, y_rows),
        in_specs=vmem_specs(2),
        out_specs=tuple(vmem_specs(4)),
    )(fine_wave, coarse_wave)
    halos = receive(rims)

    fine_velocity, coarse_velocity, *vrims = pl.pallas_call(
        functools.partial(velocity_kernel, blocks),
        out_shape=(f32((3,) + fine_wave.shape[1:]), f32((3,) + coarse_wave.shape[1:])) + halo_shapes(x_rows, y_rows),
        in_specs=vmem_specs(9) + [smem, smem],
        out_specs=tuple(vmem_specs(6)),
        scratch_shapes=[scratch_for(fine), scratch_for(coarse)],
    )(fine_wave, coarse_wave, *halos, fine_material, fine_metric, coarse_material, material_table, flags)

    vhalos = receive(vrims)
    fx_rows = 6 * (fine.chunks + coarse.chunks)
    fy_rows = round8(fine.size + coarse.size)
    stress_args = (fine_wave, fine_memory, fine_velocity, coarse_wave, coarse_memory, coarse_velocity, *vhalos,
                   fine_material, fine_mechanism, fine_metric, coarse_material, coarse_mechanism, material_table,
                   attenuation_table, flags)
    stress_specs = vmem_specs(15) + [smem, smem, smem]
    fine_face, coarse_face, *face_rims = pl.pallas_call(
        functools.partial(stress_kernel, blocks, True),
        out_shape=(
            f32((6,) + fine_wave.shape[2:]), f32((6,) + coarse_wave.shape[2:]),
            f32((fx_rows, 128)), f32((fx_rows, 128)), f32((fy_rows, 128)), f32((fy_rows, 128)),
        ),
        in_specs=stress_specs,
        out_specs=tuple(vmem_specs(6)),
        scratch_shapes=[scratch_for(fine), scratch_for(coarse)],
    )(*stress_args)
    fine_out, fine_mem, coarse_out, coarse_mem = pl.pallas_call(
        functools.partial(stress_kernel, blocks, False),
        out_shape=(f32(fine_wave.shape), f32(fine_memory.shape), f32(coarse_wave.shape), f32(coarse_memory.shape)),
        in_specs=stress_specs,
        out_specs=tuple(vmem_specs(4)),
        scratch_shapes=[scratch_for(fine), scratch_for(coarse)],
    )(*stress_args)

    fine_out, coarse_out = face_call(blocks, fine_out, coarse_out, fine_face, coarse_face, face_rims)
    return (fine_out, fine_mem, coarse_out, coarse_mem)


def solution(mesh):
    in_specs = (
        P(None, None, "gx", "gy"),
        P(None, None, "gx", "gy"),
        P(None, "gx", "gy"),
        P(None, "gx", "gy"),
        P(None, "gx", "gy"),
        P(None, None, "gx", "gy"),
        P(None, None, "gx", "gy"),
        P(None, "gx", "gy"),
        P(None, "gx", "gy"),
        P(),
        P(),
    )
    out_specs = (
        P(None, None, "gx", "gy"),
        P(None, None, "gx", "gy"),
        P(None, None, "gx", "gy"),
        P(None, None, "gx", "gy"),
    )
    return jax.shard_map(local, mesh=mesh, in_specs=in_specs, out_specs=out_specs, check_vma=False)
```

```python
import functools
import math

import jax
import jax.numpy as jnp
import numpy as np
from jax import lax
from jax.sharding import PartitionSpec as P

step_size = 0.1
penalty = 0.1 * 48.0 / 17.0
closure = [
    [-24.0 / 17.0, 59.0 / 34.0, -4.0 / 17.0, -3.0 / 34.0, 0.0, 0.0],
    [-0.5, 0.0, 0.5, 0.0, 0.0, 0.0],
    [4.0 / 43.0, -59.0 / 86.0, 0.0, 59.0 / 86.0, -4.0 / 43.0, 0.0],
    [3.0 / 98.0, 0.0, -59.0 / 98.0, 0.0, 32.0 / 49.0, -4.0 / 49.0],
]


def sbp_table(layers, spacing):
    return jnp.asarray(sbp_numpy(layers, spacing))


def sbp_numpy(layers, spacing):
    table = np.zeros((layers, layers))
    for line_at in range(4):
        for column in range(6):
            table[line_at, column] = closure[line_at][column]
            table[layers - 1 - line_at, layers - 1 - column] = -closure[line_at][column]
    for line_at in range(4, layers - 4):
        table[line_at, line_at - 2 : line_at + 3] = [
            1.0 / 12.0,
            -2.0 / 3.0,
            0.0,
            2.0 / 3.0,
            -1.0 / 12.0,
        ]
    return (table / spacing).astype(np.float32)


def shift_from(block, axis, offset):
    count = lax.axis_size(axis)
    pairs = [(i, (i + offset) % count) for i in range(count)]
    return lax.ppermute(block, axis, pairs)


def edge_flags():
    gx, gy = lax.axis_index("gx"), lax.axis_index("gy")
    nx, ny = lax.axis_size("gx"), lax.axis_size("gy")
    return jnp.stack([gx > 0, gx < nx - 1, gy > 0, gy < ny - 1]).astype(jnp.int32)


def valid_of(flags):
    return tuple(flags[k] != 0 for k in range(4))


def keep(ok, value):
    return jnp.where(ok, value, 0.0)


def packed_shift(blocks, axis, offset):
    sizes = [math.prod(b.shape) for b in blocks]
    joined = jnp.concatenate([b.reshape(-1) for b in blocks])
    moved = shift_from(joined, axis, offset)
    out, start = [], 0
    for b, size in zip(blocks, sizes):
        out.append(moved[start : start + size].reshape(b.shape))
        start += size
    return out


def exchange(blocks, width):
    x_lo = packed_shift([b[..., -width:, :] for b in blocks], "gx", 1)
    x_hi = packed_shift([b[..., :width, :] for b in blocks], "gx", -1)
    y_lo = packed_shift([b[..., -width:] for b in blocks], "gy", 1)
    y_hi = packed_shift([b[..., :width] for b in blocks], "gy", -1)
    return [(x_lo[i], x_hi[i], y_lo[i], y_hi[i]) for i in range(len(blocks))]


def central_diff(padded, along, spacing):
    length = padded.shape[along] - 4
    s = lambda o: lax.slice_in_dim(padded, o, o + length, axis=along)
    return (s(0) - 8.0 * s(1) + 8.0 * s(3) - s(4)) / (12.0 * spacing)


def diff_x(block, halo, spacing):
    x_lo, x_hi, _, _ = halo
    return central_diff(jnp.concatenate([x_lo, block, x_hi], axis=-2), block.ndim - 2, spacing)


def diff_y(block, halo, spacing):
    _, _, y_lo, y_hi = halo
    return central_diff(jnp.concatenate([y_lo, block, y_hi], axis=-1), block.ndim - 1, spacing)


def vertical_diff(fields, matrix):
    return jnp.einsum("kz,czxy->ckxy", matrix, fields, precision=lax.Precision.HIGHEST)


def lookup_table(grid_cell_index, values):
    result = jnp.zeros(grid_cell_index.shape, jnp.float32)
    for kind_at in range(values.shape[0]):
        result = jnp.where(grid_cell_index == kind_at, values[kind_at], result)
    return result


def velocity_step(wave, halo_x3, halo_y3, buoyancy, metric, matrix, spacing):
    sx = jnp.stack([wave[3], wave[6], wave[7]])
    sy = jnp.stack([wave[6], wave[4], wave[8]])
    slope_x = diff_x(sx, halo_x3, spacing)
    slope_y = diff_y(sy, halo_y3, spacing)
    slope_z = metric * vertical_diff(jnp.stack([wave[7], wave[8], wave[5]]), matrix)
    rate_x = slope_x[0] + slope_y[0] + slope_z[0]
    rate_y = slope_x[1] + slope_y[1] + slope_z[1]
    rate_z = slope_x[2] + slope_y[2] + slope_z[2]
    return wave[:3] + step_size * (buoyancy * jnp.stack([rate_x, rate_y, rate_z]))


def stress_step(wave, memory, velocity, halo, lame, shear, decay, strength, metric, matrix, spacing):
    slope_x = diff_x(velocity, halo, spacing)
    slope_y = diff_y(velocity, halo, spacing)
    slope_z = metric * vertical_diff(velocity, matrix)
    cell_volume = lame * (slope_x[0] + slope_y[1] + slope_z[2])
    rate = jnp.stack(
        [
            cell_volume + 2.0 * shear * slope_x[0],
            cell_volume + 2.0 * shear * slope_y[1],
            cell_volume + 2.0 * shear * slope_z[2],
            shear * (slope_y[0] + slope_x[1]),
            shear * (slope_z[0] + slope_x[2]),
            shear * (slope_z[1] + slope_y[2]),
        ]
    )
    memory_new = decay * memory + (1.0 - decay) * strength * rate
    stress = wave[3:] + step_size * (rate - memory_new)
    return stress, memory_new


def face_of(velocity, stress, depth):
    return jnp.stack(
        [
            velocity[0, depth],
            velocity[1, depth],
            velocity[2, depth],
            stress[4, depth],
            stress[5, depth],
            stress[2, depth],
        ]
    )


def pad_faces(faces):
    x_lo = packed_shift([f[:, -1:, :] for f in faces], "gx", 1)
    x_hi = packed_shift([f[:, :1, :] for f in faces], "gx", -1)
    faces = [jnp.concatenate([lo, f, hi], axis=1) for lo, f, hi in zip(x_lo, faces, x_hi)]
    y_lo = packed_shift([f[:, :, -1:] for f in faces], "gy", 1)
    y_hi = packed_shift([f[:, :, :1] for f in faces], "gy", -1)
    return [jnp.concatenate([lo, f, hi], axis=2) for lo, f, hi in zip(y_lo, faces, y_hi)]


def shifted(padded, offset, length, along):
    return lax.slice_in_dim(padded, offset, offset + length, axis=along)


def prolong_axis(padded, along):
    length = padded.shape[along] - 2
    left = shifted(padded, 0, length, along)
    middle = shifted(padded, 1, length, along)
    right = shifted(padded, 2, length, along)
    parts = jnp.stack(
        [(left + 2.0 * middle) / 3.0, middle, (2.0 * middle + right) / 3.0], axis=along + 1
    )
    shape = list(middle.shape)
    shape[along] = shape[along] * 3
    return parts.reshape(tuple(shape))


def split_three(padded, offset, length, along):
    part = shifted(padded, offset, 3 * length, along)
    return part.reshape(part.shape[:along] + (length, 3) + part.shape[along + 1 :])


def pick_part(parts, number, along):
    return lax.index_in_dim(parts, number, along + 1, keepdims=False)


def restrict_axis(padded, along):
    length = (padded.shape[along] - 2) // 3
    first = split_three(padded, 0, length, along)
    middle = split_three(padded, 1, length, along)
    last = split_three(padded, 2, length, along)
    return (
        pick_part(first, 0, along)
        + 2.0 * pick_part(middle, 0, along)
        + 3.0 * pick_part(middle, 1, along)
        + 2.0 * pick_part(middle, 2, along)
        + pick_part(last, 2, along)
    ) / 9.0


def assemble(velocity, stress, face, depth):
    replace = {0: face[0], 1: face[1], 2: face[2], 7: face[3], 8: face[4], 5: face[5]}
    fields = [velocity[0], velocity[1], velocity[2]] + [stress[k] for k in range(6)]
    rows = []
    for k, field in enumerate(fields):
        if k in replace:
            field = lax.dynamic_update_slice_in_dim(field, replace[k][None], depth, axis=0)
        rows.append(field)
    return jnp.stack(rows)


from jax.experimental import pallas as pl
from jax.experimental.pallas import tpu as pltpu


def sbp_rows(layers, spacing):
    table = sbp_numpy(layers, spacing)
    return [[(j, float(table[k, j])) for j in range(layers) if table[k, j] != 0.0] for k in range(layers)]


def pick(values_ref, row, index):
    result = jnp.zeros(index.shape, jnp.float32)
    for kind_at in range(values_ref.shape[1]):
        result = jnp.where(index == kind_at, values_ref[row, kind_at], result)
    return result


def fill_x(scratch, slot, lo, block, hi):
    width = lo.shape[-2]
    size = block.shape[-2]
    scratch[slot, :, 0:width, :] = lo
    scratch[slot, :, width : width + size, :] = block
    scratch[slot, :, width + size :, :] = hi


def slope_x(scratch, slot, z, size, spacing):
    s = lambda o: scratch[slot, z, o : o + size, :]
    return (s(0) - 8.0 * s(1) + 8.0 * s(3) - s(4)) / (12.0 * spacing)


def slope_y(f, lo, hi, spacing):
    n = f.shape[-1]
    lane = lax.broadcasted_iota(jnp.int32, f.shape, f.ndim - 1)
    m1 = jnp.where(lane == 0, lo[:, 1:2], pltpu.roll(f, 1, f.ndim - 1))
    m2 = jnp.where(lane == 0, lo[:, 0:1], jnp.where(lane == 1, lo[:, 1:2], pltpu.roll(f, 2, f.ndim - 1)))
    p1 = jnp.where(lane == n - 1, hi[:, 0:1], pltpu.roll(f, n - 1, f.ndim - 1))
    p2 = jnp.where(lane == n - 2, hi[:, 0:1], jnp.where(lane == n - 1, hi[:, 1:2], pltpu.roll(f, n - 2, f.ndim - 1)))
    return (m2 - 8.0 * m1 + 8.0 * p1 - p2) / (12.0 * spacing)


def slope_z(field_ref, index, row):
    total = None
    for j, weight in row:
        term = jnp.float32(weight) * field_ref[index, j]
        total = term if total is None else total + term
    return total


class Block:
    def __init__(self, shape, spacing, has_metric, x_base, y_base):
        self.layers, self.size, self.lanes = shape
        self.chunks = self.lanes // 128
        self.spacing = spacing
        self.has_metric = has_metric
        self.rows = sbp_rows(self.layers, spacing)
        self.x_base, self.y_base = x_base, y_base

    @property
    def x_rows(self):
        return 3 * self.layers * self.chunks * 2

    @property
    def y_rows(self):
        return self.layers * self.size


def plan_blocks(fine_shape, coarse_shape):
    fine = Block(fine_shape, 1.0, True, 0, 0)
    coarse = Block(coarse_shape, 3.0, False, fine.x_rows, fine.y_rows)
    fine.fx_base, fine.fy_base = 0, 0
    coarse.fx_base, coarse.fy_base = 6 * fine.chunks, fine.size
    corner_base = fine.size + coarse.size
    fine.corner_rows = (corner_base, corner_base + 1)
    coarse.corner_rows = (corner_base + 2, corner_base + 3)
    return fine, coarse, fine.x_rows + coarse.x_rows, fine.y_rows + coarse.y_rows


def round8(n):
    return -(-n // 8) * 8


def write_rims(b, src, fields, x_prev, x_next, y_prev, y_next):
    size, lanes = b.size, b.lanes
    for c, field in enumerate(fields):
        for z in range(b.layers):
            lo = src[field, z, 0:2, :]
            hi = src[field, z, size - 2 : size, :]
            for j in range(b.chunks):
                row = b.x_base + ((c * b.layers + z) * b.chunks + j) * 2
                x_prev[row : row + 2, :] = lo[:, j * 128 : (j + 1) * 128]
                x_next[row : row + 2, :] = hi[:, j * 128 : (j + 1) * 128]
    lane = lax.broadcasted_iota(jnp.int32, (size, 128), 1)
    for z in range(b.layers):
        acc_lo = jnp.zeros((size, 128), jnp.float32)
        acc_hi = jnp.zeros((size, 128), jnp.float32)
        for c, field in enumerate(fields):
            v = src[field, z]
            rl = v if c == 0 else pltpu.roll(v, 2 * c, 1)
            rh = pltpu.roll(v, (2 * c + 2) % lanes, 1)
            keep = (lane >= 2 * c) & (lane < 2 * c + 2)
            acc_lo = jnp.where(keep, rl[:, 0:128], acc_lo)
            acc_hi = jnp.where(keep, rh[:, 0:128], acc_hi)
        row = b.y_base + z * size
        y_prev[row : row + size, :] = acc_lo
        y_next[row : row + size, :] = acc_hi


def read_x_halo(b, buf, c, z):
    parts = [buf[pl.ds(b.x_base + ((c * b.layers + z) * b.chunks + j) * 2, 2), :] for j in range(b.chunks)]
    return parts[0] if len(parts) == 1 else jnp.concatenate(parts, axis=1)


def read_y_halo(b, buf, c, z, ok):
    row = b.y_base + z * b.size
    return keep(ok, buf[pl.ds(row, b.size), pl.ds(2 * c, 1)]), keep(ok, buf[pl.ds(row, b.size), pl.ds(2 * c + 1, 1)])


def fill_x2(b, scratch, slot, src, field, lo_buf, hi_buf, valid, layers=None):
    size = b.size
    if layers is None:
        scratch[slot, :, 2 : 2 + size, :] = src[field]
        layers = range(b.layers)
    else:
        for z in layers:
            scratch[slot, z, 2 : 2 + size, :] = src[field, z]
    for z in layers:
        scratch[slot, z, 0:2, :] = keep(valid[0], read_x_halo(b, lo_buf, slot, z))
        scratch[slot, z, 2 + size :, :] = keep(valid[1], read_x_halo(b, hi_buf, slot, z))


def slope_y2(f, lo, hi, spacing):
    n = f.shape[-1]
    lane = lax.broadcasted_iota(jnp.int32, f.shape, 1)
    m1 = jnp.where(lane == 0, lo[1], pltpu.roll(f, 1, 1))
    m2 = jnp.where(lane == 0, lo[0], jnp.where(lane == 1, lo[1], pltpu.roll(f, 2, 1)))
    p1 = jnp.where(lane == n - 1, hi[0], pltpu.roll(f, n - 1, 1))
    p2 = jnp.where(lane == n - 2, hi[0], jnp.where(lane == n - 1, hi[1], pltpu.roll(f, n - 2, 1)))
    return (m2 - 8.0 * m1 + 8.0 * p1 - p2) / (12.0 * spacing)


STRESS_X = (3, 6, 7)
STRESS_Y = (6, 4, 8)
VELOCITY = (0, 1, 2)


def pack_kernel(blocks, fw, cw, x_prev, x_next, y_prev, y_next):
    for b, w in zip(blocks, (fw, cw)):
        write_rims_split(b, w, x_prev, x_next, y_prev, y_next)


def write_rims_split(b, w, x_prev, x_next, y_prev, y_next):
    size, lanes = b.size, b.lanes
    for c, field in enumerate(STRESS_X):
        for z in range(b.layers):
            lo = w[field, z, 0:2, :]
            hi = w[field, z, size - 2 : size, :]
            for j in range(b.chunks):
                row = b.x_base + ((c * b.layers + z) * b.chunks + j) * 2
                x_prev[row : row + 2, :] = lo[:, j * 128 : (j + 1) * 128]
                x_next[row : row + 2, :] = hi[:, j * 128 : (j + 1) * 128]
    lane = lax.broadcasted_iota(jnp.int32, (size, 128), 1)
    for z in range(b.layers):
        acc_lo = jnp.zeros((size, 128), jnp.float32)
        acc_hi = jnp.zeros((size, 128), jnp.float32)
        for c, field in enumerate(STRESS_Y):
            v = w[field, z]
            rl = v if c == 0 else pltpu.roll(v, 2 * c, 1)
            rh = pltpu.roll(v, (2 * c + 2) % lanes, 1)
            keep = (lane >= 2 * c) & (lane < 2 * c + 2)
            acc_lo = jnp.where(keep, rl[:, 0:128], acc_lo)
            acc_hi = jnp.where(keep, rh[:, 0:128], acc_hi)
        row = b.y_base + z * size
        y_prev[row : row + size, :] = acc_lo
        y_next[row : row + size, :] = acc_hi


def velocity_block(b, w, mat, metric, table, out, sx, hx_lo, hx_hi, hy_lo, hy_hi, valid):
    for slot, field in enumerate(STRESS_X):
        fill_x2(b, sx, slot, w, field, hx_lo, hx_hi, valid)
    for z in range(b.layers):
        dx = [slope_x(sx, slot, z, b.size, b.spacing) for slot in range(3)]
        dy = [
            slope_y2(w[field, z], read_y_halo(b, hy_lo, slot, z, valid[2]), read_y_halo(b, hy_hi, slot, z, valid[3]),
                     b.spacing)
            for slot, field in enumerate(STRESS_Y)
        ]
        dz = [slope_z(w, field, b.rows[z]) for field in (7, 8, 5)]
        if metric is not None:
            m = metric[z]
            dz = [m * d for d in dz]
        buoy = pick(table, 0, mat[z])
        for k in range(3):
            out[k, z] = w[k, z] + step_size * (buoy * (dx[k] + dy[k] + dz[k]))


def velocity_kernel(blocks, fw, cw, hx_lo, hx_hi, hy_lo, hy_hi, fmat, fmetric, cmat, table, flags,
                    fvel, cvel, vx_prev, vx_next, vy_prev, vy_next, sx_f, sx_c):
    fine, coarse = blocks
    valid = valid_of(flags)
    velocity_block(fine, fw, fmat, fmetric, table, fvel, sx_f, hx_lo, hx_hi, hy_lo, hy_hi, valid)
    velocity_block(coarse, cw, cmat, None, table, cvel, sx_c, hx_lo, hx_hi, hy_lo, hy_hi, valid)
    write_rims(fine, fvel, VELOCITY, vx_prev, vx_next, vy_prev, vy_next)
    write_rims(coarse, cvel, VELOCITY, vx_prev, vx_next, vy_prev, vy_next)


def stress_block(b, depth, face_only, w, mem, vel, mat, mech, metric, mtab, atab, outputs, sx,
                 hx_lo, hx_hi, hy_lo, hy_hi, valid):
    for slot in range(3):
        fill_x2(b, sx, slot, vel, slot, hx_lo, hx_hi, valid, [depth] if face_only else None)
    for z in ([depth] if face_only else range(b.layers)):
        dx = [slope_x(sx, slot, z, b.size, b.spacing) for slot in range(3)]
        dy = [
            slope_y2(vel[slot, z], read_y_halo(b, hy_lo, slot, z, valid[2]), read_y_halo(b, hy_hi, slot, z, valid[3]),
                     b.spacing)
            for slot in range(3)
        ]
        dz = [slope_z(vel, slot, b.rows[z]) for slot in range(3)]
        if metric is not None:
            m = metric[z]
            dz = [m * d for d in dz]
        kind, mechanism = mat[z], mech[z]
        lame, shear = pick(mtab, 1, kind), pick(mtab, 2, kind)
        decay, strength = pick(atab, 0, mechanism), pick(atab, 1, mechanism)
        cell_volume = lame * (dx[0] + dy[1] + dz[2])
        rate = [
            cell_volume + 2.0 * shear * dx[0],
            cell_volume + 2.0 * shear * dy[1],
            cell_volume + 2.0 * shear * dz[2],
            shear * (dy[0] + dx[1]),
            shear * (dz[0] + dx[2]),
            shear * (dz[1] + dy[2]),
        ]
        values = [vel[k, z] for k in range(3)]
        for k in range(6):
            memory_new = decay * mem[k, z] + (1.0 - decay) * strength * rate[k]
            stress = w[3 + k, z] + step_size * (rate[k] - memory_new)
            values.append(stress)
            if not face_only:
                outputs[1][k, z] = memory_new
        if face_only:
            planes = [values[k] for k in (0, 1, 2, 7, 8, 5)]
            for i, v in enumerate(planes):
                outputs[0][i] = v
            write_face_rims(b, planes, *outputs[1])
        else:
            for k in range(9):
                outputs[0][k, z] = values[k]


def write_face_rims(b, planes, x_prev, x_next, y_prev, y_next):
    size, lanes = b.size, b.lanes
    for i, v in enumerate(planes):
        for j in range(b.chunks):
            row = b.fx_base + i * b.chunks + j
            x_prev[row : row + 1, :] = v[0:1, j * 128 : (j + 1) * 128]
            x_next[row : row + 1, :] = v[size - 1 : size, j * 128 : (j + 1) * 128]
    lane = lax.broadcasted_iota(jnp.int32, (size, 128), 1)
    acc_lo = jnp.zeros((size, 128), jnp.float32)
    acc_hi = jnp.zeros((size, 128), jnp.float32)
    for i, v in enumerate(planes):
        rl = v if i == 0 else pltpu.roll(v, i, 1)
        rh = pltpu.roll(v, (i + 1) % lanes, 1)
        acc_lo = jnp.where(lane == i, rl[:, 0:128], acc_lo)
        acc_hi = jnp.where(lane == i, rh[:, 0:128], acc_hi)
    y_prev[b.fy_base : b.fy_base + size, :] = acc_lo
    y_next[b.fy_base : b.fy_base + size, :] = acc_hi


def stress_kernel(blocks, face_only, fw, fmem, fvel, cw, cmem, cvel, hx_lo, hx_hi, hy_lo, hy_hi,
                  fmat, fmech, fmetric, cmat, cmech, mtab, atab, flags, *outs):
    fine, coarse = blocks
    valid = valid_of(flags)
    if face_only:
        fface, cface, rx_prev, rx_next, ry_prev, ry_next, sx_f, sx_c = outs
        rims = (rx_prev, rx_next, ry_prev, ry_next)
        fine_outputs, coarse_outputs = (fface, rims), (cface, rims)
    else:
        fout, fmem_out, cout, cmem_out, sx_f, sx_c = outs
        fine_outputs, coarse_outputs = (fout, fmem_out), (cout, cmem_out)
    stress_block(fine, fine.layers - 1, face_only, fw, fmem, fvel, fmat, fmech, fmetric, mtab, atab, fine_outputs,
                 sx_f, hx_lo, hx_hi, hy_lo, hy_hi, valid)
    stress_block(coarse, 0, face_only, cw, cmem, cvel, cmat, cmech, None, mtab, atab, coarse_outputs,
                 sx_c, hx_lo, hx_hi, hy_lo, hy_hi, valid)


def vmem_specs(count):
    return [pl.BlockSpec(memory_space=pltpu.VMEM)] * count


def f32(shape):
    return jax.ShapeDtypeStruct(shape, jnp.float32)


def halo_shapes(x_rows, y_rows):
    return (f32((x_rows, 128)), f32((x_rows, 128)), f32((y_rows, 128)), f32((y_rows, 128)))


def scratch_for(b):
    return pltpu.VMEM((3, b.layers, b.size + 4, b.lanes), jnp.float32)


def receive(buffers):
    x_prev, x_next, y_prev, y_next = buffers
    y_lo = shift_from(y_next, "gy", 1)
    y_hi = shift_from(y_prev, "gy", -1)
    x_lo = shift_from(x_next, "gx", 1)
    x_hi = shift_from(x_prev, "gx", -1)
    return x_lo, x_hi, y_lo, y_hi


def put_face(out, face, depth):
    out = lax.dynamic_update_slice(out, face[0:3][:, None], (0, depth, 0, 0))
    out = lax.dynamic_update_slice(out, face[5:6][:, None], (5, depth, 0, 0))
    out = lax.dynamic_update_slice(out, face[3:5][:, None], (7, depth, 0, 0))
    return out


def prolong_y_matrix(coarse_lanes):
    m = np.zeros((coarse_lanes, 3 * coarse_lanes), np.float32)
    for d in range(coarse_lanes):
        m[d, 3 * d] = 2.0 / 3.0
        m[d, 3 * d + 1] = 1.0
        m[d, 3 * d + 2] = 2.0 / 3.0
        if d >= 1:
            m[d - 1, 3 * d] = 1.0 / 3.0
        if d + 1 < coarse_lanes:
            m[d + 1, 3 * d + 2] = 1.0 / 3.0
    return m


def restrict_y_matrix(coarse_lanes):
    m = np.zeros((3 * coarse_lanes, coarse_lanes), np.float32)
    for c in range(coarse_lanes):
        for offset, weight in ((-1, 1.0), (0, 2.0), (1, 3.0), (2, 2.0), (3, 1.0)):
            f = 3 * c + offset
            if 0 <= f < 3 * coarse_lanes:
                m[f, c] = weight / 9.0
    return m


def padded_rows(b, face, hx_lo, hx_hi, hy_lo, hy_hi, valid, i):
    size = b.size

    def x_row(buf):
        parts = [buf[pl.ds(b.fx_base + i * b.chunks + j, 1), :] for j in range(b.chunks)]
        return parts[0] if len(parts) == 1 else jnp.concatenate(parts, axis=1)

    def lane_of(buf, row, ok):
        return keep(ok, buf[pl.ds(row, 1), pl.ds(i, 1)])

    x_lo_ok, x_hi_ok, y_lo_ok, y_hi_ok = valid
    lo_row, hi_row = b.corner_rows
    rows = [(keep(x_lo_ok, x_row(hx_lo)), lane_of(hy_lo, lo_row, x_lo_ok & y_lo_ok),
             lane_of(hy_hi, lo_row, x_lo_ok & y_hi_ok))]
    for x in range(size):
        rows.append((face[i, pl.ds(x, 1), :], lane_of(hy_lo, b.fy_base + x, y_lo_ok),
                     lane_of(hy_hi, b.fy_base + x, y_hi_ok)))
    rows.append((keep(x_hi_ok, x_row(hx_hi)), lane_of(hy_lo, hi_row, x_hi_ok & y_lo_ok),
                 lane_of(hy_hi, hi_row, x_hi_ok & y_hi_ok)))
    return rows


def combine(terms):
    out = []
    for part in range(3):
        total = None
        for weight, row in terms:
            v = row[part] if weight == 1.0 else weight * row[part]
            total = v if total is None else total + v
        out.append(total)
    return out


def face_kernel(blocks, fine_depth, fout_in, cout_in, fface, cface, hx_lo, hx_hi, hy_lo, hy_hi,
                py, ry, flags, fout, cout, fnew, cnew, stage_p, stage_r, sems):
    fine, coarse = blocks
    halos = (hx_lo, hx_hi, hy_lo, hy_hi, valid_of(flags))
    lane_f = lax.broadcasted_iota(jnp.int32, (1, fine.lanes), 1)
    p_lo, p_hi = [], []
    for i in range(6):
        rows = padded_rows(coarse, cface, *halos, i)
        for c in range(coarse.size):
            left, middle, right = rows[c], rows[c + 1], rows[c + 2]
            parts = [
                [(1.0, left), (2.0, middle)],
                [(1.0, middle)],
                [(2.0, middle), (1.0, right)],
            ]
            for a, terms in enumerate(parts):
                interior, lo, hi = combine(terms)
                if a != 1:
                    interior, lo, hi = interior / 3.0, lo / 3.0, hi / 3.0
                r = i * fine.size + 3 * c + a
                stage_p[pl.ds(r, 1), :] = interior
                p_lo.append(lo)
                p_hi.append(hi)
    prolonged = jnp.dot(stage_p[...], py[...], precision=lax.Precision.HIGHEST, preferred_element_type=jnp.float32)
    for i in range(6):
        for x in range(fine.size):
            r = i * fine.size + x
            value = prolonged[r : r + 1, :]
            value = value + jnp.where(lane_f == 0, p_lo[r] / 3.0, 0.0) + jnp.where(lane_f == fine.lanes - 1, p_hi[r] / 3.0, 0.0)
            own = fface[i, pl.ds(x, 1), :]
            fnew[i, 0, pl.ds(x, 1), :] = own - penalty * (own - value)
    lane_c = lax.broadcasted_iota(jnp.int32, (1, coarse.lanes), 1)
    r_lo, r_hi = [], []
    for i in range(6):
        rows = padded_rows(fine, fface, *halos, i)
        for c in range(coarse.size):
            terms = [(1.0, rows[3 * c]), (2.0, rows[3 * c + 1]), (3.0, rows[3 * c + 2]), (2.0, rows[3 * c + 3]),
                     (1.0, rows[3 * c + 4])]
            interior, lo, hi = combine(terms)
            r = i * coarse.size + c
            stage_r[pl.ds(r, 1), :] = interior / 9.0
            r_lo.append(lo / 9.0)
            r_hi.append(hi / 9.0)
    restricted = jnp.dot(stage_r[...], ry[...], precision=lax.Precision.HIGHEST, preferred_element_type=jnp.float32)
    for i in range(6):
        for c in range(coarse.size):
            r = i * coarse.size + c
            value = restricted[r : r + 1, :]
            value = value + jnp.where(lane_c == 0, r_lo[r] / 9.0, 0.0) + jnp.where(lane_c == coarse.lanes - 1, r_hi[r] / 9.0, 0.0)
            own = cface[i, pl.ds(c, 1), :]
            cnew[i, 0, pl.ds(c, 1), :] = own - penalty * (own - value)
    copies = []
    for n, (src, dst, depth) in enumerate(((fnew, fout, fine_depth), (cnew, cout, 0))):
        for k, (first, count, field) in enumerate(((0, 3, 0), (5, 1, 5), (3, 2, 7))):
            copy = pltpu.make_async_copy(
                src.at[pl.ds(first, count)], dst.at[pl.ds(field, count), pl.ds(depth, 1)], sems.at[3 * n + k]
            )
            copy.start()
            copies.append(copy)
    for copy in copies:
        copy.wait()


def diag_from(block, dx, dy):
    nx, ny = lax.axis_size("gx"), lax.axis_size("gy")
    pairs = []
    for i in range(nx):
        for j in range(ny):
            if 0 <= i + dx < nx and 0 <= j + dy < ny:
                pairs.append((i * ny + j, (i + dx) * ny + (j + dy)))
    return lax.ppermute(block, ("gx", "gy"), pairs)


def row_ends(buf, blocks, at_end):
    out = []
    for b in blocks:
        chunk = b.chunks - 1 if at_end else 0
        first = b.fx_base + chunk
        lane = 127 if at_end else 0
        out.append(lax.slice(buf, (first, lane), (first + 5 * b.chunks + 1, lane + 1), (b.chunks, 1))[:, 0])
    return jnp.stack(out)


def with_corners(y_rim, x_lo, x_hi, blocks, at_end):
    lo, hi = row_ends(x_lo, blocks, at_end), row_ends(x_hi, blocks, at_end)
    extra = jnp.stack([lo, hi], axis=1).reshape(2 * len(blocks), 6)
    extra = jnp.pad(extra, ((0, 0), (0, 128 - 6)))
    joined = jnp.concatenate([y_rim, extra])
    return jnp.pad(joined, ((0, round8(joined.shape[0]) - joined.shape[0]), (0, 0)))


def face_call(blocks, fine_out, coarse_out, fine_face, coarse_face, rims):
    fine, coarse = blocks
    x_prev, x_next, y_prev, y_next = rims
    x_lo = shift_from(x_next, "gx", 1)
    x_hi = shift_from(x_prev, "gx", -1)
    y_lo = shift_from(with_corners(y_next, x_lo, x_hi, blocks, True), "gy", 1)
    y_hi = shift_from(with_corners(y_prev, x_lo, x_hi, blocks, False), "gy", -1)
    received = (x_lo, x_hi, y_lo, y_hi)
    py = jnp.asarray(prolong_y_matrix(coarse.lanes))
    ry = jnp.asarray(restrict_y_matrix(coarse.lanes))
    anyspace = pl.BlockSpec(memory_space=pl.ANY)
    return pl.pallas_call(
        functools.partial(face_kernel, blocks, fine.layers - 1),
        out_shape=(f32(fine_out.shape), f32(coarse_out.shape)),
        in_specs=[anyspace, anyspace] + vmem_specs(8) + [pl.BlockSpec(memory_space=pltpu.SMEM)],
        out_specs=(anyspace, anyspace),
        input_output_aliases={0: 0, 1: 1},
        scratch_shapes=[
            pltpu.VMEM((6, 1, fine.size, fine.lanes), jnp.float32),
            pltpu.VMEM((6, 1, coarse.size, coarse.lanes), jnp.float32),
            pltpu.VMEM((round8(6 * fine.size), coarse.lanes), jnp.float32),
            pltpu.VMEM((round8(6 * coarse.size), fine.lanes), jnp.float32),
            pltpu.SemaphoreType.DMA((6,)),
        ],
    )(fine_out, coarse_out, fine_face, coarse_face, *received, py, ry, edge_flags())


def local(
    fine_wave,
    fine_memory,
    fine_material,
    fine_mechanism,
    fine_metric,
    coarse_wave,
    coarse_memory,
    coarse_material,
    coarse_mechanism,
    material_table,
    attenuation_table,
):
    fine, coarse, x_rows, y_rows = plan_blocks(fine_wave.shape[1:], coarse_wave.shape[1:])
    blocks = (fine, coarse)
    smem = pl.BlockSpec(memory_space=pltpu.SMEM)
    flags = edge_flags()

    rims = pl.pallas_call(
        functools.partial(pack_kernel, blocks),
        out_shape=halo_shapes(x_rows, y_rows),
        in_specs=vmem_specs(2),
        out_specs=tuple(vmem_specs(4)),
    )(fine_wave, coarse_wave)
    halos = receive(rims)

    fine_velocity, coarse_velocity, *vrims = pl.pallas_call(
        functools.partial(velocity_kernel, blocks),
        out_shape=(f32((3,) + fine_wave.shape[1:]), f32((3,) + coarse_wave.shape[1:])) + halo_shapes(x_rows, y_rows),
        in_specs=vmem_specs(9) + [smem, smem],
        out_specs=tuple(vmem_specs(6)),
        scratch_shapes=[scratch_for(fine), scratch_for(coarse)],
    )(fine_wave, coarse_wave, *halos, fine_material, fine_metric, coarse_material, material_table, flags)

    vhalos = receive(vrims)
    fx_rows = 6 * (fine.chunks + coarse.chunks)
    fy_rows = round8(fine.size + coarse.size)
    stress_args = (fine_wave, fine_memory, fine_velocity, coarse_wave, coarse_memory, coarse_velocity, *vhalos,
                   fine_material, fine_mechanism, fine_metric, coarse_material, coarse_mechanism, material_table,
                   attenuation_table, flags)
    stress_specs = vmem_specs(15) + [smem, smem, smem]
    fine_face, coarse_face, *face_rims = pl.pallas_call(
        functools.partial(stress_kernel, blocks, True),
        out_shape=(
            f32((6,) + fine_wave.shape[2:]), f32((6,) + coarse_wave.shape[2:]),
            f32((fx_rows, 128)), f32((fx_rows, 128)), f32((fy_rows, 128)), f32((fy_rows, 128)),
        ),
        in_specs=stress_specs,
        out_specs=tuple(vmem_specs(6)),
        scratch_shapes=[scratch_for(fine), scratch_for(coarse)],
    )(*stress_args)
    fine_out, fine_mem, coarse_out, coarse_mem = pl.pallas_call(
        functools.partial(stress_kernel, blocks, False),
        out_shape=(f32(fine_wave.shape), f32(fine_memory.shape), f32(coarse_wave.shape), f32(coarse_memory.shape)),
        in_specs=stress_specs,
        out_specs=tuple(vmem_specs(4)),
        scratch_shapes=[scratch_for(fine), scratch_for(coarse)],
    )(*stress_args)

    fine_out, coarse_out = face_call(blocks, fine_out, coarse_out, fine_face, coarse_face, face_rims)
    return (fine_out, fine_mem, coarse_out, coarse_mem)


def solution(mesh):
    in_specs = (
        P(None, None, "gx", "gy"),
        P(None, None, "gx", "gy"),
        P(None, "gx", "gy"),
        P(None, "gx", "gy"),
        P(None, "gx", "gy"),
        P(None, None, "gx", "gy"),
        P(None, None, "gx", "gy"),
        P(None, "gx", "gy"),
        P(None, "gx", "gy"),
        P(),
        P(),
    )
    out_specs = (
        P(None, None, "gx", "gy"),
        P(None, None, "gx", "gy"),
        P(None, None, "gx", "gy"),
        P(None, None, "gx", "gy"),
    )
    return jax.shard_map(local, mesh=mesh, in_specs=in_specs, out_specs=out_specs, check_vma=False)
```

```python
import functools
import math

import jax
import jax.numpy as jnp
import numpy as np
from jax import lax
from jax.sharding import PartitionSpec as P

step_size = 0.1
penalty = 0.1 * 48.0 / 17.0
closure = [
    [-24.0 / 17.0, 59.0 / 34.0, -4.0 / 17.0, -3.0 / 34.0, 0.0, 0.0],
    [-0.5, 0.0, 0.5, 0.0, 0.0, 0.0],
    [4.0 / 43.0, -59.0 / 86.0, 0.0, 59.0 / 86.0, -4.0 / 43.0, 0.0],
    [3.0 / 98.0, 0.0, -59.0 / 98.0, 0.0, 32.0 / 49.0, -4.0 / 49.0],
]


def sbp_table(layers, spacing):
    return jnp.asarray(sbp_numpy(layers, spacing))


def sbp_numpy(layers, spacing):
    table = np.zeros((layers, layers))
    for line_at in range(4):
        for column in range(6):
            table[line_at, column] = closure[line_at][column]
            table[layers - 1 - line_at, layers - 1 - column] = -closure[line_at][column]
    for line_at in range(4, layers - 4):
        table[line_at, line_at - 2 : line_at + 3] = [
            1.0 / 12.0,
            -2.0 / 3.0,
            0.0,
            2.0 / 3.0,
            -1.0 / 12.0,
        ]
    return (table / spacing).astype(np.float32)


def shift_from(block, axis, offset):
    count = lax.axis_size(axis)
    pairs = [(i, (i + offset) % count) for i in range(count)]
    return lax.ppermute(block, axis, pairs)


def edge_flags():
    gx, gy = lax.axis_index("gx"), lax.axis_index("gy")
    nx, ny = lax.axis_size("gx"), lax.axis_size("gy")
    return jnp.stack([gx > 0, gx < nx - 1, gy > 0, gy < ny - 1]).astype(jnp.int32)


def valid_of(flags):
    return tuple(flags[k] != 0 for k in range(4))


def keep(ok, value):
    return jnp.where(ok, value, 0.0)


def packed_shift(blocks, axis, offset):
    sizes = [math.prod(b.shape) for b in blocks]
    joined = jnp.concatenate([b.reshape(-1) for b in blocks])
    moved = shift_from(joined, axis, offset)
    out, start = [], 0
    for b, size in zip(blocks, sizes):
        out.append(moved[start : start + size].reshape(b.shape))
        start += size
    return out


def exchange(blocks, width):
    x_lo = packed_shift([b[..., -width:, :] for b in blocks], "gx", 1)
    x_hi = packed_shift([b[..., :width, :] for b in blocks], "gx", -1)
    y_lo = packed_shift([b[..., -width:] for b in blocks], "gy", 1)
    y_hi = packed_shift([b[..., :width] for b in blocks], "gy", -1)
    return [(x_lo[i], x_hi[i], y_lo[i], y_hi[i]) for i in range(len(blocks))]


def central_diff(padded, along, spacing):
    length = padded.shape[along] - 4
    s = lambda o: lax.slice_in_dim(padded, o, o + length, axis=along)
    return (s(0) - 8.0 * s(1) + 8.0 * s(3) - s(4)) / (12.0 * spacing)


def diff_x(block, halo, spacing):
    x_lo, x_hi, _, _ = halo
    return central_diff(jnp.concatenate([x_lo, block, x_hi], axis=-2), block.ndim - 2, spacing)


def diff_y(block, halo, spacing):
    _, _, y_lo, y_hi = halo
    return central_diff(jnp.concatenate([y_lo, block, y_hi], axis=-1), block.ndim - 1, spacing)


def vertical_diff(fields, matrix):
    return jnp.einsum("kz,czxy->ckxy", matrix, fields, precision=lax.Precision.HIGHEST)


def lookup_table(grid_cell_index, values):
    result = jnp.zeros(grid_cell_index.shape, jnp.float32)
    for kind_at in range(values.shape[0]):
        result = jnp.where(grid_cell_index == kind_at, values[kind_at], result)
    return result


def velocity_step(wave, halo_x3, halo_y3, buoyancy, metric, matrix, spacing):
    sx = jnp.stack([wave[3], wave[6], wave[7]])
    sy = jnp.stack([wave[6], wave[4], wave[8]])
    slope_x = diff_x(sx, halo_x3, spacing)
    slope_y = diff_y(sy, halo_y3, spacing)
    slope_z = metric * vertical_diff(jnp.stack([wave[7], wave[8], wave[5]]), matrix)
    rate_x = slope_x[0] + slope_y[0] + slope_z[0]
    rate_y = slope_x[1] + slope_y[1] + slope_z[1]
    rate_z = slope_x[2] + slope_y[2] + slope_z[2]
    return wave[:3] + step_size * (buoyancy * jnp.stack([rate_x, rate_y, rate_z]))


def stress_step(wave, memory, velocity, halo, lame, shear, decay, strength, metric, matrix, spacing):
    slope_x = diff_x(velocity, halo, spacing)
    slope_y = diff_y(velocity, halo, spacing)
    slope_z = metric * vertical_diff(velocity, matrix)
    cell_volume = lame * (slope_x[0] + slope_y[1] + slope_z[2])
    rate = jnp.stack(
        [
            cell_volume + 2.0 * shear * slope_x[0],
            cell_volume + 2.0 * shear * slope_y[1],
            cell_volume + 2.0 * shear * slope_z[2],
            shear * (slope_y[0] + slope_x[1]),
            shear * (slope_z[0] + slope_x[2]),
            shear * (slope_z[1] + slope_y[2]),
        ]
    )
    memory_new = decay * memory + (1.0 - decay) * strength * rate
    stress = wave[3:] + step_size * (rate - memory_new)
    return stress, memory_new


def face_of(velocity, stress, depth):
    return jnp.stack(
        [
            velocity[0, depth],
            velocity[1, depth],
            velocity[2, depth],
            stress[4, depth],
            stress[5, depth],
            stress[2, depth],
        ]
    )


def pad_faces(faces):
    x_lo = packed_shift([f[:, -1:, :] for f in faces], "gx", 1)
    x_hi = packed_shift([f[:, :1, :] for f in faces], "gx", -1)
    faces = [jnp.concatenate([lo, f, hi], axis=1) for lo, f, hi in zip(x_lo, faces, x_hi)]
    y_lo = packed_shift([f[:, :, -1:] for f in faces], "gy", 1)
    y_hi = packed_shift([f[:, :, :1] for f in faces], "gy", -1)
    return [jnp.concatenate([lo, f, hi], axis=2) for lo, f, hi in zip(y_lo, faces, y_hi)]


def shifted(padded, offset, length, along):
    return lax.slice_in_dim(padded, offset, offset + length, axis=along)


def prolong_axis(padded, along):
    length = padded.shape[along] - 2
    left = shifted(padded, 0, length, along)
    middle = shifted(padded, 1, length, along)
    right = shifted(padded, 2, length, along)
    parts = jnp.stack(
        [(left + 2.0 * middle) / 3.0, middle, (2.0 * middle + right) / 3.0], axis=along + 1
    )
    shape = list(middle.shape)
    shape[along] = shape[along] * 3
    return parts.reshape(tuple(shape))


def split_three(padded, offset, length, along):
    part = shifted(padded, offset, 3 * length, along)
    return part.reshape(part.shape[:along] + (length, 3) + part.shape[along + 1 :])


def pick_part(parts, number, along):
    return lax.index_in_dim(parts, number, along + 1, keepdims=False)


def restrict_axis(padded, along):
    length = (padded.shape[along] - 2) // 3
    first = split_three(padded, 0, length, along)
    middle = split_three(padded, 1, length, along)
    last = split_three(padded, 2, length, along)
    return (
        pick_part(first, 0, along)
        + 2.0 * pick_part(middle, 0, along)
        + 3.0 * pick_part(middle, 1, along)
        + 2.0 * pick_part(middle, 2, along)
        + pick_part(last, 2, along)
    ) / 9.0


def assemble(velocity, stress, face, depth):
    replace = {0: face[0], 1: face[1], 2: face[2], 7: face[3], 8: face[4], 5: face[5]}
    fields = [velocity[0], velocity[1], velocity[2]] + [stress[k] for k in range(6)]
    rows = []
    for k, field in enumerate(fields):
        if k in replace:
            field = lax.dynamic_update_slice_in_dim(field, replace[k][None], depth, axis=0)
        rows.append(field)
    return jnp.stack(rows)


from jax.experimental import pallas as pl
from jax.experimental.pallas import tpu as pltpu


def sbp_rows(layers, spacing):
    table = sbp_numpy(layers, spacing)
    return [[(j, float(table[k, j])) for j in range(layers) if table[k, j] != 0.0] for k in range(layers)]


def pick(values_ref, row, index):
    result = jnp.zeros(index.shape, jnp.float32)
    for kind_at in range(values_ref.shape[1]):
        result = jnp.where(index == kind_at, values_ref[row, kind_at], result)
    return result


def fill_x(scratch, slot, lo, block, hi):
    width = lo.shape[-2]
    size = block.shape[-2]
    scratch[slot, :, 0:width, :] = lo
    scratch[slot, :, width : width + size, :] = block
    scratch[slot, :, width + size :, :] = hi


def slope_x(scratch, slot, z, size, spacing):
    s = lambda o: scratch[slot, z, o : o + size, :]
    return (s(0) - 8.0 * s(1) + 8.0 * s(3) - s(4)) / (12.0 * spacing)


def slope_y(f, lo, hi, spacing):
    n = f.shape[-1]
    lane = lax.broadcasted_iota(jnp.int32, f.shape, f.ndim - 1)
    m1 = jnp.where(lane == 0, lo[:, 1:2], pltpu.roll(f, 1, f.ndim - 1))
    m2 = jnp.where(lane == 0, lo[:, 0:1], jnp.where(lane == 1, lo[:, 1:2], pltpu.roll(f, 2, f.ndim - 1)))
    p1 = jnp.where(lane == n - 1, hi[:, 0:1], pltpu.roll(f, n - 1, f.ndim - 1))
    p2 = jnp.where(lane == n - 2, hi[:, 0:1], jnp.where(lane == n - 1, hi[:, 1:2], pltpu.roll(f, n - 2, f.ndim - 1)))
    return (m2 - 8.0 * m1 + 8.0 * p1 - p2) / (12.0 * spacing)


def slope_z(field_ref, index, row):
    total = None
    for j, weight in row:
        term = jnp.float32(weight) * field_ref[index, j]
        total = term if total is None else total + term
    return total


class Block:
    def __init__(self, shape, spacing, has_metric, x_base, y_base):
        self.layers, self.size, self.lanes = shape
        self.chunks = self.lanes // 128
        self.spacing = spacing
        self.has_metric = has_metric
        self.rows = sbp_rows(self.layers, spacing)
        self.x_base, self.y_base = x_base, y_base

    @property
    def x_rows(self):
        return 3 * self.layers * self.chunks * 2

    @property
    def y_rows(self):
        return self.layers * self.size


def plan_blocks(fine_shape, coarse_shape):
    fine = Block(fine_shape, 1.0, True, 0, 0)
    coarse = Block(coarse_shape, 3.0, False, fine.x_rows, fine.y_rows)
    fine.fx_base, fine.fy_base = 0, 0
    coarse.fx_base, coarse.fy_base = 6 * fine.chunks, fine.size
    corner_base = fine.size + coarse.size
    fine.corner_rows = (corner_base, corner_base + 1)
    coarse.corner_rows = (corner_base + 2, corner_base + 3)
    return fine, coarse, fine.x_rows + coarse.x_rows, fine.y_rows + coarse.y_rows


def round8(n):
    return -(-n // 8) * 8


def write_rims(b, src, fields, x_prev, x_next, y_prev, y_next):
    size, lanes = b.size, b.lanes
    for c, field in enumerate(fields):
        for z in range(b.layers):
            lo = src[field, z, 0:2, :]
            hi = src[field, z, size - 2 : size, :]
            for j in range(b.chunks):
                row = b.x_base + ((c * b.layers + z) * b.chunks + j) * 2
                x_prev[row : row + 2, :] = lo[:, j * 128 : (j + 1) * 128]
                x_next[row : row + 2, :] = hi[:, j * 128 : (j + 1) * 128]
    lane = lax.broadcasted_iota(jnp.int32, (size, 128), 1)
    for z in range(b.layers):
        acc_lo = jnp.zeros((size, 128), jnp.float32)
        acc_hi = jnp.zeros((size, 128), jnp.float32)
        for c, field in enumerate(fields):
            v = src[field, z]
            rl = v if c == 0 else pltpu.roll(v, 2 * c, 1)
            rh = pltpu.roll(v, (2 * c + 2) % lanes, 1)
            keep = (lane >= 2 * c) & (lane < 2 * c + 2)
            acc_lo = jnp.where(keep, rl[:, 0:128], acc_lo)
            acc_hi = jnp.where(keep, rh[:, 0:128], acc_hi)
        row = b.y_base + z * size
        y_prev[row : row + size, :] = acc_lo
        y_next[row : row + size, :] = acc_hi


def read_x_halo(b, buf, c, z):
    parts = [buf[pl.ds(b.x_base + ((c * b.layers + z) * b.chunks + j) * 2, 2), :] for j in range(b.chunks)]
    return parts[0] if len(parts) == 1 else jnp.concatenate(parts, axis=1)


def read_y_halo(b, buf, c, z, ok):
    row = b.y_base + z * b.size
    return keep(ok, buf[pl.ds(row, b.size), pl.ds(2 * c, 1)]), keep(ok, buf[pl.ds(row, b.size), pl.ds(2 * c + 1, 1)])


def fill_x2(b, scratch, slot, src, field, lo_buf, hi_buf, valid):
    size = b.size
    scratch[slot, :, 2 : 2 + size, :] = src[field]
    for z in range(b.layers):
        scratch[slot, z, 0:2, :] = keep(valid[0], read_x_halo(b, lo_buf, slot, z))
        scratch[slot, z, 2 + size :, :] = keep(valid[1], read_x_halo(b, hi_buf, slot, z))


def slope_y2(f, lo, hi, spacing):
    n = f.shape[-1]
    lane = lax.broadcasted_iota(jnp.int32, f.shape, 1)
    m1 = jnp.where(lane == 0, lo[1], pltpu.roll(f, 1, 1))
    m2 = jnp.where(lane == 0, lo[0], jnp.where(lane == 1, lo[1], pltpu.roll(f, 2, 1)))
    p1 = jnp.where(lane == n - 1, hi[0], pltpu.roll(f, n - 1, 1))
    p2 = jnp.where(lane == n - 2, hi[0], jnp.where(lane == n - 1, hi[1], pltpu.roll(f, n - 2, 1)))
    return (m2 - 8.0 * m1 + 8.0 * p1 - p2) / (12.0 * spacing)


STRESS_X = (3, 6, 7)
STRESS_Y = (6, 4, 8)
VELOCITY = (0, 1, 2)


def pack_kernel(blocks, fw, cw, x_prev, x_next, y_prev, y_next, *scratch):
    sems = scratch[-1]
    copies, views = [], []
    for n, (b, w) in enumerate(zip(blocks, (fw, cw))):
        xs_lo, xs_hi, ys_lo, ys_hi = scratch[4 * n : 4 * n + 4]
        size, lanes = b.size, b.lanes
        jobs = []
        for c, field in enumerate(STRESS_X):
            jobs.append((w.at[field, :, pl.ds(0, 2), :], xs_lo.at[c]))
            jobs.append((w.at[field, :, pl.ds(size - 2, 2), :], xs_hi.at[c]))
        for c, field in enumerate(STRESS_Y):
            jobs.append((w.at[field, :, :, pl.ds(0, 128)], ys_lo.at[c]))
            jobs.append((w.at[field, :, :, pl.ds(lanes - 128, 128)], ys_hi.at[c]))
        for src, dst in jobs:
            copy = pltpu.make_async_copy(src, dst, sems.at[len(copies)])
            copy.start()
            copies.append(copy)
        views.append((b, xs_lo, xs_hi, ys_lo, ys_hi))
    for copy in copies:
        copy.wait()
    for b, xs_lo, xs_hi, ys_lo, ys_hi in views:
        size = b.size
        for c in range(3):
            for z in range(b.layers):
                lo = xs_lo[c, z]
                hi = xs_hi[c, z]
                for j in range(b.chunks):
                    row = b.x_base + ((c * b.layers + z) * b.chunks + j) * 2
                    x_prev[row : row + 2, :] = lo[:, j * 128 : (j + 1) * 128]
                    x_next[row : row + 2, :] = hi[:, j * 128 : (j + 1) * 128]
        lane = lax.broadcasted_iota(jnp.int32, (size, 128), 1)
        for z in range(b.layers):
            acc_lo = jnp.zeros((size, 128), jnp.float32)
            acc_hi = jnp.zeros((size, 128), jnp.float32)
            for c in range(3):
                vl = ys_lo[c, z]
                vh = ys_hi[c, z]
                rl = vl if c == 0 else pltpu.roll(vl, 2 * c, 1)
                rh = pltpu.roll(vh, (2 * c + 2) % 128, 1)
                keep_lanes = (lane >= 2 * c) & (lane < 2 * c + 2)
                acc_lo = jnp.where(keep_lanes, rl, acc_lo)
                acc_hi = jnp.where(keep_lanes, rh, acc_hi)
            row = b.y_base + z * size
            y_prev[row : row + size, :] = acc_lo
            y_next[row : row + size, :] = acc_hi


def pack_scratch(blocks):
    shapes = []
    for b in blocks:
        shapes += [
            pltpu.VMEM((3, b.layers, 2, b.lanes), jnp.float32),
            pltpu.VMEM((3, b.layers, 2, b.lanes), jnp.float32),
            pltpu.VMEM((3, b.layers, b.size, 128), jnp.float32),
            pltpu.VMEM((3, b.layers, b.size, 128), jnp.float32),
        ]
    return shapes + [pltpu.SemaphoreType.DMA((12 * len(blocks),))]


def velocity_block(b, w, mat, metric, table, out, sx, hx_lo, hx_hi, hy_lo, hy_hi, valid):
    for slot, field in enumerate(STRESS_X):
        fill_x2(b, sx, slot, w, field, hx_lo, hx_hi, valid)
    for z in range(b.layers):
        dx = [slope_x(sx, slot, z, b.size, b.spacing) for slot in range(3)]
        dy = [
            slope_y2(w[field, z], read_y_halo(b, hy_lo, slot, z, valid[2]), read_y_halo(b, hy_hi, slot, z, valid[3]),
                     b.spacing)
            for slot, field in enumerate(STRESS_Y)
        ]
        dz = [slope_z(w, field, b.rows[z]) for field in (7, 8, 5)]
        if metric is not None:
            m = metric[z]
            dz = [m * d for d in dz]
        buoy = pick(table, 0, mat[z])
        for k in range(3):
            out[k, z] = w[k, z] + step_size * (buoy * (dx[k] + dy[k] + dz[k]))


def velocity_kernel(blocks, fw, cw, hx_lo, hx_hi, hy_lo, hy_hi, fmat, fmetric, cmat, table, flags,
                    fvel, cvel, vx_prev, vx_next, vy_prev, vy_next, sx_f, sx_c):
    fine, coarse = blocks
    valid = valid_of(flags)
    velocity_block(fine, fw, fmat, fmetric, table, fvel, sx_f, hx_lo, hx_hi, hy_lo, hy_hi, valid)
    velocity_block(coarse, cw, cmat, None, table, cvel, sx_c, hx_lo, hx_hi, hy_lo, hy_hi, valid)
    write_rims(fine, fvel, VELOCITY, vx_prev, vx_next, vy_prev, vy_next)
    write_rims(coarse, cvel, VELOCITY, vx_prev, vx_next, vy_prev, vy_next)


def stress_block(b, depth, w, mem, vel, mat, mech, metric, mtab, atab, out, mem_out, face, sx,
                 hx_lo, hx_hi, hy_lo, hy_hi, face_rims, valid):
    for slot in range(3):
        fill_x2(b, sx, slot, vel, slot, hx_lo, hx_hi, valid)
    for z in range(b.layers):
        dx = [slope_x(sx, slot, z, b.size, b.spacing) for slot in range(3)]
        dy = [
            slope_y2(vel[slot, z], read_y_halo(b, hy_lo, slot, z, valid[2]), read_y_halo(b, hy_hi, slot, z, valid[3]),
                     b.spacing)
            for slot in range(3)
        ]
        dz = [slope_z(vel, slot, b.rows[z]) for slot in range(3)]
        if metric is not None:
            m = metric[z]
            dz = [m * d for d in dz]
        kind, mechanism = mat[z], mech[z]
        lame, shear = pick(mtab, 1, kind), pick(mtab, 2, kind)
        decay, strength = pick(atab, 0, mechanism), pick(atab, 1, mechanism)
        cell_volume = lame * (dx[0] + dy[1] + dz[2])
        rate = [
            cell_volume + 2.0 * shear * dx[0],
            cell_volume + 2.0 * shear * dy[1],
            cell_volume + 2.0 * shear * dz[2],
            shear * (dy[0] + dx[1]),
            shear * (dz[0] + dx[2]),
            shear * (dz[1] + dy[2]),
        ]
        values = []
        for k in range(3):
            v = vel[k, z]
            out[k, z] = v
            values.append(v)
        for k in range(6):
            memory_new = decay * mem[k, z] + (1.0 - decay) * strength * rate[k]
            mem_out[k, z] = memory_new
            stress = w[3 + k, z] + step_size * (rate[k] - memory_new)
            out[3 + k, z] = stress
            values.append(stress)
        if z == depth:
            for i, k in enumerate((0, 1, 2, 7, 8, 5)):
                face[i] = values[k]
            write_face_rims(b, [values[k] for k in (0, 1, 2, 7, 8, 5)], *face_rims)


def write_face_rims(b, planes, x_prev, x_next, y_prev, y_next):
    size, lanes = b.size, b.lanes
    for i, v in enumerate(planes):
        for j in range(b.chunks):
            row = b.fx_base + i * b.chunks + j
            x_prev[row : row + 1, :] = v[0:1, j * 128 : (j + 1) * 128]
            x_next[row : row + 1, :] = v[size - 1 : size, j * 128 : (j + 1) * 128]
    lane = lax.broadcasted_iota(jnp.int32, (size, 128), 1)
    acc_lo = jnp.zeros((size, 128), jnp.float32)
    acc_hi = jnp.zeros((size, 128), jnp.float32)
    for i, v in enumerate(planes):
        rl = v if i == 0 else pltpu.roll(v, i, 1)
        rh = pltpu.roll(v, (i + 1) % lanes, 1)
        acc_lo = jnp.where(lane == i, rl[:, 0:128], acc_lo)
        acc_hi = jnp.where(lane == i, rh[:, 0:128], acc_hi)
    y_prev[b.fy_base : b.fy_base + size, :] = acc_lo
    y_next[b.fy_base : b.fy_base + size, :] = acc_hi


def stress_kernel(blocks, fw, fmem, fvel, cw, cmem, cvel, hx_lo, hx_hi, hy_lo, hy_hi,
                  fmat, fmech, fmetric, cmat, cmech, mtab, atab, flags,
                  fout, fmem_out, fface, cout, cmem_out, cface, rx_prev, rx_next, ry_prev, ry_next, sx_f, sx_c):
    fine, coarse = blocks
    valid = valid_of(flags)
    rims = (rx_prev, rx_next, ry_prev, ry_next)
    stress_block(fine, fine.layers - 1, fw, fmem, fvel, fmat, fmech, fmetric, mtab, atab, fout, fmem_out,
                 fface, sx_f, hx_lo, hx_hi, hy_lo, hy_hi, rims, valid)
    stress_block(coarse, 0, cw, cmem, cvel, cmat, cmech, None, mtab, atab, cout, cmem_out,
                 cface, sx_c, hx_lo, hx_hi, hy_lo, hy_hi, rims, valid)


def vmem_specs(count):
    return [pl.BlockSpec(memory_space=pltpu.VMEM)] * count


def f32(shape):
    return jax.ShapeDtypeStruct(shape, jnp.float32)


def halo_shapes(x_rows, y_rows):
    return (f32((x_rows, 128)), f32((x_rows, 128)), f32((y_rows, 128)), f32((y_rows, 128)))


def scratch_for(b):
    return pltpu.VMEM((3, b.layers, b.size + 4, b.lanes), jnp.float32)


def receive(buffers):
    x_prev, x_next, y_prev, y_next = buffers
    y_lo = shift_from(y_next, "gy", 1)
    y_hi = shift_from(y_prev, "gy", -1)
    x_lo = shift_from(x_next, "gx", 1)
    x_hi = shift_from(x_prev, "gx", -1)
    return x_lo, x_hi, y_lo, y_hi


def put_face(out, face, depth):
    out = lax.dynamic_update_slice(out, face[0:3][:, None], (0, depth, 0, 0))
    out = lax.dynamic_update_slice(out, face[5:6][:, None], (5, depth, 0, 0))
    out = lax.dynamic_update_slice(out, face[3:5][:, None], (7, depth, 0, 0))
    return out


def prolong_y_matrix(coarse_lanes):
    m = np.zeros((coarse_lanes, 3 * coarse_lanes), np.float32)
    for d in range(coarse_lanes):
        m[d, 3 * d] = 2.0 / 3.0
        m[d, 3 * d + 1] = 1.0
        m[d, 3 * d + 2] = 2.0 / 3.0
        if d >= 1:
            m[d - 1, 3 * d] = 1.0 / 3.0
        if d + 1 < coarse_lanes:
            m[d + 1, 3 * d + 2] = 1.0 / 3.0
    return m


def restrict_y_matrix(coarse_lanes):
    m = np.zeros((3 * coarse_lanes, coarse_lanes), np.float32)
    for c in range(coarse_lanes):
        for offset, weight in ((-1, 1.0), (0, 2.0), (1, 3.0), (2, 2.0), (3, 1.0)):
            f = 3 * c + offset
            if 0 <= f < 3 * coarse_lanes:
                m[f, c] = weight / 9.0
    return m


def padded_rows(b, face, hx_lo, hx_hi, hy_lo, hy_hi, valid, i):
    size = b.size

    def x_row(buf):
        parts = [buf[pl.ds(b.fx_base + i * b.chunks + j, 1), :] for j in range(b.chunks)]
        return parts[0] if len(parts) == 1 else jnp.concatenate(parts, axis=1)

    def lane_of(buf, row, ok):
        return keep(ok, buf[pl.ds(row, 1), pl.ds(i, 1)])

    x_lo_ok, x_hi_ok, y_lo_ok, y_hi_ok = valid
    lo_row, hi_row = b.corner_rows
    rows = [(keep(x_lo_ok, x_row(hx_lo)), lane_of(hy_lo, lo_row, x_lo_ok & y_lo_ok),
             lane_of(hy_hi, lo_row, x_lo_ok & y_hi_ok))]
    for x in range(size):
        rows.append((face[i, pl.ds(x, 1), :], lane_of(hy_lo, b.fy_base + x, y_lo_ok),
                     lane_of(hy_hi, b.fy_base + x, y_hi_ok)))
    rows.append((keep(x_hi_ok, x_row(hx_hi)), lane_of(hy_lo, hi_row, x_hi_ok & y_lo_ok),
                 lane_of(hy_hi, hi_row, x_hi_ok & y_hi_ok)))
    return rows


def combine(terms):
    out = []
    for part in range(3):
        total = None
        for weight, row in terms:
            v = row[part] if weight == 1.0 else weight * row[part]
            total = v if total is None else total + v
        out.append(total)
    return out


def face_kernel(blocks, fine_depth, fout_in, cout_in, fface, cface, hx_lo, hx_hi, hy_lo, hy_hi,
                py, ry, flags, fout, cout, fnew, cnew, stage_p, stage_r, sems):
    fine, coarse = blocks
    halos = (hx_lo, hx_hi, hy_lo, hy_hi, valid_of(flags))
    lane_f = lax.broadcasted_iota(jnp.int32, (1, fine.lanes), 1)
    p_lo, p_hi = [], []
    for i in range(6):
        rows = padded_rows(coarse, cface, *halos, i)
        for c in range(coarse.size):
            left, middle, right = rows[c], rows[c + 1], rows[c + 2]
            parts = [
                [(1.0, left), (2.0, middle)],
                [(1.0, middle)],
                [(2.0, middle), (1.0, right)],
            ]
            for a, terms in enumerate(parts):
                interior, lo, hi = combine(terms)
                if a != 1:
                    interior, lo, hi = interior / 3.0, lo / 3.0, hi / 3.0
                r = i * fine.size + 3 * c + a
                stage_p[pl.ds(r, 1), :] = interior
                p_lo.append(lo)
                p_hi.append(hi)
    prolonged = jnp.dot(stage_p[...], py[...], precision=lax.Precision.HIGHEST, preferred_element_type=jnp.float32)
    for i in range(6):
        for x in range(fine.size):
            r = i * fine.size + x
            value = prolonged[r : r + 1, :]
            value = value + jnp.where(lane_f == 0, p_lo[r] / 3.0, 0.0) + jnp.where(lane_f == fine.lanes - 1, p_hi[r] / 3.0, 0.0)
            own = fface[i, pl.ds(x, 1), :]
            fnew[i, 0, pl.ds(x, 1), :] = own - penalty * (own - value)
    lane_c = lax.broadcasted_iota(jnp.int32, (1, coarse.lanes), 1)
    r_lo, r_hi = [], []
    for i in range(6):
        rows = padded_rows(fine, fface, *halos, i)
        for c in range(coarse.size):
            terms = [(1.0, rows[3 * c]), (2.0, rows[3 * c + 1]), (3.0, rows[3 * c + 2]), (2.0, rows[3 * c + 3]),
                     (1.0, rows[3 * c + 4])]
            interior, lo, hi = combine(terms)
            r = i * coarse.size + c
            stage_r[pl.ds(r, 1), :] = interior / 9.0
            r_lo.append(lo / 9.0)
            r_hi.append(hi / 9.0)
    restricted = jnp.dot(stage_r[...], ry[...], precision=lax.Precision.HIGHEST, preferred_element_type=jnp.float32)
    for i in range(6):
        for c in range(coarse.size):
            r = i * coarse.size + c
            value = restricted[r : r + 1, :]
            value = value + jnp.where(lane_c == 0, r_lo[r] / 9.0, 0.0) + jnp.where(lane_c == coarse.lanes - 1, r_hi[r] / 9.0, 0.0)
            own = cface[i, pl.ds(c, 1), :]
            cnew[i, 0, pl.ds(c, 1), :] = own - penalty * (own - value)
    copies = []
    for n, (src, dst, depth) in enumerate(((fnew, fout, fine_depth), (cnew, cout, 0))):
        for k, (first, count, field) in enumerate(((0, 3, 0), (5, 1, 5), (3, 2, 7))):
            copy = pltpu.make_async_copy(
                src.at[pl.ds(first, count)], dst.at[pl.ds(field, count), pl.ds(depth, 1)], sems.at[3 * n + k]
            )
            copy.start()
            copies.append(copy)
    for copy in copies:
        copy.wait()


def diag_from(block, dx, dy):
    nx, ny = lax.axis_size("gx"), lax.axis_size("gy")
    pairs = []
    for i in range(nx):
        for j in range(ny):
            if 0 <= i + dx < nx and 0 <= j + dy < ny:
                pairs.append((i * ny + j, (i + dx) * ny + (j + dy)))
    return lax.ppermute(block, ("gx", "gy"), pairs)


def row_ends(buf, blocks, at_end):
    out = []
    for b in blocks:
        chunk = b.chunks - 1 if at_end else 0
        first = b.fx_base + chunk
        lane = 127 if at_end else 0
        out.append(lax.slice(buf, (first, lane), (first + 5 * b.chunks + 1, lane + 1), (b.chunks, 1))[:, 0])
    return jnp.stack(out)


def with_corners(y_rim, x_lo, x_hi, blocks, at_end):
    lo, hi = row_ends(x_lo, blocks, at_end), row_ends(x_hi, blocks, at_end)
    extra = jnp.stack([lo, hi], axis=1).reshape(2 * len(blocks), 6)
    extra = jnp.pad(extra, ((0, 0), (0, 128 - 6)))
    joined = jnp.concatenate([y_rim, extra])
    return jnp.pad(joined, ((0, round8(joined.shape[0]) - joined.shape[0]), (0, 0)))


def face_call(blocks, fine_out, coarse_out, fine_face, coarse_face, rims):
    fine, coarse = blocks
    x_prev, x_next, y_prev, y_next = rims
    x_lo = shift_from(x_next, "gx", 1)
    x_hi = shift_from(x_prev, "gx", -1)
    y_lo = shift_from(with_corners(y_next, x_lo, x_hi, blocks, True), "gy", 1)
    y_hi = shift_from(with_corners(y_prev, x_lo, x_hi, blocks, False), "gy", -1)
    received = (x_lo, x_hi, y_lo, y_hi)
    py = jnp.asarray(prolong_y_matrix(coarse.lanes))
    ry = jnp.asarray(restrict_y_matrix(coarse.lanes))
    anyspace = pl.BlockSpec(memory_space=pl.ANY)
    return pl.pallas_call(
        functools.partial(face_kernel, blocks, fine.layers - 1),
        out_shape=(f32(fine_out.shape), f32(coarse_out.shape)),
        in_specs=[anyspace, anyspace] + vmem_specs(8) + [pl.BlockSpec(memory_space=pltpu.SMEM)],
        out_specs=(anyspace, anyspace),
        input_output_aliases={0: 0, 1: 1},
        scratch_shapes=[
            pltpu.VMEM((6, 1, fine.size, fine.lanes), jnp.float32),
            pltpu.VMEM((6, 1, coarse.size, coarse.lanes), jnp.float32),
            pltpu.VMEM((round8(6 * fine.size), coarse.lanes), jnp.float32),
            pltpu.VMEM((round8(6 * coarse.size), fine.lanes), jnp.float32),
            pltpu.SemaphoreType.DMA((6,)),
        ],
    )(fine_out, coarse_out, fine_face, coarse_face, *received, py, ry, edge_flags())


def local(
    fine_wave,
    fine_memory,
    fine_material,
    fine_mechanism,
    fine_metric,
    coarse_wave,
    coarse_memory,
    coarse_material,
    coarse_mechanism,
    material_table,
    attenuation_table,
):
    fine, coarse, x_rows, y_rows = plan_blocks(fine_wave.shape[1:], coarse_wave.shape[1:])
    blocks = (fine, coarse)
    smem = pl.BlockSpec(memory_space=pltpu.SMEM)
    flags = edge_flags()

    rims = pl.pallas_call(
        functools.partial(pack_kernel, blocks),
        out_shape=halo_shapes(x_rows, y_rows),
        in_specs=[pl.BlockSpec(memory_space=pl.ANY)] * 2,
        out_specs=tuple(vmem_specs(4)),
        scratch_shapes=pack_scratch(blocks),
    )(fine_wave, coarse_wave)
    halos = receive(rims)

    fine_velocity, coarse_velocity, *vrims = pl.pallas_call(
        functools.partial(velocity_kernel, blocks),
        out_shape=(f32((3,) + fine_wave.shape[1:]), f32((3,) + coarse_wave.shape[1:])) + halo_shapes(x_rows, y_rows),
        in_specs=vmem_specs(9) + [smem, smem],
        out_specs=tuple(vmem_specs(6)),
        scratch_shapes=[scratch_for(fine), scratch_for(coarse)],
    )(fine_wave, coarse_wave, *halos, fine_material, fine_metric, coarse_material, material_table, flags)

    vhalos = receive(vrims)
    fx_rows = 6 * (fine.chunks + coarse.chunks)
    fy_rows = round8(fine.size + coarse.size)
    fine_out, fine_mem, fine_face, coarse_out, coarse_mem, coarse_face, *face_rims = pl.pallas_call(
        functools.partial(stress_kernel, blocks),
        out_shape=(
            f32(fine_wave.shape), f32(fine_memory.shape), f32((6,) + fine_wave.shape[2:]),
            f32(coarse_wave.shape), f32(coarse_memory.shape), f32((6,) + coarse_wave.shape[2:]),
            f32((fx_rows, 128)), f32((fx_rows, 128)), f32((fy_rows, 128)), f32((fy_rows, 128)),
        ),
        in_specs=vmem_specs(15) + [smem, smem, smem],
        out_specs=tuple(vmem_specs(10)),
        scratch_shapes=[scratch_for(fine), scratch_for(coarse)],
    )(fine_wave, fine_memory, fine_velocity, coarse_wave, coarse_memory, coarse_velocity, *vhalos,
      fine_material, fine_mechanism, fine_metric, coarse_material, coarse_mechanism, material_table,
      attenuation_table, flags)

    fine_out, coarse_out = face_call(blocks, fine_out, coarse_out, fine_face, coarse_face, face_rims)
    return (fine_out, fine_mem, coarse_out, coarse_mem)


def solution(mesh):
    in_specs = (
        P(None, None, "gx", "gy"),
        P(None, None, "gx", "gy"),
        P(None, "gx", "gy"),
        P(None, "gx", "gy"),
        P(None, "gx", "gy"),
        P(None, None, "gx", "gy"),
        P(None, None, "gx", "gy"),
        P(None, "gx", "gy"),
        P(None, "gx", "gy"),
        P(),
        P(),
    )
    out_specs = (
        P(None, None, "gx", "gy"),
        P(None, None, "gx", "gy"),
        P(None, None, "gx", "gy"),
        P(None, None, "gx", "gy"),
    )
    return jax.shard_map(local, mesh=mesh, in_specs=in_specs, out_specs=out_specs, check_vma=False)
```

```python
import functools

import jax
import jax.numpy as jnp
import numpy as np
from jax import lax
from jax.sharding import PartitionSpec as P


step_size = 0.1
penalty = 0.1 * 48.0 / 17.0
closure = [
    [-24.0 / 17.0, 59.0 / 34.0, -4.0 / 17.0, -3.0 / 34.0, 0.0, 0.0],
    [-0.5, 0.0, 0.5, 0.0, 0.0, 0.0],
    [4.0 / 43.0, -59.0 / 86.0, 0.0, 59.0 / 86.0, -4.0 / 43.0, 0.0],
    [3.0 / 98.0, 0.0, -59.0 / 98.0, 0.0, 32.0 / 49.0, -4.0 / 49.0],
]


def sbp_numpy(layers, spacing):
    table = np.zeros((layers, layers))
    for line_at in range(4):
        for column in range(6):
            table[line_at, column] = closure[line_at][column]
            table[layers - 1 - line_at, layers - 1 - column] = -closure[line_at][column]
    for line_at in range(4, layers - 4):
        table[line_at, line_at - 2 : line_at + 3] = [
            1.0 / 12.0,
            -2.0 / 3.0,
            0.0,
            2.0 / 3.0,
            -1.0 / 12.0,
        ]
    return (table / spacing).astype(np.float32)


def shift_from(block, axis, offset):
    count = lax.axis_size(axis)
    pairs = [(i, (i + offset) % count) for i in range(count)]
    return lax.ppermute(block, axis, pairs)


def edge_flags():
    gx, gy = lax.axis_index("gx"), lax.axis_index("gy")
    nx, ny = lax.axis_size("gx"), lax.axis_size("gy")
    return jnp.stack([gx > 0, gx < nx - 1, gy > 0, gy < ny - 1]).astype(jnp.int32)


def valid_of(flags):
    return tuple(flags[k] != 0 for k in range(4))


def keep(ok, value):
    return jnp.where(ok, value, 0.0)


from jax.experimental import pallas as pl
from jax.experimental.pallas import tpu as pltpu


def sbp_rows(layers, spacing):
    table = sbp_numpy(layers, spacing)
    return [[(j, float(table[k, j])) for j in range(layers) if table[k, j] != 0.0] for k in range(layers)]


def pick(values_ref, row, index):
    result = jnp.zeros(index.shape, jnp.float32)
    for kind_at in range(values_ref.shape[1]):
        result = jnp.where(index == kind_at, values_ref[row, kind_at], result)
    return result


def slope_x(scratch, slot, z, size, spacing):
    s = lambda o: scratch[slot, z, o : o + size, :]
    return (s(0) - 8.0 * s(1) + 8.0 * s(3) - s(4)) / (12.0 * spacing)


def slope_z(field_ref, index, row):
    total = None
    for j, weight in row:
        term = jnp.float32(weight) * field_ref[index, j]
        total = term if total is None else total + term
    return total


class Block:
    def __init__(self, shape, spacing, x_base, y_base):
        self.layers, self.size, self.lanes = shape
        self.chunks = self.lanes // 128
        self.spacing = spacing
        self.rows = sbp_rows(self.layers, spacing)
        self.x_base, self.y_base = x_base, y_base

    @property
    def x_rows(self):
        return 3 * self.layers * self.chunks * 2

    @property
    def y_rows(self):
        return self.layers * self.size


def plan_blocks(fine_shape, coarse_shape):
    fine = Block(fine_shape, 1.0, 0, 0)
    coarse = Block(coarse_shape, 3.0, fine.x_rows, fine.y_rows)
    fine.fx_base, fine.fy_base = 0, 0
    coarse.fx_base, coarse.fy_base = 6 * fine.chunks, fine.size
    corner_base = fine.size + coarse.size
    fine.corner_rows = (corner_base, corner_base + 1)
    coarse.corner_rows = (corner_base + 2, corner_base + 3)
    return fine, coarse, fine.x_rows + coarse.x_rows, fine.y_rows + coarse.y_rows


def round8(n):
    return -(-n // 8) * 8


def write_rims(b, src, fields, x_prev, x_next, y_prev, y_next):
    size, lanes = b.size, b.lanes
    for c, field in enumerate(fields):
        for z in range(b.layers):
            lo = src[field, z, 0:2, :]
            hi = src[field, z, size - 2 : size, :]
            for j in range(b.chunks):
                row = b.x_base + ((c * b.layers + z) * b.chunks + j) * 2
                x_prev[row : row + 2, :] = lo[:, j * 128 : (j + 1) * 128]
                x_next[row : row + 2, :] = hi[:, j * 128 : (j + 1) * 128]
    lane = lax.broadcasted_iota(jnp.int32, (size, 128), 1)
    for z in range(b.layers):
        acc_lo = jnp.zeros((size, 128), jnp.float32)
        acc_hi = jnp.zeros((size, 128), jnp.float32)
        for c, field in enumerate(fields):
            v = src[field, z]
            rl = v if c == 0 else pltpu.roll(v, 2 * c, 1)
            rh = pltpu.roll(v, (2 * c + 2) % lanes, 1)
            keep = (lane >= 2 * c) & (lane < 2 * c + 2)
            acc_lo = jnp.where(keep, rl[:, 0:128], acc_lo)
            acc_hi = jnp.where(keep, rh[:, 0:128], acc_hi)
        row = b.y_base + z * size
        y_prev[row : row + size, :] = acc_lo
        y_next[row : row + size, :] = acc_hi


def read_x_halo(b, buf, c, z):
    parts = [buf[pl.ds(b.x_base + ((c * b.layers + z) * b.chunks + j) * 2, 2), :] for j in range(b.chunks)]
    return parts[0] if len(parts) == 1 else jnp.concatenate(parts, axis=1)


def read_y_halo(b, buf, c, z, ok):
    row = b.y_base + z * b.size
    return keep(ok, buf[pl.ds(row, b.size), pl.ds(2 * c, 1)]), keep(ok, buf[pl.ds(row, b.size), pl.ds(2 * c + 1, 1)])


def fill_x2(b, scratch, slot, src, field, lo_buf, hi_buf, valid):
    size = b.size
    scratch[slot, :, 2 : 2 + size, :] = src[field]
    for z in range(b.layers):
        scratch[slot, z, 0:2, :] = keep(valid[0], read_x_halo(b, lo_buf, slot, z))
        scratch[slot, z, 2 + size :, :] = keep(valid[1], read_x_halo(b, hi_buf, slot, z))


def slope_y2(f, lo, hi, spacing):
    n = f.shape[-1]
    lane = lax.broadcasted_iota(jnp.int32, f.shape, 1)
    m1 = jnp.where(lane == 0, lo[1], pltpu.roll(f, 1, 1))
    m2 = jnp.where(lane == 0, lo[0], jnp.where(lane == 1, lo[1], pltpu.roll(f, 2, 1)))
    p1 = jnp.where(lane == n - 1, hi[0], pltpu.roll(f, n - 1, 1))
    p2 = jnp.where(lane == n - 2, hi[0], jnp.where(lane == n - 1, hi[1], pltpu.roll(f, n - 2, 1)))
    return (m2 - 8.0 * m1 + 8.0 * p1 - p2) / (12.0 * spacing)


STRESS_X = (3, 6, 7)
STRESS_Y = (6, 4, 8)
VELOCITY = (0, 1, 2)


def pack_kernel(blocks, fw, cw, x_prev, x_next, y_prev, y_next):
    for b, w in zip(blocks, (fw, cw)):
        write_rims_split(b, w, x_prev, x_next, y_prev, y_next)


def write_rims_split(b, w, x_prev, x_next, y_prev, y_next):
    size, lanes = b.size, b.lanes
    for c, field in enumerate(STRESS_X):
        for z in range(b.layers):
            lo = w[field, z, 0:2, :]
            hi = w[field, z, size - 2 : size, :]
            for j in range(b.chunks):
                row = b.x_base + ((c * b.layers + z) * b.chunks + j) * 2
                x_prev[row : row + 2, :] = lo[:, j * 128 : (j + 1) * 128]
                x_next[row : row + 2, :] = hi[:, j * 128 : (j + 1) * 128]
    lane = lax.broadcasted_iota(jnp.int32, (size, 128), 1)
    for z in range(b.layers):
        acc_lo = jnp.zeros((size, 128), jnp.float32)
        acc_hi = jnp.zeros((size, 128), jnp.float32)
        for c, field in enumerate(STRESS_Y):
            v = w[field, z]
            rl = v if c == 0 else pltpu.roll(v, 2 * c, 1)
            rh = pltpu.roll(v, (2 * c + 2) % lanes, 1)
            keep = (lane >= 2 * c) & (lane < 2 * c + 2)
            acc_lo = jnp.where(keep, rl[:, 0:128], acc_lo)
            acc_hi = jnp.where(keep, rh[:, 0:128], acc_hi)
        row = b.y_base + z * size
        y_prev[row : row + size, :] = acc_lo
        y_next[row : row + size, :] = acc_hi


def velocity_block(b, w, mat, metric, table, out, sx, hx_lo, hx_hi, hy_lo, hy_hi, valid):
    for slot, field in enumerate(STRESS_X):
        fill_x2(b, sx, slot, w, field, hx_lo, hx_hi, valid)
    for z in range(b.layers):
        dx = [slope_x(sx, slot, z, b.size, b.spacing) for slot in range(3)]
        dy = [
            slope_y2(w[field, z], read_y_halo(b, hy_lo, slot, z, valid[2]), read_y_halo(b, hy_hi, slot, z, valid[3]),
                     b.spacing)
            for slot, field in enumerate(STRESS_Y)
        ]
        dz = [slope_z(w, field, b.rows[z]) for field in (7, 8, 5)]
        if metric is not None:
            m = metric[z]
            dz = [m * d for d in dz]
        buoy = pick(table, 0, mat[z])
        for k in range(3):
            out[k, z] = w[k, z] + step_size * (buoy * (dx[k] + dy[k] + dz[k]))


def velocity_kernel(blocks, fw, cw, hx_lo, hx_hi, hy_lo, hy_hi, fmat, fmetric, cmat, table, flags,
                    fvel, cvel, vx_prev, vx_next, vy_prev, vy_next, sx_f, sx_c):
    fine, coarse = blocks
    valid = valid_of(flags)
    velocity_block(fine, fw, fmat, fmetric, table, fvel, sx_f, hx_lo, hx_hi, hy_lo, hy_hi, valid)
    velocity_block(coarse, cw, cmat, None, table, cvel, sx_c, hx_lo, hx_hi, hy_lo, hy_hi, valid)
    write_rims(fine, fvel, VELOCITY, vx_prev, vx_next, vy_prev, vy_next)
    write_rims(coarse, cvel, VELOCITY, vx_prev, vx_next, vy_prev, vy_next)


def stress_block(b, depth, w, mem, vel, mat, mech, metric, mtab, atab, out, mem_out, face, sx,
                 hx_lo, hx_hi, hy_lo, hy_hi, face_rims, valid):
    for slot in range(3):
        fill_x2(b, sx, slot, vel, slot, hx_lo, hx_hi, valid)
    for z in range(b.layers):
        dx = [slope_x(sx, slot, z, b.size, b.spacing) for slot in range(3)]
        dy = [
            slope_y2(vel[slot, z], read_y_halo(b, hy_lo, slot, z, valid[2]), read_y_halo(b, hy_hi, slot, z, valid[3]),
                     b.spacing)
            for slot in range(3)
        ]
        dz = [slope_z(vel, slot, b.rows[z]) for slot in range(3)]
        if metric is not None:
            m = metric[z]
            dz = [m * d for d in dz]
        kind, mechanism = mat[z], mech[z]
        lame, shear = pick(mtab, 1, kind), pick(mtab, 2, kind)
        decay, strength = pick(atab, 0, mechanism), pick(atab, 1, mechanism)
        cell_volume = lame * (dx[0] + dy[1] + dz[2])
        rate = [
            cell_volume + 2.0 * shear * dx[0],
            cell_volume + 2.0 * shear * dy[1],
            cell_volume + 2.0 * shear * dz[2],
            shear * (dy[0] + dx[1]),
            shear * (dz[0] + dx[2]),
            shear * (dz[1] + dy[2]),
        ]
        values = []
        for k in range(3):
            v = vel[k, z]
            out[k, z] = v
            values.append(v)
        for k in range(6):
            memory_new = decay * mem[k, z] + (1.0 - decay) * strength * rate[k]
            mem_out[k, z] = memory_new
            stress = w[3 + k, z] + step_size * (rate[k] - memory_new)
            out[3 + k, z] = stress
            values.append(stress)
        if z == depth:
            for i, k in enumerate((0, 1, 2, 7, 8, 5)):
                face[i] = values[k]
            write_face_rims(b, [values[k] for k in (0, 1, 2, 7, 8, 5)], *face_rims)


def write_face_rims(b, planes, x_prev, x_next, y_prev, y_next):
    size, lanes = b.size, b.lanes
    for i, v in enumerate(planes):
        for j in range(b.chunks):
            row = b.fx_base + i * b.chunks + j
            x_prev[row : row + 1, :] = v[0:1, j * 128 : (j + 1) * 128]
            x_next[row : row + 1, :] = v[size - 1 : size, j * 128 : (j + 1) * 128]
    lane = lax.broadcasted_iota(jnp.int32, (size, 128), 1)
    acc_lo = jnp.zeros((size, 128), jnp.float32)
    acc_hi = jnp.zeros((size, 128), jnp.float32)
    for i, v in enumerate(planes):
        rl = v if i == 0 else pltpu.roll(v, i, 1)
        rh = pltpu.roll(v, (i + 1) % lanes, 1)
        acc_lo = jnp.where(lane == i, rl[:, 0:128], acc_lo)
        acc_hi = jnp.where(lane == i, rh[:, 0:128], acc_hi)
    y_prev[b.fy_base : b.fy_base + size, :] = acc_lo
    y_next[b.fy_base : b.fy_base + size, :] = acc_hi


def stress_kernel(blocks, fw, fmem, fvel, cw, cmem, cvel, hx_lo, hx_hi, hy_lo, hy_hi,
                  fmat, fmech, fmetric, cmat, cmech, mtab, atab, flags,
                  fout, fmem_out, fface, cout, cmem_out, cface, rx_prev, rx_next, ry_prev, ry_next, sx_f, sx_c):
    fine, coarse = blocks
    valid = valid_of(flags)
    rims = (rx_prev, rx_next, ry_prev, ry_next)
    stress_block(fine, fine.layers - 1, fw, fmem, fvel, fmat, fmech, fmetric, mtab, atab, fout, fmem_out,
                 fface, sx_f, hx_lo, hx_hi, hy_lo, hy_hi, rims, valid)
    stress_block(coarse, 0, cw, cmem, cvel, cmat, cmech, None, mtab, atab, cout, cmem_out,
                 cface, sx_c, hx_lo, hx_hi, hy_lo, hy_hi, rims, valid)


def vmem_specs(count):
    return [pl.BlockSpec(memory_space=pltpu.VMEM)] * count


def f32(shape):
    return jax.ShapeDtypeStruct(shape, jnp.float32)


def halo_shapes(x_rows, y_rows):
    return (f32((x_rows, 128)), f32((x_rows, 128)), f32((y_rows, 128)), f32((y_rows, 128)))


def scratch_for(b):
    return pltpu.VMEM((3, b.layers, b.size + 4, b.lanes), jnp.float32)


def receive(buffers):
    x_prev, x_next, y_prev, y_next = buffers
    y_lo = shift_from(y_next, "gy", 1)
    y_hi = shift_from(y_prev, "gy", -1)
    x_lo = shift_from(x_next, "gx", 1)
    x_hi = shift_from(x_prev, "gx", -1)
    return x_lo, x_hi, y_lo, y_hi


def prolong_y_matrix(coarse_lanes):
    m = np.zeros((coarse_lanes, 3 * coarse_lanes), np.float32)
    for d in range(coarse_lanes):
        m[d, 3 * d] = 2.0 / 3.0
        m[d, 3 * d + 1] = 1.0
        m[d, 3 * d + 2] = 2.0 / 3.0
        if d >= 1:
            m[d - 1, 3 * d] = 1.0 / 3.0
        if d + 1 < coarse_lanes:
            m[d + 1, 3 * d + 2] = 1.0 / 3.0
    return m


def restrict_y_matrix(coarse_lanes):
    m = np.zeros((3 * coarse_lanes, coarse_lanes), np.float32)
    for c in range(coarse_lanes):
        for offset, weight in ((-1, 1.0), (0, 2.0), (1, 3.0), (2, 2.0), (3, 1.0)):
            f = 3 * c + offset
            if 0 <= f < 3 * coarse_lanes:
                m[f, c] = weight / 9.0
    return m


def padded_rows(b, face, hx_lo, hx_hi, hy_lo, hy_hi, valid, i):
    size = b.size

    def x_row(buf):
        parts = [buf[pl.ds(b.fx_base + i * b.chunks + j, 1), :] for j in range(b.chunks)]
        return parts[0] if len(parts) == 1 else jnp.concatenate(parts, axis=1)

    def lane_of(buf, row, ok):
        return keep(ok, buf[pl.ds(row, 1), pl.ds(i, 1)])

    x_lo_ok, x_hi_ok, y_lo_ok, y_hi_ok = valid
    lo_row, hi_row = b.corner_rows
    rows = [(keep(x_lo_ok, x_row(hx_lo)), lane_of(hy_lo, lo_row, x_lo_ok & y_lo_ok),
             lane_of(hy_hi, lo_row, x_lo_ok & y_hi_ok))]
    for x in range(size):
        rows.append((face[i, pl.ds(x, 1), :], lane_of(hy_lo, b.fy_base + x, y_lo_ok),
                     lane_of(hy_hi, b.fy_base + x, y_hi_ok)))
    rows.append((keep(x_hi_ok, x_row(hx_hi)), lane_of(hy_lo, hi_row, x_hi_ok & y_lo_ok),
                 lane_of(hy_hi, hi_row, x_hi_ok & y_hi_ok)))
    return rows


def combine(terms):
    out = []
    for part in range(3):
        total = None
        for weight, row in terms:
            v = row[part] if weight == 1.0 else weight * row[part]
            total = v if total is None else total + v
        out.append(total)
    return out


def face_kernel(blocks, fine_depth, fout_in, cout_in, fface, cface, hx_lo, hx_hi, hy_lo, hy_hi,
                py, ry, flags, fout, cout, fnew, cnew, stage_p, stage_r, sems):
    fine, coarse = blocks
    halos = (hx_lo, hx_hi, hy_lo, hy_hi, valid_of(flags))
    lane_f = lax.broadcasted_iota(jnp.int32, (1, fine.lanes), 1)
    p_lo, p_hi = [], []
    for i in range(6):
        rows = padded_rows(coarse, cface, *halos, i)
        for c in range(coarse.size):
            left, middle, right = rows[c], rows[c + 1], rows[c + 2]
            parts = [
                [(1.0, left), (2.0, middle)],
                [(1.0, middle)],
                [(2.0, middle), (1.0, right)],
            ]
            for a, terms in enumerate(parts):
                interior, lo, hi = combine(terms)
                if a != 1:
                    interior, lo, hi = interior / 3.0, lo / 3.0, hi / 3.0
                r = i * fine.size + 3 * c + a
                stage_p[pl.ds(r, 1), :] = interior
                p_lo.append(lo)
                p_hi.append(hi)
    prolonged = jnp.dot(stage_p[...], py[...], precision=lax.Precision.HIGHEST, preferred_element_type=jnp.float32)
    for i in range(6):
        for x in range(fine.size):
            r = i * fine.size + x
            value = prolonged[r : r + 1, :]
            value = value + jnp.where(lane_f == 0, p_lo[r] / 3.0, 0.0) + jnp.where(lane_f == fine.lanes - 1, p_hi[r] / 3.0, 0.0)
            own = fface[i, pl.ds(x, 1), :]
            fnew[i, 0, pl.ds(x, 1), :] = own - penalty * (own - value)
    lane_c = lax.broadcasted_iota(jnp.int32, (1, coarse.lanes), 1)
    r_lo, r_hi = [], []
    for i in range(6):
        rows = padded_rows(fine, fface, *halos, i)
        for c in range(coarse.size):
            terms = [(1.0, rows[3 * c]), (2.0, rows[3 * c + 1]), (3.0, rows[3 * c + 2]), (2.0, rows[3 * c + 3]),
                     (1.0, rows[3 * c + 4])]
            interior, lo, hi = combine(terms)
            r = i * coarse.size + c
            stage_r[pl.ds(r, 1), :] = interior / 9.0
            r_lo.append(lo / 9.0)
            r_hi.append(hi / 9.0)
    restricted = jnp.dot(stage_r[...], ry[...], precision=lax.Precision.HIGHEST, preferred_element_type=jnp.float32)
    for i in range(6):
        for c in range(coarse.size):
            r = i * coarse.size + c
            value = restricted[r : r + 1, :]
            value = value + jnp.where(lane_c == 0, r_lo[r] / 9.0, 0.0) + jnp.where(lane_c == coarse.lanes - 1, r_hi[r] / 9.0, 0.0)
            own = cface[i, pl.ds(c, 1), :]
            cnew[i, 0, pl.ds(c, 1), :] = own - penalty * (own - value)
    copies = []
    for n, (src, dst, depth) in enumerate(((fnew, fout, fine_depth), (cnew, cout, 0))):
        for k, (first, count, field) in enumerate(((0, 3, 0), (5, 1, 5), (3, 2, 7))):
            copy = pltpu.make_async_copy(
                src.at[pl.ds(first, count)], dst.at[pl.ds(field, count), pl.ds(depth, 1)], sems.at[3 * n + k]
            )
            copy.start()
            copies.append(copy)
    for copy in copies:
        copy.wait()


def row_ends(buf, blocks, at_end):
    out = []
    for b in blocks:
        chunk = b.chunks - 1 if at_end else 0
        first = b.fx_base + chunk
        lane = 127 if at_end else 0
        out.append(lax.slice(buf, (first, lane), (first + 5 * b.chunks + 1, lane + 1), (b.chunks, 1))[:, 0])
    return jnp.stack(out)


def with_corners(y_rim, x_lo, x_hi, blocks, at_end):
    lo, hi = row_ends(x_lo, blocks, at_end), row_ends(x_hi, blocks, at_end)
    extra = jnp.stack([lo, hi], axis=1).reshape(2 * len(blocks), 6)
    extra = jnp.pad(extra, ((0, 0), (0, 128 - 6)))
    joined = jnp.concatenate([y_rim, extra])
    return jnp.pad(joined, ((0, round8(joined.shape[0]) - joined.shape[0]), (0, 0)))


def face_call(blocks, fine_out, coarse_out, fine_face, coarse_face, rims):
    fine, coarse = blocks
    x_prev, x_next, y_prev, y_next = rims
    x_lo = shift_from(x_next, "gx", 1)
    x_hi = shift_from(x_prev, "gx", -1)
    y_lo = shift_from(with_corners(y_next, x_lo, x_hi, blocks, True), "gy", 1)
    y_hi = shift_from(with_corners(y_prev, x_lo, x_hi, blocks, False), "gy", -1)
    received = (x_lo, x_hi, y_lo, y_hi)
    py = jnp.asarray(prolong_y_matrix(coarse.lanes))
    ry = jnp.asarray(restrict_y_matrix(coarse.lanes))
    anyspace = pl.BlockSpec(memory_space=pl.ANY)
    return pl.pallas_call(
        functools.partial(face_kernel, blocks, fine.layers - 1),
        out_shape=(f32(fine_out.shape), f32(coarse_out.shape)),
        in_specs=[anyspace, anyspace] + vmem_specs(8) + [pl.BlockSpec(memory_space=pltpu.SMEM)],
        out_specs=(anyspace, anyspace),
        input_output_aliases={0: 0, 1: 1},
        scratch_shapes=[
            pltpu.VMEM((6, 1, fine.size, fine.lanes), jnp.float32),
            pltpu.VMEM((6, 1, coarse.size, coarse.lanes), jnp.float32),
            pltpu.VMEM((round8(6 * fine.size), coarse.lanes), jnp.float32),
            pltpu.VMEM((round8(6 * coarse.size), fine.lanes), jnp.float32),
            pltpu.SemaphoreType.DMA((6,)),
        ],
    )(fine_out, coarse_out, fine_face, coarse_face, *received, py, ry, edge_flags())


def local(
    fine_wave,
    fine_memory,
    fine_material,
    fine_mechanism,
    fine_metric,
    coarse_wave,
    coarse_memory,
    coarse_material,
    coarse_mechanism,
    material_table,
    attenuation_table,
):
    fine, coarse, x_rows, y_rows = plan_blocks(fine_wave.shape[1:], coarse_wave.shape[1:])
    blocks = (fine, coarse)
    smem = pl.BlockSpec(memory_space=pltpu.SMEM)
    flags = edge_flags()

    rims = pl.pallas_call(
        functools.partial(pack_kernel, blocks),
        out_shape=halo_shapes(x_rows, y_rows),
        in_specs=vmem_specs(2),
        out_specs=tuple(vmem_specs(4)),
    )(fine_wave, coarse_wave)
    halos = receive(rims)

    fine_velocity, coarse_velocity, *vrims = pl.pallas_call(
        functools.partial(velocity_kernel, blocks),
        out_shape=(f32((3,) + fine_wave.shape[1:]), f32((3,) + coarse_wave.shape[1:])) + halo_shapes(x_rows, y_rows),
        in_specs=vmem_specs(9) + [smem, smem],
        out_specs=tuple(vmem_specs(6)),
        scratch_shapes=[scratch_for(fine), scratch_for(coarse)],
    )(fine_wave, coarse_wave, *halos, fine_material, fine_metric, coarse_material, material_table, flags)

    vhalos = receive(vrims)
    fx_rows = 6 * (fine.chunks + coarse.chunks)
    fy_rows = round8(fine.size + coarse.size)
    fine_out, fine_mem, fine_face, coarse_out, coarse_mem, coarse_face, *face_rims = pl.pallas_call(
        functools.partial(stress_kernel, blocks),
        out_shape=(
            f32(fine_wave.shape), f32(fine_memory.shape), f32((6,) + fine_wave.shape[2:]),
            f32(coarse_wave.shape), f32(coarse_memory.shape), f32((6,) + coarse_wave.shape[2:]),
            f32((fx_rows, 128)), f32((fx_rows, 128)), f32((fy_rows, 128)), f32((fy_rows, 128)),
        ),
        in_specs=vmem_specs(15) + [smem, smem, smem],
        out_specs=tuple(vmem_specs(10)),
        scratch_shapes=[scratch_for(fine), scratch_for(coarse)],
    )(fine_wave, fine_memory, fine_velocity, coarse_wave, coarse_memory, coarse_velocity, *vhalos,
      fine_material, fine_mechanism, fine_metric, coarse_material, coarse_mechanism, material_table,
      attenuation_table, flags)

    fine_out, coarse_out = face_call(blocks, fine_out, coarse_out, fine_face, coarse_face, face_rims)
    return (fine_out, fine_mem, coarse_out, coarse_mem)


def solution(mesh):
    in_specs = (
        P(None, None, "gx", "gy"),
        P(None, None, "gx", "gy"),
        P(None, "gx", "gy"),
        P(None, "gx", "gy"),
        P(None, "gx", "gy"),
        P(None, None, "gx", "gy"),
        P(None, None, "gx", "gy"),
        P(None, "gx", "gy"),
        P(None, "gx", "gy"),
        P(),
        P(),
    )
    out_specs = (
        P(None, None, "gx", "gy"),
        P(None, None, "gx", "gy"),
        P(None, None, "gx", "gy"),
        P(None, None, "gx", "gy"),
    )

    return jax.shard_map(local, mesh=mesh, in_specs=in_specs, out_specs=out_specs, check_vma=False)
```

```python
import functools
import math

import jax
import jax.numpy as jnp
import numpy as np
from jax import lax
from jax.sharding import PartitionSpec as P

step_size = 0.1
penalty = 0.1 * 48.0 / 17.0
closure = [
    [-24.0 / 17.0, 59.0 / 34.0, -4.0 / 17.0, -3.0 / 34.0, 0.0, 0.0],
    [-0.5, 0.0, 0.5, 0.0, 0.0, 0.0],
    [4.0 / 43.0, -59.0 / 86.0, 0.0, 59.0 / 86.0, -4.0 / 43.0, 0.0],
    [3.0 / 98.0, 0.0, -59.0 / 98.0, 0.0, 32.0 / 49.0, -4.0 / 49.0],
]


def sbp_table(layers, spacing):
    return jnp.asarray(sbp_numpy(layers, spacing))


def sbp_numpy(layers, spacing):
    table = np.zeros((layers, layers))
    for line_at in range(4):
        for column in range(6):
            table[line_at, column] = closure[line_at][column]
            table[layers - 1 - line_at, layers - 1 - column] = -closure[line_at][column]
    for line_at in range(4, layers - 4):
        table[line_at, line_at - 2 : line_at + 3] = [
            1.0 / 12.0,
            -2.0 / 3.0,
            0.0,
            2.0 / 3.0,
            -1.0 / 12.0,
        ]
    return (table / spacing).astype(np.float32)


def shift_from(block, axis, offset):
    count = lax.axis_size(axis)
    pairs = [(i, (i + offset) % count) for i in range(count)]
    return lax.ppermute(block, axis, pairs)


def edge_flags():
    gx, gy = lax.axis_index("gx"), lax.axis_index("gy")
    nx, ny = lax.axis_size("gx"), lax.axis_size("gy")
    return jnp.stack([gx > 0, gx < nx - 1, gy > 0, gy < ny - 1]).astype(jnp.int32)


def valid_of(flags):
    return tuple(flags[k] != 0 for k in range(4))


def keep(ok, value):
    return jnp.where(ok, value, 0.0)


def packed_shift(blocks, axis, offset):
    sizes = [math.prod(b.shape) for b in blocks]
    joined = jnp.concatenate([b.reshape(-1) for b in blocks])
    moved = shift_from(joined, axis, offset)
    out, start = [], 0
    for b, size in zip(blocks, sizes):
        out.append(moved[start : start + size].reshape(b.shape))
        start += size
    return out


def exchange(blocks, width):
    x_lo = packed_shift([b[..., -width:, :] for b in blocks], "gx", 1)
    x_hi = packed_shift([b[..., :width, :] for b in blocks], "gx", -1)
    y_lo = packed_shift([b[..., -width:] for b in blocks], "gy", 1)
    y_hi = packed_shift([b[..., :width] for b in blocks], "gy", -1)
    return [(x_lo[i], x_hi[i], y_lo[i], y_hi[i]) for i in range(len(blocks))]


def central_diff(padded, along, spacing):
    length = padded.shape[along] - 4
    s = lambda o: lax.slice_in_dim(padded, o, o + length, axis=along)
    return (s(0) - 8.0 * s(1) + 8.0 * s(3) - s(4)) / (12.0 * spacing)


def diff_x(block, halo, spacing):
    x_lo, x_hi, _, _ = halo
    return central_diff(jnp.concatenate([x_lo, block, x_hi], axis=-2), block.ndim - 2, spacing)


def diff_y(block, halo, spacing):
    _, _, y_lo, y_hi = halo
    return central_diff(jnp.concatenate([y_lo, block, y_hi], axis=-1), block.ndim - 1, spacing)


def vertical_diff(fields, matrix):
    return jnp.einsum("kz,czxy->ckxy", matrix, fields, precision=lax.Precision.HIGHEST)


def lookup_table(grid_cell_index, values):
    result = jnp.zeros(grid_cell_index.shape, jnp.float32)
    for kind_at in range(values.shape[0]):
        result = jnp.where(grid_cell_index == kind_at, values[kind_at], result)
    return result


def velocity_step(wave, halo_x3, halo_y3, buoyancy, metric, matrix, spacing):
    sx = jnp.stack([wave[3], wave[6], wave[7]])
    sy = jnp.stack([wave[6], wave[4], wave[8]])
    slope_x = diff_x(sx, halo_x3, spacing)
    slope_y = diff_y(sy, halo_y3, spacing)
    slope_z = metric * vertical_diff(jnp.stack([wave[7], wave[8], wave[5]]), matrix)
    rate_x = slope_x[0] + slope_y[0] + slope_z[0]
    rate_y = slope_x[1] + slope_y[1] + slope_z[1]
    rate_z = slope_x[2] + slope_y[2] + slope_z[2]
    return wave[:3] + step_size * (buoyancy * jnp.stack([rate_x, rate_y, rate_z]))


def stress_step(wave, memory, velocity, halo, lame, shear, decay, strength, metric, matrix, spacing):
    slope_x = diff_x(velocity, halo, spacing)
    slope_y = diff_y(velocity, halo, spacing)
    slope_z = metric * vertical_diff(velocity, matrix)
    cell_volume = lame * (slope_x[0] + slope_y[1] + slope_z[2])
    rate = jnp.stack(
        [
            cell_volume + 2.0 * shear * slope_x[0],
            cell_volume + 2.0 * shear * slope_y[1],
            cell_volume + 2.0 * shear * slope_z[2],
            shear * (slope_y[0] + slope_x[1]),
            shear * (slope_z[0] + slope_x[2]),
            shear * (slope_z[1] + slope_y[2]),
        ]
    )
    memory_new = decay * memory + (1.0 - decay) * strength * rate
    stress = wave[3:] + step_size * (rate - memory_new)
    return stress, memory_new


def face_of(velocity, stress, depth):
    return jnp.stack(
        [
            velocity[0, depth],
            velocity[1, depth],
            velocity[2, depth],
            stress[4, depth],
            stress[5, depth],
            stress[2, depth],
        ]
    )


def pad_faces(faces):
    x_lo = packed_shift([f[:, -1:, :] for f in faces], "gx", 1)
    x_hi = packed_shift([f[:, :1, :] for f in faces], "gx", -1)
    faces = [jnp.concatenate([lo, f, hi], axis=1) for lo, f, hi in zip(x_lo, faces, x_hi)]
    y_lo = packed_shift([f[:, :, -1:] for f in faces], "gy", 1)
    y_hi = packed_shift([f[:, :, :1] for f in faces], "gy", -1)
    return [jnp.concatenate([lo, f, hi], axis=2) for lo, f, hi in zip(y_lo, faces, y_hi)]


def shifted(padded, offset, length, along):
    return lax.slice_in_dim(padded, offset, offset + length, axis=along)


def prolong_axis(padded, along):
    length = padded.shape[along] - 2
    left = shifted(padded, 0, length, along)
    middle = shifted(padded, 1, length, along)
    right = shifted(padded, 2, length, along)
    parts = jnp.stack(
        [(left + 2.0 * middle) / 3.0, middle, (2.0 * middle + right) / 3.0], axis=along + 1
    )
    shape = list(middle.shape)
    shape[along] = shape[along] * 3
    return parts.reshape(tuple(shape))


def split_three(padded, offset, length, along):
    part = shifted(padded, offset, 3 * length, along)
    return part.reshape(part.shape[:along] + (length, 3) + part.shape[along + 1 :])


def pick_part(parts, number, along):
    return lax.index_in_dim(parts, number, along + 1, keepdims=False)


def restrict_axis(padded, along):
    length = (padded.shape[along] - 2) // 3
    first = split_three(padded, 0, length, along)
    middle = split_three(padded, 1, length, along)
    last = split_three(padded, 2, length, along)
    return (
        pick_part(first, 0, along)
        + 2.0 * pick_part(middle, 0, along)
        + 3.0 * pick_part(middle, 1, along)
        + 2.0 * pick_part(middle, 2, along)
        + pick_part(last, 2, along)
    ) / 9.0


def assemble(velocity, stress, face, depth):
    replace = {0: face[0], 1: face[1], 2: face[2], 7: face[3], 8: face[4], 5: face[5]}
    fields = [velocity[0], velocity[1], velocity[2]] + [stress[k] for k in range(6)]
    rows = []
    for k, field in enumerate(fields):
        if k in replace:
            field = lax.dynamic_update_slice_in_dim(field, replace[k][None], depth, axis=0)
        rows.append(field)
    return jnp.stack(rows)


from jax.experimental import pallas as pl
from jax.experimental.pallas import tpu as pltpu


def sbp_rows(layers, spacing):
    table = sbp_numpy(layers, spacing)
    return [[(j, float(table[k, j])) for j in range(layers) if table[k, j] != 0.0] for k in range(layers)]


def pick(values_ref, row, index):
    result = jnp.zeros(index.shape, jnp.float32)
    for kind_at in range(values_ref.shape[1]):
        result = jnp.where(index == kind_at, values_ref[row, kind_at], result)
    return result


def fill_x(scratch, slot, lo, block, hi):
    width = lo.shape[-2]
    size = block.shape[-2]
    scratch[slot, :, 0:width, :] = lo
    scratch[slot, :, width : width + size, :] = block
    scratch[slot, :, width + size :, :] = hi


def slope_x(scratch, slot, z, size, spacing):
    s = lambda o: scratch[slot, z, o : o + size, :]
    return (s(0) - 8.0 * s(1) + 8.0 * s(3) - s(4)) / (12.0 * spacing)


def slope_y(f, lo, hi, spacing):
    n = f.shape[-1]
    lane = lax.broadcasted_iota(jnp.int32, f.shape, f.ndim - 1)
    m1 = jnp.where(lane == 0, lo[:, 1:2], pltpu.roll(f, 1, f.ndim - 1))
    m2 = jnp.where(lane == 0, lo[:, 0:1], jnp.where(lane == 1, lo[:, 1:2], pltpu.roll(f, 2, f.ndim - 1)))
    p1 = jnp.where(lane == n - 1, hi[:, 0:1], pltpu.roll(f, n - 1, f.ndim - 1))
    p2 = jnp.where(lane == n - 2, hi[:, 0:1], jnp.where(lane == n - 1, hi[:, 1:2], pltpu.roll(f, n - 2, f.ndim - 1)))
    return (m2 - 8.0 * m1 + 8.0 * p1 - p2) / (12.0 * spacing)


def slope_z(field_ref, index, row):
    total = None
    for j, weight in row:
        term = jnp.float32(weight) * field_ref[index, j]
        total = term if total is None else total + term
    return total


class Block:
    def __init__(self, shape, spacing, has_metric, x_base, y_base):
        self.layers, self.size, self.lanes = shape
        self.chunks = self.lanes // 128
        self.spacing = spacing
        self.has_metric = has_metric
        self.rows = sbp_rows(self.layers, spacing)
        self.x_base, self.y_base = x_base, y_base

    @property
    def x_rows(self):
        return 3 * self.layers * self.chunks * 2

    @property
    def y_rows(self):
        return self.layers * self.size


def plan_blocks(fine_shape, coarse_shape):
    fine = Block(fine_shape, 1.0, True, 0, 0)
    coarse = Block(coarse_shape, 3.0, False, fine.x_rows, fine.y_rows)
    fine.fx_base, fine.fy_base = 0, 0
    coarse.fx_base, coarse.fy_base = 6 * fine.chunks, fine.size
    corner_base = fine.size + coarse.size
    fine.corner_rows = (corner_base, corner_base + 1)
    coarse.corner_rows = (corner_base + 2, corner_base + 3)
    return fine, coarse, fine.x_rows + coarse.x_rows, fine.y_rows + coarse.y_rows


def round8(n):
    return -(-n // 8) * 8


def write_rims(b, src, fields, x_prev, x_next, y_prev, y_next):
    size, lanes = b.size, b.lanes
    for c, field in enumerate(fields):
        for z in range(b.layers):
            lo = src[field, z, 0:2, :]
            hi = src[field, z, size - 2 : size, :]
            for j in range(b.chunks):
                row = b.x_base + ((c * b.layers + z) * b.chunks + j) * 2
                x_prev[row : row + 2, :] = lo[:, j * 128 : (j + 1) * 128]
                x_next[row : row + 2, :] = hi[:, j * 128 : (j + 1) * 128]
    lane = lax.broadcasted_iota(jnp.int32, (size, 128), 1)
    for z in range(b.layers):
        acc_lo = jnp.zeros((size, 128), jnp.float32)
        acc_hi = jnp.zeros((size, 128), jnp.float32)
        for c, field in enumerate(fields):
            v = src[field, z]
            rl = v if c == 0 else pltpu.roll(v, 2 * c, 1)
            rh = pltpu.roll(v, (2 * c + 2) % lanes, 1)
            keep = (lane >= 2 * c) & (lane < 2 * c + 2)
            acc_lo = jnp.where(keep, rl[:, 0:128], acc_lo)
            acc_hi = jnp.where(keep, rh[:, 0:128], acc_hi)
        row = b.y_base + z * size
        y_prev[row : row + size, :] = acc_lo
        y_next[row : row + size, :] = acc_hi


def read_x_halo(b, buf, c, z):
    parts = [buf[pl.ds(b.x_base + ((c * b.layers + z) * b.chunks + j) * 2, 2), :] for j in range(b.chunks)]
    return parts[0] if len(parts) == 1 else jnp.concatenate(parts, axis=1)


def read_y_halo(b, buf, c, z, ok):
    row = b.y_base + z * b.size
    return keep(ok, buf[pl.ds(row, b.size), pl.ds(2 * c, 1)]), keep(ok, buf[pl.ds(row, b.size), pl.ds(2 * c + 1, 1)])


def fill_x2(b, scratch, slot, src, field, lo_buf, hi_buf, valid):
    size = b.size
    scratch[slot, :, 2 : 2 + size, :] = src[field]
    for z in range(b.layers):
        scratch[slot, z, 0:2, :] = keep(valid[0], read_x_halo(b, lo_buf, slot, z))
        scratch[slot, z, 2 + size :, :] = keep(valid[1], read_x_halo(b, hi_buf, slot, z))


def slope_y2(f, lo, hi, spacing):
    n = f.shape[-1]
    lane = lax.broadcasted_iota(jnp.int32, f.shape, 1)
    m1 = jnp.where(lane == 0, lo[1], pltpu.roll(f, 1, 1))
    m2 = jnp.where(lane == 0, lo[0], jnp.where(lane == 1, lo[1], pltpu.roll(f, 2, 1)))
    p1 = jnp.where(lane == n - 1, hi[0], pltpu.roll(f, n - 1, 1))
    p2 = jnp.where(lane == n - 2, hi[0], jnp.where(lane == n - 1, hi[1], pltpu.roll(f, n - 2, 1)))
    return (m2 - 8.0 * m1 + 8.0 * p1 - p2) / (12.0 * spacing)


STRESS_X = (3, 6, 7)
STRESS_Y = (6, 4, 8)
VELOCITY = (0, 1, 2)


def pack_kernel(blocks, fw, cw, x_prev, x_next, y_prev, y_next):
    for b, w in zip(blocks, (fw, cw)):
        write_rims_split(b, w, x_prev, x_next, y_prev, y_next)


def write_rims_split(b, w, x_prev, x_next, y_prev, y_next):
    size, lanes = b.size, b.lanes
    for c, field in enumerate(STRESS_X):
        for z in range(b.layers):
            lo = w[field, z, 0:2, :]
            hi = w[field, z, size - 2 : size, :]
            for j in range(b.chunks):
                row = b.x_base + ((c * b.layers + z) * b.chunks + j) * 2
                x_prev[row : row + 2, :] = lo[:, j * 128 : (j + 1) * 128]
                x_next[row : row + 2, :] = hi[:, j * 128 : (j + 1) * 128]
    lane = lax.broadcasted_iota(jnp.int32, (size, 128), 1)
    for z in range(b.layers):
        acc_lo = jnp.zeros((size, 128), jnp.float32)
        acc_hi = jnp.zeros((size, 128), jnp.float32)
        for c, field in enumerate(STRESS_Y):
            v = w[field, z]
            rl = v if c == 0 else pltpu.roll(v, 2 * c, 1)
            rh = pltpu.roll(v, (2 * c + 2) % lanes, 1)
            keep = (lane >= 2 * c) & (lane < 2 * c + 2)
            acc_lo = jnp.where(keep, rl[:, 0:128], acc_lo)
            acc_hi = jnp.where(keep, rh[:, 0:128], acc_hi)
        row = b.y_base + z * size
        y_prev[row : row + size, :] = acc_lo
        y_next[row : row + size, :] = acc_hi


def velocity_block(b, w, mat, metric, table, out, sx, hx_lo, hx_hi, hy_lo, hy_hi, valid):
    for slot, field in enumerate(STRESS_X):
        fill_x2(b, sx, slot, w, field, hx_lo, hx_hi, valid)
    for z in range(b.layers):
        dx = [slope_x(sx, slot, z, b.size, b.spacing) for slot in range(3)]
        dy = [
            slope_y2(w[field, z], read_y_halo(b, hy_lo, slot, z, valid[2]), read_y_halo(b, hy_hi, slot, z, valid[3]),
                     b.spacing)
            for slot, field in enumerate(STRESS_Y)
        ]
        dz = [slope_z(w, field, b.rows[z]) for field in (7, 8, 5)]
        if metric is not None:
            m = metric[z]
            dz = [m * d for d in dz]
        buoy = pick(table, 0, mat[z])
        for k in range(3):
            out[k, z] = w[k, z] + step_size * (buoy * (dx[k] + dy[k] + dz[k]))


def velocity_kernel(blocks, fw, cw, hx_lo, hx_hi, hy_lo, hy_hi, fmat, fmetric, cmat, table, flags,
                    fvel, cvel, vx_prev, vx_next, vy_prev, vy_next, sx_f, sx_c):
    fine, coarse = blocks
    valid = valid_of(flags)
    velocity_block(fine, fw, fmat, fmetric, table, fvel, sx_f, hx_lo, hx_hi, hy_lo, hy_hi, valid)
    velocity_block(coarse, cw, cmat, None, table, cvel, sx_c, hx_lo, hx_hi, hy_lo, hy_hi, valid)
    write_rims(fine, fvel, VELOCITY, vx_prev, vx_next, vy_prev, vy_next)
    write_rims(coarse, cvel, VELOCITY, vx_prev, vx_next, vy_prev, vy_next)


def stress_block(b, depth, w, mem, vel, mat, mech, metric, mtab, atab, out, mem_out, face, sx,
                 hx_lo, hx_hi, hy_lo, hy_hi, face_rims, valid):
    for slot in range(3):
        fill_x2(b, sx, slot, vel, slot, hx_lo, hx_hi, valid)
    for z in range(b.layers):
        dx = [slope_x(sx, slot, z, b.size, b.spacing) for slot in range(3)]
        dy = [
            slope_y2(vel[slot, z], read_y_halo(b, hy_lo, slot, z, valid[2]), read_y_halo(b, hy_hi, slot, z, valid[3]),
                     b.spacing)
            for slot in range(3)
        ]
        dz = [slope_z(vel, slot, b.rows[z]) for slot in range(3)]
        if metric is not None:
            m = metric[z]
            dz = [m * d for d in dz]
        kind, mechanism = mat[z], mech[z]
        lame, shear = pick(mtab, 1, kind), pick(mtab, 2, kind)
        decay, strength = pick(atab, 0, mechanism), pick(atab, 1, mechanism)
        cell_volume = lame * (dx[0] + dy[1] + dz[2])
        rate = [
            cell_volume + 2.0 * shear * dx[0],
            cell_volume + 2.0 * shear * dy[1],
            cell_volume + 2.0 * shear * dz[2],
            shear * (dy[0] + dx[1]),
            shear * (dz[0] + dx[2]),
            shear * (dz[1] + dy[2]),
        ]
        values = []
        for k in range(3):
            v = vel[k, z]
            out[k, z] = v
            values.append(v)
        for k in range(6):
            memory_new = decay * mem[k, z] + (1.0 - decay) * strength * rate[k]
            mem_out[k, z] = memory_new
            stress = w[3 + k, z] + step_size * (rate[k] - memory_new)
            out[3 + k, z] = stress
            values.append(stress)
        if z == depth:
            for i, k in enumerate((0, 1, 2, 7, 8, 5)):
                face[i] = values[k]
            write_face_rims(b, [values[k] for k in (0, 1, 2, 7, 8, 5)], *face_rims)


def write_face_rims(b, planes, x_prev, x_next, y_prev, y_next):
    size, lanes = b.size, b.lanes
    for i, v in enumerate(planes):
        for j in range(b.chunks):
            row = b.fx_base + i * b.chunks + j
            x_prev[row : row + 1, :] = v[0:1, j * 128 : (j + 1) * 128]
            x_next[row : row + 1, :] = v[size - 1 : size, j * 128 : (j + 1) * 128]
    lane = lax.broadcasted_iota(jnp.int32, (size, 128), 1)
    acc_lo = jnp.zeros((size, 128), jnp.float32)
    acc_hi = jnp.zeros((size, 128), jnp.float32)
    for i, v in enumerate(planes):
        rl = v if i == 0 else pltpu.roll(v, i, 1)
        rh = pltpu.roll(v, (i + 1) % lanes, 1)
        acc_lo = jnp.where(lane == i, rl[:, 0:128], acc_lo)
        acc_hi = jnp.where(lane == i, rh[:, 0:128], acc_hi)
    y_prev[b.fy_base : b.fy_base + size, :] = acc_lo
    y_next[b.fy_base : b.fy_base + size, :] = acc_hi


def stress_kernel(blocks, fw, fmem, fvel, cw, cmem, cvel, hx_lo, hx_hi, hy_lo, hy_hi,
                  fmat, fmech, fmetric, cmat, cmech, mtab, atab, flags,
                  fout, fmem_out, fface, cout, cmem_out, cface, rx_prev, rx_next, ry_prev, ry_next, sx_f, sx_c):
    fine, coarse = blocks
    valid = valid_of(flags)
    rims = (rx_prev, rx_next, ry_prev, ry_next)
    stress_block(fine, fine.layers - 1, fw, fmem, fvel, fmat, fmech, fmetric, mtab, atab, fout, fmem_out,
                 fface, sx_f, hx_lo, hx_hi, hy_lo, hy_hi, rims, valid)
    stress_block(coarse, 0, cw, cmem, cvel, cmat, cmech, None, mtab, atab, cout, cmem_out,
                 cface, sx_c, hx_lo, hx_hi, hy_lo, hy_hi, rims, valid)


def vmem_specs(count):
    return [pl.BlockSpec(memory_space=pltpu.VMEM)] * count


def f32(shape):
    return jax.ShapeDtypeStruct(shape, jnp.float32)


def halo_shapes(x_rows, y_rows):
    return (f32((x_rows, 128)), f32((x_rows, 128)), f32((y_rows, 128)), f32((y_rows, 128)))


def scratch_for(b):
    return pltpu.VMEM((3, b.layers, b.size + 4, b.lanes), jnp.float32)


def receive(buffers):
    x_prev, x_next, y_prev, y_next = buffers
    y_lo = shift_from(y_next, "gy", 1)
    y_hi = shift_from(y_prev, "gy", -1)
    x_lo = shift_from(x_next, "gx", 1)
    x_hi = shift_from(x_prev, "gx", -1)
    return x_lo, x_hi, y_lo, y_hi


def put_face(out, face, depth):
    out = lax.dynamic_update_slice(out, face[0:3][:, None], (0, depth, 0, 0))
    out = lax.dynamic_update_slice(out, face[5:6][:, None], (5, depth, 0, 0))
    out = lax.dynamic_update_slice(out, face[3:5][:, None], (7, depth, 0, 0))
    return out


def prolong_y_matrix(coarse_lanes):
    m = np.zeros((coarse_lanes, 3 * coarse_lanes), np.float32)
    for d in range(coarse_lanes):
        m[d, 3 * d] = 2.0 / 3.0
        m[d, 3 * d + 1] = 1.0
        m[d, 3 * d + 2] = 2.0 / 3.0
        if d >= 1:
            m[d - 1, 3 * d] = 1.0 / 3.0
        if d + 1 < coarse_lanes:
            m[d + 1, 3 * d + 2] = 1.0 / 3.0
    return m


def restrict_y_matrix(coarse_lanes):
    m = np.zeros((3 * coarse_lanes, coarse_lanes), np.float32)
    for c in range(coarse_lanes):
        for offset, weight in ((-1, 1.0), (0, 2.0), (1, 3.0), (2, 2.0), (3, 1.0)):
            f = 3 * c + offset
            if 0 <= f < 3 * coarse_lanes:
                m[f, c] = weight / 9.0
    return m


def padded_rows(b, face, hx_lo, hx_hi, hy_lo, hy_hi, valid, i):
    size = b.size

    def x_row(buf):
        parts = [buf[pl.ds(b.fx_base + i * b.chunks + j, 1), :] for j in range(b.chunks)]
        return parts[0] if len(parts) == 1 else jnp.concatenate(parts, axis=1)

    def lane_of(buf, row, ok):
        return keep(ok, buf[pl.ds(row, 1), pl.ds(i, 1)])

    x_lo_ok, x_hi_ok, y_lo_ok, y_hi_ok = valid
    lo_row, hi_row = b.corner_rows
    rows = [(keep(x_lo_ok, x_row(hx_lo)), lane_of(hy_lo, lo_row, x_lo_ok & y_lo_ok),
             lane_of(hy_hi, lo_row, x_lo_ok & y_hi_ok))]
    for x in range(size):
        rows.append((face[i, pl.ds(x, 1), :], lane_of(hy_lo, b.fy_base + x, y_lo_ok),
                     lane_of(hy_hi, b.fy_base + x, y_hi_ok)))
    rows.append((keep(x_hi_ok, x_row(hx_hi)), lane_of(hy_lo, hi_row, x_hi_ok & y_lo_ok),
                 lane_of(hy_hi, hi_row, x_hi_ok & y_hi_ok)))
    return rows


def combine(terms):
    out = []
    for part in range(3):
        total = None
        for weight, row in terms:
            v = row[part] if weight == 1.0 else weight * row[part]
            total = v if total is None else total + v
        out.append(total)
    return out


def face_kernel(blocks, fine_depth, fout_in, cout_in, fface, cface, hx_lo, hx_hi, hy_lo, hy_hi,
                py, ry, flags, fout, cout, fnew, cnew, stage_p, stage_r, sems):
    fine, coarse = blocks
    halos = (hx_lo, hx_hi, hy_lo, hy_hi, valid_of(flags))
    lane_f = lax.broadcasted_iota(jnp.int32, (1, fine.lanes), 1)
    p_lo, p_hi = [], []
    for i in range(6):
        rows = padded_rows(coarse, cface, *halos, i)
        for c in range(coarse.size):
            left, middle, right = rows[c], rows[c + 1], rows[c + 2]
            parts = [
                [(1.0, left), (2.0, middle)],
                [(1.0, middle)],
                [(2.0, middle), (1.0, right)],
            ]
            for a, terms in enumerate(parts):
                interior, lo, hi = combine(terms)
                if a != 1:
                    interior, lo, hi = interior / 3.0, lo / 3.0, hi / 3.0
                r = i * fine.size + 3 * c + a
                stage_p[pl.ds(r, 1), :] = interior
                p_lo.append(lo)
                p_hi.append(hi)
    prolonged = jnp.dot(stage_p[...], py[...], precision=lax.Precision.HIGHEST, preferred_element_type=jnp.float32)
    for i in range(6):
        for x in range(fine.size):
            r = i * fine.size + x
            value = prolonged[r : r + 1, :]
            value = value + jnp.where(lane_f == 0, p_lo[r] / 3.0, 0.0) + jnp.where(lane_f == fine.lanes - 1, p_hi[r] / 3.0, 0.0)
            own = fface[i, pl.ds(x, 1), :]
            fnew[i, 0, pl.ds(x, 1), :] = own - penalty * (own - value)
    lane_c = lax.broadcasted_iota(jnp.int32, (1, coarse.lanes), 1)
    r_lo, r_hi = [], []
    for i in range(6):
        rows = padded_rows(fine, fface, *halos, i)
        for c in range(coarse.size):
            terms = [(1.0, rows[3 * c]), (2.0, rows[3 * c + 1]), (3.0, rows[3 * c + 2]), (2.0, rows[3 * c + 3]),
                     (1.0, rows[3 * c + 4])]
            interior, lo, hi = combine(terms)
            r = i * coarse.size + c
            stage_r[pl.ds(r, 1), :] = interior / 9.0
            r_lo.append(lo / 9.0)
            r_hi.append(hi / 9.0)
    restricted = jnp.dot(stage_r[...], ry[...], precision=lax.Precision.HIGHEST, preferred_element_type=jnp.float32)
    for i in range(6):
        for c in range(coarse.size):
            r = i * coarse.size + c
            value = restricted[r : r + 1, :]
            value = value + jnp.where(lane_c == 0, r_lo[r] / 9.0, 0.0) + jnp.where(lane_c == coarse.lanes - 1, r_hi[r] / 9.0, 0.0)
            own = cface[i, pl.ds(c, 1), :]
            cnew[i, 0, pl.ds(c, 1), :] = own - penalty * (own - value)
    copies = []
    for n, (src, dst, depth) in enumerate(((fnew, fout, fine_depth), (cnew, cout, 0))):
        for k, (first, count, field) in enumerate(((0, 3, 0), (5, 1, 5), (3, 2, 7))):
            copy = pltpu.make_async_copy(
                src.at[pl.ds(first, count)], dst.at[pl.ds(field, count), pl.ds(depth, 1)], sems.at[3 * n + k]
            )
            copy.start()
            copies.append(copy)
    for copy in copies:
        copy.wait()


def diag_from(block, dx, dy):
    nx, ny = lax.axis_size("gx"), lax.axis_size("gy")
    pairs = []
    for i in range(nx):
        for j in range(ny):
            if 0 <= i + dx < nx and 0 <= j + dy < ny:
                pairs.append((i * ny + j, (i + dx) * ny + (j + dy)))
    return lax.ppermute(block, ("gx", "gy"), pairs)


def row_ends(buf, blocks, at_end):
    out = []
    for b in blocks:
        chunk = b.chunks - 1 if at_end else 0
        first = b.fx_base + chunk
        lane = 127 if at_end else 0
        out.append(lax.slice(buf, (first, lane), (first + 5 * b.chunks + 1, lane + 1), (b.chunks, 1))[:, 0])
    return jnp.stack(out)


def with_corners(y_rim, x_lo, x_hi, blocks, at_end):
    lo, hi = row_ends(x_lo, blocks, at_end), row_ends(x_hi, blocks, at_end)
    extra = jnp.stack([lo, hi], axis=1).reshape(2 * len(blocks), 6)
    extra = jnp.pad(extra, ((0, 0), (0, 128 - 6)))
    return lax.dynamic_update_slice(y_rim, extra, (blocks[0].corner_rows[0], 0))


def face_call(blocks, fine_out, coarse_out, fine_face, coarse_face, rims):
    fine, coarse = blocks
    x_prev, x_next, y_prev, y_next = rims
    x_lo = shift_from(x_next, "gx", 1)
    x_hi = shift_from(x_prev, "gx", -1)
    y_lo = shift_from(with_corners(y_next, x_lo, x_hi, blocks, True), "gy", 1)
    y_hi = shift_from(with_corners(y_prev, x_lo, x_hi, blocks, False), "gy", -1)
    received = (x_lo, x_hi, y_lo, y_hi)
    py = jnp.asarray(prolong_y_matrix(coarse.lanes))
    ry = jnp.asarray(restrict_y_matrix(coarse.lanes))
    anyspace = pl.BlockSpec(memory_space=pl.ANY)
    return pl.pallas_call(
        functools.partial(face_kernel, blocks, fine.layers - 1),
        out_shape=(f32(fine_out.shape), f32(coarse_out.shape)),
        in_specs=[anyspace, anyspace] + vmem_specs(8) + [pl.BlockSpec(memory_space=pltpu.SMEM)],
        out_specs=(anyspace, anyspace),
        input_output_aliases={0: 0, 1: 1},
        scratch_shapes=[
            pltpu.VMEM((6, 1, fine.size, fine.lanes), jnp.float32),
            pltpu.VMEM((6, 1, coarse.size, coarse.lanes), jnp.float32),
            pltpu.VMEM((round8(6 * fine.size), coarse.lanes), jnp.float32),
            pltpu.VMEM((round8(6 * coarse.size), fine.lanes), jnp.float32),
            pltpu.SemaphoreType.DMA((6,)),
        ],
    )(fine_out, coarse_out, fine_face, coarse_face, *received, py, ry, edge_flags())


def local(
    fine_wave,
    fine_memory,
    fine_material,
    fine_mechanism,
    fine_metric,
    coarse_wave,
    coarse_memory,
    coarse_material,
    coarse_mechanism,
    material_table,
    attenuation_table,
):
    fine, coarse, x_rows, y_rows = plan_blocks(fine_wave.shape[1:], coarse_wave.shape[1:])
    blocks = (fine, coarse)
    smem = pl.BlockSpec(memory_space=pltpu.SMEM)
    flags = edge_flags()

    rims = pl.pallas_call(
        functools.partial(pack_kernel, blocks),
        out_shape=halo_shapes(x_rows, y_rows),
        in_specs=vmem_specs(2),
        out_specs=tuple(vmem_specs(4)),
    )(fine_wave, coarse_wave)
    halos = receive(rims)

    fine_velocity, coarse_velocity, *vrims = pl.pallas_call(
        functools.partial(velocity_kernel, blocks),
        out_shape=(f32((3,) + fine_wave.shape[1:]), f32((3,) + coarse_wave.shape[1:])) + halo_shapes(x_rows, y_rows),
        in_specs=vmem_specs(9) + [smem, smem],
        out_specs=tuple(vmem_specs(6)),
        scratch_shapes=[scratch_for(fine), scratch_for(coarse)],
    )(fine_wave, coarse_wave, *halos, fine_material, fine_metric, coarse_material, material_table, flags)

    vhalos = receive(vrims)
    fx_rows = 6 * (fine.chunks + coarse.chunks)
    fy_rows = round8(fine.size + coarse.size + 4)
    fine_out, fine_mem, fine_face, coarse_out, coarse_mem, coarse_face, *face_rims = pl.pallas_call(
        functools.partial(stress_kernel, blocks),
        out_shape=(
            f32(fine_wave.shape), f32(fine_memory.shape), f32((6,) + fine_wave.shape[2:]),
            f32(coarse_wave.shape), f32(coarse_memory.shape), f32((6,) + coarse_wave.shape[2:]),
            f32((fx_rows, 128)), f32((fx_rows, 128)), f32((fy_rows, 128)), f32((fy_rows, 128)),
        ),
        in_specs=vmem_specs(15) + [smem, smem, smem],
        out_specs=tuple(vmem_specs(10)),
        scratch_shapes=[scratch_for(fine), scratch_for(coarse)],
    )(fine_wave, fine_memory, fine_velocity, coarse_wave, coarse_memory, coarse_velocity, *vhalos,
      fine_material, fine_mechanism, fine_metric, coarse_material, coarse_mechanism, material_table,
      attenuation_table, flags)

    fine_out, coarse_out = face_call(blocks, fine_out, coarse_out, fine_face, coarse_face, face_rims)
    return (fine_out, fine_mem, coarse_out, coarse_mem)


def solution(mesh):
    in_specs = (
        P(None, None, "gx", "gy"),
        P(None, None, "gx", "gy"),
        P(None, "gx", "gy"),
        P(None, "gx", "gy"),
        P(None, "gx", "gy"),
        P(None, None, "gx", "gy"),
        P(None, None, "gx", "gy"),
        P(None, "gx", "gy"),
        P(None, "gx", "gy"),
        P(),
        P(),
    )
    out_specs = (
        P(None, None, "gx", "gy"),
        P(None, None, "gx", "gy"),
        P(None, None, "gx", "gy"),
        P(None, None, "gx", "gy"),
    )
    return jax.shard_map(local, mesh=mesh, in_specs=in_specs, out_specs=out_specs, check_vma=False)
```

```python
import functools
import math

import jax
import jax.numpy as jnp
import numpy as np
from jax import lax
from jax.sharding import PartitionSpec as P

step_size = 0.1
penalty = 0.1 * 48.0 / 17.0
closure = [
    [-24.0 / 17.0, 59.0 / 34.0, -4.0 / 17.0, -3.0 / 34.0, 0.0, 0.0],
    [-0.5, 0.0, 0.5, 0.0, 0.0, 0.0],
    [4.0 / 43.0, -59.0 / 86.0, 0.0, 59.0 / 86.0, -4.0 / 43.0, 0.0],
    [3.0 / 98.0, 0.0, -59.0 / 98.0, 0.0, 32.0 / 49.0, -4.0 / 49.0],
]


def sbp_table(layers, spacing):
    return jnp.asarray(sbp_numpy(layers, spacing))


def sbp_numpy(layers, spacing):
    table = np.zeros((layers, layers))
    for line_at in range(4):
        for column in range(6):
            table[line_at, column] = closure[line_at][column]
            table[layers - 1 - line_at, layers - 1 - column] = -closure[line_at][column]
    for line_at in range(4, layers - 4):
        table[line_at, line_at - 2 : line_at + 3] = [
            1.0 / 12.0,
            -2.0 / 3.0,
            0.0,
            2.0 / 3.0,
            -1.0 / 12.0,
        ]
    return (table / spacing).astype(np.float32)


def shift_from(block, axis, offset):
    count = lax.axis_size(axis)
    pairs = [(i, (i + offset) % count) for i in range(count)]
    return lax.ppermute(block, axis, pairs)


def edge_flags():
    gx, gy = lax.axis_index("gx"), lax.axis_index("gy")
    nx, ny = lax.axis_size("gx"), lax.axis_size("gy")
    return jnp.stack([gx > 0, gx < nx - 1, gy > 0, gy < ny - 1]).astype(jnp.int32)


def valid_of(flags):
    return tuple(flags[k] != 0 for k in range(4))


def keep(ok, value):
    return jnp.where(ok, value, 0.0)


def packed_shift(blocks, axis, offset):
    sizes = [math.prod(b.shape) for b in blocks]
    joined = jnp.concatenate([b.reshape(-1) for b in blocks])
    moved = shift_from(joined, axis, offset)
    out, start = [], 0
    for b, size in zip(blocks, sizes):
        out.append(moved[start : start + size].reshape(b.shape))
        start += size
    return out


def exchange(blocks, width):
    x_lo = packed_shift([b[..., -width:, :] for b in blocks], "gx", 1)
    x_hi = packed_shift([b[..., :width, :] for b in blocks], "gx", -1)
    y_lo = packed_shift([b[..., -width:] for b in blocks], "gy", 1)
    y_hi = packed_shift([b[..., :width] for b in blocks], "gy", -1)
    return [(x_lo[i], x_hi[i], y_lo[i], y_hi[i]) for i in range(len(blocks))]


def central_diff(padded, along, spacing):
    length = padded.shape[along] - 4
    s = lambda o: lax.slice_in_dim(padded, o, o + length, axis=along)
    return (s(0) - 8.0 * s(1) + 8.0 * s(3) - s(4)) / (12.0 * spacing)


def diff_x(block, halo, spacing):
    x_lo, x_hi, _, _ = halo
    return central_diff(jnp.concatenate([x_lo, block, x_hi], axis=-2), block.ndim - 2, spacing)


def diff_y(block, halo, spacing):
    _, _, y_lo, y_hi = halo
    return central_diff(jnp.concatenate([y_lo, block, y_hi], axis=-1), block.ndim - 1, spacing)


def vertical_diff(fields, matrix):
    return jnp.einsum("kz,czxy->ckxy", matrix, fields, precision=lax.Precision.HIGHEST)


def lookup_table(grid_cell_index, values):
    result = jnp.zeros(grid_cell_index.shape, jnp.float32)
    for kind_at in range(values.shape[0]):
        result = jnp.where(grid_cell_index == kind_at, values[kind_at], result)
    return result


def velocity_step(wave, halo_x3, halo_y3, buoyancy, metric, matrix, spacing):
    sx = jnp.stack([wave[3], wave[6], wave[7]])
    sy = jnp.stack([wave[6], wave[4], wave[8]])
    slope_x = diff_x(sx, halo_x3, spacing)
    slope_y = diff_y(sy, halo_y3, spacing)
    slope_z = metric * vertical_diff(jnp.stack([wave[7], wave[8], wave[5]]), matrix)
    rate_x = slope_x[0] + slope_y[0] + slope_z[0]
    rate_y = slope_x[1] + slope_y[1] + slope_z[1]
    rate_z = slope_x[2] + slope_y[2] + slope_z[2]
    return wave[:3] + step_size * (buoyancy * jnp.stack([rate_x, rate_y, rate_z]))


def stress_step(wave, memory, velocity, halo, lame, shear, decay, strength, metric, matrix, spacing):
    slope_x = diff_x(velocity, halo, spacing)
    slope_y = diff_y(velocity, halo, spacing)
    slope_z = metric * vertical_diff(velocity, matrix)
    cell_volume = lame * (slope_x[0] + slope_y[1] + slope_z[2])
    rate = jnp.stack(
        [
            cell_volume + 2.0 * shear * slope_x[0],
            cell_volume + 2.0 * shear * slope_y[1],
            cell_volume + 2.0 * shear * slope_z[2],
            shear * (slope_y[0] + slope_x[1]),
            shear * (slope_z[0] + slope_x[2]),
            shear * (slope_z[1] + slope_y[2]),
        ]
    )
    memory_new = decay * memory + (1.0 - decay) * strength * rate
    stress = wave[3:] + step_size * (rate - memory_new)
    return stress, memory_new


def face_of(velocity, stress, depth):
    return jnp.stack(
        [
            velocity[0, depth],
            velocity[1, depth],
            velocity[2, depth],
            stress[4, depth],
            stress[5, depth],
            stress[2, depth],
        ]
    )


def pad_faces(faces):
    x_lo = packed_shift([f[:, -1:, :] for f in faces], "gx", 1)
    x_hi = packed_shift([f[:, :1, :] for f in faces], "gx", -1)
    faces = [jnp.concatenate([lo, f, hi], axis=1) for lo, f, hi in zip(x_lo, faces, x_hi)]
    y_lo = packed_shift([f[:, :, -1:] for f in faces], "gy", 1)
    y_hi = packed_shift([f[:, :, :1] for f in faces], "gy", -1)
    return [jnp.concatenate([lo, f, hi], axis=2) for lo, f, hi in zip(y_lo, faces, y_hi)]


def shifted(padded, offset, length, along):
    return lax.slice_in_dim(padded, offset, offset + length, axis=along)


def prolong_axis(padded, along):
    length = padded.shape[along] - 2
    left = shifted(padded, 0, length, along)
    middle = shifted(padded, 1, length, along)
    right = shifted(padded, 2, length, along)
    parts = jnp.stack(
        [(left + 2.0 * middle) / 3.0, middle, (2.0 * middle + right) / 3.0], axis=along + 1
    )
    shape = list(middle.shape)
    shape[along] = shape[along] * 3
    return parts.reshape(tuple(shape))


def split_three(padded, offset, length, along):
    part = shifted(padded, offset, 3 * length, along)
    return part.reshape(part.shape[:along] + (length, 3) + part.shape[along + 1 :])


def pick_part(parts, number, along):
    return lax.index_in_dim(parts, number, along + 1, keepdims=False)


def restrict_axis(padded, along):
    length = (padded.shape[along] - 2) // 3
    first = split_three(padded, 0, length, along)
    middle = split_three(padded, 1, length, along)
    last = split_three(padded, 2, length, along)
    return (
        pick_part(first, 0, along)
        + 2.0 * pick_part(middle, 0, along)
        + 3.0 * pick_part(middle, 1, along)
        + 2.0 * pick_part(middle, 2, along)
        + pick_part(last, 2, along)
    ) / 9.0


def assemble(velocity, stress, face, depth):
    replace = {0: face[0], 1: face[1], 2: face[2], 7: face[3], 8: face[4], 5: face[5]}
    fields = [velocity[0], velocity[1], velocity[2]] + [stress[k] for k in range(6)]
    rows = []
    for k, field in enumerate(fields):
        if k in replace:
            field = lax.dynamic_update_slice_in_dim(field, replace[k][None], depth, axis=0)
        rows.append(field)
    return jnp.stack(rows)


from jax.experimental import pallas as pl
from jax.experimental.pallas import tpu as pltpu


def sbp_rows(layers, spacing):
    table = sbp_numpy(layers, spacing)
    return [[(j, float(table[k, j])) for j in range(layers) if table[k, j] != 0.0] for k in range(layers)]


def pick(values_ref, row, index):
    result = jnp.zeros(index.shape, jnp.float32)
    for kind_at in range(values_ref.shape[1]):
        result = jnp.where(index == kind_at, values_ref[row, kind_at], result)
    return result


def fill_x(scratch, slot, lo, block, hi):
    width = lo.shape[-2]
    size = block.shape[-2]
    scratch[slot, :, 0:width, :] = lo
    scratch[slot, :, width : width + size, :] = block
    scratch[slot, :, width + size :, :] = hi


def slope_x(scratch, slot, z, size, spacing):
    s = lambda o: scratch[slot, z, o : o + size, :]
    return (s(0) - 8.0 * s(1) + 8.0 * s(3) - s(4)) / (12.0 * spacing)


def slope_y(f, lo, hi, spacing):
    n = f.shape[-1]
    lane = lax.broadcasted_iota(jnp.int32, f.shape, f.ndim - 1)
    m1 = jnp.where(lane == 0, lo[:, 1:2], pltpu.roll(f, 1, f.ndim - 1))
    m2 = jnp.where(lane == 0, lo[:, 0:1], jnp.where(lane == 1, lo[:, 1:2], pltpu.roll(f, 2, f.ndim - 1)))
    p1 = jnp.where(lane == n - 1, hi[:, 0:1], pltpu.roll(f, n - 1, f.ndim - 1))
    p2 = jnp.where(lane == n - 2, hi[:, 0:1], jnp.where(lane == n - 1, hi[:, 1:2], pltpu.roll(f, n - 2, f.ndim - 1)))
    return (m2 - 8.0 * m1 + 8.0 * p1 - p2) / (12.0 * spacing)


def slope_z(field_ref, index, row):
    total = None
    for j, weight in row:
        term = jnp.float32(weight) * field_ref[index, j]
        total = term if total is None else total + term
    return total


class Block:
    def __init__(self, shape, spacing, has_metric, x_base, y_base):
        self.layers, self.size, self.lanes = shape
        self.chunks = self.lanes // 128
        self.spacing = spacing
        self.has_metric = has_metric
        self.rows = sbp_rows(self.layers, spacing)
        self.x_base, self.y_base = x_base, y_base

    @property
    def x_rows(self):
        return 3 * self.layers * self.chunks * 2

    @property
    def y_rows(self):
        return self.layers * self.size


def plan_blocks(fine_shape, coarse_shape):
    fine = Block(fine_shape, 1.0, True, 0, 0)
    coarse = Block(coarse_shape, 3.0, False, fine.x_rows, fine.y_rows)
    fine.fx_base, fine.fy_base = 0, 0
    coarse.fx_base, coarse.fy_base = 6 * fine.chunks, fine.size
    corner_base = fine.size + coarse.size
    fine.corner_rows = (corner_base, corner_base + 1)
    coarse.corner_rows = (corner_base + 2, corner_base + 3)
    return fine, coarse, fine.x_rows + coarse.x_rows, fine.y_rows + coarse.y_rows


def round8(n):
    return -(-n // 8) * 8


def write_rims(b, src, fields, x_prev, x_next, y_prev, y_next):
    size, lanes = b.size, b.lanes
    for c, field in enumerate(fields):
        for z in range(b.layers):
            lo = src[field, z, 0:2, :]
            hi = src[field, z, size - 2 : size, :]
            for j in range(b.chunks):
                row = b.x_base + ((c * b.layers + z) * b.chunks + j) * 2
                x_prev[row : row + 2, :] = lo[:, j * 128 : (j + 1) * 128]
                x_next[row : row + 2, :] = hi[:, j * 128 : (j + 1) * 128]
    lane = lax.broadcasted_iota(jnp.int32, (size, 128), 1)
    for z in range(b.layers):
        acc_lo = jnp.zeros((size, 128), jnp.float32)
        acc_hi = jnp.zeros((size, 128), jnp.float32)
        for c, field in enumerate(fields):
            v = src[field, z]
            rl = v if c == 0 else pltpu.roll(v, 2 * c, 1)
            rh = pltpu.roll(v, (2 * c + 2) % lanes, 1)
            keep = (lane >= 2 * c) & (lane < 2 * c + 2)
            acc_lo = jnp.where(keep, rl[:, 0:128], acc_lo)
            acc_hi = jnp.where(keep, rh[:, 0:128], acc_hi)
        row = b.y_base + z * size
        y_prev[row : row + size, :] = acc_lo
        y_next[row : row + size, :] = acc_hi


def read_x_halo(b, buf, c, z):
    parts = [buf[pl.ds(b.x_base + ((c * b.layers + z) * b.chunks + j) * 2, 2), :] for j in range(b.chunks)]
    return parts[0] if len(parts) == 1 else jnp.concatenate(parts, axis=1)


def read_y_halo(b, buf, c, z, ok):
    row = b.y_base + z * b.size
    return keep(ok, buf[pl.ds(row, b.size), pl.ds(2 * c, 1)]), keep(ok, buf[pl.ds(row, b.size), pl.ds(2 * c + 1, 1)])


def fill_x2(b, scratch, slot, src, field, lo_buf, hi_buf, valid):
    size = b.size
    scratch[slot, :, 2 : 2 + size, :] = src[field]
    for z in range(b.layers):
        scratch[slot, z, 0:2, :] = keep(valid[0], read_x_halo(b, lo_buf, slot, z))
        scratch[slot, z, 2 + size :, :] = keep(valid[1], read_x_halo(b, hi_buf, slot, z))


def slope_y2(f, lo, hi, spacing):
    n = f.shape[-1]
    lane = lax.broadcasted_iota(jnp.int32, f.shape, 1)
    m1 = jnp.where(lane == 0, lo[1], pltpu.roll(f, 1, 1))
    m2 = jnp.where(lane == 0, lo[0], jnp.where(lane == 1, lo[1], pltpu.roll(f, 2, 1)))
    p1 = jnp.where(lane == n - 1, hi[0], pltpu.roll(f, n - 1, 1))
    p2 = jnp.where(lane == n - 2, hi[0], jnp.where(lane == n - 1, hi[1], pltpu.roll(f, n - 2, 1)))
    return (m2 - 8.0 * m1 + 8.0 * p1 - p2) / (12.0 * spacing)


STRESS_X = (3, 6, 7)
STRESS_Y = (6, 4, 8)
VELOCITY = (0, 1, 2)


def pack_kernel(blocks, fw, cw, x_prev, x_next, y_prev, y_next):
    for b, w in zip(blocks, (fw, cw)):
        write_rims_split(b, w, x_prev, x_next, y_prev, y_next)


def write_rims_split(b, w, x_prev, x_next, y_prev, y_next):
    size, lanes = b.size, b.lanes
    for c, field in enumerate(STRESS_X):
        for z in range(b.layers):
            lo = w[field, z, 0:2, :]
            hi = w[field, z, size - 2 : size, :]
            for j in range(b.chunks):
                row = b.x_base + ((c * b.layers + z) * b.chunks + j) * 2
                x_prev[row : row + 2, :] = lo[:, j * 128 : (j + 1) * 128]
                x_next[row : row + 2, :] = hi[:, j * 128 : (j + 1) * 128]
    lane = lax.broadcasted_iota(jnp.int32, (size, 128), 1)
    for z in range(b.layers):
        acc_lo = jnp.zeros((size, 128), jnp.float32)
        acc_hi = jnp.zeros((size, 128), jnp.float32)
        for c, field in enumerate(STRESS_Y):
            v = w[field, z]
            rl = v if c == 0 else pltpu.roll(v, 2 * c, 1)
            rh = pltpu.roll(v, (2 * c + 2) % lanes, 1)
            keep = (lane >= 2 * c) & (lane < 2 * c + 2)
            acc_lo = jnp.where(keep, rl[:, 0:128], acc_lo)
            acc_hi = jnp.where(keep, rh[:, 0:128], acc_hi)
        row = b.y_base + z * size
        y_prev[row : row + size, :] = acc_lo
        y_next[row : row + size, :] = acc_hi


def velocity_block(b, w, mat, metric, table, out, sx, hx_lo, hx_hi, hy_lo, hy_hi, valid):
    for slot, field in enumerate(STRESS_X):
        fill_x2(b, sx, slot, w, field, hx_lo, hx_hi, valid)
    for z in range(b.layers):
        dx = [slope_x(sx, slot, z, b.size, b.spacing) for slot in range(3)]
        dy = [
            slope_y2(w[field, z], read_y_halo(b, hy_lo, slot, z, valid[2]), read_y_halo(b, hy_hi, slot, z, valid[3]),
                     b.spacing)
            for slot, field in enumerate(STRESS_Y)
        ]
        dz = [slope_z(w, field, b.rows[z]) for field in (7, 8, 5)]
        if metric is not None:
            m = metric[z]
            dz = [m * d for d in dz]
        buoy = pick(table, 0, mat[z])
        for k in range(3):
            out[k, z] = w[k, z] + step_size * (buoy * (dx[k] + dy[k] + dz[k]))


def velocity_kernel(blocks, fw, cw, hx_lo, hx_hi, hy_lo, hy_hi, fmat, fmetric, cmat, table, flags,
                    fvel, cvel, vx_prev, vx_next, vy_prev, vy_next, sx_f, sx_c):
    fine, coarse = blocks
    valid = valid_of(flags)
    velocity_block(fine, fw, fmat, fmetric, table, fvel, sx_f, hx_lo, hx_hi, hy_lo, hy_hi, valid)
    velocity_block(coarse, cw, cmat, None, table, cvel, sx_c, hx_lo, hx_hi, hy_lo, hy_hi, valid)
    write_rims(fine, fvel, VELOCITY, vx_prev, vx_next, vy_prev, vy_next)
    write_rims(coarse, cvel, VELOCITY, vx_prev, vx_next, vy_prev, vy_next)


def stress_block(b, depth, w, mem, vel, mat, mech, metric, mtab, atab, out, mem_out, face, sx,
                 hx_lo, hx_hi, hy_lo, hy_hi, face_rims, valid):
    for slot in range(3):
        fill_x2(b, sx, slot, vel, slot, hx_lo, hx_hi, valid)
    for z in range(b.layers):
        dx = [slope_x(sx, slot, z, b.size, b.spacing) for slot in range(3)]
        dy = [
            slope_y2(vel[slot, z], read_y_halo(b, hy_lo, slot, z, valid[2]), read_y_halo(b, hy_hi, slot, z, valid[3]),
                     b.spacing)
            for slot in range(3)
        ]
        dz = [slope_z(vel, slot, b.rows[z]) for slot in range(3)]
        if metric is not None:
            m = metric[z]
            dz = [m * d for d in dz]
        kind, mechanism = mat[z], mech[z]
        lame, shear = pick(mtab, 1, kind), pick(mtab, 2, kind)
        decay, strength = pick(atab, 0, mechanism), pick(atab, 1, mechanism)
        cell_volume = lame * (dx[0] + dy[1] + dz[2])
        rate = [
            cell_volume + 2.0 * shear * dx[0],
            cell_volume + 2.0 * shear * dy[1],
            cell_volume + 2.0 * shear * dz[2],
            shear * (dy[0] + dx[1]),
            shear * (dz[0] + dx[2]),
            shear * (dz[1] + dy[2]),
        ]
        values = []
        for k in range(3):
            v = vel[k, z]
            out[k, z] = v
            values.append(v)
        for k in range(6):
            memory_new = decay * mem[k, z] + (1.0 - decay) * strength * rate[k]
            mem_out[k, z] = memory_new
            stress = w[3 + k, z] + step_size * (rate[k] - memory_new)
            out[3 + k, z] = stress
            values.append(stress)
        if z == depth:
            for i, k in enumerate((0, 1, 2, 7, 8, 5)):
                face[i] = values[k]
            write_face_rims(b, [values[k] for k in (0, 1, 2, 7, 8, 5)], *face_rims)


def write_face_rims(b, planes, x_prev, x_next, y_prev, y_next):
    size, lanes = b.size, b.lanes
    for i, v in enumerate(planes):
        for j in range(b.chunks):
            row = b.fx_base + i * b.chunks + j
            x_prev[row : row + 1, :] = v[0:1, j * 128 : (j + 1) * 128]
            x_next[row : row + 1, :] = v[size - 1 : size, j * 128 : (j + 1) * 128]
    lane = lax.broadcasted_iota(jnp.int32, (size, 128), 1)
    acc_lo = jnp.zeros((size, 128), jnp.float32)
    acc_hi = jnp.zeros((size, 128), jnp.float32)
    for i, v in enumerate(planes):
        rl = v if i == 0 else pltpu.roll(v, i, 1)
        rh = pltpu.roll(v, (i + 1) % lanes, 1)
        acc_lo = jnp.where(lane == i, rl[:, 0:128], acc_lo)
        acc_hi = jnp.where(lane == i, rh[:, 0:128], acc_hi)
    y_prev[b.fy_base : b.fy_base + size, :] = acc_lo
    y_next[b.fy_base : b.fy_base + size, :] = acc_hi


def stress_kernel(blocks, fw, fmem, fvel, cw, cmem, cvel, hx_lo, hx_hi, hy_lo, hy_hi,
                  fmat, fmech, fmetric, cmat, cmech, mtab, atab, flags,
                  fout, fmem_out, fface, cout, cmem_out, cface, rx_prev, rx_next, ry_prev, ry_next, sx_f, sx_c):
    fine, coarse = blocks
    valid = valid_of(flags)
    rims = (rx_prev, rx_next, ry_prev, ry_next)
    stress_block(fine, fine.layers - 1, fw, fmem, fvel, fmat, fmech, fmetric, mtab, atab, fout, fmem_out,
                 fface, sx_f, hx_lo, hx_hi, hy_lo, hy_hi, rims, valid)
    stress_block(coarse, 0, cw, cmem, cvel, cmat, cmech, None, mtab, atab, cout, cmem_out,
                 cface, sx_c, hx_lo, hx_hi, hy_lo, hy_hi, rims, valid)


KERNEL_PARAMS = pltpu.CompilerParams()


def vmem_specs(count):
    return [pl.BlockSpec(memory_space=pltpu.VMEM)] * count


def f32(shape):
    return jax.ShapeDtypeStruct(shape, jnp.float32)


def halo_shapes(x_rows, y_rows):
    return (f32((x_rows, 128)), f32((x_rows, 128)), f32((y_rows, 128)), f32((y_rows, 128)))


def scratch_for(b):
    return pltpu.VMEM((3, b.layers, b.size + 4, b.lanes), jnp.float32)


def receive(buffers):
    x_prev, x_next, y_prev, y_next = buffers
    y_lo = shift_from(y_next, "gy", 1)
    y_hi = shift_from(y_prev, "gy", -1)
    x_lo = shift_from(x_next, "gx", 1)
    x_hi = shift_from(x_prev, "gx", -1)
    return x_lo, x_hi, y_lo, y_hi


def put_face(out, face, depth):
    out = lax.dynamic_update_slice(out, face[0:3][:, None], (0, depth, 0, 0))
    out = lax.dynamic_update_slice(out, face[5:6][:, None], (5, depth, 0, 0))
    out = lax.dynamic_update_slice(out, face[3:5][:, None], (7, depth, 0, 0))
    return out


def prolong_y_matrix(coarse_lanes):
    m = np.zeros((coarse_lanes, 3 * coarse_lanes), np.float32)
    for d in range(coarse_lanes):
        m[d, 3 * d] = 2.0 / 3.0
        m[d, 3 * d + 1] = 1.0
        m[d, 3 * d + 2] = 2.0 / 3.0
        if d >= 1:
            m[d - 1, 3 * d] = 1.0 / 3.0
        if d + 1 < coarse_lanes:
            m[d + 1, 3 * d + 2] = 1.0 / 3.0
    return m


def restrict_y_matrix(coarse_lanes):
    m = np.zeros((3 * coarse_lanes, coarse_lanes), np.float32)
    for c in range(coarse_lanes):
        for offset, weight in ((-1, 1.0), (0, 2.0), (1, 3.0), (2, 2.0), (3, 1.0)):
            f = 3 * c + offset
            if 0 <= f < 3 * coarse_lanes:
                m[f, c] = weight / 9.0
    return m


def padded_rows(b, face, hx_lo, hx_hi, hy_lo, hy_hi, valid, i):
    size = b.size

    def x_row(buf):
        parts = [buf[pl.ds(b.fx_base + i * b.chunks + j, 1), :] for j in range(b.chunks)]
        return parts[0] if len(parts) == 1 else jnp.concatenate(parts, axis=1)

    def lane_of(buf, row, ok):
        return keep(ok, buf[pl.ds(row, 1), pl.ds(i, 1)])

    x_lo_ok, x_hi_ok, y_lo_ok, y_hi_ok = valid
    lo_row, hi_row = b.corner_rows
    rows = [(keep(x_lo_ok, x_row(hx_lo)), lane_of(hy_lo, lo_row, x_lo_ok & y_lo_ok),
             lane_of(hy_hi, lo_row, x_lo_ok & y_hi_ok))]
    for x in range(size):
        rows.append((face[i, pl.ds(x, 1), :], lane_of(hy_lo, b.fy_base + x, y_lo_ok),
                     lane_of(hy_hi, b.fy_base + x, y_hi_ok)))
    rows.append((keep(x_hi_ok, x_row(hx_hi)), lane_of(hy_lo, hi_row, x_hi_ok & y_lo_ok),
                 lane_of(hy_hi, hi_row, x_hi_ok & y_hi_ok)))
    return rows


def combine(terms):
    out = []
    for part in range(3):
        total = None
        for weight, row in terms:
            v = row[part] if weight == 1.0 else weight * row[part]
            total = v if total is None else total + v
        out.append(total)
    return out


def face_kernel(blocks, fine_depth, fout_in, cout_in, fface, cface, hx_lo, hx_hi, hy_lo, hy_hi,
                py, ry, flags, fout, cout, fnew, cnew, stage_p, stage_r, sems):
    fine, coarse = blocks
    halos = (hx_lo, hx_hi, hy_lo, hy_hi, valid_of(flags))
    lane_f = lax.broadcasted_iota(jnp.int32, (1, fine.lanes), 1)
    p_lo, p_hi = [], []
    for i in range(6):
        rows = padded_rows(coarse, cface, *halos, i)
        for c in range(coarse.size):
            left, middle, right = rows[c], rows[c + 1], rows[c + 2]
            parts = [
                [(1.0, left), (2.0, middle)],
                [(1.0, middle)],
                [(2.0, middle), (1.0, right)],
            ]
            for a, terms in enumerate(parts):
                interior, lo, hi = combine(terms)
                if a != 1:
                    interior, lo, hi = interior / 3.0, lo / 3.0, hi / 3.0
                r = i * fine.size + 3 * c + a
                stage_p[pl.ds(r, 1), :] = interior
                p_lo.append(lo)
                p_hi.append(hi)
    prolonged = jnp.dot(stage_p[...], py[...], precision=lax.Precision.HIGHEST, preferred_element_type=jnp.float32)
    for i in range(6):
        for x in range(fine.size):
            r = i * fine.size + x
            value = prolonged[r : r + 1, :]
            value = value + jnp.where(lane_f == 0, p_lo[r] / 3.0, 0.0) + jnp.where(lane_f == fine.lanes - 1, p_hi[r] / 3.0, 0.0)
            own = fface[i, pl.ds(x, 1), :]
            fnew[i, 0, pl.ds(x, 1), :] = own - penalty * (own - value)
    lane_c = lax.broadcasted_iota(jnp.int32, (1, coarse.lanes), 1)
    r_lo, r_hi = [], []
    for i in range(6):
        rows = padded_rows(fine, fface, *halos, i)
        for c in range(coarse.size):
            terms = [(1.0, rows[3 * c]), (2.0, rows[3 * c + 1]), (3.0, rows[3 * c + 2]), (2.0, rows[3 * c + 3]),
                     (1.0, rows[3 * c + 4])]
            interior, lo, hi = combine(terms)
            r = i * coarse.size + c
            stage_r[pl.ds(r, 1), :] = interior / 9.0
            r_lo.append(lo / 9.0)
            r_hi.append(hi / 9.0)
    restricted = jnp.dot(stage_r[...], ry[...], precision=lax.Precision.HIGHEST, preferred_element_type=jnp.float32)
    for i in range(6):
        for c in range(coarse.size):
            r = i * coarse.size + c
            value = restricted[r : r + 1, :]
            value = value + jnp.where(lane_c == 0, r_lo[r] / 9.0, 0.0) + jnp.where(lane_c == coarse.lanes - 1, r_hi[r] / 9.0, 0.0)
            own = cface[i, pl.ds(c, 1), :]
            cnew[i, 0, pl.ds(c, 1), :] = own - penalty * (own - value)
    copies = []
    for n, (src, dst, depth) in enumerate(((fnew, fout, fine_depth), (cnew, cout, 0))):
        for k, (first, count, field) in enumerate(((0, 3, 0), (5, 1, 5), (3, 2, 7))):
            copy = pltpu.make_async_copy(
                src.at[pl.ds(first, count)], dst.at[pl.ds(field, count), pl.ds(depth, 1)], sems.at[3 * n + k]
            )
            copy.start()
            copies.append(copy)
    for copy in copies:
        copy.wait()


def diag_from(block, dx, dy):
    nx, ny = lax.axis_size("gx"), lax.axis_size("gy")
    pairs = []
    for i in range(nx):
        for j in range(ny):
            if 0 <= i + dx < nx and 0 <= j + dy < ny:
                pairs.append((i * ny + j, (i + dx) * ny + (j + dy)))
    return lax.ppermute(block, ("gx", "gy"), pairs)


def row_ends(buf, blocks, at_end):
    out = []
    for b in blocks:
        chunk = b.chunks - 1 if at_end else 0
        first = b.fx_base + chunk
        lane = 127 if at_end else 0
        out.append(lax.slice(buf, (first, lane), (first + 5 * b.chunks + 1, lane + 1), (b.chunks, 1))[:, 0])
    return jnp.stack(out)


def with_corners(y_rim, x_lo, x_hi, blocks, at_end):
    lo, hi = row_ends(x_lo, blocks, at_end), row_ends(x_hi, blocks, at_end)
    extra = jnp.stack([lo, hi], axis=1).reshape(2 * len(blocks), 6)
    extra = jnp.pad(extra, ((0, 0), (0, 128 - 6)))
    return lax.dynamic_update_slice(y_rim, extra, (blocks[0].corner_rows[0], 0))


def face_call(blocks, fine_out, coarse_out, fine_face, coarse_face, rims):
    fine, coarse = blocks
    x_prev, x_next, y_prev, y_next = rims
    x_lo = shift_from(x_next, "gx", 1)
    x_hi = shift_from(x_prev, "gx", -1)
    y_lo = shift_from(with_corners(y_next, x_lo, x_hi, blocks, True), "gy", 1)
    y_hi = shift_from(with_corners(y_prev, x_lo, x_hi, blocks, False), "gy", -1)
    received = (x_lo, x_hi, y_lo, y_hi)
    py = jnp.asarray(prolong_y_matrix(coarse.lanes))
    ry = jnp.asarray(restrict_y_matrix(coarse.lanes))
    anyspace = pl.BlockSpec(memory_space=pl.ANY)
    return pl.pallas_call(
        functools.partial(face_kernel, blocks, fine.layers - 1),
        compiler_params=KERNEL_PARAMS,
        out_shape=(f32(fine_out.shape), f32(coarse_out.shape)),
        in_specs=[anyspace, anyspace] + vmem_specs(8) + [pl.BlockSpec(memory_space=pltpu.SMEM)],
        out_specs=(anyspace, anyspace),
        input_output_aliases={0: 0, 1: 1},
        scratch_shapes=[
            pltpu.VMEM((6, 1, fine.size, fine.lanes), jnp.float32),
            pltpu.VMEM((6, 1, coarse.size, coarse.lanes), jnp.float32),
            pltpu.VMEM((round8(6 * fine.size), coarse.lanes), jnp.float32),
            pltpu.VMEM((round8(6 * coarse.size), fine.lanes), jnp.float32),
            pltpu.SemaphoreType.DMA((6,)),
        ],
    )(fine_out, coarse_out, fine_face, coarse_face, *received, py, ry, edge_flags())


def local(
    fine_wave,
    fine_memory,
    fine_material,
    fine_mechanism,
    fine_metric,
    coarse_wave,
    coarse_memory,
    coarse_material,
    coarse_mechanism,
    material_table,
    attenuation_table,
):
    fine, coarse, x_rows, y_rows = plan_blocks(fine_wave.shape[1:], coarse_wave.shape[1:])
    blocks = (fine, coarse)
    smem = pl.BlockSpec(memory_space=pltpu.SMEM)
    flags = edge_flags()

    rims = pl.pallas_call(
        functools.partial(pack_kernel, blocks),
        compiler_params=KERNEL_PARAMS,
        out_shape=halo_shapes(x_rows, y_rows),
        in_specs=vmem_specs(2),
        out_specs=tuple(vmem_specs(4)),
    )(fine_wave, coarse_wave)
    halos = receive(rims)

    fine_velocity, coarse_velocity, *vrims = pl.pallas_call(
        functools.partial(velocity_kernel, blocks),
        compiler_params=KERNEL_PARAMS,
        out_shape=(f32((3,) + fine_wave.shape[1:]), f32((3,) + coarse_wave.shape[1:])) + halo_shapes(x_rows, y_rows),
        in_specs=vmem_specs(9) + [smem, smem],
        out_specs=tuple(vmem_specs(6)),
        scratch_shapes=[scratch_for(fine), scratch_for(coarse)],
    )(fine_wave, coarse_wave, *halos, fine_material, fine_metric, coarse_material, material_table, flags)

    vhalos = receive(vrims)
    fx_rows = 6 * (fine.chunks + coarse.chunks)
    fy_rows = round8(fine.size + coarse.size + 4)
    fine_out, fine_mem, fine_face, coarse_out, coarse_mem, coarse_face, *face_rims = pl.pallas_call(
        functools.partial(stress_kernel, blocks),
        compiler_params=KERNEL_PARAMS,
        out_shape=(
            f32(fine_wave.shape), f32(fine_memory.shape), f32((6,) + fine_wave.shape[2:]),
            f32(coarse_wave.shape), f32(coarse_memory.shape), f32((6,) + coarse_wave.shape[2:]),
            f32((fx_rows, 128)), f32((fx_rows, 128)), f32((fy_rows, 128)), f32((fy_rows, 128)),
        ),
        in_specs=vmem_specs(15) + [smem, smem, smem],
        out_specs=tuple(vmem_specs(10)),
        scratch_shapes=[scratch_for(fine), scratch_for(coarse)],
    )(fine_wave, fine_memory, fine_velocity, coarse_wave, coarse_memory, coarse_velocity, *vhalos,
      fine_material, fine_mechanism, fine_metric, coarse_material, coarse_mechanism, material_table,
      attenuation_table, flags)

    fine_out, coarse_out = face_call(blocks, fine_out, coarse_out, fine_face, coarse_face, face_rims)
    return (fine_out, fine_mem, coarse_out, coarse_mem)


def solution(mesh):
    in_specs = (
        P(None, None, "gx", "gy"),
        P(None, None, "gx", "gy"),
        P(None, "gx", "gy"),
        P(None, "gx", "gy"),
        P(None, "gx", "gy"),
        P(None, None, "gx", "gy"),
        P(None, None, "gx", "gy"),
        P(None, "gx", "gy"),
        P(None, "gx", "gy"),
        P(),
        P(),
    )
    out_specs = (
        P(None, None, "gx", "gy"),
        P(None, None, "gx", "gy"),
        P(None, None, "gx", "gy"),
        P(None, None, "gx", "gy"),
    )
    return jax.shard_map(local, mesh=mesh, in_specs=in_specs, out_specs=out_specs, check_vma=False)
```

```python
import functools
import math

import jax
import jax.numpy as jnp
import numpy as np
from jax import lax
from jax.sharding import PartitionSpec as P

step_size = 0.1
penalty = 0.1 * 48.0 / 17.0
closure = [
    [-24.0 / 17.0, 59.0 / 34.0, -4.0 / 17.0, -3.0 / 34.0, 0.0, 0.0],
    [-0.5, 0.0, 0.5, 0.0, 0.0, 0.0],
    [4.0 / 43.0, -59.0 / 86.0, 0.0, 59.0 / 86.0, -4.0 / 43.0, 0.0],
    [3.0 / 98.0, 0.0, -59.0 / 98.0, 0.0, 32.0 / 49.0, -4.0 / 49.0],
]


def sbp_table(layers, spacing):
    return jnp.asarray(sbp_numpy(layers, spacing))


def sbp_numpy(layers, spacing):
    table = np.zeros((layers, layers))
    for line_at in range(4):
        for column in range(6):
            table[line_at, column] = closure[line_at][column]
            table[layers - 1 - line_at, layers - 1 - column] = -closure[line_at][column]
    for line_at in range(4, layers - 4):
        table[line_at, line_at - 2 : line_at + 3] = [
            1.0 / 12.0,
            -2.0 / 3.0,
            0.0,
            2.0 / 3.0,
            -1.0 / 12.0,
        ]
    return (table / spacing).astype(np.float32)


def shift_from(block, axis, offset):
    count = lax.axis_size(axis)
    pairs = [(i, (i + offset) % count) for i in range(count)]
    return lax.ppermute(block, axis, pairs)


def edge_flags():
    gx, gy = lax.axis_index("gx"), lax.axis_index("gy")
    nx, ny = lax.axis_size("gx"), lax.axis_size("gy")
    return jnp.stack([gx > 0, gx < nx - 1, gy > 0, gy < ny - 1]).astype(jnp.int32)


def valid_of(flags):
    return tuple(flags[k] != 0 for k in range(4))


def keep(ok, value):
    return jnp.where(ok, value, 0.0)


def packed_shift(blocks, axis, offset):
    sizes = [math.prod(b.shape) for b in blocks]
    joined = jnp.concatenate([b.reshape(-1) for b in blocks])
    moved = shift_from(joined, axis, offset)
    out, start = [], 0
    for b, size in zip(blocks, sizes):
        out.append(moved[start : start + size].reshape(b.shape))
        start += size
    return out


def exchange(blocks, width):
    x_lo = packed_shift([b[..., -width:, :] for b in blocks], "gx", 1)
    x_hi = packed_shift([b[..., :width, :] for b in blocks], "gx", -1)
    y_lo = packed_shift([b[..., -width:] for b in blocks], "gy", 1)
    y_hi = packed_shift([b[..., :width] for b in blocks], "gy", -1)
    return [(x_lo[i], x_hi[i], y_lo[i], y_hi[i]) for i in range(len(blocks))]


def central_diff(padded, along, spacing):
    length = padded.shape[along] - 4
    s = lambda o: lax.slice_in_dim(padded, o, o + length, axis=along)
    return (s(0) - 8.0 * s(1) + 8.0 * s(3) - s(4)) / (12.0 * spacing)


def diff_x(block, halo, spacing):
    x_lo, x_hi, _, _ = halo
    return central_diff(jnp.concatenate([x_lo, block, x_hi], axis=-2), block.ndim - 2, spacing)


def diff_y(block, halo, spacing):
    _, _, y_lo, y_hi = halo
    return central_diff(jnp.concatenate([y_lo, block, y_hi], axis=-1), block.ndim - 1, spacing)


def vertical_diff(fields, matrix):
    return jnp.einsum("kz,czxy->ckxy", matrix, fields, precision=lax.Precision.HIGHEST)


def lookup_table(grid_cell_index, values):
    result = jnp.zeros(grid_cell_index.shape, jnp.float32)
    for kind_at in range(values.shape[0]):
        result = jnp.where(grid_cell_index == kind_at, values[kind_at], result)
    return result


def velocity_step(wave, halo_x3, halo_y3, buoyancy, metric, matrix, spacing):
    sx = jnp.stack([wave[3], wave[6], wave[7]])
    sy = jnp.stack([wave[6], wave[4], wave[8]])
    slope_x = diff_x(sx, halo_x3, spacing)
    slope_y = diff_y(sy, halo_y3, spacing)
    slope_z = metric * vertical_diff(jnp.stack([wave[7], wave[8], wave[5]]), matrix)
    rate_x = slope_x[0] + slope_y[0] + slope_z[0]
    rate_y = slope_x[1] + slope_y[1] + slope_z[1]
    rate_z = slope_x[2] + slope_y[2] + slope_z[2]
    return wave[:3] + step_size * (buoyancy * jnp.stack([rate_x, rate_y, rate_z]))


def stress_step(wave, memory, velocity, halo, lame, shear, decay, strength, metric, matrix, spacing):
    slope_x = diff_x(velocity, halo, spacing)
    slope_y = diff_y(velocity, halo, spacing)
    slope_z = metric * vertical_diff(velocity, matrix)
    cell_volume = lame * (slope_x[0] + slope_y[1] + slope_z[2])
    rate = jnp.stack(
        [
            cell_volume + 2.0 * shear * slope_x[0],
            cell_volume + 2.0 * shear * slope_y[1],
            cell_volume + 2.0 * shear * slope_z[2],
            shear * (slope_y[0] + slope_x[1]),
            shear * (slope_z[0] + slope_x[2]),
            shear * (slope_z[1] + slope_y[2]),
        ]
    )
    memory_new = decay * memory + (1.0 - decay) * strength * rate
    stress = wave[3:] + step_size * (rate - memory_new)
    return stress, memory_new


def face_of(velocity, stress, depth):
    return jnp.stack(
        [
            velocity[0, depth],
            velocity[1, depth],
            velocity[2, depth],
            stress[4, depth],
            stress[5, depth],
            stress[2, depth],
        ]
    )


def pad_faces(faces):
    x_lo = packed_shift([f[:, -1:, :] for f in faces], "gx", 1)
    x_hi = packed_shift([f[:, :1, :] for f in faces], "gx", -1)
    faces = [jnp.concatenate([lo, f, hi], axis=1) for lo, f, hi in zip(x_lo, faces, x_hi)]
    y_lo = packed_shift([f[:, :, -1:] for f in faces], "gy", 1)
    y_hi = packed_shift([f[:, :, :1] for f in faces], "gy", -1)
    return [jnp.concatenate([lo, f, hi], axis=2) for lo, f, hi in zip(y_lo, faces, y_hi)]


def shifted(padded, offset, length, along):
    return lax.slice_in_dim(padded, offset, offset + length, axis=along)


def prolong_axis(padded, along):
    length = padded.shape[along] - 2
    left = shifted(padded, 0, length, along)
    middle = shifted(padded, 1, length, along)
    right = shifted(padded, 2, length, along)
    parts = jnp.stack(
        [(left + 2.0 * middle) / 3.0, middle, (2.0 * middle + right) / 3.0], axis=along + 1
    )
    shape = list(middle.shape)
    shape[along] = shape[along] * 3
    return parts.reshape(tuple(shape))


def split_three(padded, offset, length, along):
    part = shifted(padded, offset, 3 * length, along)
    return part.reshape(part.shape[:along] + (length, 3) + part.shape[along + 1 :])


def pick_part(parts, number, along):
    return lax.index_in_dim(parts, number, along + 1, keepdims=False)


def restrict_axis(padded, along):
    length = (padded.shape[along] - 2) // 3
    first = split_three(padded, 0, length, along)
    middle = split_three(padded, 1, length, along)
    last = split_three(padded, 2, length, along)
    return (
        pick_part(first, 0, along)
        + 2.0 * pick_part(middle, 0, along)
        + 3.0 * pick_part(middle, 1, along)
        + 2.0 * pick_part(middle, 2, along)
        + pick_part(last, 2, along)
    ) / 9.0


def assemble(velocity, stress, face, depth):
    replace = {0: face[0], 1: face[1], 2: face[2], 7: face[3], 8: face[4], 5: face[5]}
    fields = [velocity[0], velocity[1], velocity[2]] + [stress[k] for k in range(6)]
    rows = []
    for k, field in enumerate(fields):
        if k in replace:
            field = lax.dynamic_update_slice_in_dim(field, replace[k][None], depth, axis=0)
        rows.append(field)
    return jnp.stack(rows)


from jax.experimental import pallas as pl
from jax.experimental.pallas import tpu as pltpu


def sbp_rows(layers, spacing):
    table = sbp_numpy(layers, spacing)
    return [[(j, float(table[k, j])) for j in range(layers) if table[k, j] != 0.0] for k in range(layers)]


def pick(values_ref, row, index):
    level = [values_ref[row, kind_at] for kind_at in range(values_ref.shape[1])]
    bit = 0
    while len(level) > 1:
        on = (index & (1 << bit)) != 0
        level = [jnp.where(on, level[k + 1], level[k]) for k in range(0, len(level), 2)]
        bit += 1
    return level[0]


def fill_x(scratch, slot, lo, block, hi):
    width = lo.shape[-2]
    size = block.shape[-2]
    scratch[slot, :, 0:width, :] = lo
    scratch[slot, :, width : width + size, :] = block
    scratch[slot, :, width + size :, :] = hi


def slope_x(scratch, slot, z, size, spacing):
    s = lambda o: scratch[slot, z, o : o + size, :]
    return (s(0) - 8.0 * s(1) + 8.0 * s(3) - s(4)) / (12.0 * spacing)


def slope_y(f, lo, hi, spacing):
    n = f.shape[-1]
    lane = lax.broadcasted_iota(jnp.int32, f.shape, f.ndim - 1)
    m1 = jnp.where(lane == 0, lo[:, 1:2], pltpu.roll(f, 1, f.ndim - 1))
    m2 = jnp.where(lane == 0, lo[:, 0:1], jnp.where(lane == 1, lo[:, 1:2], pltpu.roll(f, 2, f.ndim - 1)))
    p1 = jnp.where(lane == n - 1, hi[:, 0:1], pltpu.roll(f, n - 1, f.ndim - 1))
    p2 = jnp.where(lane == n - 2, hi[:, 0:1], jnp.where(lane == n - 1, hi[:, 1:2], pltpu.roll(f, n - 2, f.ndim - 1)))
    return (m2 - 8.0 * m1 + 8.0 * p1 - p2) / (12.0 * spacing)


def slope_z(field_ref, index, row):
    total = None
    for j, weight in row:
        term = jnp.float32(weight) * field_ref[index, j]
        total = term if total is None else total + term
    return total


class Block:
    def __init__(self, shape, spacing, has_metric, x_base, y_base):
        self.layers, self.size, self.lanes = shape
        self.chunks = self.lanes // 128
        self.spacing = spacing
        self.has_metric = has_metric
        self.rows = sbp_rows(self.layers, spacing)
        self.x_base, self.y_base = x_base, y_base

    @property
    def x_rows(self):
        return 3 * self.layers * self.chunks * 2

    @property
    def y_rows(self):
        return self.layers * self.size


def plan_blocks(fine_shape, coarse_shape):
    fine = Block(fine_shape, 1.0, True, 0, 0)
    coarse = Block(coarse_shape, 3.0, False, fine.x_rows, fine.y_rows)
    fine.fx_base, fine.fy_base = 0, 0
    coarse.fx_base, coarse.fy_base = 6 * fine.chunks, fine.size
    corner_base = fine.size + coarse.size
    fine.corner_rows = (corner_base, corner_base + 1)
    coarse.corner_rows = (corner_base + 2, corner_base + 3)
    return fine, coarse, fine.x_rows + coarse.x_rows, fine.y_rows + coarse.y_rows


def round8(n):
    return -(-n // 8) * 8


def write_rims(b, src, fields, x_prev, x_next, y_prev, y_next):
    size, lanes = b.size, b.lanes
    for c, field in enumerate(fields):
        for z in range(b.layers):
            lo = src[field, z, 0:2, :]
            hi = src[field, z, size - 2 : size, :]
            for j in range(b.chunks):
                row = b.x_base + ((c * b.layers + z) * b.chunks + j) * 2
                x_prev[row : row + 2, :] = lo[:, j * 128 : (j + 1) * 128]
                x_next[row : row + 2, :] = hi[:, j * 128 : (j + 1) * 128]
    lane = lax.broadcasted_iota(jnp.int32, (size, 128), 1)
    for z in range(b.layers):
        acc_lo = jnp.zeros((size, 128), jnp.float32)
        acc_hi = jnp.zeros((size, 128), jnp.float32)
        for c, field in enumerate(fields):
            v = src[field, z]
            rl = v if c == 0 else pltpu.roll(v, 2 * c, 1)
            rh = pltpu.roll(v, (2 * c + 2) % lanes, 1)
            keep = (lane >= 2 * c) & (lane < 2 * c + 2)
            acc_lo = jnp.where(keep, rl[:, 0:128], acc_lo)
            acc_hi = jnp.where(keep, rh[:, 0:128], acc_hi)
        row = b.y_base + z * size
        y_prev[row : row + size, :] = acc_lo
        y_next[row : row + size, :] = acc_hi


def read_x_halo(b, buf, c, z):
    parts = [buf[pl.ds(b.x_base + ((c * b.layers + z) * b.chunks + j) * 2, 2), :] for j in range(b.chunks)]
    return parts[0] if len(parts) == 1 else jnp.concatenate(parts, axis=1)


def read_y_halo(b, buf, c, z, ok):
    row = b.y_base + z * b.size
    return keep(ok, buf[pl.ds(row, b.size), pl.ds(2 * c, 1)]), keep(ok, buf[pl.ds(row, b.size), pl.ds(2 * c + 1, 1)])


def fill_x2(b, scratch, slot, src, field, lo_buf, hi_buf, valid):
    size = b.size
    scratch[slot, :, 2 : 2 + size, :] = src[field]
    for z in range(b.layers):
        scratch[slot, z, 0:2, :] = keep(valid[0], read_x_halo(b, lo_buf, slot, z))
        scratch[slot, z, 2 + size :, :] = keep(valid[1], read_x_halo(b, hi_buf, slot, z))


def slope_y2(f, lo, hi, spacing):
    n = f.shape[-1]
    lane = lax.broadcasted_iota(jnp.int32, f.shape, 1)
    m1 = jnp.where(lane == 0, lo[1], pltpu.roll(f, 1, 1))
    m2 = jnp.where(lane == 0, lo[0], jnp.where(lane == 1, lo[1], pltpu.roll(f, 2, 1)))
    p1 = jnp.where(lane == n - 1, hi[0], pltpu.roll(f, n - 1, 1))
    p2 = jnp.where(lane == n - 2, hi[0], jnp.where(lane == n - 1, hi[1], pltpu.roll(f, n - 2, 1)))
    return (m2 - 8.0 * m1 + 8.0 * p1 - p2) / (12.0 * spacing)


STRESS_X = (3, 6, 7)
STRESS_Y = (6, 4, 8)
VELOCITY = (0, 1, 2)


def pack_kernel(blocks, fw, cw, x_prev, x_next, y_prev, y_next):
    for b, w in zip(blocks, (fw, cw)):
        write_rims_split(b, w, x_prev, x_next, y_prev, y_next)


def write_rims_split(b, w, x_prev, x_next, y_prev, y_next):
    size, lanes = b.size, b.lanes
    for c, field in enumerate(STRESS_X):
        for z in range(b.layers):
            lo = w[field, z, 0:2, :]
            hi = w[field, z, size - 2 : size, :]
            for j in range(b.chunks):
                row = b.x_base + ((c * b.layers + z) * b.chunks + j) * 2
                x_prev[row : row + 2, :] = lo[:, j * 128 : (j + 1) * 128]
                x_next[row : row + 2, :] = hi[:, j * 128 : (j + 1) * 128]
    lane = lax.broadcasted_iota(jnp.int32, (size, 128), 1)
    for z in range(b.layers):
        acc_lo = jnp.zeros((size, 128), jnp.float32)
        acc_hi = jnp.zeros((size, 128), jnp.float32)
        for c, field in enumerate(STRESS_Y):
            v = w[field, z]
            rl = v if c == 0 else pltpu.roll(v, 2 * c, 1)
            rh = pltpu.roll(v, (2 * c + 2) % lanes, 1)
            keep = (lane >= 2 * c) & (lane < 2 * c + 2)
            acc_lo = jnp.where(keep, rl[:, 0:128], acc_lo)
            acc_hi = jnp.where(keep, rh[:, 0:128], acc_hi)
        row = b.y_base + z * size
        y_prev[row : row + size, :] = acc_lo
        y_next[row : row + size, :] = acc_hi


def velocity_block(b, w, mat, metric, table, out, sx, hx_lo, hx_hi, hy_lo, hy_hi, valid):
    for slot, field in enumerate(STRESS_X):
        fill_x2(b, sx, slot, w, field, hx_lo, hx_hi, valid)
    for z in range(b.layers):
        dx = [slope_x(sx, slot, z, b.size, b.spacing) for slot in range(3)]
        dy = [
            slope_y2(w[field, z], read_y_halo(b, hy_lo, slot, z, valid[2]), read_y_halo(b, hy_hi, slot, z, valid[3]),
                     b.spacing)
            for slot, field in enumerate(STRESS_Y)
        ]
        dz = [slope_z(w, field, b.rows[z]) for field in (7, 8, 5)]
        if metric is not None:
            m = metric[z]
            dz = [m * d for d in dz]
        buoy = pick(table, 0, mat[z])
        for k in range(3):
            out[k, z] = w[k, z] + step_size * (buoy * (dx[k] + dy[k] + dz[k]))


def velocity_kernel(blocks, fw, cw, hx_lo, hx_hi, hy_lo, hy_hi, fmat, fmetric, cmat, table, flags,
                    fvel, cvel, vx_prev, vx_next, vy_prev, vy_next, sx_f, sx_c):
    fine, coarse = blocks
    valid = valid_of(flags)
    velocity_block(fine, fw, fmat, fmetric, table, fvel, sx_f, hx_lo, hx_hi, hy_lo, hy_hi, valid)
    velocity_block(coarse, cw, cmat, None, table, cvel, sx_c, hx_lo, hx_hi, hy_lo, hy_hi, valid)
    write_rims(fine, fvel, VELOCITY, vx_prev, vx_next, vy_prev, vy_next)
    write_rims(coarse, cvel, VELOCITY, vx_prev, vx_next, vy_prev, vy_next)


def stress_block(b, depth, w, mem, vel, mat, mech, metric, mtab, atab, out, mem_out, face, sx,
                 hx_lo, hx_hi, hy_lo, hy_hi, face_rims, valid):
    for slot in range(3):
        fill_x2(b, sx, slot, vel, slot, hx_lo, hx_hi, valid)
    for z in range(b.layers):
        dx = [slope_x(sx, slot, z, b.size, b.spacing) for slot in range(3)]
        dy = [
            slope_y2(vel[slot, z], read_y_halo(b, hy_lo, slot, z, valid[2]), read_y_halo(b, hy_hi, slot, z, valid[3]),
                     b.spacing)
            for slot in range(3)
        ]
        dz = [slope_z(vel, slot, b.rows[z]) for slot in range(3)]
        if metric is not None:
            m = metric[z]
            dz = [m * d for d in dz]
        kind, mechanism = mat[z], mech[z]
        lame, shear = pick(mtab, 1, kind), pick(mtab, 2, kind)
        decay, strength = pick(atab, 0, mechanism), pick(atab, 1, mechanism)
        cell_volume = lame * (dx[0] + dy[1] + dz[2])
        rate = [
            cell_volume + 2.0 * shear * dx[0],
            cell_volume + 2.0 * shear * dy[1],
            cell_volume + 2.0 * shear * dz[2],
            shear * (dy[0] + dx[1]),
            shear * (dz[0] + dx[2]),
            shear * (dz[1] + dy[2]),
        ]
        values = []
        for k in range(3):
            v = vel[k, z]
            out[k, z] = v
            values.append(v)
        for k in range(6):
            memory_new = decay * mem[k, z] + (1.0 - decay) * strength * rate[k]
            mem_out[k, z] = memory_new
            stress = w[3 + k, z] + step_size * (rate[k] - memory_new)
            out[3 + k, z] = stress
            values.append(stress)
        if z == depth:
            for i, k in enumerate((0, 1, 2, 7, 8, 5)):
                face[i] = values[k]
            write_face_rims(b, [values[k] for k in (0, 1, 2, 7, 8, 5)], *face_rims)


def write_face_rims(b, planes, x_prev, x_next, y_prev, y_next):
    size, lanes = b.size, b.lanes
    for i, v in enumerate(planes):
        for j in range(b.chunks):
            row = b.fx_base + i * b.chunks + j
            x_prev[row : row + 1, :] = v[0:1, j * 128 : (j + 1) * 128]
            x_next[row : row + 1, :] = v[size - 1 : size, j * 128 : (j + 1) * 128]
    lane = lax.broadcasted_iota(jnp.int32, (size, 128), 1)
    acc_lo = jnp.zeros((size, 128), jnp.float32)
    acc_hi = jnp.zeros((size, 128), jnp.float32)
    for i, v in enumerate(planes):
        rl = v if i == 0 else pltpu.roll(v, i, 1)
        rh = pltpu.roll(v, (i + 1) % lanes, 1)
        acc_lo = jnp.where(lane == i, rl[:, 0:128], acc_lo)
        acc_hi = jnp.where(lane == i, rh[:, 0:128], acc_hi)
    y_prev[b.fy_base : b.fy_base + size, :] = acc_lo
    y_next[b.fy_base : b.fy_base + size, :] = acc_hi


def stress_kernel(blocks, fw, fmem, fvel, cw, cmem, cvel, hx_lo, hx_hi, hy_lo, hy_hi,
                  fmat, fmech, fmetric, cmat, cmech, mtab, atab, flags,
                  fout, fmem_out, fface, cout, cmem_out, cface, rx_prev, rx_next, ry_prev, ry_next, sx_f, sx_c):
    fine, coarse = blocks
    valid = valid_of(flags)
    rims = (rx_prev, rx_next, ry_prev, ry_next)
    stress_block(fine, fine.layers - 1, fw, fmem, fvel, fmat, fmech, fmetric, mtab, atab, fout, fmem_out,
                 fface, sx_f, hx_lo, hx_hi, hy_lo, hy_hi, rims, valid)
    stress_block(coarse, 0, cw, cmem, cvel, cmat, cmech, None, mtab, atab, cout, cmem_out,
                 cface, sx_c, hx_lo, hx_hi, hy_lo, hy_hi, rims, valid)


def vmem_specs(count):
    return [pl.BlockSpec(memory_space=pltpu.VMEM)] * count


def f32(shape):
    return jax.ShapeDtypeStruct(shape, jnp.float32)


def halo_shapes(x_rows, y_rows):
    return (f32((x_rows, 128)), f32((x_rows, 128)), f32((y_rows, 128)), f32((y_rows, 128)))


def scratch_for(b):
    return pltpu.VMEM((3, b.layers, b.size + 4, b.lanes), jnp.float32)


def receive(buffers):
    x_prev, x_next, y_prev, y_next = buffers
    y_lo = shift_from(y_next, "gy", 1)
    y_hi = shift_from(y_prev, "gy", -1)
    x_lo = shift_from(x_next, "gx", 1)
    x_hi = shift_from(x_prev, "gx", -1)
    return x_lo, x_hi, y_lo, y_hi


def put_face(out, face, depth):
    out = lax.dynamic_update_slice(out, face[0:3][:, None], (0, depth, 0, 0))
    out = lax.dynamic_update_slice(out, face[5:6][:, None], (5, depth, 0, 0))
    out = lax.dynamic_update_slice(out, face[3:5][:, None], (7, depth, 0, 0))
    return out


def prolong_y_matrix(coarse_lanes):
    m = np.zeros((coarse_lanes, 3 * coarse_lanes), np.float32)
    for d in range(coarse_lanes):
        m[d, 3 * d] = 2.0 / 3.0
        m[d, 3 * d + 1] = 1.0
        m[d, 3 * d + 2] = 2.0 / 3.0
        if d >= 1:
            m[d - 1, 3 * d] = 1.0 / 3.0
        if d + 1 < coarse_lanes:
            m[d + 1, 3 * d + 2] = 1.0 / 3.0
    return m


def restrict_y_matrix(coarse_lanes):
    m = np.zeros((3 * coarse_lanes, coarse_lanes), np.float32)
    for c in range(coarse_lanes):
        for offset, weight in ((-1, 1.0), (0, 2.0), (1, 3.0), (2, 2.0), (3, 1.0)):
            f = 3 * c + offset
            if 0 <= f < 3 * coarse_lanes:
                m[f, c] = weight / 9.0
    return m


def padded_rows(b, face, hx_lo, hx_hi, hy_lo, hy_hi, valid, i):
    size = b.size

    def x_row(buf):
        parts = [buf[pl.ds(b.fx_base + i * b.chunks + j, 1), :] for j in range(b.chunks)]
        return parts[0] if len(parts) == 1 else jnp.concatenate(parts, axis=1)

    def lane_of(buf, row, ok):
        return keep(ok, buf[pl.ds(row, 1), pl.ds(i, 1)])

    x_lo_ok, x_hi_ok, y_lo_ok, y_hi_ok = valid
    lo_row, hi_row = b.corner_rows
    rows = [(keep(x_lo_ok, x_row(hx_lo)), lane_of(hy_lo, lo_row, x_lo_ok & y_lo_ok),
             lane_of(hy_hi, lo_row, x_lo_ok & y_hi_ok))]
    for x in range(size):
        rows.append((face[i, pl.ds(x, 1), :], lane_of(hy_lo, b.fy_base + x, y_lo_ok),
                     lane_of(hy_hi, b.fy_base + x, y_hi_ok)))
    rows.append((keep(x_hi_ok, x_row(hx_hi)), lane_of(hy_lo, hi_row, x_hi_ok & y_lo_ok),
                 lane_of(hy_hi, hi_row, x_hi_ok & y_hi_ok)))
    return rows


def combine(terms):
    out = []
    for part in range(3):
        total = None
        for weight, row in terms:
            v = row[part] if weight == 1.0 else weight * row[part]
            total = v if total is None else total + v
        out.append(total)
    return out


def face_kernel(blocks, fine_depth, fout_in, cout_in, fface, cface, hx_lo, hx_hi, hy_lo, hy_hi,
                py, ry, flags, fout, cout, fnew, cnew, stage_p, stage_r, sems):
    fine, coarse = blocks
    halos = (hx_lo, hx_hi, hy_lo, hy_hi, valid_of(flags))
    lane_f = lax.broadcasted_iota(jnp.int32, (1, fine.lanes), 1)
    p_lo, p_hi = [], []
    for i in range(6):
        rows = padded_rows(coarse, cface, *halos, i)
        for c in range(coarse.size):
            left, middle, right = rows[c], rows[c + 1], rows[c + 2]
            parts = [
                [(1.0, left), (2.0, middle)],
                [(1.0, middle)],
                [(2.0, middle), (1.0, right)],
            ]
            for a, terms in enumerate(parts):
                interior, lo, hi = combine(terms)
                if a != 1:
                    interior, lo, hi = interior / 3.0, lo / 3.0, hi / 3.0
                r = i * fine.size + 3 * c + a
                stage_p[pl.ds(r, 1), :] = interior
                p_lo.append(lo)
                p_hi.append(hi)
    prolonged = jnp.dot(stage_p[...], py[...], precision=lax.Precision.HIGHEST, preferred_element_type=jnp.float32)
    for i in range(6):
        for x in range(fine.size):
            r = i * fine.size + x
            value = prolonged[r : r + 1, :]
            value = value + jnp.where(lane_f == 0, p_lo[r] / 3.0, 0.0) + jnp.where(lane_f == fine.lanes - 1, p_hi[r] / 3.0, 0.0)
            own = fface[i, pl.ds(x, 1), :]
            fnew[i, 0, pl.ds(x, 1), :] = own - penalty * (own - value)
    lane_c = lax.broadcasted_iota(jnp.int32, (1, coarse.lanes), 1)
    r_lo, r_hi = [], []
    for i in range(6):
        rows = padded_rows(fine, fface, *halos, i)
        for c in range(coarse.size):
            terms = [(1.0, rows[3 * c]), (2.0, rows[3 * c + 1]), (3.0, rows[3 * c + 2]), (2.0, rows[3 * c + 3]),
                     (1.0, rows[3 * c + 4])]
            interior, lo, hi = combine(terms)
            r = i * coarse.size + c
            stage_r[pl.ds(r, 1), :] = interior / 9.0
            r_lo.append(lo / 9.0)
            r_hi.append(hi / 9.0)
    restricted = jnp.dot(stage_r[...], ry[...], precision=lax.Precision.HIGHEST, preferred_element_type=jnp.float32)
    for i in range(6):
        for c in range(coarse.size):
            r = i * coarse.size + c
            value = restricted[r : r + 1, :]
            value = value + jnp.where(lane_c == 0, r_lo[r] / 9.0, 0.0) + jnp.where(lane_c == coarse.lanes - 1, r_hi[r] / 9.0, 0.0)
            own = cface[i, pl.ds(c, 1), :]
            cnew[i, 0, pl.ds(c, 1), :] = own - penalty * (own - value)
    copies = []
    for n, (src, dst, depth) in enumerate(((fnew, fout, fine_depth), (cnew, cout, 0))):
        for k, (first, count, field) in enumerate(((0, 3, 0), (5, 1, 5), (3, 2, 7))):
            copy = pltpu.make_async_copy(
                src.at[pl.ds(first, count)], dst.at[pl.ds(field, count), pl.ds(depth, 1)], sems.at[3 * n + k]
            )
            copy.start()
            copies.append(copy)
    for copy in copies:
        copy.wait()


def diag_from(block, dx, dy):
    nx, ny = lax.axis_size("gx"), lax.axis_size("gy")
    pairs = []
    for i in range(nx):
        for j in range(ny):
            if 0 <= i + dx < nx and 0 <= j + dy < ny:
                pairs.append((i * ny + j, (i + dx) * ny + (j + dy)))
    return lax.ppermute(block, ("gx", "gy"), pairs)


def row_ends(buf, blocks, at_end):
    out = []
    for b in blocks:
        chunk = b.chunks - 1 if at_end else 0
        first = b.fx_base + chunk
        lane = 127 if at_end else 0
        out.append(lax.slice(buf, (first, lane), (first + 5 * b.chunks + 1, lane + 1), (b.chunks, 1))[:, 0])
    return jnp.stack(out)


def with_corners(y_rim, x_lo, x_hi, blocks, at_end):
    lo, hi = row_ends(x_lo, blocks, at_end), row_ends(x_hi, blocks, at_end)
    extra = jnp.stack([lo, hi], axis=1).reshape(2 * len(blocks), 6)
    extra = jnp.pad(extra, ((0, 0), (0, 128 - 6)))
    return lax.dynamic_update_slice(y_rim, extra, (blocks[0].corner_rows[0], 0))


def face_call(blocks, fine_out, coarse_out, fine_face, coarse_face, rims):
    fine, coarse = blocks
    x_prev, x_next, y_prev, y_next = rims
    x_lo = shift_from(x_next, "gx", 1)
    x_hi = shift_from(x_prev, "gx", -1)
    y_lo = shift_from(with_corners(y_next, x_lo, x_hi, blocks, True), "gy", 1)
    y_hi = shift_from(with_corners(y_prev, x_lo, x_hi, blocks, False), "gy", -1)
    received = (x_lo, x_hi, y_lo, y_hi)
    py = jnp.asarray(prolong_y_matrix(coarse.lanes))
    ry = jnp.asarray(restrict_y_matrix(coarse.lanes))
    anyspace = pl.BlockSpec(memory_space=pl.ANY)
    return pl.pallas_call(
        functools.partial(face_kernel, blocks, fine.layers - 1),
        out_shape=(f32(fine_out.shape), f32(coarse_out.shape)),
        in_specs=[anyspace, anyspace] + vmem_specs(8) + [pl.BlockSpec(memory_space=pltpu.SMEM)],
        out_specs=(anyspace, anyspace),
        input_output_aliases={0: 0, 1: 1},
        scratch_shapes=[
            pltpu.VMEM((6, 1, fine.size, fine.lanes), jnp.float32),
            pltpu.VMEM((6, 1, coarse.size, coarse.lanes), jnp.float32),
            pltpu.VMEM((round8(6 * fine.size), coarse.lanes), jnp.float32),
            pltpu.VMEM((round8(6 * coarse.size), fine.lanes), jnp.float32),
            pltpu.SemaphoreType.DMA((6,)),
        ],
    )(fine_out, coarse_out, fine_face, coarse_face, *received, py, ry, edge_flags())


def local(
    fine_wave,
    fine_memory,
    fine_material,
    fine_mechanism,
    fine_metric,
    coarse_wave,
    coarse_memory,
    coarse_material,
    coarse_mechanism,
    material_table,
    attenuation_table,
):
    fine, coarse, x_rows, y_rows = plan_blocks(fine_wave.shape[1:], coarse_wave.shape[1:])
    blocks = (fine, coarse)
    smem = pl.BlockSpec(memory_space=pltpu.SMEM)
    flags = edge_flags()

    rims = pl.pallas_call(
        functools.partial(pack_kernel, blocks),
        out_shape=halo_shapes(x_rows, y_rows),
        in_specs=vmem_specs(2),
        out_specs=tuple(vmem_specs(4)),
    )(fine_wave, coarse_wave)
    halos = receive(rims)

    fine_velocity, coarse_velocity, *vrims = pl.pallas_call(
        functools.partial(velocity_kernel, blocks),
        out_shape=(f32((3,) + fine_wave.shape[1:]), f32((3,) + coarse_wave.shape[1:])) + halo_shapes(x_rows, y_rows),
        in_specs=vmem_specs(9) + [smem, smem],
        out_specs=tuple(vmem_specs(6)),
        scratch_shapes=[scratch_for(fine), scratch_for(coarse)],
    )(fine_wave, coarse_wave, *halos, fine_material, fine_metric, coarse_material, material_table, flags)

    vhalos = receive(vrims)
    fx_rows = 6 * (fine.chunks + coarse.chunks)
    fy_rows = round8(fine.size + coarse.size + 4)
    fine_out, fine_mem, fine_face, coarse_out, coarse_mem, coarse_face, *face_rims = pl.pallas_call(
        functools.partial(stress_kernel, blocks),
        out_shape=(
            f32(fine_wave.shape), f32(fine_memory.shape), f32((6,) + fine_wave.shape[2:]),
            f32(coarse_wave.shape), f32(coarse_memory.shape), f32((6,) + coarse_wave.shape[2:]),
            f32((fx_rows, 128)), f32((fx_rows, 128)), f32((fy_rows, 128)), f32((fy_rows, 128)),
        ),
        in_specs=vmem_specs(15) + [smem, smem, smem],
        out_specs=tuple(vmem_specs(10)),
        scratch_shapes=[scratch_for(fine), scratch_for(coarse)],
    )(fine_wave, fine_memory, fine_velocity, coarse_wave, coarse_memory, coarse_velocity, *vhalos,
      fine_material, fine_mechanism, fine_metric, coarse_material, coarse_mechanism, material_table,
      attenuation_table, flags)

    fine_out, coarse_out = face_call(blocks, fine_out, coarse_out, fine_face, coarse_face, face_rims)
    return (fine_out, fine_mem, coarse_out, coarse_mem)


def solution(mesh):
    in_specs = (
        P(None, None, "gx", "gy"),
        P(None, None, "gx", "gy"),
        P(None, "gx", "gy"),
        P(None, "gx", "gy"),
        P(None, "gx", "gy"),
        P(None, None, "gx", "gy"),
        P(None, None, "gx", "gy"),
        P(None, "gx", "gy"),
        P(None, "gx", "gy"),
        P(),
        P(),
    )
    out_specs = (
        P(None, None, "gx", "gy"),
        P(None, None, "gx", "gy"),
        P(None, None, "gx", "gy"),
        P(None, None, "gx", "gy"),
    )
    return jax.shard_map(local, mesh=mesh, in_specs=in_specs, out_specs=out_specs, check_vma=False)
```
